32 devices in a mesh: groups: 1, blk: 8 (over z, y), seg: 2 (over x), freq: 2 (over core).
Axes of the slice: x: 2, y: 2, z: 4, core: 2. Of those that a mesh axis runs over, the one named last changes fastest.
Arguments:
- raw: bfloat16 [64, 64, 16384], P(('groups', 'blk'), 'seg', 'freq'), may hold values from -6 to 6
- taps: float32 [128], replicated, may hold values from -0.5 to 0.5
- send_list: int32 [8, 8, 2], P(('groups', 'blk')), may hold values from 0 to 8, as said below
- recv_row: int32 [8, 8, 2], P(('groups', 'blk')), may hold values from 0 to 16, as said below
Outputs:
- cross_spectra: float32 [2, 256, 128, 128], P(None, ('seg', 'freq'), ('groups', 'blk'))
The draws below stay inside these ranges and needn't reach their ends.
Inputs may be any that keep to these rules, and one draw needn't show every extreme that they name: send_list[s, o, k] is the local sensing point of source s that goes to owner o in slot k, or 8 for an empty slot; a source names each of its points at most once; the filled slots of a pair come first; some source fills all 2 slots to one owner. recv_row[o, s, k] is the row of owner o that receives slot k of source s, and it is 16 exactly where send_list[s, o, k] is 8; an owner's filled rows are 0 to its count - 1, each once, rising with source and then slot; some owner holds exactly 16 rows.
All inputs are finite; a program needn't handle non-finite values.
Results may differ from the reference program's by a relative error of at most 0.0029.
Values may be sent and summed in bfloat16 or wider, within the bound.
No kernel may reach another device: no remote copies, remote signals or barrier semaphores. Data moves between devices by JAX's collectives and lax.ppermute only.
A program may use at most 128 MiB of HBM per device.

```python
import math
import jax
import jax.numpy as jnp
from jax import lax

SEG_LEN = 16384
BINS = 256
BAND_LO = 128
HW = 4
TAPS = 128
SECT = 8
OWN = 16
CAP = 2
CH_RAW = 64
CHANNELS = 128
SEGS = 64
N_BLK = 8


def routing_tables(key):
    base = jax.random.fold_in(key, 4099)
    keys = jax.random.split(base, 5)
    hot_owner = jax.random.randint(keys[0], (), 0, N_BLK)
    hot_turn = jax.random.randint(keys[1], (), 0, N_BLK)
    source_ids = jnp.arange(N_BLK, dtype=jnp.int32)
    hot_source = (source_ids - hot_turn) % N_BLK < OWN // CAP
    local_order = jax.vmap(lambda sub_key: jax.random.permutation(sub_key, SECT))(jax.random.split(keys[2], N_BLK))
    local_order = local_order.astype(jnp.int32)
    other_pick = jax.random.randint(keys[3], (N_BLK, SECT), 0, N_BLK - 1)
    other_owner = other_pick + (other_pick >= hot_owner).astype(jnp.int32)
    active = jax.random.randint(keys[4], (N_BLK, SECT), 0, 8) != 0
    position = jnp.arange(SECT, dtype=jnp.int32)[None, :]
    to_hot = hot_source[:, None] & (position < CAP)
    owner = jnp.where(to_hot, hot_owner, jnp.where(active, other_owner, N_BLK)).astype(jnp.int32)
    owner_ids = jnp.arange(N_BLK, dtype=jnp.int32)
    owner_onehot = (owner[:, :, None] == owner_ids[None, None, :]).astype(jnp.int32)
    pair_rank = jnp.sum((jnp.cumsum(owner_onehot, axis=1) - 1) * owner_onehot, axis=2)
    keeping = (owner < N_BLK) & (pair_rank < CAP)
    kept_onehot = owner_onehot * keeping[:, :, None].astype(jnp.int32)
    flat_kept = kept_onehot.reshape(N_BLK * SECT, N_BLK)
    owner_rank = jnp.sum((jnp.cumsum(flat_kept, axis=0) - 1) * flat_kept, axis=1).reshape(N_BLK, SECT)
    keeping = keeping & (owner_rank < OWN)
    final_onehot = owner_onehot * keeping[:, :, None].astype(jnp.int32)
    slot_rank = jnp.sum((jnp.cumsum(final_onehot, axis=1) - 1) * final_onehot, axis=2)
    flat_final = final_onehot.reshape(N_BLK * SECT, N_BLK)
    row_rank = jnp.sum((jnp.cumsum(flat_final, axis=0) - 1) * flat_final, axis=1).reshape(N_BLK, SECT)
    slot_onehot = (slot_rank[:, :, None] == jnp.arange(CAP, dtype=jnp.int32)[None, None, :]).astype(jnp.int32)
    marked = final_onehot[:, :, :, None] * slot_onehot[:, :, None, :]
    sends = SECT + jnp.sum(marked * (local_order[:, :, None, None] - SECT), axis=1)
    receives = OWN + jnp.sum(marked * (row_rank[:, :, None, None] - OWN), axis=1)
    return (sends.astype(jnp.int32), jnp.transpose(receives, (1, 0, 2)).astype(jnp.int32))


def draw_send_list(key, part):
    return routing_tables(key)[0]


def draw_recv_row(key, part):
    return routing_tables(key)[1]


def block_scale(stream_key, extent, cuts, smallest, largest):
    factor_of = 1.0
    for axis_at, parts in cuts:
        steps = jax.random.uniform(jax.random.fold_in(jax.random.fold_in(stream_key, 6), axis_at), (parts,), jnp.float32, smallest / len(cuts), largest / len(cuts))
        factor_of = factor_of * jnp.repeat(jnp.exp(steps), extent[axis_at] // parts).reshape((-1,) + (1,) * (len(extent) - 1 - axis_at))
    return factor_of


def noise(stream_key, dims, scale, reach, cuts=(), kind=jnp.bfloat16):
    result = jax.random.normal(stream_key, dims, jnp.float32) * scale
    if len(cuts) > 0:
        result = block_scale(stream_key, dims, cuts, -0.22, 0.18) * result
    return jnp.clip(result, min=-reach, max=reach).astype(kind)


def setup_inputs(seed: int = 0, part: int = 0) -> dict:
    key_list = jax.random.split(jax.random.key(seed), 5)
    own_keys = jax.random.split(jax.random.fold_in(key_list[4], part), 5)
    raw = noise(own_keys[0], (CH_RAW, SEGS, SEG_LEN), 1.0, 6.0, ((0, 8), (1, 2), (2, 2)))
    taps = noise(key_list[1], (TAPS,), TAPS ** -0.5, 0.5, (), jnp.float32)
    send_list = draw_send_list(jax.random.fold_in(jax.random.fold_in(key_list[4], part), 71), part)
    recv_row = draw_recv_row(jax.random.fold_in(jax.random.fold_in(key_list[4], part), 71), part)
    return {"raw": raw, "taps": taps, "send_list": send_list, "recv_row": recv_row}


WHITEN_FLOOR = 0.25
TWO_PI = 2.0 * math.pi

def dft_tables(band_index, sample_index):
    wavenumber = BAND_LO + band_index
    phase_int = wavenumber[:, None] * sample_index[None, :] % SEG_LEN
    angles = phase_int.astype(jnp.float32) * (TWO_PI / SEG_LEN)
    norm_scale = 1.0 / math.sqrt(SEG_LEN)
    cos_part = (jnp.cos(angles) * norm_scale).astype(jnp.bfloat16)
    sin_part = (-jnp.sin(angles) * norm_scale).astype(jnp.bfloat16)
    return (cos_part, sin_part)

def response(band_index, taps):
    wavenumber = BAND_LO + band_index
    lag_index = jnp.arange(taps.shape[0], dtype=jnp.int32)
    phase_int = wavenumber[:, None] * lag_index[None, :] % SEG_LEN
    angles = phase_int.astype(jnp.float32) * (TWO_PI / SEG_LEN)
    real_part = jnp.dot(jnp.cos(angles), taps, precision=lax.Precision.HIGHEST)
    imag_part = jnp.dot(-jnp.sin(angles), taps, precision=lax.Precision.HIGHEST)
    return (real_part, imag_part)

def reference(raw, taps, send_list, recv_row):
    bins_all = jnp.arange(BINS, dtype=jnp.int32)
    cos_table, sin_table = dft_tables(bins_all, jnp.arange(SEG_LEN, dtype=jnp.int32))
    response_re, response_im = response(bins_all, taps)
    low_edge = jnp.maximum(bins_all - HW, 0)
    high_edge = jnp.minimum(bins_all + HW, BINS - 1)
    counted = (high_edge - low_edge + 1).astype(jnp.float32)

    def whiten_source(source_raw):
        flat_records = source_raw.reshape(SECT * SEGS, SEG_LEN)
        real_part = jnp.dot(flat_records, cos_table.T, preferred_element_type=jnp.float32)
        imag_part = jnp.dot(flat_records, sin_table.T, preferred_element_type=jnp.float32)
        amplitude = jnp.sqrt(real_part * real_part + imag_part * imag_part + 1e-06)
        padded = jnp.pad(amplitude, ((0, 0), (HW, HW)))
        window_sum = padded[:, 0:BINS]
        for offset_step in range(1, 2 * HW + 1):
            window_sum = window_sum + padded[:, offset_step:offset_step + BINS]
        smooth = window_sum / counted[None, :]
        divisor = jnp.maximum(smooth, WHITEN_FLOOR)
        scaled_re = real_part / divisor
        scaled_im = imag_part / divisor
        white_re = scaled_re * response_re[None, :] - scaled_im * response_im[None, :]
        white_im = scaled_re * response_im[None, :] + scaled_im * response_re[None, :]
        whitened = jnp.stack([white_re, white_im], axis=-1).astype(jnp.bfloat16)
        return whitened.reshape(SECT, SEGS, BINS, 2)
    whitened = lax.map(whiten_source, raw.reshape(N_BLK, SECT, SEGS, SEG_LEN))
    whitened = whitened.reshape(CH_RAW, SEGS, BINS, 2)
    source_ids = jnp.arange(N_BLK, dtype=jnp.int32)
    owner_ids = jnp.arange(N_BLK, dtype=jnp.int32)
    chosen = jnp.transpose(send_list, (1, 0, 2))
    valid = (chosen < SECT) & (recv_row < OWN)
    channel = jnp.where(valid, source_ids[None, :, None] * SECT + chosen, 0).astype(jnp.int32)
    target = jnp.where(valid, owner_ids[:, None, None] * OWN + recv_row, CHANNELS).astype(jnp.int32)
    source_of = jnp.zeros((CHANNELS + 1,), jnp.int32).at[target.reshape(-1)].set(channel.reshape(-1))
    filled = jnp.zeros((CHANNELS + 1,), jnp.int32).at[target.reshape(-1)].set(1)
    gathered = whitened[source_of[:CHANNELS]]
    routed = jnp.where(filled[:CHANNELS][:, None, None, None] == 1, gathered, jnp.zeros_like(gathered))
    real_rows = routed[..., 0].astype(jnp.float32)
    imag_rows = routed[..., 1].astype(jnp.float32)
    highest = lax.Precision.HIGHEST
    cross_re = jnp.einsum('isb,jsb->bij', real_rows, real_rows, precision=highest)
    cross_re = cross_re + jnp.einsum('isb,jsb->bij', imag_rows, imag_rows, precision=highest)
    cross_im = jnp.einsum('isb,jsb->bij', imag_rows, real_rows, precision=highest)
    cross_im = cross_im - jnp.einsum('isb,jsb->bij', real_rows, imag_rows, precision=highest)
    return jnp.stack([cross_re, cross_im]) / jnp.float32(SEGS)
```

```python
import math

import jax
import jax.numpy as jnp
from jax import lax
from jax.sharding import PartitionSpec as P

SEG_LEN = 16384
BINS = 256
BAND_LO = 128
HW = 4
OWN = 16


WHITEN_FLOOR = 0.25
TWO_PI = 2.0 * math.pi


def swapped(value, axis, distance):
    mask = 2**distance
    pairs = [(source, source ^ mask) for source in range(lax.axis_size(axis))]
    return lax.ppermute(value, axis, pairs)


def dft_tables(band_index, sample_index):
    wavenumber = BAND_LO + band_index
    phase_int = wavenumber[:, None] * sample_index[None, :] % SEG_LEN
    angles = phase_int.astype(jnp.float32) * (TWO_PI / SEG_LEN)
    norm_scale = 1.0 / math.sqrt(SEG_LEN)
    cos_part = (jnp.cos(angles) * norm_scale).astype(jnp.bfloat16)
    sin_part = (-jnp.sin(angles) * norm_scale).astype(jnp.bfloat16)
    return (cos_part, sin_part)


def dft_tables_fast(band_index, first_sample, count):
    lanes = 128
    wavenumber = BAND_LO + band_index
    coarse = (first_sample + lanes * jnp.arange(count // lanes, dtype=jnp.int32))
    fine = jnp.arange(lanes, dtype=jnp.int32)
    coarse_angle = (wavenumber[:, None] * coarse[None, :] % SEG_LEN).astype(jnp.float32) * (
        TWO_PI / SEG_LEN
    )
    fine_angle = (wavenumber[:, None] * fine[None, :] % SEG_LEN).astype(jnp.float32) * (
        TWO_PI / SEG_LEN
    )
    cos_a = jnp.cos(coarse_angle)[:, :, None]
    sin_a = jnp.sin(coarse_angle)[:, :, None]
    cos_b = jnp.cos(fine_angle)[:, None, :]
    sin_b = jnp.sin(fine_angle)[:, None, :]
    norm_scale = 1.0 / math.sqrt(SEG_LEN)
    cos_sum = cos_a * cos_b - sin_a * sin_b
    sin_sum = sin_a * cos_b + cos_a * sin_b
    rows = band_index.shape[0]
    cos_part = (cos_sum * norm_scale).astype(jnp.bfloat16).reshape(rows, count)
    sin_part = (-sin_sum * norm_scale).astype(jnp.bfloat16).reshape(rows, count)
    return (cos_part, sin_part)


def response(band_index, taps):
    wavenumber = BAND_LO + band_index
    lag_index = jnp.arange(taps.shape[0], dtype=jnp.int32)
    phase_int = wavenumber[:, None] * lag_index[None, :] % SEG_LEN
    angles = phase_int.astype(jnp.float32) * (TWO_PI / SEG_LEN)
    real_part = jnp.dot(jnp.cos(angles), taps, precision=lax.Precision.HIGHEST)
    imag_part = jnp.dot(-jnp.sin(angles), taps, precision=lax.Precision.HIGHEST)
    return (real_part, imag_part)


def per_device(raw, taps, send_list, recv_row):
    owners_count = lax.axis_size("blk")
    seg_count = lax.axis_size("seg")
    freq_count = lax.axis_size("freq")
    freq_rank = lax.axis_index("freq")
    sections, seg_dev, half_len = raw.shape
    records = raw.reshape(sections * seg_dev, half_len)
    device_bins = BINS // freq_count
    block_bins = device_bins // seg_count
    capacity = send_list.shape[2]

    def band_of(row_ids):
        owner_core = row_ids // device_bins
        local_row = row_ids % device_bins
        return (
            local_row // block_bins * freq_count + owner_core
        ) * block_bins + local_row % block_bins

    band_rows = band_of(jnp.arange(device_bins * freq_count, dtype=jnp.int32))
    cos_part, sin_part = dft_tables_fast(band_rows, freq_rank * half_len, half_len)
    contract = (((1,), (1,)), ((), ()))
    real_all = lax.dot_general(cos_part, records, contract, preferred_element_type=jnp.float32)
    imag_all = lax.dot_general(sin_part, records, contract, preferred_element_type=jnp.float32)
    blocks = jnp.stack([real_all, imag_all], axis=1)
    blocks = blocks.reshape(freq_count, device_bins, 2, records.shape[0])
    if freq_count == 2:
        kept = jnp.where(freq_rank == 0, blocks[0], blocks[1])
        sent = jnp.where(freq_rank == 0, blocks[1], blocks[0])
        spectra = kept + swapped(sent, "freq", 0)
    else:
        spectra = lax.psum_scatter(
            blocks.reshape(device_bins * freq_count, 2, records.shape[0]),
            "freq",
            scatter_dimension=0,
            tiled=True,
        )
    real_part = spectra[:, 0]
    imag_part = spectra[:, 1]
    amplitude = jnp.sqrt(real_part * real_part + imag_part * imag_part + 1e-06)
    amp_blocks = amplitude.reshape(seg_count, block_bins, -1)
    band_rims = jnp.stack([amp_blocks[:, :HW], amp_blocks[:, block_bins - HW :]])
    partner = swapped(band_rims, "freq", 0)
    zero_rim = jnp.zeros_like(partner[1][:1])
    right_prev = jnp.concatenate([zero_rim, partner[1][:-1]], axis=0)
    left_next = jnp.concatenate([partner[0][1:], zero_rim], axis=0)
    first_core = freq_rank == 0
    lower_rim = jnp.where(first_core, right_prev, partner[1])
    upper_rim = jnp.where(first_core, partner[0], left_next)
    padded = jnp.concatenate([lower_rim, amp_blocks, upper_rim], axis=1)
    window_sum = padded[:, 0:block_bins]
    for offset_step in range(1, 2 * HW + 1):
        window_sum = window_sum + padded[:, offset_step : offset_step + block_bins]
    span_ids = jnp.arange(seg_count, dtype=jnp.int32)[:, None]
    offsets = jnp.arange(block_bins, dtype=jnp.int32)[None, :]
    position = (span_ids * freq_count + freq_rank) * block_bins + offsets
    counted = jnp.minimum(position + HW, BINS - 1) - jnp.maximum(position - HW, 0) + 1
    smooth = window_sum / counted.astype(jnp.float32)[:, :, None]
    divisor = jnp.maximum(smooth, WHITEN_FLOOR).reshape(device_bins, -1)
    local_bins = freq_rank * device_bins + jnp.arange(device_bins, dtype=jnp.int32)
    response_re, response_im = response(band_of(local_bins), taps)
    scaled_re = real_part / divisor
    scaled_im = imag_part / divisor
    white_re = scaled_re * response_re[:, None] - scaled_im * response_im[:, None]
    white_im = scaled_re * response_im[:, None] + scaled_im * response_re[:, None]
    whitened = jnp.stack([white_re, white_im], axis=1).astype(jnp.bfloat16)
    whitened = whitened.reshape(device_bins, 2, sections, seg_dev)
    slot_ids = send_list.reshape(-1)
    picker = (slot_ids[:, None] == jnp.arange(sections, dtype=jnp.int32)[None, :]).astype(
        jnp.bfloat16
    )
    packed = jnp.einsum(
        "pc,fxcn->pxnf", picker, whitened, preferred_element_type=jnp.float32
    ).astype(jnp.bfloat16)
    packed = packed.reshape(owners_count, capacity, 2, seg_dev, device_bins)
    arrived = lax.all_to_all(packed, "blk", split_axis=0, concat_axis=0, tiled=True)
    arrived = arrived.reshape(owners_count * capacity, 2, seg_dev, device_bins)
    row_targets = recv_row.reshape(-1)
    placer = (jnp.arange(OWN, dtype=jnp.int32)[:, None] == row_targets[None, :]).astype(
        jnp.bfloat16
    )
    own_block = jnp.einsum(
        "rp,pxnf->xnrf", placer, arrived, preferred_element_type=jnp.float32
    ).astype(jnp.bfloat16)
    incoming = lax.all_gather(own_block, "blk", axis=2, tiled=True)
    cross_re = jnp.einsum("xnif,xnjf->fij", own_block, incoming, preferred_element_type=jnp.float32)
    cross_im = jnp.einsum(
        "nif,njf->fij", own_block[1], incoming[0], preferred_element_type=jnp.float32
    )
    cross_im = cross_im - jnp.einsum(
        "nif,njf->fij", own_block[0], incoming[1], preferred_element_type=jnp.float32
    )
    pair_block = jnp.stack([cross_re, cross_im])
    stacked = lax.psum_scatter(pair_block, "seg", scatter_dimension=1, tiled=True)
    return stacked / jnp.float32(seg_dev * seg_count)


def solution(mesh):
    placed = (
        P(("groups", "blk"), "seg", "freq"),
        P(),
        P(("groups", "blk"), None, None),
        P(("groups", "blk"), None, None),
    )
    return jax.shard_map(
        per_device,
        mesh=mesh,
        in_specs=placed,
        out_specs=P(None, ("seg", "freq"), ("groups", "blk"), None),
        check_vma=False,
    )
```

```python
import math

import jax
import jax.numpy as jnp
from jax import lax
from jax.sharding import PartitionSpec as P

SEG_LEN = 16384
BINS = 256
BAND_LO = 128
HW = 4
OWN = 16


WHITEN_FLOOR = 0.25
TWO_PI = 2.0 * math.pi


def swapped(value, axis, distance):
    mask = 2**distance
    pairs = [(source, source ^ mask) for source in range(lax.axis_size(axis))]
    return lax.ppermute(value, axis, pairs)


def dft_tables(band_index, sample_index):
    wavenumber = BAND_LO + band_index
    phase_int = wavenumber[:, None] * sample_index[None, :] % SEG_LEN
    angles = phase_int.astype(jnp.float32) * (TWO_PI / SEG_LEN)
    norm_scale = 1.0 / math.sqrt(SEG_LEN)
    cos_part = (jnp.cos(angles) * norm_scale).astype(jnp.bfloat16)
    sin_part = (-jnp.sin(angles) * norm_scale).astype(jnp.bfloat16)
    return (cos_part, sin_part)


def dft_tables_fast(band_index, first_sample, count):
    lanes = 128
    wavenumber = BAND_LO + band_index
    coarse = (first_sample + lanes * jnp.arange(count // lanes, dtype=jnp.int32))
    fine = jnp.arange(lanes, dtype=jnp.int32)
    coarse_angle = (wavenumber[:, None] * coarse[None, :] % SEG_LEN).astype(jnp.float32) * (
        TWO_PI / SEG_LEN
    )
    fine_angle = (wavenumber[:, None] * fine[None, :] % SEG_LEN).astype(jnp.float32) * (
        TWO_PI / SEG_LEN
    )
    cos_a = jnp.cos(coarse_angle)[:, :, None]
    sin_a = jnp.sin(coarse_angle)[:, :, None]
    cos_b = jnp.cos(fine_angle)[:, None, :]
    sin_b = jnp.sin(fine_angle)[:, None, :]
    norm_scale = 1.0 / math.sqrt(SEG_LEN)
    cos_sum = cos_a * cos_b - sin_a * sin_b
    sin_sum = sin_a * cos_b + cos_a * sin_b
    rows = band_index.shape[0]
    cos_part = (cos_sum * norm_scale).astype(jnp.bfloat16).reshape(rows, count)
    sin_part = (-sin_sum * norm_scale).astype(jnp.bfloat16).reshape(rows, count)
    return (cos_part, sin_part)


def response(band_index, taps):
    wavenumber = BAND_LO + band_index
    lag_index = jnp.arange(taps.shape[0], dtype=jnp.int32)
    phase_int = wavenumber[:, None] * lag_index[None, :] % SEG_LEN
    angles = phase_int.astype(jnp.float32) * (TWO_PI / SEG_LEN)
    real_part = jnp.dot(jnp.cos(angles), taps, precision=lax.Precision.HIGHEST)
    imag_part = jnp.dot(-jnp.sin(angles), taps, precision=lax.Precision.HIGHEST)
    return (real_part, imag_part)


def per_device(raw, taps, send_list, recv_row):
    owners_count = lax.axis_size("blk")
    seg_count = lax.axis_size("seg")
    freq_count = lax.axis_size("freq")
    freq_rank = lax.axis_index("freq")
    sections, seg_dev, half_len = raw.shape
    records = raw.reshape(sections * seg_dev, half_len)
    device_bins = BINS // freq_count
    block_bins = device_bins // seg_count
    capacity = send_list.shape[2]

    def band_of(row_ids):
        owner_core = row_ids // device_bins
        local_row = row_ids % device_bins
        return (
            local_row // block_bins * freq_count + owner_core
        ) * block_bins + local_row % block_bins

    band_rows = band_of(jnp.arange(device_bins * freq_count, dtype=jnp.int32))
    cos_part, sin_part = dft_tables_fast(band_rows, freq_rank * half_len, half_len)
    contract = (((1,), (1,)), ((), ()))
    real_all = lax.dot_general(cos_part, records, contract, preferred_element_type=jnp.float32)
    imag_all = lax.dot_general(sin_part, records, contract, preferred_element_type=jnp.float32)
    blocks = jnp.stack([real_all, imag_all], axis=1)
    blocks = blocks.reshape(freq_count, device_bins, 2, records.shape[0])
    if freq_count == 2:
        kept = jnp.where(freq_rank == 0, blocks[0], blocks[1])
        sent = jnp.where(freq_rank == 0, blocks[1], blocks[0])
        spectra = kept + swapped(sent, "freq", 0)
    else:
        spectra = lax.psum_scatter(
            blocks.reshape(device_bins * freq_count, 2, records.shape[0]),
            "freq",
            scatter_dimension=0,
            tiled=True,
        )
    real_part = spectra[:, 0]
    imag_part = spectra[:, 1]
    amplitude = jnp.sqrt(real_part * real_part + imag_part * imag_part + 1e-06)
    amp_blocks = amplitude.reshape(seg_count, block_bins, -1)
    band_rims = jnp.stack([amp_blocks[:, :HW], amp_blocks[:, block_bins - HW :]])
    partner = swapped(band_rims, "freq", 0)
    zero_rim = jnp.zeros_like(partner[1][:1])
    right_prev = jnp.concatenate([zero_rim, partner[1][:-1]], axis=0)
    left_next = jnp.concatenate([partner[0][1:], zero_rim], axis=0)
    first_core = freq_rank == 0
    lower_rim = jnp.where(first_core, right_prev, partner[1])
    upper_rim = jnp.where(first_core, partner[0], left_next)
    padded = jnp.concatenate([lower_rim, amp_blocks, upper_rim], axis=1)
    window_sum = padded[:, 0:block_bins]
    for offset_step in range(1, 2 * HW + 1):
        window_sum = window_sum + padded[:, offset_step : offset_step + block_bins]
    span_ids = jnp.arange(seg_count, dtype=jnp.int32)[:, None]
    offsets = jnp.arange(block_bins, dtype=jnp.int32)[None, :]
    position = (span_ids * freq_count + freq_rank) * block_bins + offsets
    counted = jnp.minimum(position + HW, BINS - 1) - jnp.maximum(position - HW, 0) + 1
    smooth = window_sum / counted.astype(jnp.float32)[:, :, None]
    divisor = jnp.maximum(smooth, WHITEN_FLOOR).reshape(device_bins, -1)
    local_bins = freq_rank * device_bins + jnp.arange(device_bins, dtype=jnp.int32)
    response_re, response_im = response(band_of(local_bins), taps)
    scaled_re = real_part / divisor
    scaled_im = imag_part / divisor
    white_re = scaled_re * response_re[:, None] - scaled_im * response_im[:, None]
    white_im = scaled_re * response_im[:, None] + scaled_im * response_re[:, None]
    whitened = jnp.stack([white_re, white_im], axis=1).astype(jnp.bfloat16)
    whitened = whitened.reshape(seg_count, block_bins, 2, sections, seg_dev)
    whitened = jnp.transpose(whitened, (0, 1, 3, 2, 4))
    seg_rank = lax.axis_index("seg")
    pieces = [lax.dynamic_index_in_dim(whitened, seg_rank, axis=0, keepdims=False)]
    for shift in range(1, seg_count):
        outgoing = lax.dynamic_index_in_dim(
            whitened, (seg_rank + shift) % seg_count, axis=0, keepdims=False
        )
        pairs = [(source, (source + shift) % seg_count) for source in range(seg_count)]
        pieces.append(lax.ppermute(outgoing, "seg", pairs))
    local = jnp.stack(pieces, axis=3).reshape(block_bins, sections, -1)
    all_segs = seg_dev * seg_count
    gathered = lax.all_gather(local, "blk", axis=1, tiled=True)
    tables = lax.all_gather(jnp.stack([send_list, recv_row]), "blk", axis=1, tiled=True)
    send_all = tables[0]
    recv_all = tables[1]
    rows_count = owners_count * OWN
    chans_count = owners_count * sections
    chosen = jnp.transpose(send_all, (1, 0, 2))
    valid = (chosen < sections) & (recv_all < OWN)
    source_ids = jnp.arange(owners_count, dtype=jnp.int32)[None, :, None]
    owner_ids = jnp.arange(owners_count, dtype=jnp.int32)[:, None, None]
    channel = jnp.where(valid, source_ids * sections + chosen, -1).reshape(-1)
    target = jnp.where(valid, owner_ids * OWN + recv_all, -1).reshape(-1)
    row_hot = (target[:, None] == jnp.arange(rows_count, dtype=jnp.int32)[None, :]).astype(
        jnp.bfloat16
    )
    chan_hot = (channel[:, None] == jnp.arange(chans_count, dtype=jnp.int32)[None, :]).astype(
        jnp.bfloat16
    )
    selector = jnp.einsum(
        "er,ec->rc", row_hot, chan_hot, preferred_element_type=jnp.float32
    ).astype(jnp.bfloat16)
    routed = jnp.einsum(
        "rc,bcq->brq", selector, gathered, preferred_element_type=jnp.float32
    ).astype(jnp.bfloat16)
    blk_rank = lax.axis_index("blk")
    own = lax.dynamic_slice_in_dim(routed, blk_rank * OWN, OWN, axis=1)
    own_re = own[..., :all_segs]
    own_im = own[..., all_segs:]
    rotated = jnp.concatenate([own_im, -own_re], axis=-1)
    lhs = jnp.concatenate([own, rotated], axis=1)
    cross = jnp.einsum("bpq,bjq->bpj", lhs, routed, preferred_element_type=jnp.float32)
    cross = cross.reshape(block_bins, 2, OWN, rows_count)
    return jnp.transpose(cross, (1, 0, 2, 3)) / jnp.float32(all_segs)


def solution(mesh):
    placed = (
        P(("groups", "blk"), "seg", "freq"),
        P(),
        P(("groups", "blk"), None, None),
        P(("groups", "blk"), None, None),
    )
    return jax.shard_map(
        per_device,
        mesh=mesh,
        in_specs=placed,
        out_specs=P(None, ("seg", "freq"), ("groups", "blk"), None),
        check_vma=False,
    )
```

```python
import math

import jax
import jax.numpy as jnp
from jax import lax
from jax.sharding import PartitionSpec as P

SEG_LEN = 16384
BINS = 256
BAND_LO = 128
HW = 4
OWN = 16


WHITEN_FLOOR = 0.25
TWO_PI = 2.0 * math.pi


def swapped(value, axis, distance):
    mask = 2**distance
    pairs = [(source, source ^ mask) for source in range(lax.axis_size(axis))]
    return lax.ppermute(value, axis, pairs)


def dft_tables(band_index, sample_index):
    wavenumber = BAND_LO + band_index
    phase_int = wavenumber[:, None] * sample_index[None, :] % SEG_LEN
    angles = phase_int.astype(jnp.float32) * (TWO_PI / SEG_LEN)
    norm_scale = 1.0 / math.sqrt(SEG_LEN)
    cos_part = (jnp.cos(angles) * norm_scale).astype(jnp.bfloat16)
    sin_part = (-jnp.sin(angles) * norm_scale).astype(jnp.bfloat16)
    return (cos_part, sin_part)


def dft_tables_fast(band_index, first_sample, count):
    lanes = 128
    wavenumber = BAND_LO + band_index
    coarse = (first_sample + lanes * jnp.arange(count // lanes, dtype=jnp.int32))
    fine = jnp.arange(lanes, dtype=jnp.int32)
    coarse_angle = (wavenumber[:, None] * coarse[None, :] % SEG_LEN).astype(jnp.float32) * (
        TWO_PI / SEG_LEN
    )
    fine_angle = (wavenumber[:, None] * fine[None, :] % SEG_LEN).astype(jnp.float32) * (
        TWO_PI / SEG_LEN
    )
    cos_a = jnp.cos(coarse_angle)[:, :, None]
    sin_a = jnp.sin(coarse_angle)[:, :, None]
    cos_b = jnp.cos(fine_angle)[:, None, :]
    sin_b = jnp.sin(fine_angle)[:, None, :]
    norm_scale = 1.0 / math.sqrt(SEG_LEN)
    cos_sum = cos_a * cos_b - sin_a * sin_b
    sin_sum = sin_a * cos_b + cos_a * sin_b
    rows = band_index.shape[0]
    cos_part = (cos_sum * norm_scale).astype(jnp.bfloat16).reshape(rows, count)
    sin_part = (-sin_sum * norm_scale).astype(jnp.bfloat16).reshape(rows, count)
    return (cos_part, sin_part)


def response(band_index, taps):
    wavenumber = BAND_LO + band_index
    lag_index = jnp.arange(taps.shape[0], dtype=jnp.int32)
    phase_int = wavenumber[:, None] * lag_index[None, :] % SEG_LEN
    angles = phase_int.astype(jnp.float32) * (TWO_PI / SEG_LEN)
    real_part = jnp.dot(jnp.cos(angles), taps, precision=lax.Precision.HIGHEST)
    imag_part = jnp.dot(-jnp.sin(angles), taps, precision=lax.Precision.HIGHEST)
    return (real_part, imag_part)


def per_device(raw, taps, send_list, recv_row):
    owners_count = lax.axis_size("blk")
    seg_count = lax.axis_size("seg")
    freq_count = lax.axis_size("freq")
    freq_rank = lax.axis_index("freq")
    sections, seg_dev, half_len = raw.shape
    records = raw.reshape(sections * seg_dev, half_len)
    device_bins = BINS // freq_count
    block_bins = device_bins // seg_count
    capacity = send_list.shape[2]

    def band_of(row_ids):
        owner_core = row_ids // device_bins
        local_row = row_ids % device_bins
        return (
            local_row // block_bins * freq_count + owner_core
        ) * block_bins + local_row % block_bins

    band_rows = band_of(jnp.arange(device_bins * freq_count, dtype=jnp.int32))
    cos_part, sin_part = dft_tables_fast(band_rows, freq_rank * half_len, half_len)
    contract = (((1,), (1,)), ((), ()))
    real_all = lax.dot_general(cos_part, records, contract, preferred_element_type=jnp.float32)
    imag_all = lax.dot_general(sin_part, records, contract, preferred_element_type=jnp.float32)
    blocks = jnp.stack([real_all, imag_all], axis=1)
    blocks = blocks.reshape(freq_count, device_bins, 2, records.shape[0])
    if freq_count == 2:
        kept = jnp.where(freq_rank == 0, blocks[0], blocks[1])
        sent = jnp.where(freq_rank == 0, blocks[1], blocks[0])
        spectra = kept + swapped(sent, "freq", 0)
    else:
        spectra = lax.psum_scatter(
            blocks.reshape(device_bins * freq_count, 2, records.shape[0]),
            "freq",
            scatter_dimension=0,
            tiled=True,
        )
    real_part = spectra[:, 0]
    imag_part = spectra[:, 1]
    amplitude = jnp.sqrt(real_part * real_part + imag_part * imag_part + 1e-06)
    amp_blocks = amplitude.reshape(seg_count, block_bins, -1)
    band_rims = jnp.stack([amp_blocks[:, :HW], amp_blocks[:, block_bins - HW :]])
    partner = swapped(band_rims, "freq", 0)
    zero_rim = jnp.zeros_like(partner[1][:1])
    right_prev = jnp.concatenate([zero_rim, partner[1][:-1]], axis=0)
    left_next = jnp.concatenate([partner[0][1:], zero_rim], axis=0)
    first_core = freq_rank == 0
    lower_rim = jnp.where(first_core, right_prev, partner[1])
    upper_rim = jnp.where(first_core, partner[0], left_next)
    padded = jnp.concatenate([lower_rim, amp_blocks, upper_rim], axis=1)
    window_sum = padded[:, 0:block_bins]
    for offset_step in range(1, 2 * HW + 1):
        window_sum = window_sum + padded[:, offset_step : offset_step + block_bins]
    span_ids = jnp.arange(seg_count, dtype=jnp.int32)[:, None]
    offsets = jnp.arange(block_bins, dtype=jnp.int32)[None, :]
    position = (span_ids * freq_count + freq_rank) * block_bins + offsets
    counted = jnp.minimum(position + HW, BINS - 1) - jnp.maximum(position - HW, 0) + 1
    smooth = window_sum / counted.astype(jnp.float32)[:, :, None]
    divisor = jnp.maximum(smooth, WHITEN_FLOOR).reshape(device_bins, -1)
    local_bins = freq_rank * device_bins + jnp.arange(device_bins, dtype=jnp.int32)
    response_re, response_im = response(band_of(local_bins), taps)
    scaled_re = real_part / divisor
    scaled_im = imag_part / divisor
    white_re = scaled_re * response_re[:, None] - scaled_im * response_im[:, None]
    white_im = scaled_re * response_im[:, None] + scaled_im * response_re[:, None]
    whitened = jnp.stack([white_re, white_im], axis=1).astype(jnp.bfloat16)
    whitened = whitened.reshape(seg_count, block_bins, 2, sections, seg_dev)
    whitened = jnp.transpose(whitened, (0, 1, 3, 2, 4))
    seg_rank = lax.axis_index("seg")
    pieces = [lax.dynamic_index_in_dim(whitened, seg_rank, axis=0, keepdims=False)]
    for shift in range(1, seg_count):
        outgoing = lax.dynamic_index_in_dim(
            whitened, (seg_rank + shift) % seg_count, axis=0, keepdims=False
        )
        pairs = [(source, (source + shift) % seg_count) for source in range(seg_count)]
        pieces.append(lax.ppermute(outgoing, "seg", pairs))
    local = jnp.stack(pieces, axis=3).reshape(block_bins, sections, -1)
    all_segs = seg_dev * seg_count
    table_width = local.shape[-1]
    table = jnp.concatenate([send_list[0], recv_row[0]], axis=1).reshape(-1)
    table_len = table.shape[0]
    slab = jnp.pad(table.astype(jnp.bfloat16), (0, sections * table_width - table_len))
    carried = jnp.concatenate([local, slab.reshape(1, sections, table_width)], axis=0)
    everything = lax.all_gather(carried, "blk", axis=0, tiled=False)
    gathered = everything[:, :block_bins]
    table_part = everything[:, block_bins].reshape(owners_count, -1)[:, :table_len]
    table_part = table_part.astype(jnp.int32).reshape(owners_count, owners_count, 2 * capacity)
    send_all = table_part[..., :capacity]
    recv_all = table_part[..., capacity:]
    rows_count = owners_count * OWN
    chans_count = owners_count * sections
    chosen = jnp.transpose(send_all, (1, 0, 2))
    valid = (chosen < sections) & (recv_all < OWN)
    source_ids = jnp.arange(owners_count, dtype=jnp.int32)[None, :, None]
    owner_ids = jnp.arange(owners_count, dtype=jnp.int32)[:, None, None]
    channel = jnp.where(valid, source_ids * sections + chosen, -1).reshape(-1)
    target = jnp.where(valid, owner_ids * OWN + recv_all, -1).reshape(-1)
    row_hot = (target[:, None] == jnp.arange(rows_count, dtype=jnp.int32)[None, :]).astype(
        jnp.bfloat16
    )
    chan_hot = (channel[:, None] == jnp.arange(chans_count, dtype=jnp.int32)[None, :]).astype(
        jnp.bfloat16
    )
    selector = jnp.einsum(
        "er,ec->rc", row_hot, chan_hot, preferred_element_type=jnp.float32
    ).astype(jnp.bfloat16)
    selector = selector.reshape(rows_count, owners_count, sections)
    routed = jnp.einsum(
        "rsc,sbcq->brq", selector, gathered, preferred_element_type=jnp.float32
    ).astype(jnp.bfloat16)
    blk_rank = lax.axis_index("blk")
    own = lax.dynamic_slice_in_dim(routed, blk_rank * OWN, OWN, axis=1)
    own_re = own[..., :all_segs]
    own_im = own[..., all_segs:]
    rotated = jnp.concatenate([own_im, -own_re], axis=-1)
    lhs = jnp.concatenate([own, rotated], axis=1)
    cross = jnp.einsum("bpq,bjq->bpj", lhs, routed, preferred_element_type=jnp.float32)
    cross = cross.reshape(block_bins, 2, OWN, rows_count)
    return jnp.transpose(cross, (1, 0, 2, 3)) / jnp.float32(all_segs)


def solution(mesh):
    placed = (
        P(("groups", "blk"), "seg", "freq"),
        P(),
        P(("groups", "blk"), None, None),
        P(("groups", "blk"), None, None),
    )
    return jax.shard_map(
        per_device,
        mesh=mesh,
        in_specs=placed,
        out_specs=P(None, ("seg", "freq"), ("groups", "blk"), None),
        check_vma=False,
    )
```

```python
import math

import jax
import jax.numpy as jnp
from jax import lax
from jax.sharding import PartitionSpec as P

SEG_LEN = 16384
BINS = 256
BAND_LO = 128
HW = 4
OWN = 16


WHITEN_FLOOR = 0.25
TWO_PI = 2.0 * math.pi


def swapped(value, axis, distance):
    mask = 2**distance
    pairs = [(source, source ^ mask) for source in range(lax.axis_size(axis))]
    return lax.ppermute(value, axis, pairs)


def dft_tables(band_index, sample_index):
    wavenumber = BAND_LO + band_index
    phase_int = wavenumber[:, None] * sample_index[None, :] % SEG_LEN
    angles = phase_int.astype(jnp.float32) * (TWO_PI / SEG_LEN)
    norm_scale = 1.0 / math.sqrt(SEG_LEN)
    cos_part = (jnp.cos(angles) * norm_scale).astype(jnp.bfloat16)
    sin_part = (-jnp.sin(angles) * norm_scale).astype(jnp.bfloat16)
    return (cos_part, sin_part)


def dft_tables_fast(band_index, first_sample, count):
    lanes = 128
    wavenumber = BAND_LO + band_index
    coarse = (first_sample + lanes * jnp.arange(count // lanes, dtype=jnp.int32))
    fine = jnp.arange(lanes, dtype=jnp.int32)
    coarse_angle = (wavenumber[:, None] * coarse[None, :] % SEG_LEN).astype(jnp.float32) * (
        TWO_PI / SEG_LEN
    )
    fine_angle = (wavenumber[:, None] * fine[None, :] % SEG_LEN).astype(jnp.float32) * (
        TWO_PI / SEG_LEN
    )
    cos_a = jnp.cos(coarse_angle)[:, :, None]
    sin_a = jnp.sin(coarse_angle)[:, :, None]
    cos_b = jnp.cos(fine_angle)[:, None, :]
    sin_b = jnp.sin(fine_angle)[:, None, :]
    norm_scale = 1.0 / math.sqrt(SEG_LEN)
    cos_sum = cos_a * cos_b - sin_a * sin_b
    sin_sum = sin_a * cos_b + cos_a * sin_b
    rows = band_index.shape[0]
    cos_part = (cos_sum * norm_scale).astype(jnp.bfloat16).reshape(rows, count)
    sin_part = (-sin_sum * norm_scale).astype(jnp.bfloat16).reshape(rows, count)
    return (cos_part, sin_part)


def response(band_index, taps):
    wavenumber = BAND_LO + band_index
    lag_index = jnp.arange(taps.shape[0], dtype=jnp.int32)
    phase_int = wavenumber[:, None] * lag_index[None, :] % SEG_LEN
    angles = phase_int.astype(jnp.float32) * (TWO_PI / SEG_LEN)
    real_part = jnp.dot(jnp.cos(angles), taps, precision=lax.Precision.HIGHEST)
    imag_part = jnp.dot(-jnp.sin(angles), taps, precision=lax.Precision.HIGHEST)
    return (real_part, imag_part)


def gather_blocks(carried, count, rank):
    if count & (count - 1) != 0:
        return lax.all_gather(carried, "blk", axis=0, tiled=False)
    masks = []
    step = count // 2
    while step >= 1:
        masks.append(step)
        step //= 2
    if not masks:
        return carried[None]
    first = masks[0]
    rest = masks[1:]
    pairs = [(source, source ^ first) for source in range(count)]
    held = jnp.stack([carried, lax.ppermute(carried, "blk", pairs)], axis=0)
    split = (held.shape[1] + 1) // 2
    halves = [held[:, :split], held[:, split:]]
    orders = [rest, rest[::-1]]
    results = []
    for part, order in zip(halves, orders):
        done = [first]
        for mask in order:
            pairs = [(source, source ^ mask) for source in range(count)]
            arrived = lax.ppermute(part, "blk", pairs)
            done.append(mask)
            axis = sorted(done, reverse=True).index(mask)
            part = jnp.stack([part, arrived], axis=axis)
        results.append(part.reshape((count,) + part.shape[len(masks):]))
    return jnp.concatenate(results, axis=1)


def per_device(raw, taps, send_list, recv_row):
    owners_count = lax.axis_size("blk")
    seg_count = lax.axis_size("seg")
    freq_count = lax.axis_size("freq")
    freq_rank = lax.axis_index("freq")
    sections, seg_dev, half_len = raw.shape
    records = raw.reshape(sections * seg_dev, half_len)
    device_bins = BINS // freq_count
    block_bins = device_bins // seg_count
    capacity = send_list.shape[2]

    def band_of(row_ids):
        owner_core = row_ids // device_bins
        local_row = row_ids % device_bins
        return (
            local_row // block_bins * freq_count + owner_core
        ) * block_bins + local_row % block_bins

    band_rows = band_of(jnp.arange(device_bins * freq_count, dtype=jnp.int32))
    cos_part, sin_part = dft_tables_fast(band_rows, freq_rank * half_len, half_len)
    contract = (((1,), (1,)), ((), ()))
    real_all = lax.dot_general(cos_part, records, contract, preferred_element_type=jnp.float32)
    imag_all = lax.dot_general(sin_part, records, contract, preferred_element_type=jnp.float32)
    blocks = jnp.stack([real_all, imag_all], axis=1)
    blocks = blocks.reshape(freq_count, device_bins, 2, records.shape[0])
    if freq_count == 2:
        kept = jnp.where(freq_rank == 0, blocks[0], blocks[1])
        sent = jnp.where(freq_rank == 0, blocks[1], blocks[0])
        spectra = kept + swapped(sent, "freq", 0)
    else:
        spectra = lax.psum_scatter(
            blocks.reshape(device_bins * freq_count, 2, records.shape[0]),
            "freq",
            scatter_dimension=0,
            tiled=True,
        )
    real_part = spectra[:, 0]
    imag_part = spectra[:, 1]
    amplitude = jnp.sqrt(real_part * real_part + imag_part * imag_part + 1e-06)
    amp_blocks = amplitude.reshape(seg_count, block_bins, -1)
    band_rims = jnp.stack([amp_blocks[:, :HW], amp_blocks[:, block_bins - HW :]])
    partner = swapped(band_rims, "freq", 0)
    zero_rim = jnp.zeros_like(partner[1][:1])
    right_prev = jnp.concatenate([zero_rim, partner[1][:-1]], axis=0)
    left_next = jnp.concatenate([partner[0][1:], zero_rim], axis=0)
    first_core = freq_rank == 0
    lower_rim = jnp.where(first_core, right_prev, partner[1])
    upper_rim = jnp.where(first_core, partner[0], left_next)
    padded = jnp.concatenate([lower_rim, amp_blocks, upper_rim], axis=1)
    window_sum = padded[:, 0:block_bins]
    for offset_step in range(1, 2 * HW + 1):
        window_sum = window_sum + padded[:, offset_step : offset_step + block_bins]
    span_ids = jnp.arange(seg_count, dtype=jnp.int32)[:, None]
    offsets = jnp.arange(block_bins, dtype=jnp.int32)[None, :]
    position = (span_ids * freq_count + freq_rank) * block_bins + offsets
    counted = jnp.minimum(position + HW, BINS - 1) - jnp.maximum(position - HW, 0) + 1
    smooth = window_sum / counted.astype(jnp.float32)[:, :, None]
    divisor = jnp.maximum(smooth, WHITEN_FLOOR).reshape(device_bins, -1)
    local_bins = freq_rank * device_bins + jnp.arange(device_bins, dtype=jnp.int32)
    response_re, response_im = response(band_of(local_bins), taps)
    scaled_re = real_part / divisor
    scaled_im = imag_part / divisor
    white_re = scaled_re * response_re[:, None] - scaled_im * response_im[:, None]
    white_im = scaled_re * response_im[:, None] + scaled_im * response_re[:, None]
    whitened = jnp.stack([white_re, white_im], axis=1).astype(jnp.bfloat16)
    whitened = whitened.reshape(seg_count, block_bins, 2, sections, seg_dev)
    whitened = jnp.transpose(whitened, (0, 1, 3, 2, 4))
    seg_rank = lax.axis_index("seg")
    pieces = [lax.dynamic_index_in_dim(whitened, seg_rank, axis=0, keepdims=False)]
    for shift in range(1, seg_count):
        outgoing = lax.dynamic_index_in_dim(
            whitened, (seg_rank + shift) % seg_count, axis=0, keepdims=False
        )
        pairs = [(source, (source + shift) % seg_count) for source in range(seg_count)]
        pieces.append(lax.ppermute(outgoing, "seg", pairs))
    local = jnp.stack(pieces, axis=3).reshape(block_bins, sections, -1)
    all_segs = seg_dev * seg_count
    table_width = local.shape[-1]
    table = jnp.concatenate([send_list[0], recv_row[0]], axis=1).reshape(-1)
    table_len = table.shape[0]
    slab = jnp.pad(table.astype(jnp.bfloat16), (0, sections * table_width - table_len))
    carried = jnp.concatenate([local, slab.reshape(1, sections, table_width)], axis=0)
    blk_rank = lax.axis_index("blk")
    everything = gather_blocks(carried, owners_count, blk_rank)
    gathered = everything[:, :block_bins]
    table_part = everything[:, block_bins].reshape(owners_count, -1)[:, :table_len]
    table_part = table_part.astype(jnp.int32).reshape(owners_count, owners_count, 2 * capacity)
    if owners_count & (owners_count - 1) == 0:
        source_of = blk_rank ^ jnp.arange(owners_count, dtype=jnp.int32)
        table_part = jnp.take(table_part, source_of, axis=0)
    send_all = table_part[..., :capacity]
    recv_all = table_part[..., capacity:]
    rows_count = owners_count * OWN
    chans_count = owners_count * sections
    chosen = jnp.transpose(send_all, (1, 0, 2))
    valid = (chosen < sections) & (recv_all < OWN)
    source_ids = jnp.arange(owners_count, dtype=jnp.int32)[None, :, None]
    owner_ids = jnp.arange(owners_count, dtype=jnp.int32)[:, None, None]
    channel = jnp.where(valid, source_ids * sections + chosen, -1).reshape(-1)
    target = jnp.where(valid, owner_ids * OWN + recv_all, -1).reshape(-1)
    row_hot = (target[:, None] == jnp.arange(rows_count, dtype=jnp.int32)[None, :]).astype(
        jnp.bfloat16
    )
    chan_hot = (channel[:, None] == jnp.arange(chans_count, dtype=jnp.int32)[None, :]).astype(
        jnp.bfloat16
    )
    selector = jnp.einsum(
        "er,ec->rc", row_hot, chan_hot, preferred_element_type=jnp.float32
    ).astype(jnp.bfloat16)
    selector = selector.reshape(rows_count, owners_count, sections)
    if owners_count & (owners_count - 1) == 0:
        selector = jnp.take(selector, source_of, axis=1)
    routed = jnp.einsum(
        "rsc,sbcq->brq", selector, gathered, preferred_element_type=jnp.float32
    ).astype(jnp.bfloat16)
    own = lax.dynamic_slice_in_dim(routed, blk_rank * OWN, OWN, axis=1)
    own_re = own[..., :all_segs]
    own_im = own[..., all_segs:]
    rotated = jnp.concatenate([own_im, -own_re], axis=-1)
    lhs = jnp.concatenate([own, rotated], axis=1)
    cross = jnp.einsum("bpq,bjq->bpj", lhs, routed, preferred_element_type=jnp.float32)
    cross = cross.reshape(block_bins, 2, OWN, rows_count)
    return jnp.transpose(cross, (1, 0, 2, 3)) / jnp.float32(all_segs)


def solution(mesh):
    placed = (
        P(("groups", "blk"), "seg", "freq"),
        P(),
        P(("groups", "blk"), None, None),
        P(("groups", "blk"), None, None),
    )
    return jax.shard_map(
        per_device,
        mesh=mesh,
        in_specs=placed,
        out_specs=P(None, ("seg", "freq"), ("groups", "blk"), None),
        check_vma=False,
    )
```

```python
import math

import jax
import jax.numpy as jnp
from jax import lax
from jax.sharding import PartitionSpec as P

SEG_LEN = 16384
BINS = 256
BAND_LO = 128
HW = 4
OWN = 16


WHITEN_FLOOR = 0.25
TWO_PI = 2.0 * math.pi


def swapped(value, axis, distance):
    mask = 2**distance
    pairs = [(source, source ^ mask) for source in range(lax.axis_size(axis))]
    return lax.ppermute(value, axis, pairs)


def dft_tables(band_index, sample_index):
    wavenumber = BAND_LO + band_index
    phase_int = wavenumber[:, None] * sample_index[None, :] % SEG_LEN
    angles = phase_int.astype(jnp.float32) * (TWO_PI / SEG_LEN)
    norm_scale = 1.0 / math.sqrt(SEG_LEN)
    cos_part = (jnp.cos(angles) * norm_scale).astype(jnp.bfloat16)
    sin_part = (-jnp.sin(angles) * norm_scale).astype(jnp.bfloat16)
    return (cos_part, sin_part)


def dft_tables_fast(band_index, first_sample, count):
    lanes = 128
    wavenumber = BAND_LO + band_index
    coarse = (first_sample + lanes * jnp.arange(count // lanes, dtype=jnp.int32))
    fine = jnp.arange(lanes, dtype=jnp.int32)
    coarse_angle = (wavenumber[:, None] * coarse[None, :] % SEG_LEN).astype(jnp.float32) * (
        TWO_PI / SEG_LEN
    )
    fine_angle = (wavenumber[:, None] * fine[None, :] % SEG_LEN).astype(jnp.float32) * (
        TWO_PI / SEG_LEN
    )
    cos_a = jnp.cos(coarse_angle)[:, :, None]
    sin_a = jnp.sin(coarse_angle)[:, :, None]
    cos_b = jnp.cos(fine_angle)[:, None, :]
    sin_b = jnp.sin(fine_angle)[:, None, :]
    norm_scale = 1.0 / math.sqrt(SEG_LEN)
    cos_sum = cos_a * cos_b - sin_a * sin_b
    sin_sum = sin_a * cos_b + cos_a * sin_b
    rows = band_index.shape[0]
    cos_part = (cos_sum * norm_scale).astype(jnp.bfloat16).reshape(rows, count)
    sin_part = (-sin_sum * norm_scale).astype(jnp.bfloat16).reshape(rows, count)
    return (cos_part, sin_part)


def response(band_index, taps):
    wavenumber = BAND_LO + band_index
    lag_index = jnp.arange(taps.shape[0], dtype=jnp.int32)
    phase_int = wavenumber[:, None] * lag_index[None, :] % SEG_LEN
    angles = phase_int.astype(jnp.float32) * (TWO_PI / SEG_LEN)
    real_part = jnp.dot(jnp.cos(angles), taps, precision=lax.Precision.HIGHEST)
    imag_part = jnp.dot(-jnp.sin(angles), taps, precision=lax.Precision.HIGHEST)
    return (real_part, imag_part)


def gather_blocks(carried, count, rank):
    if count & (count - 1) != 0:
        return lax.all_gather(carried, "blk", axis=0, tiled=False)
    masks = []
    step = count // 2
    while step >= 1:
        masks.append(step)
        step //= 2
    if not masks:
        return carried[None]
    first = masks[0]
    rest = masks[1:]
    pairs = [(source, source ^ first) for source in range(count)]
    held = jnp.stack([carried, lax.ppermute(carried, "blk", pairs)], axis=0)
    split = (held.shape[1] + 1) // 2
    halves = [held[:, :split], held[:, split:]]
    orders = [rest, rest[::-1]]
    results = []
    for part, order in zip(halves, orders):
        done = [first]
        for mask in order:
            pairs = [(source, source ^ mask) for source in range(count)]
            arrived = lax.ppermute(part, "blk", pairs)
            done.append(mask)
            axis = sorted(done, reverse=True).index(mask)
            part = jnp.stack([part, arrived], axis=axis)
        results.append(part.reshape((count,) + part.shape[len(masks):]))
    return jnp.concatenate(results, axis=1)


def per_device(raw, taps, send_list, recv_row):
    owners_count = lax.axis_size("blk")
    seg_count = lax.axis_size("seg")
    freq_count = lax.axis_size("freq")
    freq_rank = lax.axis_index("freq")
    sections, seg_dev, half_len = raw.shape
    records = raw.reshape(sections * seg_dev, half_len)
    device_bins = BINS // freq_count
    block_bins = device_bins // seg_count
    capacity = send_list.shape[2]

    def band_of(row_ids):
        owner_core = row_ids // device_bins
        local_row = row_ids % device_bins
        return (
            local_row // block_bins * freq_count + owner_core
        ) * block_bins + local_row % block_bins

    band_rows = band_of(jnp.arange(device_bins * freq_count, dtype=jnp.int32))
    cos_part, sin_part = dft_tables_fast(band_rows, freq_rank * half_len, half_len)
    contract = (((1,), (1,)), ((), ()))
    real_all = lax.dot_general(cos_part, records, contract, preferred_element_type=jnp.float32)
    imag_all = lax.dot_general(sin_part, records, contract, preferred_element_type=jnp.float32)
    blocks = jnp.stack([real_all, imag_all], axis=1)
    blocks = blocks.reshape(freq_count, device_bins, 2, records.shape[0])
    if freq_count == 2:
        kept = jnp.where(freq_rank == 0, blocks[0], blocks[1])
        sent = jnp.where(freq_rank == 0, blocks[1], blocks[0])
        spectra = kept + swapped(sent, "freq", 0)
    else:
        spectra = lax.psum_scatter(
            blocks.reshape(device_bins * freq_count, 2, records.shape[0]),
            "freq",
            scatter_dimension=0,
            tiled=True,
        )
    real_part = spectra[:, 0]
    imag_part = spectra[:, 1]
    amplitude = jnp.sqrt(real_part * real_part + imag_part * imag_part + 1e-06)
    amp_blocks = amplitude.reshape(seg_count, block_bins, -1)
    band_rims = jnp.stack([amp_blocks[:, :HW], amp_blocks[:, block_bins - HW :]])
    partner = swapped(band_rims, "freq", 0)
    zero_rim = jnp.zeros_like(partner[1][:1])
    right_prev = jnp.concatenate([zero_rim, partner[1][:-1]], axis=0)
    left_next = jnp.concatenate([partner[0][1:], zero_rim], axis=0)
    first_core = freq_rank == 0
    lower_rim = jnp.where(first_core, right_prev, partner[1])
    upper_rim = jnp.where(first_core, partner[0], left_next)
    padded = jnp.concatenate([lower_rim, amp_blocks, upper_rim], axis=1)
    window_sum = padded[:, 0:block_bins]
    for offset_step in range(1, 2 * HW + 1):
        window_sum = window_sum + padded[:, offset_step : offset_step + block_bins]
    span_ids = jnp.arange(seg_count, dtype=jnp.int32)[:, None]
    offsets = jnp.arange(block_bins, dtype=jnp.int32)[None, :]
    position = (span_ids * freq_count + freq_rank) * block_bins + offsets
    counted = jnp.minimum(position + HW, BINS - 1) - jnp.maximum(position - HW, 0) + 1
    smooth = window_sum / counted.astype(jnp.float32)[:, :, None]
    divisor = jnp.maximum(smooth, WHITEN_FLOOR).reshape(device_bins, -1)
    local_bins = freq_rank * device_bins + jnp.arange(device_bins, dtype=jnp.int32)
    response_re, response_im = response(band_of(local_bins), taps)
    scaled_re = real_part / divisor
    scaled_im = imag_part / divisor
    white_re = scaled_re * response_re[:, None] - scaled_im * response_im[:, None]
    white_im = scaled_re * response_im[:, None] + scaled_im * response_re[:, None]
    whitened = jnp.stack([white_re, white_im], axis=1).astype(jnp.bfloat16)
    whitened = whitened.reshape(seg_count, block_bins, 2, sections, seg_dev)
    whitened = jnp.transpose(whitened, (0, 3, 1, 2, 4))
    seg_rank = lax.axis_index("seg")
    pieces = [lax.dynamic_index_in_dim(whitened, seg_rank, axis=0, keepdims=False)]
    for shift in range(1, seg_count):
        outgoing = lax.dynamic_index_in_dim(
            whitened, (seg_rank + shift) % seg_count, axis=0, keepdims=False
        )
        pairs = [(source, (source + shift) % seg_count) for source in range(seg_count)]
        flat = outgoing.reshape(sections, -1)
        pieces.append(lax.ppermute(flat, "seg", pairs).reshape(outgoing.shape))
    local = jnp.stack(pieces, axis=3).reshape(sections, block_bins, -1)
    all_segs = seg_dev * seg_count
    table_width = local.shape[-1]
    table = jnp.concatenate([send_list[0], recv_row[0]], axis=1).reshape(-1)
    table_len = table.shape[0]
    slab = jnp.pad(table.astype(jnp.bfloat16), (0, sections * table_width - table_len))
    carried = jnp.concatenate([local, slab.reshape(sections, 1, table_width)], axis=1)
    blk_rank = lax.axis_index("blk")
    everything = gather_blocks(carried.reshape(sections, -1), owners_count, blk_rank)
    everything = everything.reshape(owners_count, sections, block_bins + 1, table_width)
    gathered = everything[:, :, :block_bins]
    table_part = everything[:, :, block_bins].reshape(owners_count, -1)[:, :table_len]
    table_part = table_part.astype(jnp.int32).reshape(owners_count, owners_count, 2 * capacity)
    if owners_count & (owners_count - 1) == 0:
        source_of = blk_rank ^ jnp.arange(owners_count, dtype=jnp.int32)
        table_part = jnp.take(table_part, source_of, axis=0)
    send_all = table_part[..., :capacity]
    recv_all = table_part[..., capacity:]
    rows_count = owners_count * OWN
    chans_count = owners_count * sections
    chosen = jnp.transpose(send_all, (1, 0, 2))
    valid = (chosen < sections) & (recv_all < OWN)
    source_ids = jnp.arange(owners_count, dtype=jnp.int32)[None, :, None]
    owner_ids = jnp.arange(owners_count, dtype=jnp.int32)[:, None, None]
    channel = jnp.where(valid, source_ids * sections + chosen, -1).reshape(-1)
    target = jnp.where(valid, owner_ids * OWN + recv_all, -1).reshape(-1)
    row_hot = (target[:, None] == jnp.arange(rows_count, dtype=jnp.int32)[None, :]).astype(
        jnp.bfloat16
    )
    chan_hot = (channel[:, None] == jnp.arange(chans_count, dtype=jnp.int32)[None, :]).astype(
        jnp.bfloat16
    )
    selector = jnp.einsum(
        "er,ec->rc", row_hot, chan_hot, preferred_element_type=jnp.float32
    ).astype(jnp.bfloat16)
    selector = selector.reshape(rows_count, owners_count, sections)
    if owners_count & (owners_count - 1) == 0:
        selector = jnp.take(selector, source_of, axis=1)
    routed = jnp.einsum(
        "rsc,scbq->brq", selector, gathered, preferred_element_type=jnp.float32
    ).astype(jnp.bfloat16)
    own = lax.dynamic_slice_in_dim(routed, blk_rank * OWN, OWN, axis=1)
    own_re = own[..., :all_segs]
    own_im = own[..., all_segs:]
    rotated = jnp.concatenate([own_im, -own_re], axis=-1)
    lhs = jnp.concatenate([own, rotated], axis=1)
    cross = jnp.einsum("bpq,bjq->bpj", lhs, routed, preferred_element_type=jnp.float32)
    cross = cross.reshape(block_bins, 2, OWN, rows_count)
    return jnp.transpose(cross, (1, 0, 2, 3)) / jnp.float32(all_segs)


def solution(mesh):
    placed = (
        P(("groups", "blk"), "seg", "freq"),
        P(),
        P(("groups", "blk"), None, None),
        P(("groups", "blk"), None, None),
    )
    return jax.shard_map(
        per_device,
        mesh=mesh,
        in_specs=placed,
        out_specs=P(None, ("seg", "freq"), ("groups", "blk"), None),
        check_vma=False,
    )
```

```python
import math

import jax
import jax.numpy as jnp
from jax import lax
from jax.sharding import PartitionSpec as P

SEG_LEN = 16384
BINS = 256
BAND_LO = 128
HW = 4
OWN = 16


WHITEN_FLOOR = 0.25
TWO_PI = 2.0 * math.pi


def swapped(value, axis, distance):
    mask = 2**distance
    pairs = [(source, source ^ mask) for source in range(lax.axis_size(axis))]
    return lax.ppermute(value, axis, pairs)


def dft_tables(band_index, sample_index):
    wavenumber = BAND_LO + band_index
    phase_int = wavenumber[:, None] * sample_index[None, :] % SEG_LEN
    angles = phase_int.astype(jnp.float32) * (TWO_PI / SEG_LEN)
    norm_scale = 1.0 / math.sqrt(SEG_LEN)
    cos_part = (jnp.cos(angles) * norm_scale).astype(jnp.bfloat16)
    sin_part = (-jnp.sin(angles) * norm_scale).astype(jnp.bfloat16)
    return (cos_part, sin_part)


def dft_tables_fast(band_index, first_sample, count):
    lanes = 128
    wavenumber = BAND_LO + band_index
    coarse = (first_sample + lanes * jnp.arange(count // lanes, dtype=jnp.int32))
    fine = jnp.arange(lanes, dtype=jnp.int32)
    coarse_angle = (wavenumber[:, None] * coarse[None, :] % SEG_LEN).astype(jnp.float32) * (
        TWO_PI / SEG_LEN
    )
    fine_angle = (wavenumber[:, None] * fine[None, :] % SEG_LEN).astype(jnp.float32) * (
        TWO_PI / SEG_LEN
    )
    cos_a = jnp.cos(coarse_angle)[:, :, None]
    sin_a = jnp.sin(coarse_angle)[:, :, None]
    cos_b = jnp.cos(fine_angle)[:, None, :]
    sin_b = jnp.sin(fine_angle)[:, None, :]
    norm_scale = 1.0 / math.sqrt(SEG_LEN)
    cos_sum = cos_a * cos_b - sin_a * sin_b
    sin_sum = sin_a * cos_b + cos_a * sin_b
    rows = band_index.shape[0]
    cos_part = (cos_sum * norm_scale).astype(jnp.bfloat16).reshape(rows, count)
    sin_part = (-sin_sum * norm_scale).astype(jnp.bfloat16).reshape(rows, count)
    return (cos_part, sin_part)


def response(band_index, taps):
    wavenumber = BAND_LO + band_index
    lag_index = jnp.arange(taps.shape[0], dtype=jnp.int32)
    phase_int = wavenumber[:, None] * lag_index[None, :] % SEG_LEN
    angles = phase_int.astype(jnp.float32) * (TWO_PI / SEG_LEN)
    real_part = jnp.dot(jnp.cos(angles), taps, precision=lax.Precision.HIGHEST)
    imag_part = jnp.dot(-jnp.sin(angles), taps, precision=lax.Precision.HIGHEST)
    return (real_part, imag_part)


def gather_blocks(carried, count, rank):
    if count & (count - 1) != 0:
        return lax.all_gather(carried, "blk", axis=0, tiled=False)
    masks = []
    step = count // 2
    while step >= 1:
        masks.append(step)
        step //= 2
    if not masks:
        return carried[None]
    first = masks[0]
    rest = masks[1:]
    pairs = [(source, source ^ first) for source in range(count)]
    held = jnp.stack([carried, lax.ppermute(carried, "blk", pairs)], axis=0)
    split = (held.shape[1] + 1) // 2
    halves = [held[:, :split], held[:, split:]]
    orders = [rest, rest[::-1]]
    results = []
    for part, order in zip(halves, orders):
        done = [first]
        for mask in order:
            pairs = [(source, source ^ mask) for source in range(count)]
            arrived = lax.ppermute(part, "blk", pairs)
            done.append(mask)
            axis = sorted(done, reverse=True).index(mask)
            part = jnp.stack([part, arrived], axis=axis)
        results.append(part.reshape((count,) + part.shape[len(masks):]))
    return jnp.concatenate(results, axis=1)


def per_device(raw, taps, send_list, recv_row):
    owners_count = lax.axis_size("blk")
    seg_count = lax.axis_size("seg")
    freq_count = lax.axis_size("freq")
    freq_rank = lax.axis_index("freq")
    seg_rank = lax.axis_index("seg")
    blk_rank = lax.axis_index("blk")
    sections, seg_dev, half_len = raw.shape
    device_bins = BINS // freq_count
    block_bins = device_bins // seg_count
    capacity = send_list.shape[2]
    all_segs = seg_dev * seg_count
    table_width = 2 * all_segs

    def band_of(row_ids):
        owner_core = row_ids // device_bins
        local_row = row_ids % device_bins
        return (
            local_row // block_bins * freq_count + owner_core
        ) * block_bins + local_row % block_bins

    band_rows = band_of(jnp.arange(device_bins * freq_count, dtype=jnp.int32))
    cos_part, sin_part = dft_tables_fast(band_rows, freq_rank * half_len, half_len)
    contract = (((1,), (1,)), ((), ()))
    local_bins = freq_rank * device_bins + jnp.arange(device_bins, dtype=jnp.int32)
    response_re, response_im = response(band_of(local_bins), taps)
    span_ids = jnp.arange(seg_count, dtype=jnp.int32)[:, None]
    offsets = jnp.arange(block_bins, dtype=jnp.int32)[None, :]
    position = (span_ids * freq_count + freq_rank) * block_bins + offsets
    counted = jnp.minimum(position + HW, BINS - 1) - jnp.maximum(position - HW, 0) + 1
    table = jnp.concatenate([send_list[0], recv_row[0]], axis=1).reshape(-1)
    table_len = table.shape[0]
    slab = jnp.pad(table.astype(jnp.bfloat16), (0, sections * table_width - table_len))
    slab = slab.reshape(sections, 1, table_width)

    def whiten_part(part_raw):
        part_sections = part_raw.shape[0]
        records = part_raw.reshape(part_sections * seg_dev, half_len)
        real_all = lax.dot_general(cos_part, records, contract, preferred_element_type=jnp.float32)
        imag_all = lax.dot_general(sin_part, records, contract, preferred_element_type=jnp.float32)
        blocks = jnp.stack([real_all, imag_all], axis=1)
        blocks = blocks.reshape(freq_count, device_bins, 2, records.shape[0])
        if freq_count == 2:
            kept = jnp.where(freq_rank == 0, blocks[0], blocks[1])
            sent = jnp.where(freq_rank == 0, blocks[1], blocks[0])
            spectra = kept + swapped(sent, "freq", 0)
        else:
            spectra = lax.psum_scatter(
                blocks.reshape(device_bins * freq_count, 2, records.shape[0]),
                "freq",
                scatter_dimension=0,
                tiled=True,
            )
        real_part = spectra[:, 0]
        imag_part = spectra[:, 1]
        amplitude = jnp.sqrt(real_part * real_part + imag_part * imag_part + 1e-06)
        amp_blocks = amplitude.reshape(seg_count, block_bins, -1)
        band_rims = jnp.stack([amp_blocks[:, :HW], amp_blocks[:, block_bins - HW :]])
        partner = swapped(band_rims, "freq", 0)
        zero_rim = jnp.zeros_like(partner[1][:1])
        right_prev = jnp.concatenate([zero_rim, partner[1][:-1]], axis=0)
        left_next = jnp.concatenate([partner[0][1:], zero_rim], axis=0)
        first_core = freq_rank == 0
        lower_rim = jnp.where(first_core, right_prev, partner[1])
        upper_rim = jnp.where(first_core, partner[0], left_next)
        padded = jnp.concatenate([lower_rim, amp_blocks, upper_rim], axis=1)
        window_sum = padded[:, 0:block_bins]
        for offset_step in range(1, 2 * HW + 1):
            window_sum = window_sum + padded[:, offset_step : offset_step + block_bins]
        smooth = window_sum / counted.astype(jnp.float32)[:, :, None]
        divisor = jnp.maximum(smooth, WHITEN_FLOOR).reshape(device_bins, -1)
        scaled_re = real_part / divisor
        scaled_im = imag_part / divisor
        white_re = scaled_re * response_re[:, None] - scaled_im * response_im[:, None]
        white_im = scaled_re * response_im[:, None] + scaled_im * response_re[:, None]
        whitened = jnp.stack([white_re, white_im], axis=1).astype(jnp.bfloat16)
        whitened = whitened.reshape(seg_count, block_bins, 2, part_sections, seg_dev)
        return jnp.transpose(whitened, (0, 3, 1, 2, 4))

    def exchange_part(whitened):
        part_sections = whitened.shape[1]
        pieces = [lax.dynamic_index_in_dim(whitened, seg_rank, axis=0, keepdims=False)]
        for shift in range(1, seg_count):
            outgoing = lax.dynamic_index_in_dim(
                whitened, (seg_rank + shift) % seg_count, axis=0, keepdims=False
            )
            pairs = [(source, (source + shift) % seg_count) for source in range(seg_count)]
            flat = outgoing.reshape(part_sections, -1)
            pieces.append(lax.ppermute(flat, "seg", pairs).reshape(outgoing.shape))
        return jnp.stack(pieces, axis=3).reshape(part_sections, block_bins, -1)

    parts = 2 if sections % 4 == 0 else 1
    part_len = sections // parts
    gathered_parts = []
    next_raw = raw[:part_len]
    for part in range(parts):
        lo = part * part_len
        whitened = whiten_part(next_raw)
        if part + 1 < parts:
            next_raw, whitened = lax.optimization_barrier(
                (raw[lo + part_len : lo + 2 * part_len], whitened)
            )
        local = exchange_part(whitened)
        carried = jnp.concatenate([local, slab[lo : lo + part_len]], axis=1)
        moved = gather_blocks(carried.reshape(part_len, -1), owners_count, blk_rank)
        gathered_parts.append(
            moved.reshape(owners_count, part_len, block_bins + 1, table_width)
        )
    everything = jnp.concatenate(gathered_parts, axis=1)
    gathered = everything[:, :, :block_bins]
    table_part = everything[:, :, block_bins].reshape(owners_count, -1)[:, :table_len]
    table_part = table_part.astype(jnp.int32).reshape(owners_count, owners_count, 2 * capacity)
    if owners_count & (owners_count - 1) == 0:
        source_of = blk_rank ^ jnp.arange(owners_count, dtype=jnp.int32)
        table_part = jnp.take(table_part, source_of, axis=0)
    send_all = table_part[..., :capacity]
    recv_all = table_part[..., capacity:]
    rows_count = owners_count * OWN
    chans_count = owners_count * sections
    chosen = jnp.transpose(send_all, (1, 0, 2))
    valid = (chosen < sections) & (recv_all < OWN)
    source_ids = jnp.arange(owners_count, dtype=jnp.int32)[None, :, None]
    owner_ids = jnp.arange(owners_count, dtype=jnp.int32)[:, None, None]
    channel = jnp.where(valid, source_ids * sections + chosen, -1).reshape(-1)
    target = jnp.where(valid, owner_ids * OWN + recv_all, -1).reshape(-1)
    row_hot = (target[:, None] == jnp.arange(rows_count, dtype=jnp.int32)[None, :]).astype(
        jnp.bfloat16
    )
    chan_hot = (channel[:, None] == jnp.arange(chans_count, dtype=jnp.int32)[None, :]).astype(
        jnp.bfloat16
    )
    selector = jnp.einsum(
        "er,ec->rc", row_hot, chan_hot, preferred_element_type=jnp.float32
    ).astype(jnp.bfloat16)
    selector = selector.reshape(rows_count, owners_count, sections)
    if owners_count & (owners_count - 1) == 0:
        selector = jnp.take(selector, source_of, axis=1)
    routed = jnp.einsum(
        "rsc,scbq->brq", selector, gathered, preferred_element_type=jnp.float32
    ).astype(jnp.bfloat16)
    own = lax.dynamic_slice_in_dim(routed, blk_rank * OWN, OWN, axis=1)
    own_re = own[..., :all_segs]
    own_im = own[..., all_segs:]
    rotated = jnp.concatenate([own_im, -own_re], axis=-1)
    lhs = jnp.concatenate([own, rotated], axis=1)
    cross = jnp.einsum("bpq,bjq->bpj", lhs, routed, preferred_element_type=jnp.float32)
    cross = cross.reshape(block_bins, 2, OWN, rows_count)
    return jnp.transpose(cross, (1, 0, 2, 3)) / jnp.float32(all_segs)


def solution(mesh):
    placed = (
        P(("groups", "blk"), "seg", "freq"),
        P(),
        P(("groups", "blk"), None, None),
        P(("groups", "blk"), None, None),
    )
    return jax.shard_map(
        per_device,
        mesh=mesh,
        in_specs=placed,
        out_specs=P(None, ("seg", "freq"), ("groups", "blk"), None),
        check_vma=False,
    )
```

```python
import math

import jax
import jax.numpy as jnp
from jax import lax
from jax.experimental import pallas as pl
from jax.experimental.pallas import tpu as pltpu
from jax.sharding import PartitionSpec as P

SEG_LEN = 16384
BINS = 256
BAND_LO = 128
HW = 4
OWN = 16


WHITEN_FLOOR = 0.25
TWO_PI = 2.0 * math.pi


def swapped(value, axis, distance):
    mask = 2**distance
    pairs = [(source, source ^ mask) for source in range(lax.axis_size(axis))]
    return lax.ppermute(value, axis, pairs)


def dft_tables(band_index, sample_index):
    wavenumber = BAND_LO + band_index
    phase_int = wavenumber[:, None] * sample_index[None, :] % SEG_LEN
    angles = phase_int.astype(jnp.float32) * (TWO_PI / SEG_LEN)
    norm_scale = 1.0 / math.sqrt(SEG_LEN)
    cos_part = (jnp.cos(angles) * norm_scale).astype(jnp.bfloat16)
    sin_part = (-jnp.sin(angles) * norm_scale).astype(jnp.bfloat16)
    return (cos_part, sin_part)


def dft_tables_fast(band_index, first_sample, count):
    lanes = 128
    wavenumber = BAND_LO + band_index
    coarse = (first_sample + lanes * jnp.arange(count // lanes, dtype=jnp.int32))
    fine = jnp.arange(lanes, dtype=jnp.int32)
    coarse_angle = (wavenumber[:, None] * coarse[None, :] % SEG_LEN).astype(jnp.float32) * (
        TWO_PI / SEG_LEN
    )
    fine_angle = (wavenumber[:, None] * fine[None, :] % SEG_LEN).astype(jnp.float32) * (
        TWO_PI / SEG_LEN
    )
    cos_a = jnp.cos(coarse_angle)[:, :, None]
    sin_a = jnp.sin(coarse_angle)[:, :, None]
    cos_b = jnp.cos(fine_angle)[:, None, :]
    sin_b = jnp.sin(fine_angle)[:, None, :]
    norm_scale = 1.0 / math.sqrt(SEG_LEN)
    cos_sum = cos_a * cos_b - sin_a * sin_b
    sin_sum = sin_a * cos_b + cos_a * sin_b
    rows = band_index.shape[0]
    cos_part = (cos_sum * norm_scale).astype(jnp.bfloat16).reshape(rows, count)
    sin_part = (-sin_sum * norm_scale).astype(jnp.bfloat16).reshape(rows, count)
    return (cos_part, sin_part)


def response(band_index, taps):
    wavenumber = BAND_LO + band_index
    lag_index = jnp.arange(taps.shape[0], dtype=jnp.int32)
    phase_int = wavenumber[:, None] * lag_index[None, :] % SEG_LEN
    angles = phase_int.astype(jnp.float32) * (TWO_PI / SEG_LEN)
    real_part = jnp.dot(jnp.cos(angles), taps, precision=lax.Precision.HIGHEST)
    imag_part = jnp.dot(-jnp.sin(angles), taps, precision=lax.Precision.HIGHEST)
    return (real_part, imag_part)


def dft_kernel(rec_ref, cos_a_ref, nsin_a_ref, cos_b_ref, sin_b_ref, re_ref, im_ref):
    step = pl.program_id(0)
    lanes = cos_b_ref.shape[0]
    per_step = rec_ref.shape[1] // lanes

    @pl.when(step == 0)
    def _():
        re_ref[...] = jnp.zeros_like(re_ref)
        im_ref[...] = jnp.zeros_like(im_ref)

    cos_b = cos_b_ref[...]
    sin_b = sin_b_ref[...]
    cos_tiles = []
    sin_tiles = []
    for inner in range(per_step):
        row = step * per_step + inner
        cos_a = cos_a_ref[pl.ds(row, 1), :]
        nsin_a = nsin_a_ref[pl.ds(row, 1), :]
        cos_tiles.append((cos_a * cos_b + nsin_a * sin_b).astype(jnp.bfloat16))
        sin_tiles.append((nsin_a * cos_b - cos_a * sin_b).astype(jnp.bfloat16))
    cos_tile = jnp.concatenate(cos_tiles, axis=0)
    sin_tile = jnp.concatenate(sin_tiles, axis=0)
    rec = rec_ref[...]
    re_ref[...] += jnp.dot(rec, cos_tile, preferred_element_type=jnp.float32)
    im_ref[...] += jnp.dot(rec, sin_tile, preferred_element_type=jnp.float32)


def dft_fused(records, band_index, first_sample):
    lanes = 128
    chunk = 512
    count = records.shape[1]
    wavenumber = BAND_LO + band_index
    coarse = first_sample + lanes * jnp.arange(count // lanes, dtype=jnp.int32)
    fine = jnp.arange(lanes, dtype=jnp.int32)
    coarse_angle = (coarse[:, None] * wavenumber[None, :] % SEG_LEN).astype(jnp.float32) * (
        TWO_PI / SEG_LEN
    )
    fine_angle = (fine[:, None] * wavenumber[None, :] % SEG_LEN).astype(jnp.float32) * (
        TWO_PI / SEG_LEN
    )
    norm_scale = 1.0 / math.sqrt(SEG_LEN)
    cos_a = jnp.cos(coarse_angle)
    nsin_a = -jnp.sin(coarse_angle)
    cos_b = jnp.cos(fine_angle) * norm_scale
    sin_b = jnp.sin(fine_angle) * norm_scale
    rows = records.shape[0]
    bins = band_index.shape[0]
    full = lambda step: (0, 0)
    return pl.pallas_call(
        dft_kernel,
        grid=(count // chunk,),
        in_specs=[
            pl.BlockSpec((rows, chunk), lambda step: (0, step)),
            pl.BlockSpec(cos_a.shape, full),
            pl.BlockSpec(nsin_a.shape, full),
            pl.BlockSpec(cos_b.shape, full),
            pl.BlockSpec(sin_b.shape, full),
        ],
        out_specs=[pl.BlockSpec((rows, bins), full), pl.BlockSpec((rows, bins), full)],
        out_shape=[
            jax.ShapeDtypeStruct((rows, bins), jnp.float32),
            jax.ShapeDtypeStruct((rows, bins), jnp.float32),
        ],
        compiler_params=pltpu.CompilerParams(dimension_semantics=("arbitrary",)),
    )(records, cos_a, nsin_a, cos_b, sin_b)


def gather_blocks(carried, count, rank):
    if count & (count - 1) != 0:
        return lax.all_gather(carried, "blk", axis=0, tiled=False)
    masks = []
    step = count // 2
    while step >= 1:
        masks.append(step)
        step //= 2
    if not masks:
        return carried[None]
    first = masks[0]
    rest = masks[1:]
    pairs = [(source, source ^ first) for source in range(count)]
    held = jnp.stack([carried, lax.ppermute(carried, "blk", pairs)], axis=0)
    split = (held.shape[1] + 1) // 2
    halves = [held[:, :split], held[:, split:]]
    orders = [rest, rest[::-1]]
    results = []
    for part, order in zip(halves, orders):
        done = [first]
        for mask in order:
            pairs = [(source, source ^ mask) for source in range(count)]
            arrived = lax.ppermute(part, "blk", pairs)
            done.append(mask)
            axis = sorted(done, reverse=True).index(mask)
            part = jnp.stack([part, arrived], axis=axis)
        results.append(part.reshape((count,) + part.shape[len(masks):]))
    return jnp.concatenate(results, axis=1)


def per_device(raw, taps, send_list, recv_row):
    owners_count = lax.axis_size("blk")
    seg_count = lax.axis_size("seg")
    freq_count = lax.axis_size("freq")
    freq_rank = lax.axis_index("freq")
    sections, seg_dev, half_len = raw.shape
    records = raw.reshape(sections * seg_dev, half_len)
    device_bins = BINS // freq_count
    block_bins = device_bins // seg_count
    capacity = send_list.shape[2]

    def band_of(row_ids):
        owner_core = row_ids // device_bins
        local_row = row_ids % device_bins
        return (
            local_row // block_bins * freq_count + owner_core
        ) * block_bins + local_row % block_bins

    band_rows = band_of(jnp.arange(device_bins * freq_count, dtype=jnp.int32))
    real_t, imag_t = dft_fused(records, band_rows, freq_rank * half_len)
    real_all = real_t.T
    imag_all = imag_t.T
    blocks = jnp.stack([real_all, imag_all], axis=1)
    blocks = blocks.reshape(freq_count, device_bins, 2, records.shape[0])
    if freq_count == 2:
        kept = jnp.where(freq_rank == 0, blocks[0], blocks[1])
        sent = jnp.where(freq_rank == 0, blocks[1], blocks[0])
        spectra = kept + swapped(sent, "freq", 0)
    else:
        spectra = lax.psum_scatter(
            blocks.reshape(device_bins * freq_count, 2, records.shape[0]),
            "freq",
            scatter_dimension=0,
            tiled=True,
        )
    real_part = spectra[:, 0]
    imag_part = spectra[:, 1]
    amplitude = jnp.sqrt(real_part * real_part + imag_part * imag_part + 1e-06)
    amp_blocks = amplitude.reshape(seg_count, block_bins, -1)
    band_rims = jnp.stack([amp_blocks[:, :HW], amp_blocks[:, block_bins - HW :]])
    partner = swapped(band_rims, "freq", 0)
    zero_rim = jnp.zeros_like(partner[1][:1])
    right_prev = jnp.concatenate([zero_rim, partner[1][:-1]], axis=0)
    left_next = jnp.concatenate([partner[0][1:], zero_rim], axis=0)
    first_core = freq_rank == 0
    lower_rim = jnp.where(first_core, right_prev, partner[1])
    upper_rim = jnp.where(first_core, partner[0], left_next)
    padded = jnp.concatenate([lower_rim, amp_blocks, upper_rim], axis=1)
    window_sum = padded[:, 0:block_bins]
    for offset_step in range(1, 2 * HW + 1):
        window_sum = window_sum + padded[:, offset_step : offset_step + block_bins]
    span_ids = jnp.arange(seg_count, dtype=jnp.int32)[:, None]
    offsets = jnp.arange(block_bins, dtype=jnp.int32)[None, :]
    position = (span_ids * freq_count + freq_rank) * block_bins + offsets
    counted = jnp.minimum(position + HW, BINS - 1) - jnp.maximum(position - HW, 0) + 1
    smooth = window_sum / counted.astype(jnp.float32)[:, :, None]
    divisor = jnp.maximum(smooth, WHITEN_FLOOR).reshape(device_bins, -1)
    local_bins = freq_rank * device_bins + jnp.arange(device_bins, dtype=jnp.int32)
    response_re, response_im = response(band_of(local_bins), taps)
    scaled_re = real_part / divisor
    scaled_im = imag_part / divisor
    white_re = scaled_re * response_re[:, None] - scaled_im * response_im[:, None]
    white_im = scaled_re * response_im[:, None] + scaled_im * response_re[:, None]
    whitened = jnp.stack([white_re, white_im], axis=1).astype(jnp.bfloat16)
    whitened = whitened.reshape(seg_count, block_bins, 2, sections, seg_dev)
    whitened = jnp.transpose(whitened, (0, 3, 1, 2, 4))
    seg_rank = lax.axis_index("seg")
    pieces = [lax.dynamic_index_in_dim(whitened, seg_rank, axis=0, keepdims=False)]
    for shift in range(1, seg_count):
        outgoing = lax.dynamic_index_in_dim(
            whitened, (seg_rank + shift) % seg_count, axis=0, keepdims=False
        )
        pairs = [(source, (source + shift) % seg_count) for source in range(seg_count)]
        flat = outgoing.reshape(sections, -1)
        pieces.append(lax.ppermute(flat, "seg", pairs).reshape(outgoing.shape))
    local = jnp.stack(pieces, axis=3).reshape(sections, block_bins, -1)
    all_segs = seg_dev * seg_count
    table_width = local.shape[-1]
    table = jnp.concatenate([send_list[0], recv_row[0]], axis=1).reshape(-1)
    table_len = table.shape[0]
    slab = jnp.pad(table.astype(jnp.bfloat16), (0, sections * table_width - table_len))
    carried = jnp.concatenate([local, slab.reshape(sections, 1, table_width)], axis=1)
    blk_rank = lax.axis_index("blk")
    everything = gather_blocks(carried.reshape(sections, -1), owners_count, blk_rank)
    everything = everything.reshape(owners_count, sections, block_bins + 1, table_width)
    gathered = everything[:, :, :block_bins]
    table_part = everything[:, :, block_bins].reshape(owners_count, -1)[:, :table_len]
    table_part = table_part.astype(jnp.int32).reshape(owners_count, owners_count, 2 * capacity)
    if owners_count & (owners_count - 1) == 0:
        source_of = blk_rank ^ jnp.arange(owners_count, dtype=jnp.int32)
        table_part = jnp.take(table_part, source_of, axis=0)
    send_all = table_part[..., :capacity]
    recv_all = table_part[..., capacity:]
    rows_count = owners_count * OWN
    chans_count = owners_count * sections
    chosen = jnp.transpose(send_all, (1, 0, 2))
    valid = (chosen < sections) & (recv_all < OWN)
    source_ids = jnp.arange(owners_count, dtype=jnp.int32)[None, :, None]
    owner_ids = jnp.arange(owners_count, dtype=jnp.int32)[:, None, None]
    channel = jnp.where(valid, source_ids * sections + chosen, -1).reshape(-1)
    target = jnp.where(valid, owner_ids * OWN + recv_all, -1).reshape(-1)
    row_hot = (target[:, None] == jnp.arange(rows_count, dtype=jnp.int32)[None, :]).astype(
        jnp.bfloat16
    )
    chan_hot = (channel[:, None] == jnp.arange(chans_count, dtype=jnp.int32)[None, :]).astype(
        jnp.bfloat16
    )
    selector = jnp.einsum(
        "er,ec->rc", row_hot, chan_hot, preferred_element_type=jnp.float32
    ).astype(jnp.bfloat16)
    selector = selector.reshape(rows_count, owners_count, sections)
    if owners_count & (owners_count - 1) == 0:
        selector = jnp.take(selector, source_of, axis=1)
    routed = jnp.einsum(
        "rsc,scbq->brq", selector, gathered, preferred_element_type=jnp.float32
    ).astype(jnp.bfloat16)
    own = lax.dynamic_slice_in_dim(routed, blk_rank * OWN, OWN, axis=1)
    own_re = own[..., :all_segs]
    own_im = own[..., all_segs:]
    rotated = jnp.concatenate([own_im, -own_re], axis=-1)
    lhs = jnp.concatenate([own, rotated], axis=1)
    cross = jnp.einsum("bpq,bjq->bpj", lhs, routed, preferred_element_type=jnp.float32)
    cross = cross.reshape(block_bins, 2, OWN, rows_count)
    return jnp.transpose(cross, (1, 0, 2, 3)) / jnp.float32(all_segs)


def solution(mesh):
    placed = (
        P(("groups", "blk"), "seg", "freq"),
        P(),
        P(("groups", "blk"), None, None),
        P(("groups", "blk"), None, None),
    )
    return jax.shard_map(
        per_device,
        mesh=mesh,
        in_specs=placed,
        out_specs=P(None, ("seg", "freq"), ("groups", "blk"), None),
        check_vma=False,
    )
```

```python
import math

import jax
import jax.numpy as jnp
from jax import lax
from jax.experimental import pallas as pl
from jax.experimental.pallas import tpu as pltpu
from jax.sharding import PartitionSpec as P

SEG_LEN = 16384
BINS = 256
BAND_LO = 128
HW = 4
OWN = 16


WHITEN_FLOOR = 0.25
TWO_PI = 2.0 * math.pi


def swapped(value, axis, distance):
    mask = 2**distance
    pairs = [(source, source ^ mask) for source in range(lax.axis_size(axis))]
    return lax.ppermute(value, axis, pairs)


def dft_tables(band_index, sample_index):
    wavenumber = BAND_LO + band_index
    phase_int = wavenumber[:, None] * sample_index[None, :] % SEG_LEN
    angles = phase_int.astype(jnp.float32) * (TWO_PI / SEG_LEN)
    norm_scale = 1.0 / math.sqrt(SEG_LEN)
    cos_part = (jnp.cos(angles) * norm_scale).astype(jnp.bfloat16)
    sin_part = (-jnp.sin(angles) * norm_scale).astype(jnp.bfloat16)
    return (cos_part, sin_part)


def dft_tables_fast(band_index, first_sample, count):
    lanes = 128
    wavenumber = BAND_LO + band_index
    coarse = (first_sample + lanes * jnp.arange(count // lanes, dtype=jnp.int32))
    fine = jnp.arange(lanes, dtype=jnp.int32)
    coarse_angle = (wavenumber[:, None] * coarse[None, :] % SEG_LEN).astype(jnp.float32) * (
        TWO_PI / SEG_LEN
    )
    fine_angle = (wavenumber[:, None] * fine[None, :] % SEG_LEN).astype(jnp.float32) * (
        TWO_PI / SEG_LEN
    )
    cos_a = jnp.cos(coarse_angle)[:, :, None]
    sin_a = jnp.sin(coarse_angle)[:, :, None]
    cos_b = jnp.cos(fine_angle)[:, None, :]
    sin_b = jnp.sin(fine_angle)[:, None, :]
    norm_scale = 1.0 / math.sqrt(SEG_LEN)
    cos_sum = cos_a * cos_b - sin_a * sin_b
    sin_sum = sin_a * cos_b + cos_a * sin_b
    rows = band_index.shape[0]
    cos_part = (cos_sum * norm_scale).astype(jnp.bfloat16).reshape(rows, count)
    sin_part = (-sin_sum * norm_scale).astype(jnp.bfloat16).reshape(rows, count)
    return (cos_part, sin_part)


def response(band_index, taps):
    wavenumber = BAND_LO + band_index
    lag_index = jnp.arange(taps.shape[0], dtype=jnp.int32)
    phase_int = wavenumber[:, None] * lag_index[None, :] % SEG_LEN
    angles = phase_int.astype(jnp.float32) * (TWO_PI / SEG_LEN)
    real_part = jnp.dot(jnp.cos(angles), taps, precision=lax.Precision.HIGHEST)
    imag_part = jnp.dot(-jnp.sin(angles), taps, precision=lax.Precision.HIGHEST)
    return (real_part, imag_part)


def dft_kernel(rec_ref, cos_a_ref, nsin_a_ref, cos_b_ref, sin_b_ref, re_ref, im_ref):
    step = pl.program_id(0)
    lanes = cos_b_ref.shape[0]
    group = 8
    groups = rec_ref.shape[1] // (group * lanes)

    @pl.when(step == 0)
    def _():
        re_ref[...] = jnp.zeros_like(re_ref)
        im_ref[...] = jnp.zeros_like(im_ref)

    def one_group(index, carry):
        row = pl.multiple_of((step * groups + index) * group, group)
        cos_a = cos_a_ref[pl.ds(row, group), :]
        nsin_a = nsin_a_ref[pl.ds(row, group), :]
        cos_b = cos_b_ref[...]
        sin_b = sin_b_ref[...]
        for pair in range(group // 2):
            cos_parts = []
            sin_parts = []
            for half in range(2):
                at = 2 * pair + half
                ca = cos_a[at : at + 1]
                sa = nsin_a[at : at + 1]
                cos_parts.append(ca * cos_b + sa * sin_b)
                sin_parts.append(sa * cos_b - ca * sin_b)
            cos_tile = jnp.concatenate(cos_parts, axis=0).astype(jnp.bfloat16)
            sin_tile = jnp.concatenate(sin_parts, axis=0).astype(jnp.bfloat16)
            first = pl.multiple_of((index * group + 2 * pair) * lanes, 2 * lanes)
            rec = rec_ref[:, pl.ds(first, 2 * lanes)]
            re_ref[...] += jnp.dot(rec, cos_tile, preferred_element_type=jnp.float32)
            im_ref[...] += jnp.dot(rec, sin_tile, preferred_element_type=jnp.float32)
        return carry

    lax.fori_loop(0, groups, one_group, 0)


def dft_fused(records, band_index, first_sample):
    lanes = 128
    chunk = 2048
    count = records.shape[1]
    wavenumber = BAND_LO + band_index
    coarse = first_sample + lanes * jnp.arange(count // lanes, dtype=jnp.int32)
    fine = jnp.arange(lanes, dtype=jnp.int32)
    coarse_angle = (coarse[:, None] * wavenumber[None, :] % SEG_LEN).astype(jnp.float32) * (
        TWO_PI / SEG_LEN
    )
    fine_angle = (fine[:, None] * wavenumber[None, :] % SEG_LEN).astype(jnp.float32) * (
        TWO_PI / SEG_LEN
    )
    norm_scale = 1.0 / math.sqrt(SEG_LEN)
    cos_a = jnp.cos(coarse_angle)
    nsin_a = -jnp.sin(coarse_angle)
    cos_b = jnp.cos(fine_angle) * norm_scale
    sin_b = jnp.sin(fine_angle) * norm_scale
    rows = records.shape[0]
    bins = band_index.shape[0]
    full = lambda step: (0, 0)
    return pl.pallas_call(
        dft_kernel,
        grid=(count // chunk,),
        in_specs=[
            pl.BlockSpec((rows, chunk), lambda step: (0, step)),
            pl.BlockSpec(cos_a.shape, full),
            pl.BlockSpec(nsin_a.shape, full),
            pl.BlockSpec(cos_b.shape, full),
            pl.BlockSpec(sin_b.shape, full),
        ],
        out_specs=[pl.BlockSpec((rows, bins), full), pl.BlockSpec((rows, bins), full)],
        out_shape=[
            jax.ShapeDtypeStruct((rows, bins), jnp.float32),
            jax.ShapeDtypeStruct((rows, bins), jnp.float32),
        ],
        compiler_params=pltpu.CompilerParams(dimension_semantics=("arbitrary",)),
    )(records, cos_a, nsin_a, cos_b, sin_b)


def gather_blocks(carried, count, rank):
    if count & (count - 1) != 0:
        return lax.all_gather(carried, "blk", axis=0, tiled=False)
    masks = []
    step = count // 2
    while step >= 1:
        masks.append(step)
        step //= 2
    if not masks:
        return carried[None]
    first = masks[0]
    rest = masks[1:]
    pairs = [(source, source ^ first) for source in range(count)]
    held = jnp.stack([carried, lax.ppermute(carried, "blk", pairs)], axis=0)
    split = (held.shape[1] + 1) // 2
    halves = [held[:, :split], held[:, split:]]
    orders = [rest, rest[::-1]]
    results = []
    for part, order in zip(halves, orders):
        done = [first]
        for mask in order:
            pairs = [(source, source ^ mask) for source in range(count)]
            arrived = lax.ppermute(part, "blk", pairs)
            done.append(mask)
            axis = sorted(done, reverse=True).index(mask)
            part = jnp.stack([part, arrived], axis=axis)
        results.append(part.reshape((count,) + part.shape[len(masks):]))
    return jnp.concatenate(results, axis=1)


def per_device(raw, taps, send_list, recv_row):
    owners_count = lax.axis_size("blk")
    seg_count = lax.axis_size("seg")
    freq_count = lax.axis_size("freq")
    freq_rank = lax.axis_index("freq")
    sections, seg_dev, half_len = raw.shape
    records = raw.reshape(sections * seg_dev, half_len)
    device_bins = BINS // freq_count
    block_bins = device_bins // seg_count
    capacity = send_list.shape[2]

    def band_of(row_ids):
        owner_core = row_ids // device_bins
        local_row = row_ids % device_bins
        return (
            local_row // block_bins * freq_count + owner_core
        ) * block_bins + local_row % block_bins

    band_rows = band_of(jnp.arange(device_bins * freq_count, dtype=jnp.int32))
    real_t, imag_t = dft_fused(records, band_rows, freq_rank * half_len)
    real_all = real_t.T
    imag_all = imag_t.T
    blocks = jnp.stack([real_all, imag_all], axis=1)
    blocks = blocks.reshape(freq_count, device_bins, 2, records.shape[0])
    if freq_count == 2:
        kept = jnp.where(freq_rank == 0, blocks[0], blocks[1])
        sent = jnp.where(freq_rank == 0, blocks[1], blocks[0])
        spectra = kept + swapped(sent, "freq", 0)
    else:
        spectra = lax.psum_scatter(
            blocks.reshape(device_bins * freq_count, 2, records.shape[0]),
            "freq",
            scatter_dimension=0,
            tiled=True,
        )
    real_part = spectra[:, 0]
    imag_part = spectra[:, 1]
    amplitude = jnp.sqrt(real_part * real_part + imag_part * imag_part + 1e-06)
    amp_blocks = amplitude.reshape(seg_count, block_bins, -1)
    band_rims = jnp.stack([amp_blocks[:, :HW], amp_blocks[:, block_bins - HW :]])
    partner = swapped(band_rims, "freq", 0)
    zero_rim = jnp.zeros_like(partner[1][:1])
    right_prev = jnp.concatenate([zero_rim, partner[1][:-1]], axis=0)
    left_next = jnp.concatenate([partner[0][1:], zero_rim], axis=0)
    first_core = freq_rank == 0
    lower_rim = jnp.where(first_core, right_prev, partner[1])
    upper_rim = jnp.where(first_core, partner[0], left_next)
    padded = jnp.concatenate([lower_rim, amp_blocks, upper_rim], axis=1)
    window_sum = padded[:, 0:block_bins]
    for offset_step in range(1, 2 * HW + 1):
        window_sum = window_sum + padded[:, offset_step : offset_step + block_bins]
    span_ids = jnp.arange(seg_count, dtype=jnp.int32)[:, None]
    offsets = jnp.arange(block_bins, dtype=jnp.int32)[None, :]
    position = (span_ids * freq_count + freq_rank) * block_bins + offsets
    counted = jnp.minimum(position + HW, BINS - 1) - jnp.maximum(position - HW, 0) + 1
    smooth = window_sum / counted.astype(jnp.float32)[:, :, None]
    divisor = jnp.maximum(smooth, WHITEN_FLOOR).reshape(device_bins, -1)
    local_bins = freq_rank * device_bins + jnp.arange(device_bins, dtype=jnp.int32)
    response_re, response_im = response(band_of(local_bins), taps)
    scaled_re = real_part / divisor
    scaled_im = imag_part / divisor
    white_re = scaled_re * response_re[:, None] - scaled_im * response_im[:, None]
    white_im = scaled_re * response_im[:, None] + scaled_im * response_re[:, None]
    whitened = jnp.stack([white_re, white_im], axis=1).astype(jnp.bfloat16)
    whitened = whitened.reshape(seg_count, block_bins, 2, sections, seg_dev)
    whitened = jnp.transpose(whitened, (0, 3, 1, 2, 4))
    seg_rank = lax.axis_index("seg")
    pieces = [lax.dynamic_index_in_dim(whitened, seg_rank, axis=0, keepdims=False)]
    for shift in range(1, seg_count):
        outgoing = lax.dynamic_index_in_dim(
            whitened, (seg_rank + shift) % seg_count, axis=0, keepdims=False
        )
        pairs = [(source, (source + shift) % seg_count) for source in range(seg_count)]
        flat = outgoing.reshape(sections, -1)
        pieces.append(lax.ppermute(flat, "seg", pairs).reshape(outgoing.shape))
    local = jnp.stack(pieces, axis=3).reshape(sections, block_bins, -1)
    all_segs = seg_dev * seg_count
    table_width = local.shape[-1]
    table = jnp.concatenate([send_list[0], recv_row[0]], axis=1).reshape(-1)
    table_len = table.shape[0]
    slab = jnp.pad(table.astype(jnp.bfloat16), (0, sections * table_width - table_len))
    carried = jnp.concatenate([local, slab.reshape(sections, 1, table_width)], axis=1)
    blk_rank = lax.axis_index("blk")
    everything = gather_blocks(carried.reshape(sections, -1), owners_count, blk_rank)
    everything = everything.reshape(owners_count, sections, block_bins + 1, table_width)
    gathered = everything[:, :, :block_bins]
    table_part = everything[:, :, block_bins].reshape(owners_count, -1)[:, :table_len]
    table_part = table_part.astype(jnp.int32).reshape(owners_count, owners_count, 2 * capacity)
    if owners_count & (owners_count - 1) == 0:
        source_of = blk_rank ^ jnp.arange(owners_count, dtype=jnp.int32)
        table_part = jnp.take(table_part, source_of, axis=0)
    send_all = table_part[..., :capacity]
    recv_all = table_part[..., capacity:]
    rows_count = owners_count * OWN
    chans_count = owners_count * sections
    chosen = jnp.transpose(send_all, (1, 0, 2))
    valid = (chosen < sections) & (recv_all < OWN)
    source_ids = jnp.arange(owners_count, dtype=jnp.int32)[None, :, None]
    owner_ids = jnp.arange(owners_count, dtype=jnp.int32)[:, None, None]
    channel = jnp.where(valid, source_ids * sections + chosen, -1).reshape(-1)
    target = jnp.where(valid, owner_ids * OWN + recv_all, -1).reshape(-1)
    row_hot = (target[:, None] == jnp.arange(rows_count, dtype=jnp.int32)[None, :]).astype(
        jnp.bfloat16
    )
    chan_hot = (channel[:, None] == jnp.arange(chans_count, dtype=jnp.int32)[None, :]).astype(
        jnp.bfloat16
    )
    selector = jnp.einsum(
        "er,ec->rc", row_hot, chan_hot, preferred_element_type=jnp.float32
    ).astype(jnp.bfloat16)
    selector = selector.reshape(rows_count, owners_count, sections)
    if owners_count & (owners_count - 1) == 0:
        selector = jnp.take(selector, source_of, axis=1)
    routed = jnp.einsum(
        "rsc,scbq->brq", selector, gathered, preferred_element_type=jnp.float32
    ).astype(jnp.bfloat16)
    own = lax.dynamic_slice_in_dim(routed, blk_rank * OWN, OWN, axis=1)
    own_re = own[..., :all_segs]
    own_im = own[..., all_segs:]
    rotated = jnp.concatenate([own_im, -own_re], axis=-1)
    lhs = jnp.concatenate([own, rotated], axis=1)
    cross = jnp.einsum("bpq,bjq->bpj", lhs, routed, preferred_element_type=jnp.float32)
    cross = cross.reshape(block_bins, 2, OWN, rows_count)
    return jnp.transpose(cross, (1, 0, 2, 3)) / jnp.float32(all_segs)


def solution(mesh):
    placed = (
        P(("groups", "blk"), "seg", "freq"),
        P(),
        P(("groups", "blk"), None, None),
        P(("groups", "blk"), None, None),
    )
    return jax.shard_map(
        per_device,
        mesh=mesh,
        in_specs=placed,
        out_specs=P(None, ("seg", "freq"), ("groups", "blk"), None),
        check_vma=False,
    )
```

```python
import math

import jax
import jax.numpy as jnp
from jax import lax
from jax.experimental import pallas as pl
from jax.experimental.pallas import tpu as pltpu
from jax.sharding import PartitionSpec as P

SEG_LEN = 16384
BINS = 256
BAND_LO = 128
HW = 4
OWN = 16


WHITEN_FLOOR = 0.25
TWO_PI = 2.0 * math.pi


def swapped(value, axis, distance):
    mask = 2**distance
    pairs = [(source, source ^ mask) for source in range(lax.axis_size(axis))]
    return lax.ppermute(value, axis, pairs)


def dft_tables(band_index, sample_index):
    wavenumber = BAND_LO + band_index
    phase_int = wavenumber[:, None] * sample_index[None, :] % SEG_LEN
    angles = phase_int.astype(jnp.float32) * (TWO_PI / SEG_LEN)
    norm_scale = 1.0 / math.sqrt(SEG_LEN)
    cos_part = (jnp.cos(angles) * norm_scale).astype(jnp.bfloat16)
    sin_part = (-jnp.sin(angles) * norm_scale).astype(jnp.bfloat16)
    return (cos_part, sin_part)


def dft_tables_fast(band_index, first_sample, count):
    lanes = 128
    wavenumber = BAND_LO + band_index
    coarse = (first_sample + lanes * jnp.arange(count // lanes, dtype=jnp.int32))
    fine = jnp.arange(lanes, dtype=jnp.int32)
    coarse_angle = (wavenumber[:, None] * coarse[None, :] % SEG_LEN).astype(jnp.float32) * (
        TWO_PI / SEG_LEN
    )
    fine_angle = (wavenumber[:, None] * fine[None, :] % SEG_LEN).astype(jnp.float32) * (
        TWO_PI / SEG_LEN
    )
    cos_a = jnp.cos(coarse_angle)[:, :, None]
    sin_a = jnp.sin(coarse_angle)[:, :, None]
    cos_b = jnp.cos(fine_angle)[:, None, :]
    sin_b = jnp.sin(fine_angle)[:, None, :]
    norm_scale = 1.0 / math.sqrt(SEG_LEN)
    cos_sum = cos_a * cos_b - sin_a * sin_b
    sin_sum = sin_a * cos_b + cos_a * sin_b
    rows = band_index.shape[0]
    cos_part = (cos_sum * norm_scale).astype(jnp.bfloat16).reshape(rows, count)
    sin_part = (-sin_sum * norm_scale).astype(jnp.bfloat16).reshape(rows, count)
    return (cos_part, sin_part)


def response(band_index, taps):
    wavenumber = BAND_LO + band_index
    lag_index = jnp.arange(taps.shape[0], dtype=jnp.int32)
    phase_int = wavenumber[:, None] * lag_index[None, :] % SEG_LEN
    angles = phase_int.astype(jnp.float32) * (TWO_PI / SEG_LEN)
    real_part = jnp.dot(jnp.cos(angles), taps, precision=lax.Precision.HIGHEST)
    imag_part = jnp.dot(-jnp.sin(angles), taps, precision=lax.Precision.HIGHEST)
    return (real_part, imag_part)


def dft_kernel(rec_ref, cos_a_ref, nsin_a_ref, cos_b_ref, sin_b_ref, re_ref, im_ref):
    step = pl.program_id(0)
    lanes = cos_b_ref.shape[0]
    group = 8
    groups = rec_ref.shape[1] // (group * lanes)

    @pl.when(step == 0)
    def _():
        re_ref[...] = jnp.zeros_like(re_ref)
        im_ref[...] = jnp.zeros_like(im_ref)

    def one_group(index, carry):
        row = pl.multiple_of((step * groups + index) * group, group)
        cos_a = cos_a_ref[pl.ds(row, group), :]
        nsin_a = nsin_a_ref[pl.ds(row, group), :]
        cos_b = cos_b_ref[...]
        sin_b = sin_b_ref[...]
        for pair in range(group // 2):
            cos_parts = []
            sin_parts = []
            for half in range(2):
                at = 2 * pair + half
                ca = cos_a[at : at + 1]
                sa = nsin_a[at : at + 1]
                cos_parts.append(ca * cos_b + sa * sin_b)
                sin_parts.append(sa * cos_b - ca * sin_b)
            cos_tile = jnp.concatenate(cos_parts, axis=0).astype(jnp.bfloat16)
            sin_tile = jnp.concatenate(sin_parts, axis=0).astype(jnp.bfloat16)
            first = pl.multiple_of((index * group + 2 * pair) * lanes, 2 * lanes)
            rec = rec_ref[:, pl.ds(first, 2 * lanes)]
            re_ref[...] += jnp.dot(rec, cos_tile, preferred_element_type=jnp.float32)
            im_ref[...] += jnp.dot(rec, sin_tile, preferred_element_type=jnp.float32)
        return carry

    lax.fori_loop(0, groups, one_group, 0)


def dft_fused(records, band_index, first_sample):
    lanes = 128
    chunk = 2048
    count = records.shape[1]
    wavenumber = BAND_LO + band_index
    coarse = first_sample + lanes * jnp.arange(count // lanes, dtype=jnp.int32)
    fine = jnp.arange(lanes, dtype=jnp.int32)
    coarse_angle = (coarse[:, None] * wavenumber[None, :] % SEG_LEN).astype(jnp.float32) * (
        TWO_PI / SEG_LEN
    )
    fine_angle = (fine[:, None] * wavenumber[None, :] % SEG_LEN).astype(jnp.float32) * (
        TWO_PI / SEG_LEN
    )
    norm_scale = 1.0 / math.sqrt(SEG_LEN)
    cos_a = jnp.cos(coarse_angle)
    nsin_a = -jnp.sin(coarse_angle)
    cos_b = jnp.cos(fine_angle) * norm_scale
    sin_b = jnp.sin(fine_angle) * norm_scale
    rows = records.shape[0]
    bins = band_index.shape[0]
    full = lambda step: (0, 0)
    return pl.pallas_call(
        dft_kernel,
        grid=(count // chunk,),
        in_specs=[
            pl.BlockSpec((rows, chunk), lambda step: (0, step)),
            pl.BlockSpec(cos_a.shape, full),
            pl.BlockSpec(nsin_a.shape, full),
            pl.BlockSpec(cos_b.shape, full),
            pl.BlockSpec(sin_b.shape, full),
        ],
        out_specs=[pl.BlockSpec((rows, bins), full), pl.BlockSpec((rows, bins), full)],
        out_shape=[
            jax.ShapeDtypeStruct((rows, bins), jnp.float32),
            jax.ShapeDtypeStruct((rows, bins), jnp.float32),
        ],
        compiler_params=pltpu.CompilerParams(dimension_semantics=("arbitrary",)),
    )(records, cos_a, nsin_a, cos_b, sin_b)


def gather_blocks(carried, count, rank, split_halves=True):
    if count & (count - 1) != 0:
        return lax.all_gather(carried, "blk", axis=0, tiled=False)
    masks = []
    step = count // 2
    while step >= 1:
        masks.append(step)
        step //= 2
    if not masks:
        return carried[None]
    first = masks[0]
    rest = masks[1:]
    pairs = [(source, source ^ first) for source in range(count)]
    held = jnp.stack([carried, lax.ppermute(carried, "blk", pairs)], axis=0)
    if split_halves:
        split = (held.shape[1] + 1) // 2
        halves = [held[:, :split], held[:, split:]]
        orders = [rest, rest[::-1]]
    else:
        halves = [held]
        orders = [rest]
    results = []
    for part, order in zip(halves, orders):
        done = [first]
        for mask in order:
            pairs = [(source, source ^ mask) for source in range(count)]
            arrived = lax.ppermute(part, "blk", pairs)
            done.append(mask)
            axis = sorted(done, reverse=True).index(mask)
            part = jnp.stack([part, arrived], axis=axis)
        results.append(part.reshape((count,) + part.shape[len(masks):]))
    return jnp.concatenate(results, axis=1)


def per_device(raw, taps, send_list, recv_row):
    owners_count = lax.axis_size("blk")
    seg_count = lax.axis_size("seg")
    freq_count = lax.axis_size("freq")
    freq_rank = lax.axis_index("freq")
    sections, seg_dev, half_len = raw.shape
    records = raw.reshape(sections * seg_dev, half_len)
    device_bins = BINS // freq_count
    block_bins = device_bins // seg_count
    capacity = send_list.shape[2]

    def band_of(row_ids):
        owner_core = row_ids // device_bins
        local_row = row_ids % device_bins
        return (
            local_row // block_bins * freq_count + owner_core
        ) * block_bins + local_row % block_bins

    blk_rank = lax.axis_index("blk")
    table = jnp.concatenate([send_list[0], recv_row[0]], axis=1)
    table_part = gather_blocks(table, owners_count, blk_rank, split_halves=False)
    if owners_count & (owners_count - 1) == 0:
        source_of = blk_rank ^ jnp.arange(owners_count, dtype=jnp.int32)
        table_part = jnp.take(table_part, source_of, axis=0)
    send_all = table_part[..., :capacity]
    recv_all = table_part[..., capacity:]
    band_rows = band_of(jnp.arange(device_bins * freq_count, dtype=jnp.int32))
    real_t, imag_t = dft_fused(records, band_rows, freq_rank * half_len)
    real_all = real_t.T
    imag_all = imag_t.T
    blocks = jnp.stack([real_all, imag_all], axis=1)
    blocks = blocks.reshape(freq_count, device_bins, 2, records.shape[0])
    if freq_count == 2:
        kept = jnp.where(freq_rank == 0, blocks[0], blocks[1])
        sent = jnp.where(freq_rank == 0, blocks[1], blocks[0])
        spectra = kept + swapped(sent, "freq", 0)
    else:
        spectra = lax.psum_scatter(
            blocks.reshape(device_bins * freq_count, 2, records.shape[0]),
            "freq",
            scatter_dimension=0,
            tiled=True,
        )
    real_part = spectra[:, 0]
    imag_part = spectra[:, 1]
    amplitude = jnp.sqrt(real_part * real_part + imag_part * imag_part + 1e-06)
    amp_blocks = amplitude.reshape(seg_count, block_bins, -1)
    band_rims = jnp.stack([amp_blocks[:, :HW], amp_blocks[:, block_bins - HW :]])
    partner = swapped(band_rims, "freq", 0)
    zero_rim = jnp.zeros_like(partner[1][:1])
    right_prev = jnp.concatenate([zero_rim, partner[1][:-1]], axis=0)
    left_next = jnp.concatenate([partner[0][1:], zero_rim], axis=0)
    first_core = freq_rank == 0
    lower_rim = jnp.where(first_core, right_prev, partner[1])
    upper_rim = jnp.where(first_core, partner[0], left_next)
    padded = jnp.concatenate([lower_rim, amp_blocks, upper_rim], axis=1)
    window_sum = padded[:, 0:block_bins]
    for offset_step in range(1, 2 * HW + 1):
        window_sum = window_sum + padded[:, offset_step : offset_step + block_bins]
    span_ids = jnp.arange(seg_count, dtype=jnp.int32)[:, None]
    offsets = jnp.arange(block_bins, dtype=jnp.int32)[None, :]
    position = (span_ids * freq_count + freq_rank) * block_bins + offsets
    counted = jnp.minimum(position + HW, BINS - 1) - jnp.maximum(position - HW, 0) + 1
    smooth = window_sum / counted.astype(jnp.float32)[:, :, None]
    divisor = jnp.maximum(smooth, WHITEN_FLOOR).reshape(device_bins, -1)
    local_bins = freq_rank * device_bins + jnp.arange(device_bins, dtype=jnp.int32)
    response_re, response_im = response(band_of(local_bins), taps)
    scaled_re = real_part / divisor
    scaled_im = imag_part / divisor
    white_re = scaled_re * response_re[:, None] - scaled_im * response_im[:, None]
    white_im = scaled_re * response_im[:, None] + scaled_im * response_re[:, None]
    whitened = jnp.stack([white_re, white_im], axis=1).astype(jnp.bfloat16)
    whitened = whitened.reshape(seg_count, block_bins, 2, sections, seg_dev)
    whitened = jnp.transpose(whitened, (0, 3, 1, 2, 4))
    seg_rank = lax.axis_index("seg")
    pieces = [lax.dynamic_index_in_dim(whitened, seg_rank, axis=0, keepdims=False)]
    for shift in range(1, seg_count):
        outgoing = lax.dynamic_index_in_dim(
            whitened, (seg_rank + shift) % seg_count, axis=0, keepdims=False
        )
        pairs = [(source, (source + shift) % seg_count) for source in range(seg_count)]
        flat = outgoing.reshape(sections, -1)
        pieces.append(lax.ppermute(flat, "seg", pairs).reshape(outgoing.shape))
    local = jnp.stack(pieces, axis=3).reshape(sections, block_bins, -1)
    all_segs = seg_dev * seg_count
    table_width = local.shape[-1]
    everything = gather_blocks(local.reshape(sections, -1), owners_count, blk_rank)
    gathered = everything.reshape(owners_count, sections, block_bins, table_width)
    rows_count = owners_count * OWN
    chans_count = owners_count * sections
    chosen = jnp.transpose(send_all, (1, 0, 2))
    valid = (chosen < sections) & (recv_all < OWN)
    source_ids = jnp.arange(owners_count, dtype=jnp.int32)[None, :, None]
    owner_ids = jnp.arange(owners_count, dtype=jnp.int32)[:, None, None]
    channel = jnp.where(valid, source_ids * sections + chosen, -1).reshape(-1)
    target = jnp.where(valid, owner_ids * OWN + recv_all, -1).reshape(-1)
    row_hot = (target[:, None] == jnp.arange(rows_count, dtype=jnp.int32)[None, :]).astype(
        jnp.bfloat16
    )
    chan_hot = (channel[:, None] == jnp.arange(chans_count, dtype=jnp.int32)[None, :]).astype(
        jnp.bfloat16
    )
    selector = jnp.einsum(
        "er,ec->rc", row_hot, chan_hot, preferred_element_type=jnp.float32
    ).astype(jnp.bfloat16)
    selector = selector.reshape(rows_count, owners_count, sections)
    if owners_count & (owners_count - 1) == 0:
        selector = jnp.take(selector, source_of, axis=1)
    routed = jnp.einsum(
        "rsc,scbq->brq", selector, gathered, preferred_element_type=jnp.float32
    ).astype(jnp.bfloat16)
    own = lax.dynamic_slice_in_dim(routed, blk_rank * OWN, OWN, axis=1)
    own_re = own[..., :all_segs]
    own_im = own[..., all_segs:]
    rotated = jnp.concatenate([own_im, -own_re], axis=-1)
    cross_re = jnp.einsum("biq,bjq->bij", own, routed, preferred_element_type=jnp.float32)
    cross_im = jnp.einsum("biq,bjq->bij", rotated, routed, preferred_element_type=jnp.float32)
    return jnp.stack([cross_re, cross_im]) / jnp.float32(all_segs)


def solution(mesh):
    placed = (
        P(("groups", "blk"), "seg", "freq"),
        P(),
        P(("groups", "blk"), None, None),
        P(("groups", "blk"), None, None),
    )
    return jax.shard_map(
        per_device,
        mesh=mesh,
        in_specs=placed,
        out_specs=P(None, ("seg", "freq"), ("groups", "blk"), None),
        check_vma=False,
    )
```

```python
import math

import jax
import jax.numpy as jnp
from jax import lax
from jax.experimental import pallas as pl
from jax.experimental.pallas import tpu as pltpu
from jax.sharding import PartitionSpec as P

SEG_LEN = 16384
BINS = 256
BAND_LO = 128
HW = 4
OWN = 16


WHITEN_FLOOR = 0.25
TWO_PI = 2.0 * math.pi


def swapped(value, axis, distance):
    mask = 2**distance
    pairs = [(source, source ^ mask) for source in range(lax.axis_size(axis))]
    return lax.ppermute(value, axis, pairs)


def dft_tables(band_index, sample_index):
    wavenumber = BAND_LO + band_index
    phase_int = wavenumber[:, None] * sample_index[None, :] % SEG_LEN
    angles = phase_int.astype(jnp.float32) * (TWO_PI / SEG_LEN)
    norm_scale = 1.0 / math.sqrt(SEG_LEN)
    cos_part = (jnp.cos(angles) * norm_scale).astype(jnp.bfloat16)
    sin_part = (-jnp.sin(angles) * norm_scale).astype(jnp.bfloat16)
    return (cos_part, sin_part)


def dft_tables_fast(band_index, first_sample, count):
    lanes = 128
    wavenumber = BAND_LO + band_index
    coarse = (first_sample + lanes * jnp.arange(count // lanes, dtype=jnp.int32))
    fine = jnp.arange(lanes, dtype=jnp.int32)
    coarse_angle = (wavenumber[:, None] * coarse[None, :] % SEG_LEN).astype(jnp.float32) * (
        TWO_PI / SEG_LEN
    )
    fine_angle = (wavenumber[:, None] * fine[None, :] % SEG_LEN).astype(jnp.float32) * (
        TWO_PI / SEG_LEN
    )
    cos_a = jnp.cos(coarse_angle)[:, :, None]
    sin_a = jnp.sin(coarse_angle)[:, :, None]
    cos_b = jnp.cos(fine_angle)[:, None, :]
    sin_b = jnp.sin(fine_angle)[:, None, :]
    norm_scale = 1.0 / math.sqrt(SEG_LEN)
    cos_sum = cos_a * cos_b - sin_a * sin_b
    sin_sum = sin_a * cos_b + cos_a * sin_b
    rows = band_index.shape[0]
    cos_part = (cos_sum * norm_scale).astype(jnp.bfloat16).reshape(rows, count)
    sin_part = (-sin_sum * norm_scale).astype(jnp.bfloat16).reshape(rows, count)
    return (cos_part, sin_part)


def response(band_index, taps):
    wavenumber = BAND_LO + band_index
    lag_index = jnp.arange(taps.shape[0], dtype=jnp.int32)
    phase_int = wavenumber[:, None] * lag_index[None, :] % SEG_LEN
    angles = phase_int.astype(jnp.float32) * (TWO_PI / SEG_LEN)
    real_part = jnp.dot(jnp.cos(angles), taps, precision=lax.Precision.HIGHEST)
    imag_part = jnp.dot(-jnp.sin(angles), taps, precision=lax.Precision.HIGHEST)
    return (real_part, imag_part)


def dft_kernel(rec_ref, cos_a_ref, nsin_a_ref, cos_b_ref, sin_b_ref, re_ref, im_ref):
    step = pl.program_id(0)
    lanes = cos_b_ref.shape[0]
    group = 8
    groups = rec_ref.shape[1] // (group * lanes)

    @pl.when(step == 0)
    def _():
        re_ref[...] = jnp.zeros_like(re_ref)
        im_ref[...] = jnp.zeros_like(im_ref)

    def one_group(index, carry):
        row = pl.multiple_of((step * groups + index) * group, group)
        cos_a = cos_a_ref[pl.ds(row, group), :]
        nsin_a = nsin_a_ref[pl.ds(row, group), :]
        cos_b = cos_b_ref[...]
        sin_b = sin_b_ref[...]
        for pair in range(group // 2):
            cos_parts = []
            sin_parts = []
            for half in range(2):
                at = 2 * pair + half
                ca = cos_a[at : at + 1]
                sa = nsin_a[at : at + 1]
                cos_parts.append(ca * cos_b + sa * sin_b)
                sin_parts.append(sa * cos_b - ca * sin_b)
            cos_tile = jnp.concatenate(cos_parts, axis=0).astype(jnp.bfloat16)
            sin_tile = jnp.concatenate(sin_parts, axis=0).astype(jnp.bfloat16)
            first = pl.multiple_of((index * group + 2 * pair) * lanes, 2 * lanes)
            rec = rec_ref[:, pl.ds(first, 2 * lanes)]
            re_ref[...] += jnp.dot(rec, cos_tile, preferred_element_type=jnp.float32)
            im_ref[...] += jnp.dot(rec, sin_tile, preferred_element_type=jnp.float32)
        return carry

    lax.fori_loop(0, groups, one_group, 0)


def dft_fused(records, band_index, first_sample):
    lanes = 128
    chunk = 2048
    count = records.shape[1]
    wavenumber = BAND_LO + band_index
    norm_scale = 1.0 / math.sqrt(SEG_LEN)

    def cos_sin(steps):
        angle = (steps[:, None] * wavenumber[None, :] % SEG_LEN).astype(jnp.float32) * (
            TWO_PI / SEG_LEN
        )
        return jnp.cos(angle), jnp.sin(angle)

    def combined(outer_steps, inner_steps):
        outer_cos, outer_sin = cos_sin(outer_steps)
        inner_cos, inner_sin = cos_sin(inner_steps)
        width = wavenumber.shape[0]
        cos_sum = outer_cos[:, None] * inner_cos[None] - outer_sin[:, None] * inner_sin[None]
        sin_sum = outer_sin[:, None] * inner_cos[None] + outer_cos[:, None] * inner_sin[None]
        return cos_sum.reshape(-1, width), sin_sum.reshape(-1, width)

    coarse_count = count // lanes
    coarse_outer = coarse_count // 8 if coarse_count % 8 == 0 else 1
    coarse_inner = coarse_count // coarse_outer
    cos_a, sin_a = combined(
        first_sample + lanes * coarse_inner * jnp.arange(coarse_outer, dtype=jnp.int32),
        lanes * jnp.arange(coarse_inner, dtype=jnp.int32),
    )
    nsin_a = -sin_a
    cos_b, sin_b = combined(
        16 * jnp.arange(lanes // 16, dtype=jnp.int32), jnp.arange(16, dtype=jnp.int32)
    )
    cos_b = cos_b * norm_scale
    sin_b = sin_b * norm_scale
    rows = records.shape[0]
    bins = band_index.shape[0]
    full = lambda step: (0, 0)
    return pl.pallas_call(
        dft_kernel,
        grid=(count // chunk,),
        in_specs=[
            pl.BlockSpec((rows, chunk), lambda step: (0, step)),
            pl.BlockSpec(cos_a.shape, full),
            pl.BlockSpec(nsin_a.shape, full),
            pl.BlockSpec(cos_b.shape, full),
            pl.BlockSpec(sin_b.shape, full),
        ],
        out_specs=[pl.BlockSpec((rows, bins), full), pl.BlockSpec((rows, bins), full)],
        out_shape=[
            jax.ShapeDtypeStruct((rows, bins), jnp.float32),
            jax.ShapeDtypeStruct((rows, bins), jnp.float32),
        ],
        compiler_params=pltpu.CompilerParams(dimension_semantics=("arbitrary",)),
    )(records, cos_a, nsin_a, cos_b, sin_b)


def gather_blocks(carried, count, rank):
    if count & (count - 1) != 0:
        return lax.all_gather(carried, "blk", axis=0, tiled=False)
    masks = []
    step = count // 2
    while step >= 1:
        masks.append(step)
        step //= 2
    if not masks:
        return carried[None]
    first = masks[0]
    rest = masks[1:]
    pairs = [(source, source ^ first) for source in range(count)]
    held = jnp.stack([carried, lax.ppermute(carried, "blk", pairs)], axis=0)
    split = (held.shape[1] + 1) // 2
    halves = [held[:, :split], held[:, split:]]
    orders = [rest, rest[::-1]]
    results = []
    for part, order in zip(halves, orders):
        done = [first]
        for mask in order:
            pairs = [(source, source ^ mask) for source in range(count)]
            arrived = lax.ppermute(part, "blk", pairs)
            done.append(mask)
            axis = sorted(done, reverse=True).index(mask)
            part = jnp.stack([part, arrived], axis=axis)
        results.append(part.reshape((count,) + part.shape[len(masks):]))
    return jnp.concatenate(results, axis=1)


def per_device(raw, taps, send_list, recv_row):
    owners_count = lax.axis_size("blk")
    seg_count = lax.axis_size("seg")
    freq_count = lax.axis_size("freq")
    freq_rank = lax.axis_index("freq")
    sections, seg_dev, half_len = raw.shape
    records = raw.reshape(sections * seg_dev, half_len)
    device_bins = BINS // freq_count
    block_bins = device_bins // seg_count
    capacity = send_list.shape[2]

    def band_of(row_ids):
        owner_core = row_ids // device_bins
        local_row = row_ids % device_bins
        return (
            local_row // block_bins * freq_count + owner_core
        ) * block_bins + local_row % block_bins

    band_rows = band_of(jnp.arange(device_bins * freq_count, dtype=jnp.int32))
    real_t, imag_t = dft_fused(records, band_rows, freq_rank * half_len)
    real_all = real_t.T
    imag_all = imag_t.T
    blocks = jnp.stack([real_all, imag_all], axis=1)
    blocks = blocks.reshape(freq_count, device_bins, 2, records.shape[0])
    if freq_count == 2:
        kept = jnp.where(freq_rank == 0, blocks[0], blocks[1])
        sent = jnp.where(freq_rank == 0, blocks[1], blocks[0])
        spectra = kept + swapped(sent, "freq", 0)
    else:
        spectra = lax.psum_scatter(
            blocks.reshape(device_bins * freq_count, 2, records.shape[0]),
            "freq",
            scatter_dimension=0,
            tiled=True,
        )
    real_part = spectra[:, 0]
    imag_part = spectra[:, 1]
    amplitude = jnp.sqrt(real_part * real_part + imag_part * imag_part + 1e-06)
    amp_blocks = amplitude.reshape(seg_count, block_bins, -1)
    band_rims = jnp.stack([amp_blocks[:, :HW], amp_blocks[:, block_bins - HW :]])
    partner = swapped(band_rims, "freq", 0)
    zero_rim = jnp.zeros_like(partner[1][:1])
    right_prev = jnp.concatenate([zero_rim, partner[1][:-1]], axis=0)
    left_next = jnp.concatenate([partner[0][1:], zero_rim], axis=0)
    first_core = freq_rank == 0
    lower_rim = jnp.where(first_core, right_prev, partner[1])
    upper_rim = jnp.where(first_core, partner[0], left_next)
    padded = jnp.concatenate([lower_rim, amp_blocks, upper_rim], axis=1)
    window_sum = padded[:, 0:block_bins]
    for offset_step in range(1, 2 * HW + 1):
        window_sum = window_sum + padded[:, offset_step : offset_step + block_bins]
    span_ids = jnp.arange(seg_count, dtype=jnp.int32)[:, None]
    offsets = jnp.arange(block_bins, dtype=jnp.int32)[None, :]
    position = (span_ids * freq_count + freq_rank) * block_bins + offsets
    counted = jnp.minimum(position + HW, BINS - 1) - jnp.maximum(position - HW, 0) + 1
    smooth = window_sum / counted.astype(jnp.float32)[:, :, None]
    divisor = jnp.maximum(smooth, WHITEN_FLOOR).reshape(device_bins, -1)
    local_bins = freq_rank * device_bins + jnp.arange(device_bins, dtype=jnp.int32)
    response_re, response_im = response(band_of(local_bins), taps)
    scaled_re = real_part / divisor
    scaled_im = imag_part / divisor
    white_re = scaled_re * response_re[:, None] - scaled_im * response_im[:, None]
    white_im = scaled_re * response_im[:, None] + scaled_im * response_re[:, None]
    whitened = jnp.stack([white_re, white_im], axis=1).astype(jnp.bfloat16)
    whitened = whitened.reshape(seg_count, block_bins, 2, sections, seg_dev)
    whitened = jnp.transpose(whitened, (0, 3, 1, 2, 4))
    seg_rank = lax.axis_index("seg")
    pieces = [lax.dynamic_index_in_dim(whitened, seg_rank, axis=0, keepdims=False)]
    for shift in range(1, seg_count):
        outgoing = lax.dynamic_index_in_dim(
            whitened, (seg_rank + shift) % seg_count, axis=0, keepdims=False
        )
        pairs = [(source, (source + shift) % seg_count) for source in range(seg_count)]
        flat = outgoing.reshape(sections, -1)
        pieces.append(lax.ppermute(flat, "seg", pairs).reshape(outgoing.shape))
    local = jnp.stack(pieces, axis=3).reshape(sections, block_bins, -1)
    all_segs = seg_dev * seg_count
    table_width = local.shape[-1]
    table = jnp.concatenate([send_list[0], recv_row[0]], axis=1).reshape(-1)
    table_len = table.shape[0]
    slab = jnp.pad(table.astype(jnp.bfloat16), (0, sections * table_width - table_len))
    carried = jnp.concatenate([local, slab.reshape(sections, 1, table_width)], axis=1)
    blk_rank = lax.axis_index("blk")
    everything = gather_blocks(carried.reshape(sections, -1), owners_count, blk_rank)
    everything = everything.reshape(owners_count, sections, block_bins + 1, table_width)
    gathered = everything[:, :, :block_bins]
    table_part = everything[:, :, block_bins].reshape(owners_count, -1)[:, :table_len]
    table_part = table_part.astype(jnp.int32).reshape(owners_count, owners_count, 2 * capacity)
    position_ids = jnp.arange(owners_count, dtype=jnp.int32)
    if owners_count & (owners_count - 1) == 0:
        source_of = blk_rank ^ position_ids
        unpermute = (source_of[:, None] == position_ids[None, :]).astype(jnp.int32)
        table_part = jnp.sum(unpermute[:, :, None, None] * table_part[None], axis=1)
    else:
        source_of = position_ids
    send_all = table_part[..., :capacity]
    recv_all = table_part[..., capacity:]
    rows_count = owners_count * OWN
    chans_count = owners_count * sections
    chosen = jnp.transpose(send_all, (1, 0, 2))
    valid = (chosen < sections) & (recv_all < OWN)
    source_ids = (blk_rank ^ position_ids if owners_count & (owners_count - 1) == 0 else position_ids)[None, :, None]
    owner_ids = jnp.arange(owners_count, dtype=jnp.int32)[:, None, None]
    channel = jnp.where(valid, source_ids * sections + chosen, -1).reshape(-1)
    target = jnp.where(valid, owner_ids * OWN + recv_all, -1).reshape(-1)
    row_hot = (target[:, None] == jnp.arange(rows_count, dtype=jnp.int32)[None, :]).astype(
        jnp.bfloat16
    )
    chan_hot = (channel[:, None] == jnp.arange(chans_count, dtype=jnp.int32)[None, :]).astype(
        jnp.bfloat16
    )
    selector = jnp.einsum(
        "er,ec->rc", row_hot, chan_hot, preferred_element_type=jnp.float32
    ).astype(jnp.bfloat16)
    selector = selector.reshape(rows_count, owners_count, sections)
    routed = jnp.einsum(
        "rsc,scbq->brq", selector, gathered, preferred_element_type=jnp.float32
    ).astype(jnp.bfloat16)
    own = lax.dynamic_slice_in_dim(routed, blk_rank * OWN, OWN, axis=1)
    own_re = own[..., :all_segs]
    own_im = own[..., all_segs:]
    rotated = jnp.concatenate([own_im, -own_re], axis=-1)
    lhs = jnp.concatenate([own, rotated], axis=1)
    cross = jnp.einsum("bpq,bjq->bpj", lhs, routed, preferred_element_type=jnp.float32)
    cross = cross.reshape(block_bins, 2, OWN, rows_count)
    return jnp.transpose(cross, (1, 0, 2, 3)) / jnp.float32(all_segs)


def solution(mesh):
    placed = (
        P(("groups", "blk"), "seg", "freq"),
        P(),
        P(("groups", "blk"), None, None),
        P(("groups", "blk"), None, None),
    )
    return jax.shard_map(
        per_device,
        mesh=mesh,
        in_specs=placed,
        out_specs=P(None, ("seg", "freq"), ("groups", "blk"), None),
        check_vma=False,
    )
```

```python
import math

import jax
import jax.numpy as jnp
from jax import lax
from jax.experimental import pallas as pl
from jax.experimental.pallas import tpu as pltpu
from jax.sharding import PartitionSpec as P

SEG_LEN = 16384
BINS = 256
BAND_LO = 128
HW = 4
OWN = 16


WHITEN_FLOOR = 0.25
TWO_PI = 2.0 * math.pi


def swapped(value, axis, distance):
    mask = 2**distance
    pairs = [(source, source ^ mask) for source in range(lax.axis_size(axis))]
    return lax.ppermute(value, axis, pairs)


def dft_tables(band_index, sample_index):
    wavenumber = BAND_LO + band_index
    phase_int = wavenumber[:, None] * sample_index[None, :] % SEG_LEN
    angles = phase_int.astype(jnp.float32) * (TWO_PI / SEG_LEN)
    norm_scale = 1.0 / math.sqrt(SEG_LEN)
    cos_part = (jnp.cos(angles) * norm_scale).astype(jnp.bfloat16)
    sin_part = (-jnp.sin(angles) * norm_scale).astype(jnp.bfloat16)
    return (cos_part, sin_part)


def dft_tables_fast(band_index, first_sample, count):
    lanes = 128
    wavenumber = BAND_LO + band_index
    coarse = (first_sample + lanes * jnp.arange(count // lanes, dtype=jnp.int32))
    fine = jnp.arange(lanes, dtype=jnp.int32)
    coarse_angle = (wavenumber[:, None] * coarse[None, :] % SEG_LEN).astype(jnp.float32) * (
        TWO_PI / SEG_LEN
    )
    fine_angle = (wavenumber[:, None] * fine[None, :] % SEG_LEN).astype(jnp.float32) * (
        TWO_PI / SEG_LEN
    )
    cos_a = jnp.cos(coarse_angle)[:, :, None]
    sin_a = jnp.sin(coarse_angle)[:, :, None]
    cos_b = jnp.cos(fine_angle)[:, None, :]
    sin_b = jnp.sin(fine_angle)[:, None, :]
    norm_scale = 1.0 / math.sqrt(SEG_LEN)
    cos_sum = cos_a * cos_b - sin_a * sin_b
    sin_sum = sin_a * cos_b + cos_a * sin_b
    rows = band_index.shape[0]
    cos_part = (cos_sum * norm_scale).astype(jnp.bfloat16).reshape(rows, count)
    sin_part = (-sin_sum * norm_scale).astype(jnp.bfloat16).reshape(rows, count)
    return (cos_part, sin_part)


def response(band_index, taps):
    wavenumber = BAND_LO + band_index
    lag_index = jnp.arange(taps.shape[0], dtype=jnp.int32)
    phase_int = wavenumber[:, None] * lag_index[None, :] % SEG_LEN
    angles = phase_int.astype(jnp.float32) * (TWO_PI / SEG_LEN)
    real_part = jnp.dot(jnp.cos(angles), taps, precision=lax.Precision.HIGHEST)
    imag_part = jnp.dot(-jnp.sin(angles), taps, precision=lax.Precision.HIGHEST)
    return (real_part, imag_part)


def dft_kernel(rec_ref, cos_a_ref, nsin_a_ref, cos_b_ref, sin_b_ref, re_ref, im_ref):
    step = pl.program_id(0)
    lanes = cos_b_ref.shape[0]
    group = 8
    groups = rec_ref.shape[1] // (group * lanes)

    @pl.when(step == 0)
    def _():
        re_ref[...] = jnp.zeros_like(re_ref)
        im_ref[...] = jnp.zeros_like(im_ref)

    def one_group(index, carry):
        row = pl.multiple_of((step * groups + index) * group, group)
        cos_a = cos_a_ref[pl.ds(row, group), :]
        nsin_a = nsin_a_ref[pl.ds(row, group), :]
        cos_b = cos_b_ref[...]
        sin_b = sin_b_ref[...]
        for pair in range(group // 2):
            cos_parts = []
            sin_parts = []
            for half in range(2):
                at = 2 * pair + half
                ca = cos_a[at : at + 1]
                sa = nsin_a[at : at + 1]
                cos_parts.append(ca * cos_b + sa * sin_b)
                sin_parts.append(sa * cos_b - ca * sin_b)
            cos_tile = jnp.concatenate(cos_parts, axis=0).astype(jnp.bfloat16)
            sin_tile = jnp.concatenate(sin_parts, axis=0).astype(jnp.bfloat16)
            first = pl.multiple_of((index * group + 2 * pair) * lanes, 2 * lanes)
            rec = rec_ref[:, pl.ds(first, 2 * lanes)]
            re_ref[...] += jnp.dot(rec, cos_tile, preferred_element_type=jnp.float32)
            im_ref[...] += jnp.dot(rec, sin_tile, preferred_element_type=jnp.float32)
        return carry

    lax.fori_loop(0, groups, one_group, 0)


def dft_fused(records, band_index, first_sample):
    lanes = 128
    chunk = 2048
    count = records.shape[1]
    wavenumber = BAND_LO + band_index
    norm_scale = 1.0 / math.sqrt(SEG_LEN)

    def cos_sin(steps):
        angle = (steps[:, None] * wavenumber[None, :] % SEG_LEN).astype(jnp.float32) * (
            TWO_PI / SEG_LEN
        )
        return jnp.cos(angle), jnp.sin(angle)

    def combined(outer_steps, inner_steps):
        outer_cos, outer_sin = cos_sin(outer_steps)
        inner_cos, inner_sin = cos_sin(inner_steps)
        width = wavenumber.shape[0]
        cos_sum = outer_cos[:, None] * inner_cos[None] - outer_sin[:, None] * inner_sin[None]
        sin_sum = outer_sin[:, None] * inner_cos[None] + outer_cos[:, None] * inner_sin[None]
        return cos_sum.reshape(-1, width), sin_sum.reshape(-1, width)

    coarse_count = count // lanes
    coarse_outer = coarse_count // 8 if coarse_count % 8 == 0 else 1
    coarse_inner = coarse_count // coarse_outer
    cos_a, sin_a = combined(
        first_sample + lanes * coarse_inner * jnp.arange(coarse_outer, dtype=jnp.int32),
        lanes * jnp.arange(coarse_inner, dtype=jnp.int32),
    )
    nsin_a = -sin_a
    cos_b, sin_b = combined(
        16 * jnp.arange(lanes // 16, dtype=jnp.int32), jnp.arange(16, dtype=jnp.int32)
    )
    cos_b = cos_b * norm_scale
    sin_b = sin_b * norm_scale
    rows = records.shape[0]
    bins = band_index.shape[0]
    full = lambda step: (0, 0)
    return pl.pallas_call(
        dft_kernel,
        grid=(count // chunk,),
        in_specs=[
            pl.BlockSpec((rows, chunk), lambda step: (0, step)),
            pl.BlockSpec(cos_a.shape, full),
            pl.BlockSpec(nsin_a.shape, full),
            pl.BlockSpec(cos_b.shape, full),
            pl.BlockSpec(sin_b.shape, full),
        ],
        out_specs=[pl.BlockSpec((rows, bins), full), pl.BlockSpec((rows, bins), full)],
        out_shape=[
            jax.ShapeDtypeStruct((rows, bins), jnp.float32),
            jax.ShapeDtypeStruct((rows, bins), jnp.float32),
        ],
        compiler_params=pltpu.CompilerParams(dimension_semantics=("arbitrary",)),
    )(records, cos_a, nsin_a, cos_b, sin_b)


def gather_blocks(carried, count, rank):
    if count & (count - 1) != 0:
        return lax.all_gather(carried, "blk", axis=0, tiled=False)
    masks = []
    step = count // 2
    while step >= 1:
        masks.append(step)
        step //= 2
    if not masks:
        return carried[None]
    first = masks[0]
    rest = masks[1:]
    pairs = [(source, source ^ first) for source in range(count)]
    held = jnp.stack([carried, lax.ppermute(carried, "blk", pairs)], axis=0)
    split = (held.shape[1] + 1) // 2
    halves = [held[:, :split], held[:, split:]]
    orders = [rest, rest[::-1]]
    results = []
    for part, order in zip(halves, orders):
        done = [first]
        for mask in order:
            pairs = [(source, source ^ mask) for source in range(count)]
            arrived = lax.ppermute(part, "blk", pairs)
            done.append(mask)
            axis = sorted(done, reverse=True).index(mask)
            part = jnp.stack([part, arrived], axis=axis)
        results.append(part.reshape((count,) + part.shape[len(masks):]))
    return jnp.concatenate(results, axis=1)


def per_device(raw, taps, send_list, recv_row):
    owners_count = lax.axis_size("blk")
    seg_count = lax.axis_size("seg")
    freq_count = lax.axis_size("freq")
    freq_rank = lax.axis_index("freq")
    sections, seg_dev, half_len = raw.shape
    records = raw.reshape(sections * seg_dev, half_len)
    device_bins = BINS // freq_count
    block_bins = device_bins // seg_count
    capacity = send_list.shape[2]

    def band_of(row_ids):
        owner_core = row_ids // device_bins
        local_row = row_ids % device_bins
        return (
            local_row // block_bins * freq_count + owner_core
        ) * block_bins + local_row % block_bins

    blk_rank = lax.axis_index("blk")
    seg_rank = lax.axis_index("seg")
    all_segs = seg_dev * seg_count
    table = jnp.concatenate([send_list[0], recv_row[0]], axis=1).reshape(-1)
    table_len = table.shape[0]
    phased = seg_count == 2 and freq_count == 2 and owners_count & (owners_count - 1) == 0
    if phased:
        gathered, table_raw = phased_exchange(
            records, taps, table, sections, seg_dev, half_len, owners_count, freq_rank, seg_rank, blk_rank
        )
    else:
        gathered, table_raw = plain_exchange(
            records, taps, table, sections, seg_dev, half_len, owners_count, freq_rank, seg_rank, blk_rank,
            seg_count, freq_count,
        )
    table_part = table_raw.astype(jnp.int32).reshape(owners_count, owners_count, 2 * capacity)
    return finish(gathered, table_part, owners_count, sections, block_bins, all_segs, capacity, blk_rank)


def amplitude_of(pair):
    return jnp.sqrt(pair[:, 0] * pair[:, 0] + pair[:, 1] * pair[:, 1] + 1e-06)


def whiten_block(spectra, lower_rim, upper_rim, block_index, taps):
    block_bins = spectra.shape[0]
    real_part = spectra[:, 0]
    imag_part = spectra[:, 1]
    amplitude = jnp.sqrt(real_part * real_part + imag_part * imag_part + 1e-06)
    padded = jnp.concatenate([lower_rim, amplitude, upper_rim], axis=0)
    window_sum = padded[0:block_bins]
    for offset_step in range(1, 2 * HW + 1):
        window_sum = window_sum + padded[offset_step : offset_step + block_bins]
    position = block_index * block_bins + jnp.arange(block_bins, dtype=jnp.int32)
    counted = jnp.minimum(position + HW, BINS - 1) - jnp.maximum(position - HW, 0) + 1
    smooth = window_sum / counted.astype(jnp.float32)[:, None]
    divisor = jnp.maximum(smooth, WHITEN_FLOOR)
    response_re, response_im = response(position, taps)
    scaled_re = real_part / divisor
    scaled_im = imag_part / divisor
    white_re = scaled_re * response_re[:, None] - scaled_im * response_im[:, None]
    white_im = scaled_re * response_im[:, None] + scaled_im * response_re[:, None]
    return jnp.stack([white_re, white_im], axis=1).astype(jnp.bfloat16)


def phased_exchange(records, taps, table, sections, seg_dev, half_len, owners_count, freq_rank, seg_rank, blk_rank):
    block_bins = BINS // 4
    pair_bins = 2 * block_bins
    rec_count = records.shape[0]
    contract = (((1,), (1,)), ((), ()))
    first_sample = freq_rank * half_len
    first_core = freq_rank == 0

    def pair_partials(source, pair_seg):
        bins = pair_bins * pair_seg + jnp.arange(pair_bins, dtype=jnp.int32)
        real_t, imag_t = dft_fused(source, bins, first_sample)
        both = jnp.stack([real_t.T, imag_t.T], axis=1)
        halves = both.reshape(2, block_bins, 2, rec_count)
        kept = jnp.where(first_core, halves[0], halves[1])
        sent = jnp.where(first_core, halves[1], halves[0])
        return kept, sent

    def edges_of(block):
        return jnp.concatenate([block[:HW], block[block_bins - HW :]], axis=0)

    rim_bins = pair_bins - HW + HW * seg_rank + jnp.arange(HW, dtype=jnp.int32)
    rim_cos, rim_sin = dft_tables_fast(rim_bins, first_sample, half_len)
    rim_part = jnp.stack(
        [
            lax.dot_general(rim_cos, records, contract, preferred_element_type=jnp.float32),
            lax.dot_general(rim_sin, records, contract, preferred_element_type=jnp.float32),
        ],
        axis=1,
    )
    zero_rim = jnp.zeros((HW, rec_count), jnp.float32)

    kept_a, sent_a = pair_partials(records, 1 - seg_rank)
    message_a = jnp.concatenate([sent_a, edges_of(kept_a), rim_part], axis=0)
    arrived_a = swapped(message_a, "freq", 0)
    mine_a = kept_a + arrived_a[:block_bins]
    partner_a = amplitude_of(edges_of(sent_a) + arrived_a[block_bins : block_bins + 2 * HW])
    outer_a = amplitude_of(rim_part + arrived_a[block_bins + 2 * HW :])
    outer_a = jnp.where(freq_rank == seg_rank, outer_a, zero_rim)
    lower_a = jnp.where(first_core, outer_a, partner_a[HW:])
    upper_a = jnp.where(first_core, partner_a[:HW], outer_a)
    white_a = whiten_block(mine_a, lower_a, upper_a, 2 * (1 - seg_rank) + freq_rank, taps)
    white_a = white_a.reshape(block_bins, 2, sections, seg_dev)
    outgoing = jnp.transpose(white_a, (2, 0, 1, 3)).reshape(sections, -1)
    source_b, outgoing = lax.optimization_barrier((records, outgoing))
    received = lax.ppermute(outgoing, "seg", [(0, 1), (1, 0)])
    table_width = 2 * 2 * seg_dev
    slab = jnp.pad(table.astype(jnp.bfloat16), (0, sections * table_width - table.shape[0]))
    carried_a = jnp.concatenate([received, slab.reshape(sections, table_width)], axis=1)
    moved_a = gather_blocks(carried_a, owners_count, blk_rank)

    kept_b, sent_b = pair_partials(source_b, seg_rank)
    message_b = jnp.concatenate([sent_b, edges_of(kept_b)], axis=0)
    arrived_b = swapped(message_b, "freq", 0)
    mine_b = kept_b + arrived_b[:block_bins]
    partner_b = amplitude_of(edges_of(sent_b) + arrived_b[block_bins:])
    outer_b = jnp.where(first_core, partner_a[HW:], partner_a[:HW])
    outer_b = jnp.where(freq_rank != seg_rank, outer_b, zero_rim)
    lower_b = jnp.where(first_core, outer_b, partner_b[HW:])
    upper_b = jnp.where(first_core, partner_b[:HW], outer_b)
    white_b = whiten_block(mine_b, lower_b, upper_b, 2 * seg_rank + freq_rank, taps)
    white_b = white_b.reshape(block_bins, 2, sections, seg_dev)
    carried_b = jnp.transpose(white_b, (2, 0, 1, 3)).reshape(sections, -1)
    moved_b = gather_blocks(carried_b, owners_count, blk_rank)

    data_width = carried_b.shape[1]
    data_a = moved_a[:, :, :data_width].reshape(owners_count, sections, block_bins, 2, seg_dev)
    data_b = moved_b.reshape(owners_count, sections, block_bins, 2, seg_dev)
    gathered = jnp.concatenate([data_a, data_b], axis=-1)
    gathered = gathered.reshape(owners_count, sections, block_bins, 4 * seg_dev)
    table_raw = moved_a[:, :, data_width:].reshape(owners_count, -1)[:, : table.shape[0]]
    return gathered, table_raw


def plain_exchange(records, taps, table, sections, seg_dev, half_len, owners_count, freq_rank, seg_rank, blk_rank,
                   seg_count, freq_count):
    device_bins = BINS // freq_count
    block_bins = device_bins // seg_count

    def band_of(row_ids):
        owner_core = row_ids // device_bins
        local_row = row_ids % device_bins
        return (
            local_row // block_bins * freq_count + owner_core
        ) * block_bins + local_row % block_bins

    band_rows = band_of(jnp.arange(device_bins * freq_count, dtype=jnp.int32))
    real_t, imag_t = dft_fused(records, band_rows, freq_rank * half_len)
    real_all = real_t.T
    imag_all = imag_t.T
    blocks = jnp.stack([real_all, imag_all], axis=1)
    blocks = blocks.reshape(freq_count, device_bins, 2, records.shape[0])
    if freq_count == 2:
        kept = jnp.where(freq_rank == 0, blocks[0], blocks[1])
        sent = jnp.where(freq_rank == 0, blocks[1], blocks[0])
        spectra = kept + swapped(sent, "freq", 0)
    else:
        spectra = lax.psum_scatter(
            blocks.reshape(device_bins * freq_count, 2, records.shape[0]),
            "freq",
            scatter_dimension=0,
            tiled=True,
        )
    real_part = spectra[:, 0]
    imag_part = spectra[:, 1]
    amplitude = jnp.sqrt(real_part * real_part + imag_part * imag_part + 1e-06)
    amp_blocks = amplitude.reshape(seg_count, block_bins, -1)
    band_rims = jnp.stack([amp_blocks[:, :HW], amp_blocks[:, block_bins - HW :]])
    partner = swapped(band_rims, "freq", 0)
    zero_rim = jnp.zeros_like(partner[1][:1])
    right_prev = jnp.concatenate([zero_rim, partner[1][:-1]], axis=0)
    left_next = jnp.concatenate([partner[0][1:], zero_rim], axis=0)
    first_core = freq_rank == 0
    lower_rim = jnp.where(first_core, right_prev, partner[1])
    upper_rim = jnp.where(first_core, partner[0], left_next)
    padded = jnp.concatenate([lower_rim, amp_blocks, upper_rim], axis=1)
    window_sum = padded[:, 0:block_bins]
    for offset_step in range(1, 2 * HW + 1):
        window_sum = window_sum + padded[:, offset_step : offset_step + block_bins]
    span_ids = jnp.arange(seg_count, dtype=jnp.int32)[:, None]
    offsets = jnp.arange(block_bins, dtype=jnp.int32)[None, :]
    position = (span_ids * freq_count + freq_rank) * block_bins + offsets
    counted = jnp.minimum(position + HW, BINS - 1) - jnp.maximum(position - HW, 0) + 1
    smooth = window_sum / counted.astype(jnp.float32)[:, :, None]
    divisor = jnp.maximum(smooth, WHITEN_FLOOR).reshape(device_bins, -1)
    local_bins = freq_rank * device_bins + jnp.arange(device_bins, dtype=jnp.int32)
    response_re, response_im = response(band_of(local_bins), taps)
    scaled_re = real_part / divisor
    scaled_im = imag_part / divisor
    white_re = scaled_re * response_re[:, None] - scaled_im * response_im[:, None]
    white_im = scaled_re * response_im[:, None] + scaled_im * response_re[:, None]
    whitened = jnp.stack([white_re, white_im], axis=1).astype(jnp.bfloat16)
    whitened = whitened.reshape(seg_count, block_bins, 2, sections, seg_dev)
    whitened = jnp.transpose(whitened, (0, 3, 1, 2, 4))
    pieces = [lax.dynamic_index_in_dim(whitened, seg_rank, axis=0, keepdims=False)]
    for shift in range(1, seg_count):
        outgoing = lax.dynamic_index_in_dim(
            whitened, (seg_rank + shift) % seg_count, axis=0, keepdims=False
        )
        pairs = [(source, (source + shift) % seg_count) for source in range(seg_count)]
        flat = outgoing.reshape(sections, -1)
        pieces.append(lax.ppermute(flat, "seg", pairs).reshape(outgoing.shape))
    local = jnp.stack(pieces, axis=3).reshape(sections, block_bins, -1)
    table_width = local.shape[-1]
    table_len = table.shape[0]
    slab = jnp.pad(table.astype(jnp.bfloat16), (0, sections * table_width - table_len))
    carried = jnp.concatenate([local, slab.reshape(sections, 1, table_width)], axis=1)
    everything = gather_blocks(carried.reshape(sections, -1), owners_count, blk_rank)
    everything = everything.reshape(owners_count, sections, block_bins + 1, table_width)
    gathered = everything[:, :, :block_bins]
    table_raw = everything[:, :, block_bins].reshape(owners_count, -1)[:, :table_len]
    return gathered, table_raw


def finish(gathered, table_part, owners_count, sections, block_bins, all_segs, capacity, blk_rank):
    position_ids = jnp.arange(owners_count, dtype=jnp.int32)
    if owners_count & (owners_count - 1) == 0:
        source_of = blk_rank ^ position_ids
        unpermute = (source_of[:, None] == position_ids[None, :]).astype(jnp.int32)
        table_part = jnp.sum(unpermute[:, :, None, None] * table_part[None], axis=1)
    else:
        source_of = position_ids
    send_all = table_part[..., :capacity]
    recv_all = table_part[..., capacity:]
    rows_count = owners_count * OWN
    chans_count = owners_count * sections
    chosen = jnp.transpose(send_all, (1, 0, 2))
    valid = (chosen < sections) & (recv_all < OWN)
    source_ids = (blk_rank ^ position_ids if owners_count & (owners_count - 1) == 0 else position_ids)[None, :, None]
    owner_ids = jnp.arange(owners_count, dtype=jnp.int32)[:, None, None]
    channel = jnp.where(valid, source_ids * sections + chosen, -1).reshape(-1)
    target = jnp.where(valid, owner_ids * OWN + recv_all, -1).reshape(-1)
    row_hot = (target[:, None] == jnp.arange(rows_count, dtype=jnp.int32)[None, :]).astype(
        jnp.bfloat16
    )
    chan_hot = (channel[:, None] == jnp.arange(chans_count, dtype=jnp.int32)[None, :]).astype(
        jnp.bfloat16
    )
    selector = jnp.einsum(
        "er,ec->rc", row_hot, chan_hot, preferred_element_type=jnp.float32
    ).astype(jnp.bfloat16)
    selector = selector.reshape(rows_count, owners_count, sections)
    routed = jnp.einsum(
        "rsc,scbq->brq", selector, gathered, preferred_element_type=jnp.float32
    ).astype(jnp.bfloat16)
    own = lax.dynamic_slice_in_dim(routed, blk_rank * OWN, OWN, axis=1)
    own_re = own[..., :all_segs]
    own_im = own[..., all_segs:]
    rotated = jnp.concatenate([own_im, -own_re], axis=-1)
    lhs = jnp.concatenate([own, rotated], axis=1)
    cross = jnp.einsum("bpq,bjq->bpj", lhs, routed, preferred_element_type=jnp.float32)
    cross = cross.reshape(block_bins, 2, OWN, rows_count)
    return jnp.transpose(cross, (1, 0, 2, 3)) / jnp.float32(all_segs)


def solution(mesh):
    placed = (
        P(("groups", "blk"), "seg", "freq"),
        P(),
        P(("groups", "blk"), None, None),
        P(("groups", "blk"), None, None),
    )
    return jax.shard_map(
        per_device,
        mesh=mesh,
        in_specs=placed,
        out_specs=P(None, ("seg", "freq"), ("groups", "blk"), None),
        check_vma=False,
    )
```

```python
import math

import jax
import jax.numpy as jnp
from jax import lax
from jax.experimental import pallas as pl
from jax.experimental.pallas import tpu as pltpu
from jax.sharding import PartitionSpec as P

SEG_LEN = 16384
BINS = 256
BAND_LO = 128
HW = 4
OWN = 16


WHITEN_FLOOR = 0.25
TWO_PI = 2.0 * math.pi


def swapped(value, axis, distance):
    mask = 2**distance
    pairs = [(source, source ^ mask) for source in range(lax.axis_size(axis))]
    return lax.ppermute(value, axis, pairs)


def dft_tables(band_index, sample_index):
    wavenumber = BAND_LO + band_index
    phase_int = wavenumber[:, None] * sample_index[None, :] % SEG_LEN
    angles = phase_int.astype(jnp.float32) * (TWO_PI / SEG_LEN)
    norm_scale = 1.0 / math.sqrt(SEG_LEN)
    cos_part = (jnp.cos(angles) * norm_scale).astype(jnp.bfloat16)
    sin_part = (-jnp.sin(angles) * norm_scale).astype(jnp.bfloat16)
    return (cos_part, sin_part)


def dft_tables_fast(band_index, first_sample, count):
    lanes = 128
    wavenumber = BAND_LO + band_index
    coarse = (first_sample + lanes * jnp.arange(count // lanes, dtype=jnp.int32))
    fine = jnp.arange(lanes, dtype=jnp.int32)
    coarse_angle = (wavenumber[:, None] * coarse[None, :] % SEG_LEN).astype(jnp.float32) * (
        TWO_PI / SEG_LEN
    )
    fine_angle = (wavenumber[:, None] * fine[None, :] % SEG_LEN).astype(jnp.float32) * (
        TWO_PI / SEG_LEN
    )
    cos_a = jnp.cos(coarse_angle)[:, :, None]
    sin_a = jnp.sin(coarse_angle)[:, :, None]
    cos_b = jnp.cos(fine_angle)[:, None, :]
    sin_b = jnp.sin(fine_angle)[:, None, :]
    norm_scale = 1.0 / math.sqrt(SEG_LEN)
    cos_sum = cos_a * cos_b - sin_a * sin_b
    sin_sum = sin_a * cos_b + cos_a * sin_b
    rows = band_index.shape[0]
    cos_part = (cos_sum * norm_scale).astype(jnp.bfloat16).reshape(rows, count)
    sin_part = (-sin_sum * norm_scale).astype(jnp.bfloat16).reshape(rows, count)
    return (cos_part, sin_part)


def response(band_index, taps):
    wavenumber = BAND_LO + band_index
    lag_index = jnp.arange(taps.shape[0], dtype=jnp.int32)
    phase_int = wavenumber[:, None] * lag_index[None, :] % SEG_LEN
    angles = phase_int.astype(jnp.float32) * (TWO_PI / SEG_LEN)
    real_part = jnp.dot(jnp.cos(angles), taps, precision=lax.Precision.HIGHEST)
    imag_part = jnp.dot(-jnp.sin(angles), taps, precision=lax.Precision.HIGHEST)
    return (real_part, imag_part)


def dft_kernel(rec_ref, cos_a_ref, nsin_a_ref, cos_b_ref, sin_b_ref, re_ref, im_ref):
    step = pl.program_id(0)
    lanes = cos_b_ref.shape[0]
    group = 8
    groups = rec_ref.shape[1] // (group * lanes)

    @pl.when(step == 0)
    def _():
        re_ref[...] = jnp.zeros_like(re_ref)
        im_ref[...] = jnp.zeros_like(im_ref)

    def one_group(index, carry):
        row = pl.multiple_of((step * groups + index) * group, group)
        cos_a = cos_a_ref[pl.ds(row, group), :]
        nsin_a = nsin_a_ref[pl.ds(row, group), :]
        cos_b = cos_b_ref[...]
        sin_b = sin_b_ref[...]
        for pair in range(group // 2):
            cos_parts = []
            sin_parts = []
            for half in range(2):
                at = 2 * pair + half
                ca = cos_a[at : at + 1]
                sa = nsin_a[at : at + 1]
                cos_parts.append(ca * cos_b + sa * sin_b)
                sin_parts.append(sa * cos_b - ca * sin_b)
            cos_tile = jnp.concatenate(cos_parts, axis=0).astype(jnp.bfloat16)
            sin_tile = jnp.concatenate(sin_parts, axis=0).astype(jnp.bfloat16)
            first = pl.multiple_of((index * group + 2 * pair) * lanes, 2 * lanes)
            rec = rec_ref[:, pl.ds(first, 2 * lanes)]
            re_ref[...] += jnp.dot(rec, cos_tile, preferred_element_type=jnp.float32)
            im_ref[...] += jnp.dot(rec, sin_tile, preferred_element_type=jnp.float32)
        return carry

    lax.fori_loop(0, groups, one_group, 0)


def dft_fused(records, band_index, first_sample):
    lanes = 128
    chunk = 2048
    count = records.shape[1]
    wavenumber = BAND_LO + band_index
    norm_scale = 1.0 / math.sqrt(SEG_LEN)

    def cos_sin(steps):
        angle = (steps[:, None] * wavenumber[None, :] % SEG_LEN).astype(jnp.float32) * (
            TWO_PI / SEG_LEN
        )
        return jnp.cos(angle), jnp.sin(angle)

    def combined(outer_steps, inner_steps):
        outer_cos, outer_sin = cos_sin(outer_steps)
        inner_cos, inner_sin = cos_sin(inner_steps)
        width = wavenumber.shape[0]
        cos_sum = outer_cos[:, None] * inner_cos[None] - outer_sin[:, None] * inner_sin[None]
        sin_sum = outer_sin[:, None] * inner_cos[None] + outer_cos[:, None] * inner_sin[None]
        return cos_sum.reshape(-1, width), sin_sum.reshape(-1, width)

    coarse_count = count // lanes
    coarse_outer = coarse_count // 8 if coarse_count % 8 == 0 else 1
    coarse_inner = coarse_count // coarse_outer
    cos_a, sin_a = combined(
        first_sample + lanes * coarse_inner * jnp.arange(coarse_outer, dtype=jnp.int32),
        lanes * jnp.arange(coarse_inner, dtype=jnp.int32),
    )
    nsin_a = -sin_a
    cos_b, sin_b = combined(
        16 * jnp.arange(lanes // 16, dtype=jnp.int32), jnp.arange(16, dtype=jnp.int32)
    )
    cos_b = cos_b * norm_scale
    sin_b = sin_b * norm_scale
    rows = records.shape[0]
    bins = band_index.shape[0]
    full = lambda step: (0, 0)
    return pl.pallas_call(
        dft_kernel,
        grid=(count // chunk,),
        in_specs=[
            pl.BlockSpec((rows, chunk), lambda step: (0, step)),
            pl.BlockSpec(cos_a.shape, full),
            pl.BlockSpec(nsin_a.shape, full),
            pl.BlockSpec(cos_b.shape, full),
            pl.BlockSpec(sin_b.shape, full),
        ],
        out_specs=[pl.BlockSpec((rows, bins), full), pl.BlockSpec((rows, bins), full)],
        out_shape=[
            jax.ShapeDtypeStruct((rows, bins), jnp.float32),
            jax.ShapeDtypeStruct((rows, bins), jnp.float32),
        ],
        compiler_params=pltpu.CompilerParams(dimension_semantics=("arbitrary",)),
    )(records, cos_a, nsin_a, cos_b, sin_b)


def gather_blocks(carried, count, rank):
    if count & (count - 1) != 0:
        return lax.all_gather(carried, "blk", axis=0, tiled=False)
    masks = []
    step = count // 2
    while step >= 1:
        masks.append(step)
        step //= 2
    if not masks:
        return carried[None]
    first = masks[0]
    rest = masks[1:]
    pairs = [(source, source ^ first) for source in range(count)]
    held = jnp.stack([carried, lax.ppermute(carried, "blk", pairs)], axis=0)
    split = (held.shape[1] + 1) // 2
    halves = [held[:, :split], held[:, split:]]
    orders = [rest, rest[::-1]]
    results = []
    for part, order in zip(halves, orders):
        done = [first]
        for mask in order:
            pairs = [(source, source ^ mask) for source in range(count)]
            arrived = lax.ppermute(part, "blk", pairs)
            done.append(mask)
            axis = sorted(done, reverse=True).index(mask)
            part = jnp.stack([part, arrived], axis=axis)
        results.append(part.reshape((count,) + part.shape[len(masks):]))
    return jnp.concatenate(results, axis=1)


def per_device(raw, taps, send_list, recv_row):
    owners_count = lax.axis_size("blk")
    seg_count = lax.axis_size("seg")
    freq_count = lax.axis_size("freq")
    freq_rank = lax.axis_index("freq")
    sections, seg_dev, half_len = raw.shape
    records = raw.reshape(sections * seg_dev, half_len)
    device_bins = BINS // freq_count
    block_bins = device_bins // seg_count
    capacity = send_list.shape[2]

    def band_of(row_ids):
        owner_core = row_ids // device_bins
        local_row = row_ids % device_bins
        return (
            local_row // block_bins * freq_count + owner_core
        ) * block_bins + local_row % block_bins

    band_rows = band_of(jnp.arange(device_bins * freq_count, dtype=jnp.int32))
    real_t, imag_t = dft_fused(records, band_rows, freq_rank * half_len)
    real_all = real_t.T
    imag_all = imag_t.T
    blocks = jnp.stack([real_all, imag_all], axis=1)
    blocks = blocks.reshape(freq_count, device_bins, 2, records.shape[0])
    if freq_count == 2:
        kept = jnp.where(freq_rank == 0, blocks[0], blocks[1])
        sent = jnp.where(freq_rank == 0, blocks[1], blocks[0])
        kept_blocks = kept.reshape(seg_count, block_bins, 2, -1)
        sent_blocks = sent.reshape(seg_count, block_bins, 2, -1)
        own_edges = jnp.concatenate(
            [kept_blocks[:, :HW], kept_blocks[:, block_bins - HW :]], axis=1
        ).reshape(seg_count * 2 * HW, 2, -1)
        message = jnp.concatenate([sent, own_edges], axis=0)
        arrived = swapped(message, "freq", 0)
        spectra = kept + arrived[:device_bins]
        their_edges = jnp.concatenate(
            [sent_blocks[:, :HW], sent_blocks[:, block_bins - HW :]], axis=1
        ).reshape(seg_count * 2 * HW, 2, -1)
        edge_spectra = (their_edges + arrived[device_bins:]).reshape(seg_count, 2, HW, 2, -1)
        partner = jnp.transpose(
            jnp.sqrt(
                edge_spectra[..., 0, :] * edge_spectra[..., 0, :]
                + edge_spectra[..., 1, :] * edge_spectra[..., 1, :]
                + 1e-06
            ),
            (1, 0, 2, 3),
        )
    else:
        spectra = lax.psum_scatter(
            blocks.reshape(device_bins * freq_count, 2, records.shape[0]),
            "freq",
            scatter_dimension=0,
            tiled=True,
        )
    real_part = spectra[:, 0]
    imag_part = spectra[:, 1]
    amplitude = jnp.sqrt(real_part * real_part + imag_part * imag_part + 1e-06)
    amp_blocks = amplitude.reshape(seg_count, block_bins, -1)
    if freq_count != 2:
        band_rims = jnp.stack([amp_blocks[:, :HW], amp_blocks[:, block_bins - HW :]])
        partner = swapped(band_rims, "freq", 0)
    zero_rim = jnp.zeros_like(partner[1][:1])
    right_prev = jnp.concatenate([zero_rim, partner[1][:-1]], axis=0)
    left_next = jnp.concatenate([partner[0][1:], zero_rim], axis=0)
    first_core = freq_rank == 0
    lower_rim = jnp.where(first_core, right_prev, partner[1])
    upper_rim = jnp.where(first_core, partner[0], left_next)
    padded = jnp.concatenate([lower_rim, amp_blocks, upper_rim], axis=1)
    window_sum = padded[:, 0:block_bins]
    for offset_step in range(1, 2 * HW + 1):
        window_sum = window_sum + padded[:, offset_step : offset_step + block_bins]
    span_ids = jnp.arange(seg_count, dtype=jnp.int32)[:, None]
    offsets = jnp.arange(block_bins, dtype=jnp.int32)[None, :]
    position = (span_ids * freq_count + freq_rank) * block_bins + offsets
    counted = jnp.minimum(position + HW, BINS - 1) - jnp.maximum(position - HW, 0) + 1
    smooth = window_sum / counted.astype(jnp.float32)[:, :, None]
    divisor = jnp.maximum(smooth, WHITEN_FLOOR).reshape(device_bins, -1)
    local_bins = freq_rank * device_bins + jnp.arange(device_bins, dtype=jnp.int32)
    response_re, response_im = response(band_of(local_bins), taps)
    scaled_re = real_part / divisor
    scaled_im = imag_part / divisor
    white_re = scaled_re * response_re[:, None] - scaled_im * response_im[:, None]
    white_im = scaled_re * response_im[:, None] + scaled_im * response_re[:, None]
    whitened = jnp.stack([white_re, white_im], axis=1).astype(jnp.bfloat16)
    whitened = whitened.reshape(seg_count, block_bins, 2, sections, seg_dev)
    whitened = jnp.transpose(whitened, (0, 3, 1, 2, 4))
    seg_rank = lax.axis_index("seg")
    pieces = [lax.dynamic_index_in_dim(whitened, seg_rank, axis=0, keepdims=False)]
    for shift in range(1, seg_count):
        outgoing = lax.dynamic_index_in_dim(
            whitened, (seg_rank + shift) % seg_count, axis=0, keepdims=False
        )
        pairs = [(source, (source + shift) % seg_count) for source in range(seg_count)]
        flat = outgoing.reshape(sections, -1)
        pieces.append(lax.ppermute(flat, "seg", pairs).reshape(outgoing.shape))
    local = jnp.stack(pieces, axis=3).reshape(sections, block_bins, -1)
    all_segs = seg_dev * seg_count
    table_width = local.shape[-1]
    table = jnp.concatenate([send_list[0], recv_row[0]], axis=1).reshape(-1)
    table_len = table.shape[0]
    slab = jnp.pad(table.astype(jnp.bfloat16), (0, sections * table_width - table_len))
    carried = jnp.concatenate([local, slab.reshape(sections, 1, table_width)], axis=1)
    blk_rank = lax.axis_index("blk")
    everything = gather_blocks(carried.reshape(sections, -1), owners_count, blk_rank)
    everything = everything.reshape(owners_count, sections, block_bins + 1, table_width)
    gathered = everything[:, :, :block_bins]
    table_part = everything[:, :, block_bins].reshape(owners_count, -1)[:, :table_len]
    table_part = table_part.astype(jnp.int32).reshape(owners_count, owners_count, 2 * capacity)
    position_ids = jnp.arange(owners_count, dtype=jnp.int32)
    if owners_count & (owners_count - 1) == 0:
        source_of = blk_rank ^ position_ids
        unpermute = (source_of[:, None] == position_ids[None, :]).astype(jnp.int32)
        table_part = jnp.sum(unpermute[:, :, None, None] * table_part[None], axis=1)
    else:
        source_of = position_ids
    send_all = table_part[..., :capacity]
    recv_all = table_part[..., capacity:]
    rows_count = owners_count * OWN
    chans_count = owners_count * sections
    chosen = jnp.transpose(send_all, (1, 0, 2))
    valid = (chosen < sections) & (recv_all < OWN)
    source_ids = (blk_rank ^ position_ids if owners_count & (owners_count - 1) == 0 else position_ids)[None, :, None]
    owner_ids = jnp.arange(owners_count, dtype=jnp.int32)[:, None, None]
    channel = jnp.where(valid, source_ids * sections + chosen, -1).reshape(-1)
    target = jnp.where(valid, owner_ids * OWN + recv_all, -1).reshape(-1)
    row_hot = (target[:, None] == jnp.arange(rows_count, dtype=jnp.int32)[None, :]).astype(
        jnp.bfloat16
    )
    chan_hot = (channel[:, None] == jnp.arange(chans_count, dtype=jnp.int32)[None, :]).astype(
        jnp.bfloat16
    )
    selector = jnp.einsum(
        "er,ec->rc", row_hot, chan_hot, preferred_element_type=jnp.float32
    ).astype(jnp.bfloat16)
    selector = selector.reshape(rows_count, owners_count, sections)
    routed = jnp.einsum(
        "rsc,scbq->brq", selector, gathered, preferred_element_type=jnp.float32
    ).astype(jnp.bfloat16)
    own = lax.dynamic_slice_in_dim(routed, blk_rank * OWN, OWN, axis=1)
    own_re = own[..., :all_segs]
    own_im = own[..., all_segs:]
    rotated = jnp.concatenate([own_im, -own_re], axis=-1)
    lhs = jnp.concatenate([own, rotated], axis=1)
    cross = jnp.einsum("bpq,bjq->bpj", lhs, routed, preferred_element_type=jnp.float32)
    cross = cross.reshape(block_bins, 2, OWN, rows_count)
    return jnp.transpose(cross, (1, 0, 2, 3)) / jnp.float32(all_segs)


def solution(mesh):
    placed = (
        P(("groups", "blk"), "seg", "freq"),
        P(),
        P(("groups", "blk"), None, None),
        P(("groups", "blk"), None, None),
    )
    return jax.shard_map(
        per_device,
        mesh=mesh,
        in_specs=placed,
        out_specs=P(None, ("seg", "freq"), ("groups", "blk"), None),
        check_vma=False,
    )
```

```python
import math

import jax
import jax.numpy as jnp
from jax import lax
from jax.experimental import pallas as pl
from jax.experimental.pallas import tpu as pltpu
from jax.sharding import PartitionSpec as P

SEG_LEN = 16384
BINS = 256
BAND_LO = 128
HW = 4
OWN = 16


WHITEN_FLOOR = 0.25
TWO_PI = 2.0 * math.pi


def swapped(value, axis, distance):
    mask = 2**distance
    pairs = [(source, source ^ mask) for source in range(lax.axis_size(axis))]
    return lax.ppermute(value, axis, pairs)


def dft_tables(band_index, sample_index):
    wavenumber = BAND_LO + band_index
    phase_int = wavenumber[:, None] * sample_index[None, :] % SEG_LEN
    angles = phase_int.astype(jnp.float32) * (TWO_PI / SEG_LEN)
    norm_scale = 1.0 / math.sqrt(SEG_LEN)
    cos_part = (jnp.cos(angles) * norm_scale).astype(jnp.bfloat16)
    sin_part = (-jnp.sin(angles) * norm_scale).astype(jnp.bfloat16)
    return (cos_part, sin_part)


def dft_tables_fast(band_index, first_sample, count):
    lanes = 128
    wavenumber = BAND_LO + band_index
    coarse = (first_sample + lanes * jnp.arange(count // lanes, dtype=jnp.int32))
    fine = jnp.arange(lanes, dtype=jnp.int32)
    coarse_angle = (wavenumber[:, None] * coarse[None, :] % SEG_LEN).astype(jnp.float32) * (
        TWO_PI / SEG_LEN
    )
    fine_angle = (wavenumber[:, None] * fine[None, :] % SEG_LEN).astype(jnp.float32) * (
        TWO_PI / SEG_LEN
    )
    cos_a = jnp.cos(coarse_angle)[:, :, None]
    sin_a = jnp.sin(coarse_angle)[:, :, None]
    cos_b = jnp.cos(fine_angle)[:, None, :]
    sin_b = jnp.sin(fine_angle)[:, None, :]
    norm_scale = 1.0 / math.sqrt(SEG_LEN)
    cos_sum = cos_a * cos_b - sin_a * sin_b
    sin_sum = sin_a * cos_b + cos_a * sin_b
    rows = band_index.shape[0]
    cos_part = (cos_sum * norm_scale).astype(jnp.bfloat16).reshape(rows, count)
    sin_part = (-sin_sum * norm_scale).astype(jnp.bfloat16).reshape(rows, count)
    return (cos_part, sin_part)


def response(band_index, taps):
    wavenumber = BAND_LO + band_index
    lag_index = jnp.arange(taps.shape[0], dtype=jnp.int32)
    phase_int = wavenumber[:, None] * lag_index[None, :] % SEG_LEN
    angles = phase_int.astype(jnp.float32) * (TWO_PI / SEG_LEN)
    real_part = jnp.dot(jnp.cos(angles), taps, precision=lax.Precision.HIGHEST)
    imag_part = jnp.dot(-jnp.sin(angles), taps, precision=lax.Precision.HIGHEST)
    return (real_part, imag_part)


def dft_kernel(rec_ref, cos_a_ref, nsin_a_ref, cos_b_ref, sin_b_ref, re_ref, im_ref):
    step = pl.program_id(0)
    lanes = cos_b_ref.shape[0]
    group = 8
    groups = rec_ref.shape[1] // (group * lanes)

    @pl.when(step == 0)
    def _():
        re_ref[...] = jnp.zeros_like(re_ref)
        im_ref[...] = jnp.zeros_like(im_ref)

    def one_group(index, carry):
        row = pl.multiple_of((step * groups + index) * group, group)
        cos_a = cos_a_ref[pl.ds(row, group), :]
        nsin_a = nsin_a_ref[pl.ds(row, group), :]
        cos_b = cos_b_ref[...]
        sin_b = sin_b_ref[...]
        for pair in range(group // 2):
            cos_parts = []
            sin_parts = []
            for half in range(2):
                at = 2 * pair + half
                ca = cos_a[at : at + 1]
                sa = nsin_a[at : at + 1]
                cos_parts.append(ca * cos_b + sa * sin_b)
                sin_parts.append(sa * cos_b - ca * sin_b)
            cos_tile = jnp.concatenate(cos_parts, axis=0).astype(jnp.bfloat16)
            sin_tile = jnp.concatenate(sin_parts, axis=0).astype(jnp.bfloat16)
            first = pl.multiple_of((index * group + 2 * pair) * lanes, 2 * lanes)
            rec = rec_ref[:, pl.ds(first, 2 * lanes)]
            re_ref[...] += jnp.dot(rec, cos_tile, preferred_element_type=jnp.float32)
            im_ref[...] += jnp.dot(rec, sin_tile, preferred_element_type=jnp.float32)
        return carry

    lax.fori_loop(0, groups, one_group, 0)


def dft_fused(records, band_index, first_sample):
    lanes = 128
    chunk = 2048
    count = records.shape[1]
    wavenumber = BAND_LO + band_index
    norm_scale = 1.0 / math.sqrt(SEG_LEN)

    def cos_sin(steps):
        angle = (steps[:, None] * wavenumber[None, :] % SEG_LEN).astype(jnp.float32) * (
            TWO_PI / SEG_LEN
        )
        return jnp.cos(angle), jnp.sin(angle)

    def combined(outer_steps, inner_steps):
        outer_cos, outer_sin = cos_sin(outer_steps)
        inner_cos, inner_sin = cos_sin(inner_steps)
        width = wavenumber.shape[0]
        cos_sum = outer_cos[:, None] * inner_cos[None] - outer_sin[:, None] * inner_sin[None]
        sin_sum = outer_sin[:, None] * inner_cos[None] + outer_cos[:, None] * inner_sin[None]
        return cos_sum.reshape(-1, width), sin_sum.reshape(-1, width)

    coarse_count = count // lanes
    coarse_outer = coarse_count // 8 if coarse_count % 8 == 0 else 1
    coarse_inner = coarse_count // coarse_outer
    cos_a, sin_a = combined(
        first_sample + lanes * coarse_inner * jnp.arange(coarse_outer, dtype=jnp.int32),
        lanes * jnp.arange(coarse_inner, dtype=jnp.int32),
    )
    nsin_a = -sin_a
    cos_b, sin_b = combined(
        16 * jnp.arange(lanes // 16, dtype=jnp.int32), jnp.arange(16, dtype=jnp.int32)
    )
    cos_b = cos_b * norm_scale
    sin_b = sin_b * norm_scale
    rows = records.shape[0]
    bins = band_index.shape[0]
    full = lambda step: (0, 0)
    return pl.pallas_call(
        dft_kernel,
        grid=(count // chunk,),
        in_specs=[
            pl.BlockSpec((rows, chunk), lambda step: (0, step)),
            pl.BlockSpec(cos_a.shape, full),
            pl.BlockSpec(nsin_a.shape, full),
            pl.BlockSpec(cos_b.shape, full),
            pl.BlockSpec(sin_b.shape, full),
        ],
        out_specs=[pl.BlockSpec((rows, bins), full), pl.BlockSpec((rows, bins), full)],
        out_shape=[
            jax.ShapeDtypeStruct((rows, bins), jnp.float32),
            jax.ShapeDtypeStruct((rows, bins), jnp.float32),
        ],
        compiler_params=pltpu.CompilerParams(dimension_semantics=("arbitrary",)),
    )(records, cos_a, nsin_a, cos_b, sin_b)


def gather_blocks(carried, count, rank):
    if count & (count - 1) != 0:
        return lax.all_gather(carried, "blk", axis=0, tiled=False)
    masks = []
    step = count // 2
    while step >= 1:
        masks.append(step)
        step //= 2
    if not masks:
        return carried[None]
    first = masks[0]
    rest = masks[1:]
    pairs = [(source, source ^ first) for source in range(count)]
    held = jnp.stack([carried, lax.ppermute(carried, "blk", pairs)], axis=0)
    split = (held.shape[1] + 1) // 2
    halves = [held[:, :split], held[:, split:]]
    orders = [rest, rest[::-1]]
    results = []
    for part, order in zip(halves, orders):
        done = [first]
        for mask in order:
            pairs = [(source, source ^ mask) for source in range(count)]
            arrived = lax.ppermute(part, "blk", pairs)
            done.append(mask)
            axis = sorted(done, reverse=True).index(mask)
            part = jnp.stack([part, arrived], axis=axis)
        results.append(part.reshape((count,) + part.shape[len(masks):]))
    return jnp.concatenate(results, axis=1)


def per_device(raw, taps, send_list, recv_row):
    owners_count = lax.axis_size("blk")
    seg_count = lax.axis_size("seg")
    freq_count = lax.axis_size("freq")
    freq_rank = lax.axis_index("freq")
    sections, seg_dev, half_len = raw.shape
    records = raw.reshape(sections * seg_dev, half_len)
    device_bins = BINS // freq_count
    block_bins = device_bins // seg_count
    capacity = send_list.shape[2]

    def band_of(row_ids):
        owner_core = row_ids // device_bins
        local_row = row_ids % device_bins
        return (
            local_row // block_bins * freq_count + owner_core
        ) * block_bins + local_row % block_bins

    band_rows = band_of(jnp.arange(device_bins * freq_count, dtype=jnp.int32))
    real_t, imag_t = dft_fused(records, band_rows, freq_rank * half_len)
    real_all = real_t.T
    imag_all = imag_t.T
    blocks = jnp.stack([real_all, imag_all], axis=1)
    blocks = blocks.reshape(freq_count, device_bins, 2, records.shape[0])
    if freq_count == 2:
        kept = jnp.where(freq_rank == 0, blocks[0], blocks[1])
        sent = jnp.where(freq_rank == 0, blocks[1], blocks[0])
        kept_blocks = kept.reshape(seg_count, block_bins, 2, -1)
        sent_blocks = sent.reshape(seg_count, block_bins, 2, -1)
        own_edges = jnp.concatenate(
            [kept_blocks[:, :HW], kept_blocks[:, block_bins - HW :]], axis=1
        ).reshape(seg_count * 2 * HW, 2, -1)
        message = jnp.concatenate([sent, own_edges], axis=0)
        arrived = swapped(message, "freq", 0)
        spectra = kept + arrived[:device_bins]
        their_edges = jnp.concatenate(
            [sent_blocks[:, :HW], sent_blocks[:, block_bins - HW :]], axis=1
        ).reshape(seg_count * 2 * HW, 2, -1)
        edge_spectra = (their_edges + arrived[device_bins:]).reshape(seg_count, 2, HW, 2, -1)
        partner = jnp.transpose(
            jnp.sqrt(
                edge_spectra[..., 0, :] * edge_spectra[..., 0, :]
                + edge_spectra[..., 1, :] * edge_spectra[..., 1, :]
                + 1e-06
            ),
            (1, 0, 2, 3),
        )
    else:
        spectra = lax.psum_scatter(
            blocks.reshape(device_bins * freq_count, 2, records.shape[0]),
            "freq",
            scatter_dimension=0,
            tiled=True,
        )
    real_part = spectra[:, 0]
    imag_part = spectra[:, 1]
    amplitude = jnp.sqrt(real_part * real_part + imag_part * imag_part + 1e-06)
    amp_blocks = amplitude.reshape(seg_count, block_bins, -1)
    if freq_count != 2:
        band_rims = jnp.stack([amp_blocks[:, :HW], amp_blocks[:, block_bins - HW :]])
        partner = swapped(band_rims, "freq", 0)
    zero_rim = jnp.zeros_like(partner[1][:1])
    right_prev = jnp.concatenate([zero_rim, partner[1][:-1]], axis=0)
    left_next = jnp.concatenate([partner[0][1:], zero_rim], axis=0)
    first_core = freq_rank == 0
    lower_rim = jnp.where(first_core, right_prev, partner[1])
    upper_rim = jnp.where(first_core, partner[0], left_next)
    padded = jnp.concatenate([lower_rim, amp_blocks, upper_rim], axis=1)
    window_sum = padded[:, 0:block_bins]
    for offset_step in range(1, 2 * HW + 1):
        window_sum = window_sum + padded[:, offset_step : offset_step + block_bins]
    span_ids = jnp.arange(seg_count, dtype=jnp.int32)[:, None]
    offsets = jnp.arange(block_bins, dtype=jnp.int32)[None, :]
    position = (span_ids * freq_count + freq_rank) * block_bins + offsets
    counted = jnp.minimum(position + HW, BINS - 1) - jnp.maximum(position - HW, 0) + 1
    smooth = window_sum / counted.astype(jnp.float32)[:, :, None]
    divisor = jnp.maximum(smooth, WHITEN_FLOOR).reshape(device_bins, -1)
    local_bins = freq_rank * device_bins + jnp.arange(device_bins, dtype=jnp.int32)
    response_re, response_im = response(band_of(local_bins), taps)
    scaled_re = real_part / divisor
    scaled_im = imag_part / divisor
    white_re = scaled_re * response_re[:, None] - scaled_im * response_im[:, None]
    white_im = scaled_re * response_im[:, None] + scaled_im * response_re[:, None]
    whitened = jnp.stack([white_re, white_im], axis=1).astype(jnp.bfloat16)
    whitened = whitened.reshape(seg_count, block_bins, 2, sections, seg_dev)
    whitened = jnp.transpose(whitened, (0, 3, 1, 2, 4))
    seg_rank = lax.axis_index("seg")
    pieces = [lax.dynamic_index_in_dim(whitened, seg_rank, axis=0, keepdims=False)]
    for shift in range(1, seg_count):
        outgoing = lax.dynamic_index_in_dim(
            whitened, (seg_rank + shift) % seg_count, axis=0, keepdims=False
        )
        pairs = [(source, (source + shift) % seg_count) for source in range(seg_count)]
        flat = outgoing.reshape(sections, -1)
        pieces.append(lax.ppermute(flat, "seg", pairs).reshape(outgoing.shape))
    all_segs = seg_dev * seg_count
    table = jnp.concatenate([send_list[0], recv_row[0]], axis=1).reshape(-1)
    table_len = table.shape[0]
    piece_width = block_bins * 2 * seg_dev
    slab_width = 128
    slab = jnp.pad(table.astype(jnp.bfloat16), (0, sections * slab_width - table_len))
    blk_rank = lax.axis_index("blk")
    moved = []
    for index, piece in enumerate(pieces):
        flat = piece.reshape(sections, -1)
        if index == 0:
            flat = jnp.concatenate([flat, slab.reshape(sections, slab_width)], axis=1)
        moved.append(gather_blocks(flat, owners_count, blk_rank))
    table_part = moved[0][:, :, piece_width:].reshape(owners_count, -1)[:, :table_len]
    table_part = table_part.astype(jnp.int32).reshape(owners_count, owners_count, 2 * capacity)
    position_ids = jnp.arange(owners_count, dtype=jnp.int32)
    if owners_count & (owners_count - 1) == 0:
        source_of = blk_rank ^ position_ids
        unpermute = (source_of[:, None] == position_ids[None, :]).astype(jnp.int32)
        table_part = jnp.sum(unpermute[:, :, None, None] * table_part[None], axis=1)
    else:
        source_of = position_ids
    send_all = table_part[..., :capacity]
    recv_all = table_part[..., capacity:]
    rows_count = owners_count * OWN
    chans_count = owners_count * sections
    chosen = jnp.transpose(send_all, (1, 0, 2))
    valid = (chosen < sections) & (recv_all < OWN)
    source_ids = (blk_rank ^ position_ids if owners_count & (owners_count - 1) == 0 else position_ids)[None, :, None]
    owner_ids = jnp.arange(owners_count, dtype=jnp.int32)[:, None, None]
    channel = jnp.where(valid, source_ids * sections + chosen, -1).reshape(-1)
    target = jnp.where(valid, owner_ids * OWN + recv_all, -1).reshape(-1)
    row_hot = (target[:, None] == jnp.arange(rows_count, dtype=jnp.int32)[None, :]).astype(
        jnp.bfloat16
    )
    chan_hot = (channel[:, None] == jnp.arange(chans_count, dtype=jnp.int32)[None, :]).astype(
        jnp.bfloat16
    )
    selector = jnp.einsum(
        "er,ec->rc", row_hot, chan_hot, preferred_element_type=jnp.float32
    ).astype(jnp.bfloat16)
    selector = selector.reshape(rows_count, owners_count, sections)
    cross = None
    for chain in moved:
        data = chain[:, :, :piece_width].reshape(owners_count, sections, block_bins, 2 * seg_dev)
        routed = jnp.einsum(
            "rsc,scbq->brq", selector, data, preferred_element_type=jnp.float32
        ).astype(jnp.bfloat16)
        own = lax.dynamic_slice_in_dim(routed, blk_rank * OWN, OWN, axis=1)
        own_re = own[..., :seg_dev]
        own_im = own[..., seg_dev:]
        rotated = jnp.concatenate([own_im, -own_re], axis=-1)
        lhs = jnp.concatenate([own, rotated], axis=1)
        part = jnp.einsum("bpq,bjq->bpj", lhs, routed, preferred_element_type=jnp.float32)
        cross = part if cross is None else cross + part
    cross = cross.reshape(block_bins, 2, OWN, rows_count)
    return jnp.transpose(cross, (1, 0, 2, 3)) / jnp.float32(all_segs)


def solution(mesh):
    placed = (
        P(("groups", "blk"), "seg", "freq"),
        P(),
        P(("groups", "blk"), None, None),
        P(("groups", "blk"), None, None),
    )
    return jax.shard_map(
        per_device,
        mesh=mesh,
        in_specs=placed,
        out_specs=P(None, ("seg", "freq"), ("groups", "blk"), None),
        check_vma=False,
    )
```

```python
import math

import jax
import jax.numpy as jnp
from jax import lax
from jax.experimental import pallas as pl
from jax.experimental.pallas import tpu as pltpu
from jax.sharding import PartitionSpec as P

SEG_LEN = 16384
BINS = 256
BAND_LO = 128
HW = 4
OWN = 16


WHITEN_FLOOR = 0.25
TWO_PI = 2.0 * math.pi


def swapped(value, axis, distance):
    mask = 2**distance
    pairs = [(source, source ^ mask) for source in range(lax.axis_size(axis))]
    return lax.ppermute(value, axis, pairs)


def dft_tables(band_index, sample_index):
    wavenumber = BAND_LO + band_index
    phase_int = wavenumber[:, None] * sample_index[None, :] % SEG_LEN
    angles = phase_int.astype(jnp.float32) * (TWO_PI / SEG_LEN)
    norm_scale = 1.0 / math.sqrt(SEG_LEN)
    cos_part = (jnp.cos(angles) * norm_scale).astype(jnp.bfloat16)
    sin_part = (-jnp.sin(angles) * norm_scale).astype(jnp.bfloat16)
    return (cos_part, sin_part)


def dft_tables_fast(band_index, first_sample, count):
    lanes = 128
    wavenumber = BAND_LO + band_index
    coarse = (first_sample + lanes * jnp.arange(count // lanes, dtype=jnp.int32))
    fine = jnp.arange(lanes, dtype=jnp.int32)
    coarse_angle = (wavenumber[:, None] * coarse[None, :] % SEG_LEN).astype(jnp.float32) * (
        TWO_PI / SEG_LEN
    )
    fine_angle = (wavenumber[:, None] * fine[None, :] % SEG_LEN).astype(jnp.float32) * (
        TWO_PI / SEG_LEN
    )
    cos_a = jnp.cos(coarse_angle)[:, :, None]
    sin_a = jnp.sin(coarse_angle)[:, :, None]
    cos_b = jnp.cos(fine_angle)[:, None, :]
    sin_b = jnp.sin(fine_angle)[:, None, :]
    norm_scale = 1.0 / math.sqrt(SEG_LEN)
    cos_sum = cos_a * cos_b - sin_a * sin_b
    sin_sum = sin_a * cos_b + cos_a * sin_b
    rows = band_index.shape[0]
    cos_part = (cos_sum * norm_scale).astype(jnp.bfloat16).reshape(rows, count)
    sin_part = (-sin_sum * norm_scale).astype(jnp.bfloat16).reshape(rows, count)
    return (cos_part, sin_part)


def response(band_index, taps):
    wavenumber = BAND_LO + band_index
    lag_index = jnp.arange(taps.shape[0], dtype=jnp.int32)
    phase_int = wavenumber[:, None] * lag_index[None, :] % SEG_LEN
    angles = phase_int.astype(jnp.float32) * (TWO_PI / SEG_LEN)
    real_part = jnp.dot(jnp.cos(angles), taps, precision=lax.Precision.HIGHEST)
    imag_part = jnp.dot(-jnp.sin(angles), taps, precision=lax.Precision.HIGHEST)
    return (real_part, imag_part)


def dft_kernel(rec_ref, cos_a_ref, nsin_a_ref, cos_b_ref, sin_b_ref, re_ref, im_ref):
    step = pl.program_id(0)
    lanes = cos_b_ref.shape[0]
    group = 8
    groups = rec_ref.shape[1] // (group * lanes)

    @pl.when(step == 0)
    def _():
        re_ref[...] = jnp.zeros_like(re_ref)
        im_ref[...] = jnp.zeros_like(im_ref)

    def one_group(index, carry):
        row = pl.multiple_of((step * groups + index) * group, group)
        cos_a = cos_a_ref[pl.ds(row, group), :]
        nsin_a = nsin_a_ref[pl.ds(row, group), :]
        cos_b = cos_b_ref[...]
        sin_b = sin_b_ref[...]
        for pair in range(group // 2):
            cos_parts = []
            sin_parts = []
            for half in range(2):
                at = 2 * pair + half
                ca = cos_a[at : at + 1]
                sa = nsin_a[at : at + 1]
                cos_parts.append(ca * cos_b + sa * sin_b)
                sin_parts.append(sa * cos_b - ca * sin_b)
            cos_tile = jnp.concatenate(cos_parts, axis=0).astype(jnp.bfloat16)
            sin_tile = jnp.concatenate(sin_parts, axis=0).astype(jnp.bfloat16)
            first = pl.multiple_of((index * group + 2 * pair) * lanes, 2 * lanes)
            rec = rec_ref[:, pl.ds(first, 2 * lanes)]
            re_ref[...] += jnp.dot(rec, cos_tile, preferred_element_type=jnp.float32)
            im_ref[...] += jnp.dot(rec, sin_tile, preferred_element_type=jnp.float32)
        return carry

    lax.fori_loop(0, groups, one_group, 0)


def dft_fused(records, band_index, first_sample):
    lanes = 128
    chunk = 2048
    count = records.shape[1]
    wavenumber = BAND_LO + band_index
    norm_scale = 1.0 / math.sqrt(SEG_LEN)

    def cos_sin(steps):
        angle = (steps[:, None] * wavenumber[None, :] % SEG_LEN).astype(jnp.float32) * (
            TWO_PI / SEG_LEN
        )
        return jnp.cos(angle), jnp.sin(angle)

    def combined(outer_steps, inner_steps):
        outer_cos, outer_sin = cos_sin(outer_steps)
        inner_cos, inner_sin = cos_sin(inner_steps)
        width = wavenumber.shape[0]
        cos_sum = outer_cos[:, None] * inner_cos[None] - outer_sin[:, None] * inner_sin[None]
        sin_sum = outer_sin[:, None] * inner_cos[None] + outer_cos[:, None] * inner_sin[None]
        return cos_sum.reshape(-1, width), sin_sum.reshape(-1, width)

    coarse_count = count // lanes
    coarse_outer = coarse_count // 8 if coarse_count % 8 == 0 else 1
    coarse_inner = coarse_count // coarse_outer
    cos_a, sin_a = combined(
        first_sample + lanes * coarse_inner * jnp.arange(coarse_outer, dtype=jnp.int32),
        lanes * jnp.arange(coarse_inner, dtype=jnp.int32),
    )
    nsin_a = -sin_a
    cos_b, sin_b = combined(
        16 * jnp.arange(lanes // 16, dtype=jnp.int32), jnp.arange(16, dtype=jnp.int32)
    )
    cos_b = cos_b * norm_scale
    sin_b = sin_b * norm_scale
    rows = records.shape[0]
    bins = band_index.shape[0]
    full = lambda step: (0, 0)
    return pl.pallas_call(
        dft_kernel,
        grid=(count // chunk,),
        in_specs=[
            pl.BlockSpec((rows, chunk), lambda step: (0, step)),
            pl.BlockSpec(cos_a.shape, full),
            pl.BlockSpec(nsin_a.shape, full),
            pl.BlockSpec(cos_b.shape, full),
            pl.BlockSpec(sin_b.shape, full),
        ],
        out_specs=[pl.BlockSpec((rows, bins), full), pl.BlockSpec((rows, bins), full)],
        out_shape=[
            jax.ShapeDtypeStruct((rows, bins), jnp.float32),
            jax.ShapeDtypeStruct((rows, bins), jnp.float32),
        ],
        compiler_params=pltpu.CompilerParams(dimension_semantics=("arbitrary",)),
    )(records, cos_a, nsin_a, cos_b, sin_b)


def gather_blocks(carried, count, rank, held=None):
    if count & (count - 1) != 0:
        return lax.all_gather(carried, "blk", axis=0, tiled=False)
    masks = []
    step = count // 2
    while step >= 1:
        masks.append(step)
        step //= 2
    if not masks:
        return carried[None]
    first = masks[0]
    rest = masks[1:]
    if held is None:
        pairs = [(source, source ^ first) for source in range(count)]
        held = jnp.stack([carried, lax.ppermute(carried, "blk", pairs)], axis=0)
    split = (held.shape[1] + 1) // 2
    halves = [held[:, :split], held[:, split:]]
    orders = [rest, rest[::-1]]
    results = []
    for part, order in zip(halves, orders):
        done = [first]
        for mask in order:
            pairs = [(source, source ^ mask) for source in range(count)]
            arrived = lax.ppermute(part, "blk", pairs)
            done.append(mask)
            axis = sorted(done, reverse=True).index(mask)
            part = jnp.stack([part, arrived], axis=axis)
        results.append(part.reshape((count,) + part.shape[len(masks):]))
    return jnp.concatenate(results, axis=1)


def per_device(raw, taps, send_list, recv_row):
    owners_count = lax.axis_size("blk")
    seg_count = lax.axis_size("seg")
    freq_count = lax.axis_size("freq")
    freq_rank = lax.axis_index("freq")
    sections, seg_dev, half_len = raw.shape
    records = raw.reshape(sections * seg_dev, half_len)
    device_bins = BINS // freq_count
    block_bins = device_bins // seg_count
    capacity = send_list.shape[2]

    def band_of(row_ids):
        owner_core = row_ids // device_bins
        local_row = row_ids % device_bins
        return (
            local_row // block_bins * freq_count + owner_core
        ) * block_bins + local_row % block_bins

    band_rows = band_of(jnp.arange(device_bins * freq_count, dtype=jnp.int32))
    real_t, imag_t = dft_fused(records, band_rows, freq_rank * half_len)
    real_all = real_t.T
    imag_all = imag_t.T
    blocks = jnp.stack([real_all, imag_all], axis=1)
    blocks = blocks.reshape(freq_count, device_bins, 2, records.shape[0])
    if freq_count == 2:
        kept = jnp.where(freq_rank == 0, blocks[0], blocks[1])
        sent = jnp.where(freq_rank == 0, blocks[1], blocks[0])
        kept_blocks = kept.reshape(seg_count, block_bins, 2, -1)
        sent_blocks = sent.reshape(seg_count, block_bins, 2, -1)
        own_edges = jnp.concatenate(
            [kept_blocks[:, :HW], kept_blocks[:, block_bins - HW :]], axis=1
        ).reshape(seg_count * 2 * HW, 2, -1)
        message = jnp.concatenate([sent, own_edges], axis=0)
        arrived = swapped(message, "freq", 0)
        spectra = kept + arrived[:device_bins]
        their_edges = jnp.concatenate(
            [sent_blocks[:, :HW], sent_blocks[:, block_bins - HW :]], axis=1
        ).reshape(seg_count * 2 * HW, 2, -1)
        edge_spectra = (their_edges + arrived[device_bins:]).reshape(seg_count, 2, HW, 2, -1)
        partner = jnp.transpose(
            jnp.sqrt(
                edge_spectra[..., 0, :] * edge_spectra[..., 0, :]
                + edge_spectra[..., 1, :] * edge_spectra[..., 1, :]
                + 1e-06
            ),
            (1, 0, 2, 3),
        )
    else:
        spectra = lax.psum_scatter(
            blocks.reshape(device_bins * freq_count, 2, records.shape[0]),
            "freq",
            scatter_dimension=0,
            tiled=True,
        )
    real_part = spectra[:, 0]
    imag_part = spectra[:, 1]
    amplitude = jnp.sqrt(real_part * real_part + imag_part * imag_part + 1e-06)
    amp_blocks = amplitude.reshape(seg_count, block_bins, -1)
    if freq_count != 2:
        band_rims = jnp.stack([amp_blocks[:, :HW], amp_blocks[:, block_bins - HW :]])
        partner = swapped(band_rims, "freq", 0)
    zero_rim = jnp.zeros_like(partner[1][:1])
    right_prev = jnp.concatenate([zero_rim, partner[1][:-1]], axis=0)
    left_next = jnp.concatenate([partner[0][1:], zero_rim], axis=0)
    first_core = freq_rank == 0
    lower_rim = jnp.where(first_core, right_prev, partner[1])
    upper_rim = jnp.where(first_core, partner[0], left_next)
    padded = jnp.concatenate([lower_rim, amp_blocks, upper_rim], axis=1)
    window_sum = padded[:, 0:block_bins]
    for offset_step in range(1, 2 * HW + 1):
        window_sum = window_sum + padded[:, offset_step : offset_step + block_bins]
    span_ids = jnp.arange(seg_count, dtype=jnp.int32)[:, None]
    offsets = jnp.arange(block_bins, dtype=jnp.int32)[None, :]
    position = (span_ids * freq_count + freq_rank) * block_bins + offsets
    counted = jnp.minimum(position + HW, BINS - 1) - jnp.maximum(position - HW, 0) + 1
    smooth = window_sum / counted.astype(jnp.float32)[:, :, None]
    divisor = jnp.maximum(smooth, WHITEN_FLOOR).reshape(device_bins, -1)
    local_bins = freq_rank * device_bins + jnp.arange(device_bins, dtype=jnp.int32)
    response_re, response_im = response(band_of(local_bins), taps)
    scaled_re = real_part / divisor
    scaled_im = imag_part / divisor
    white_re = scaled_re * response_re[:, None] - scaled_im * response_im[:, None]
    white_im = scaled_re * response_im[:, None] + scaled_im * response_re[:, None]
    whitened = jnp.stack([white_re, white_im], axis=1).astype(jnp.bfloat16)
    whitened = whitened.reshape(seg_count, block_bins, 2, sections, seg_dev)
    whitened = jnp.transpose(whitened, (0, 3, 1, 2, 4))
    seg_rank = lax.axis_index("seg")
    all_segs = seg_dev * seg_count
    table = jnp.concatenate([send_list[0], recv_row[0]], axis=1).reshape(-1)
    table_len = table.shape[0]
    blk_rank = lax.axis_index("blk")
    fused_round = seg_count == 2 and owners_count >= 2 and owners_count & (owners_count - 1) == 0
    if fused_round:
        piece_width = block_bins * 2 * seg_dev
        slab_width = 128
        slab = jnp.pad(table.astype(jnp.bfloat16), (0, sections * slab_width - table_len))
        keep = lax.dynamic_index_in_dim(whitened, seg_rank, axis=0, keepdims=False)
        other = lax.dynamic_index_in_dim(whitened, 1 - seg_rank, axis=0, keepdims=False)
        keep_flat = jnp.concatenate(
            [keep.reshape(sections, -1), slab.reshape(sections, slab_width)], axis=1
        )
        other_flat = other.reshape(sections, -1)
        first = owners_count // 2
        from_blk = lax.ppermute(
            keep_flat, "blk", [(source, source ^ first) for source in range(owners_count)]
        )
        from_seg = lax.ppermute(other_flat, "seg", [(0, 1), (1, 0)])
        diagonal = [
            (source * 2 + side, (source ^ first) * 2 + 1 - side)
            for source in range(owners_count)
            for side in range(2)
        ]
        from_diagonal = lax.ppermute(other_flat, ("blk", "seg"), diagonal)
        held = jnp.stack(
            [
                jnp.concatenate([keep_flat, from_seg], axis=1),
                jnp.concatenate([from_blk, from_diagonal], axis=1),
            ],
            axis=0,
        )
        moved = gather_blocks(None, owners_count, blk_rank, held=held)
        halves = [moved[:, :, :piece_width], moved[:, :, piece_width + slab_width :]]
        table_part = moved[:, :, piece_width : piece_width + slab_width]
        table_part = table_part.reshape(owners_count, -1)[:, :table_len]
        half_segs = seg_dev
    else:
        pieces = [lax.dynamic_index_in_dim(whitened, seg_rank, axis=0, keepdims=False)]
        for shift in range(1, seg_count):
            outgoing = lax.dynamic_index_in_dim(
                whitened, (seg_rank + shift) % seg_count, axis=0, keepdims=False
            )
            pairs = [(source, (source + shift) % seg_count) for source in range(seg_count)]
            flat = outgoing.reshape(sections, -1)
            pieces.append(lax.ppermute(flat, "seg", pairs).reshape(outgoing.shape))
        local = jnp.stack(pieces, axis=3).reshape(sections, block_bins, -1)
        table_width = local.shape[-1]
        slab = jnp.pad(table.astype(jnp.bfloat16), (0, sections * table_width - table_len))
        carried = jnp.concatenate([local, slab.reshape(sections, 1, table_width)], axis=1)
        everything = gather_blocks(carried.reshape(sections, -1), owners_count, blk_rank)
        everything = everything.reshape(owners_count, sections, block_bins + 1, table_width)
        halves = [everything[:, :, :block_bins]]
        table_part = everything[:, :, block_bins].reshape(owners_count, -1)[:, :table_len]
        half_segs = all_segs
    table_part = table_part.astype(jnp.int32).reshape(owners_count, owners_count, 2 * capacity)
    position_ids = jnp.arange(owners_count, dtype=jnp.int32)
    if owners_count & (owners_count - 1) == 0:
        source_of = blk_rank ^ position_ids
        unpermute = (source_of[:, None] == position_ids[None, :]).astype(jnp.int32)
        table_part = jnp.sum(unpermute[:, :, None, None] * table_part[None], axis=1)
    else:
        source_of = position_ids
    send_all = table_part[..., :capacity]
    recv_all = table_part[..., capacity:]
    rows_count = owners_count * OWN
    chans_count = owners_count * sections
    chosen = jnp.transpose(send_all, (1, 0, 2))
    valid = (chosen < sections) & (recv_all < OWN)
    source_ids = (blk_rank ^ position_ids if owners_count & (owners_count - 1) == 0 else position_ids)[None, :, None]
    owner_ids = jnp.arange(owners_count, dtype=jnp.int32)[:, None, None]
    channel = jnp.where(valid, source_ids * sections + chosen, -1).reshape(-1)
    target = jnp.where(valid, owner_ids * OWN + recv_all, -1).reshape(-1)
    row_hot = (target[:, None] == jnp.arange(rows_count, dtype=jnp.int32)[None, :]).astype(
        jnp.bfloat16
    )
    chan_hot = (channel[:, None] == jnp.arange(chans_count, dtype=jnp.int32)[None, :]).astype(
        jnp.bfloat16
    )
    selector = jnp.einsum(
        "er,ec->rc", row_hot, chan_hot, preferred_element_type=jnp.float32
    ).astype(jnp.bfloat16)
    selector = selector.reshape(rows_count, owners_count, sections)
    cross = None
    for half in halves:
        data = half.reshape(owners_count, sections, block_bins, 2 * half_segs)
        routed = jnp.einsum(
            "rsc,scbq->brq", selector, data, preferred_element_type=jnp.float32
        ).astype(jnp.bfloat16)
        own = lax.dynamic_slice_in_dim(routed, blk_rank * OWN, OWN, axis=1)
        own_re = own[..., :half_segs]
        own_im = own[..., half_segs:]
        rotated = jnp.concatenate([own_im, -own_re], axis=-1)
        lhs = jnp.concatenate([own, rotated], axis=1)
        part = jnp.einsum("bpq,bjq->bpj", lhs, routed, preferred_element_type=jnp.float32)
        cross = part if cross is None else cross + part
    cross = cross.reshape(block_bins, 2, OWN, rows_count)
    return jnp.transpose(cross, (1, 0, 2, 3)) / jnp.float32(all_segs)


def solution(mesh):
    placed = (
        P(("groups", "blk"), "seg", "freq"),
        P(),
        P(("groups", "blk"), None, None),
        P(("groups", "blk"), None, None),
    )
    return jax.shard_map(
        per_device,
        mesh=mesh,
        in_specs=placed,
        out_specs=P(None, ("seg", "freq"), ("groups", "blk"), None),
        check_vma=False,
    )
```

```python
import math

import jax
import jax.numpy as jnp
from jax import lax
from jax.experimental import pallas as pl
from jax.experimental.pallas import tpu as pltpu
from jax.sharding import PartitionSpec as P

SEG_LEN = 16384
BINS = 256
BAND_LO = 128
HW = 4
OWN = 16


WHITEN_FLOOR = 0.25
TWO_PI = 2.0 * math.pi


def swapped(value, axis, distance):
    mask = 2**distance
    pairs = [(source, source ^ mask) for source in range(lax.axis_size(axis))]
    return lax.ppermute(value, axis, pairs)


def dft_tables(band_index, sample_index):
    wavenumber = BAND_LO + band_index
    phase_int = wavenumber[:, None] * sample_index[None, :] % SEG_LEN
    angles = phase_int.astype(jnp.float32) * (TWO_PI / SEG_LEN)
    norm_scale = 1.0 / math.sqrt(SEG_LEN)
    cos_part = (jnp.cos(angles) * norm_scale).astype(jnp.bfloat16)
    sin_part = (-jnp.sin(angles) * norm_scale).astype(jnp.bfloat16)
    return (cos_part, sin_part)


def dft_tables_fast(band_index, first_sample, count):
    lanes = 128
    wavenumber = BAND_LO + band_index
    coarse = (first_sample + lanes * jnp.arange(count // lanes, dtype=jnp.int32))
    fine = jnp.arange(lanes, dtype=jnp.int32)
    coarse_angle = (wavenumber[:, None] * coarse[None, :] % SEG_LEN).astype(jnp.float32) * (
        TWO_PI / SEG_LEN
    )
    fine_angle = (wavenumber[:, None] * fine[None, :] % SEG_LEN).astype(jnp.float32) * (
        TWO_PI / SEG_LEN
    )
    cos_a = jnp.cos(coarse_angle)[:, :, None]
    sin_a = jnp.sin(coarse_angle)[:, :, None]
    cos_b = jnp.cos(fine_angle)[:, None, :]
    sin_b = jnp.sin(fine_angle)[:, None, :]
    norm_scale = 1.0 / math.sqrt(SEG_LEN)
    cos_sum = cos_a * cos_b - sin_a * sin_b
    sin_sum = sin_a * cos_b + cos_a * sin_b
    rows = band_index.shape[0]
    cos_part = (cos_sum * norm_scale).astype(jnp.bfloat16).reshape(rows, count)
    sin_part = (-sin_sum * norm_scale).astype(jnp.bfloat16).reshape(rows, count)
    return (cos_part, sin_part)


def response(band_index, taps):
    wavenumber = BAND_LO + band_index
    lag_index = jnp.arange(taps.shape[0], dtype=jnp.int32)
    phase_int = wavenumber[:, None] * lag_index[None, :] % SEG_LEN
    angles = phase_int.astype(jnp.float32) * (TWO_PI / SEG_LEN)
    real_part = jnp.dot(jnp.cos(angles), taps, precision=lax.Precision.HIGHEST)
    imag_part = jnp.dot(-jnp.sin(angles), taps, precision=lax.Precision.HIGHEST)
    return (real_part, imag_part)


def dft_kernel(rec_ref, cos_a_ref, nsin_a_ref, cos_b_ref, sin_b_ref, re_ref, im_ref):
    step = pl.program_id(0)
    lanes = cos_b_ref.shape[0]
    group = 8
    groups = rec_ref.shape[1] // (group * lanes)

    @pl.when(step == 0)
    def _():
        re_ref[...] = jnp.zeros_like(re_ref)
        im_ref[...] = jnp.zeros_like(im_ref)

    def one_group(index, carry):
        row = pl.multiple_of((step * groups + index) * group, group)
        cos_a = cos_a_ref[pl.ds(row, group), :]
        nsin_a = nsin_a_ref[pl.ds(row, group), :]
        cos_b = cos_b_ref[...]
        sin_b = sin_b_ref[...]
        for pair in range(group // 2):
            cos_parts = []
            sin_parts = []
            for half in range(2):
                at = 2 * pair + half
                ca = cos_a[at : at + 1]
                sa = nsin_a[at : at + 1]
                cos_parts.append(ca * cos_b + sa * sin_b)
                sin_parts.append(sa * cos_b - ca * sin_b)
            cos_tile = jnp.concatenate(cos_parts, axis=0).astype(jnp.bfloat16)
            sin_tile = jnp.concatenate(sin_parts, axis=0).astype(jnp.bfloat16)
            first = pl.multiple_of((index * group + 2 * pair) * lanes, 2 * lanes)
            rec = rec_ref[:, pl.ds(first, 2 * lanes)]
            re_ref[...] += jnp.dot(rec, cos_tile, preferred_element_type=jnp.float32)
            im_ref[...] += jnp.dot(rec, sin_tile, preferred_element_type=jnp.float32)
        return carry

    lax.fori_loop(0, groups, one_group, 0)


def dft_fused(records, band_index, first_sample):
    lanes = 128
    chunk = 2048
    count = records.shape[1]
    wavenumber = BAND_LO + band_index
    norm_scale = 1.0 / math.sqrt(SEG_LEN)

    def cos_sin(steps):
        angle = (steps[:, None] * wavenumber[None, :] % SEG_LEN).astype(jnp.float32) * (
            TWO_PI / SEG_LEN
        )
        return jnp.cos(angle), jnp.sin(angle)

    def combined(outer_steps, inner_steps):
        outer_cos, outer_sin = cos_sin(outer_steps)
        inner_cos, inner_sin = cos_sin(inner_steps)
        width = wavenumber.shape[0]
        cos_sum = outer_cos[:, None] * inner_cos[None] - outer_sin[:, None] * inner_sin[None]
        sin_sum = outer_sin[:, None] * inner_cos[None] + outer_cos[:, None] * inner_sin[None]
        return cos_sum.reshape(-1, width), sin_sum.reshape(-1, width)

    coarse_count = count // lanes
    coarse_outer = coarse_count // 8 if coarse_count % 8 == 0 else 1
    coarse_inner = coarse_count // coarse_outer
    cos_a, sin_a = combined(
        first_sample + lanes * coarse_inner * jnp.arange(coarse_outer, dtype=jnp.int32),
        lanes * jnp.arange(coarse_inner, dtype=jnp.int32),
    )
    nsin_a = -sin_a
    cos_b, sin_b = combined(
        16 * jnp.arange(lanes // 16, dtype=jnp.int32), jnp.arange(16, dtype=jnp.int32)
    )
    cos_b = cos_b * norm_scale
    sin_b = sin_b * norm_scale
    rows = records.shape[0]
    bins = band_index.shape[0]
    full = lambda step: (0, 0)
    return pl.pallas_call(
        dft_kernel,
        grid=(count // chunk,),
        in_specs=[
            pl.BlockSpec((rows, chunk), lambda step: (0, step)),
            pl.BlockSpec(cos_a.shape, full),
            pl.BlockSpec(nsin_a.shape, full),
            pl.BlockSpec(cos_b.shape, full),
            pl.BlockSpec(sin_b.shape, full),
        ],
        out_specs=[pl.BlockSpec((rows, bins), full), pl.BlockSpec((rows, bins), full)],
        out_shape=[
            jax.ShapeDtypeStruct((rows, bins), jnp.float32),
            jax.ShapeDtypeStruct((rows, bins), jnp.float32),
        ],
        compiler_params=pltpu.CompilerParams(dimension_semantics=("arbitrary",)),
    )(records, cos_a, nsin_a, cos_b, sin_b)


def gather_blocks(carried, count, rank, held=None):
    if count & (count - 1) != 0:
        return lax.all_gather(carried, "blk", axis=0, tiled=False)
    masks = []
    step = count // 2
    while step >= 1:
        masks.append(step)
        step //= 2
    if not masks:
        return carried[None]
    first = masks[0]
    rest = masks[1:]
    if held is None:
        pairs = [(source, source ^ first) for source in range(count)]
        held = jnp.stack([carried, lax.ppermute(carried, "blk", pairs)], axis=0)
    split = (held.shape[1] + 1) // 2
    halves = [held[:, :split], held[:, split:]]
    orders = [rest, rest[::-1]]
    results = []
    for part, order in zip(halves, orders):
        done = [first]
        for mask in order:
            pairs = [(source, source ^ mask) for source in range(count)]
            arrived = lax.ppermute(part, "blk", pairs)
            done.append(mask)
            axis = sorted(done, reverse=True).index(mask)
            part = jnp.stack([part, arrived], axis=axis)
        results.append(part.reshape((count,) + part.shape[len(masks):]))
    return jnp.concatenate(results, axis=1)


def per_device(raw, taps, send_list, recv_row):
    owners_count = lax.axis_size("blk")
    seg_count = lax.axis_size("seg")
    freq_count = lax.axis_size("freq")
    freq_rank = lax.axis_index("freq")
    sections, seg_dev, half_len = raw.shape
    records = raw.reshape(sections * seg_dev, half_len)
    device_bins = BINS // freq_count
    block_bins = device_bins // seg_count
    capacity = send_list.shape[2]

    def band_of(row_ids):
        owner_core = row_ids // device_bins
        local_row = row_ids % device_bins
        return (
            local_row // block_bins * freq_count + owner_core
        ) * block_bins + local_row % block_bins

    band_rows = band_of(jnp.arange(device_bins * freq_count, dtype=jnp.int32))
    real_t, imag_t = dft_fused(records, band_rows, freq_rank * half_len)
    real_all = real_t.T
    imag_all = imag_t.T
    blocks = jnp.stack([real_all, imag_all], axis=1)
    blocks = blocks.reshape(freq_count, device_bins, 2, records.shape[0])
    if freq_count == 2:
        kept = jnp.where(freq_rank == 0, blocks[0], blocks[1])
        sent = jnp.where(freq_rank == 0, blocks[1], blocks[0])
        kept_blocks = kept.reshape(seg_count, block_bins, 2, -1)
        sent_blocks = sent.reshape(seg_count, block_bins, 2, -1)
        own_edges = jnp.concatenate(
            [kept_blocks[:, :HW], kept_blocks[:, block_bins - HW :]], axis=1
        ).reshape(seg_count * 2 * HW, 2, -1)
        message = jnp.concatenate([sent, own_edges], axis=0)
        arrived = swapped(message, "freq", 0)
        spectra = kept + arrived[:device_bins]
        their_edges = jnp.concatenate(
            [sent_blocks[:, :HW], sent_blocks[:, block_bins - HW :]], axis=1
        ).reshape(seg_count * 2 * HW, 2, -1)
        edge_spectra = (their_edges + arrived[device_bins:]).reshape(seg_count, 2, HW, 2, -1)
        partner = jnp.transpose(
            jnp.sqrt(
                edge_spectra[..., 0, :] * edge_spectra[..., 0, :]
                + edge_spectra[..., 1, :] * edge_spectra[..., 1, :]
                + 1e-06
            ),
            (1, 0, 2, 3),
        )
    else:
        spectra = lax.psum_scatter(
            blocks.reshape(device_bins * freq_count, 2, records.shape[0]),
            "freq",
            scatter_dimension=0,
            tiled=True,
        )
    real_part = spectra[:, 0]
    imag_part = spectra[:, 1]
    amplitude = jnp.sqrt(real_part * real_part + imag_part * imag_part + 1e-06)
    amp_blocks = amplitude.reshape(seg_count, block_bins, -1)
    if freq_count != 2:
        band_rims = jnp.stack([amp_blocks[:, :HW], amp_blocks[:, block_bins - HW :]])
        partner = swapped(band_rims, "freq", 0)
    zero_rim = jnp.zeros_like(partner[1][:1])
    right_prev = jnp.concatenate([zero_rim, partner[1][:-1]], axis=0)
    left_next = jnp.concatenate([partner[0][1:], zero_rim], axis=0)
    first_core = freq_rank == 0
    lower_rim = jnp.where(first_core, right_prev, partner[1])
    upper_rim = jnp.where(first_core, partner[0], left_next)
    padded = jnp.concatenate([lower_rim, amp_blocks, upper_rim], axis=1)
    window_sum = padded[:, 0:block_bins]
    for offset_step in range(1, 2 * HW + 1):
        window_sum = window_sum + padded[:, offset_step : offset_step + block_bins]
    span_ids = jnp.arange(seg_count, dtype=jnp.int32)[:, None]
    offsets = jnp.arange(block_bins, dtype=jnp.int32)[None, :]
    position = (span_ids * freq_count + freq_rank) * block_bins + offsets
    counted = jnp.minimum(position + HW, BINS - 1) - jnp.maximum(position - HW, 0) + 1
    smooth = window_sum / counted.astype(jnp.float32)[:, :, None]
    divisor = jnp.maximum(smooth, WHITEN_FLOOR).reshape(device_bins, -1)
    local_bins = freq_rank * device_bins + jnp.arange(device_bins, dtype=jnp.int32)
    response_re, response_im = response(band_of(local_bins), taps)
    scaled_re = real_part / divisor
    scaled_im = imag_part / divisor
    white_re = scaled_re * response_re[:, None] - scaled_im * response_im[:, None]
    white_im = scaled_re * response_im[:, None] + scaled_im * response_re[:, None]
    whitened = jnp.stack([white_re, white_im], axis=1).astype(jnp.bfloat16)
    whitened = whitened.reshape(seg_count, block_bins, 2, sections, seg_dev)
    whitened = jnp.transpose(whitened, (0, 3, 1, 2, 4))
    seg_rank = lax.axis_index("seg")
    all_segs = seg_dev * seg_count
    table = jnp.concatenate([send_list[0], recv_row[0]], axis=1).reshape(-1)
    table_len = table.shape[0]
    blk_rank = lax.axis_index("blk")
    fused_round = seg_count == 2 and owners_count >= 2 and owners_count & (owners_count - 1) == 0
    if fused_round:
        piece_width = block_bins * 2 * seg_dev
        slab_width = 128
        slab = jnp.pad(table.astype(jnp.bfloat16), (0, sections * slab_width - table_len))
        keep = lax.dynamic_index_in_dim(whitened, seg_rank, axis=0, keepdims=False)
        other = lax.dynamic_index_in_dim(whitened, 1 - seg_rank, axis=0, keepdims=False)
        keep_flat = jnp.concatenate(
            [keep.reshape(sections, -1), slab.reshape(sections, slab_width)], axis=1
        )
        other_flat = other.reshape(sections, -1)
        first = owners_count // 2
        from_blk = lax.ppermute(
            keep_flat, "blk", [(source, source ^ first) for source in range(owners_count)]
        )
        from_seg = lax.ppermute(other_flat, "seg", [(0, 1), (1, 0)])
        diagonal = [
            (source * 2 + side, (source ^ first) * 2 + 1 - side)
            for source in range(owners_count)
            for side in range(2)
        ]
        from_diagonal = lax.ppermute(other_flat, ("blk", "seg"), diagonal)

        def interleave(mine_segs, their_segs, table_slab):
            lanes_in = 2 * seg_dev
            joined = jnp.concatenate(
                [
                    mine_segs.reshape(sections, block_bins, lanes_in),
                    their_segs.reshape(sections, block_bins, lanes_in),
                ],
                axis=2,
            ).reshape(sections, -1)
            return jnp.concatenate([joined, table_slab], axis=1)

        held = jnp.stack(
            [
                interleave(keep_flat[:, :piece_width], from_seg, keep_flat[:, piece_width:]),
                interleave(from_blk[:, :piece_width], from_diagonal, from_blk[:, piece_width:]),
            ],
            axis=0,
        )
        moved = gather_blocks(None, owners_count, blk_rank, held=held)
        halves = [moved[:, :, : 2 * piece_width]]
        table_part = moved[:, :, 2 * piece_width :]
        table_part = table_part.reshape(owners_count, -1)[:, :table_len]
        half_segs = all_segs
        chunk_segs = seg_dev
    else:
        pieces = [lax.dynamic_index_in_dim(whitened, seg_rank, axis=0, keepdims=False)]
        for shift in range(1, seg_count):
            outgoing = lax.dynamic_index_in_dim(
                whitened, (seg_rank + shift) % seg_count, axis=0, keepdims=False
            )
            pairs = [(source, (source + shift) % seg_count) for source in range(seg_count)]
            flat = outgoing.reshape(sections, -1)
            pieces.append(lax.ppermute(flat, "seg", pairs).reshape(outgoing.shape))
        local = jnp.stack(pieces, axis=3).reshape(sections, block_bins, -1)
        table_width = local.shape[-1]
        slab = jnp.pad(table.astype(jnp.bfloat16), (0, sections * table_width - table_len))
        carried = jnp.concatenate([local, slab.reshape(sections, 1, table_width)], axis=1)
        everything = gather_blocks(carried.reshape(sections, -1), owners_count, blk_rank)
        everything = everything.reshape(owners_count, sections, block_bins + 1, table_width)
        halves = [everything[:, :, :block_bins]]
        table_part = everything[:, :, block_bins].reshape(owners_count, -1)[:, :table_len]
        half_segs = all_segs
        chunk_segs = all_segs
    table_part = table_part.astype(jnp.int32).reshape(owners_count, owners_count, 2 * capacity)
    position_ids = jnp.arange(owners_count, dtype=jnp.int32)
    if owners_count & (owners_count - 1) == 0:
        source_of = blk_rank ^ position_ids
        unpermute = (source_of[:, None] == position_ids[None, :]).astype(jnp.int32)
        table_part = jnp.sum(unpermute[:, :, None, None] * table_part[None], axis=1)
    else:
        source_of = position_ids
    send_all = table_part[..., :capacity]
    recv_all = table_part[..., capacity:]
    rows_count = owners_count * OWN
    chans_count = owners_count * sections
    chosen = jnp.transpose(send_all, (1, 0, 2))
    valid = (chosen < sections) & (recv_all < OWN)
    source_ids = (blk_rank ^ position_ids if owners_count & (owners_count - 1) == 0 else position_ids)[None, :, None]
    owner_ids = jnp.arange(owners_count, dtype=jnp.int32)[:, None, None]
    channel = jnp.where(valid, source_ids * sections + chosen, -1).reshape(-1)
    target = jnp.where(valid, owner_ids * OWN + recv_all, -1).reshape(-1)
    row_hot = (target[:, None] == jnp.arange(rows_count, dtype=jnp.int32)[None, :]).astype(
        jnp.bfloat16
    )
    chan_hot = (channel[:, None] == jnp.arange(chans_count, dtype=jnp.int32)[None, :]).astype(
        jnp.bfloat16
    )
    selector = jnp.einsum(
        "er,ec->rc", row_hot, chan_hot, preferred_element_type=jnp.float32
    ).astype(jnp.bfloat16)
    selector = selector.reshape(rows_count, owners_count, sections)
    cross = None
    for half in halves:
        data = half.reshape(owners_count, sections, block_bins, 2 * half_segs)
        routed = jnp.einsum(
            "rsc,scbq->brq", selector, data, preferred_element_type=jnp.float32
        ).astype(jnp.bfloat16)
        own = lax.dynamic_slice_in_dim(routed, blk_rank * OWN, OWN, axis=1)
        own_parts = own.reshape(own.shape[:-1] + (-1, 2, chunk_segs))
        rotated = jnp.stack([own_parts[..., 1, :], -own_parts[..., 0, :]], axis=-2)
        rotated = rotated.reshape(own.shape)
        lhs = jnp.concatenate([own, rotated], axis=1)
        part = jnp.einsum("bpq,bjq->bpj", lhs, routed, preferred_element_type=jnp.float32)
        cross = part if cross is None else cross + part
    cross = cross.reshape(block_bins, 2, OWN, rows_count)
    return jnp.transpose(cross, (1, 0, 2, 3)) / jnp.float32(all_segs)


def solution(mesh):
    placed = (
        P(("groups", "blk"), "seg", "freq"),
        P(),
        P(("groups", "blk"), None, None),
        P(("groups", "blk"), None, None),
    )
    return jax.shard_map(
        per_device,
        mesh=mesh,
        in_specs=placed,
        out_specs=P(None, ("seg", "freq"), ("groups", "blk"), None),
        check_vma=False,
    )
```

```python
import math

import jax
import jax.numpy as jnp
from jax import lax
from jax.experimental import pallas as pl
from jax.experimental.pallas import tpu as pltpu
from jax.sharding import PartitionSpec as P

SEG_LEN = 16384
BINS = 256
BAND_LO = 128
HW = 4
OWN = 16


WHITEN_FLOOR = 0.25
TWO_PI = 2.0 * math.pi


def swapped(value, axis, distance):
    mask = 2**distance
    pairs = [(source, source ^ mask) for source in range(lax.axis_size(axis))]
    return lax.ppermute(value, axis, pairs)


def dft_tables(band_index, sample_index):
    wavenumber = BAND_LO + band_index
    phase_int = wavenumber[:, None] * sample_index[None, :] % SEG_LEN
    angles = phase_int.astype(jnp.float32) * (TWO_PI / SEG_LEN)
    norm_scale = 1.0 / math.sqrt(SEG_LEN)
    cos_part = (jnp.cos(angles) * norm_scale).astype(jnp.bfloat16)
    sin_part = (-jnp.sin(angles) * norm_scale).astype(jnp.bfloat16)
    return (cos_part, sin_part)


def dft_tables_fast(band_index, first_sample, count):
    lanes = 128
    wavenumber = BAND_LO + band_index
    coarse = (first_sample + lanes * jnp.arange(count // lanes, dtype=jnp.int32))
    fine = jnp.arange(lanes, dtype=jnp.int32)
    coarse_angle = (wavenumber[:, None] * coarse[None, :] % SEG_LEN).astype(jnp.float32) * (
        TWO_PI / SEG_LEN
    )
    fine_angle = (wavenumber[:, None] * fine[None, :] % SEG_LEN).astype(jnp.float32) * (
        TWO_PI / SEG_LEN
    )
    cos_a = jnp.cos(coarse_angle)[:, :, None]
    sin_a = jnp.sin(coarse_angle)[:, :, None]
    cos_b = jnp.cos(fine_angle)[:, None, :]
    sin_b = jnp.sin(fine_angle)[:, None, :]
    norm_scale = 1.0 / math.sqrt(SEG_LEN)
    cos_sum = cos_a * cos_b - sin_a * sin_b
    sin_sum = sin_a * cos_b + cos_a * sin_b
    rows = band_index.shape[0]
    cos_part = (cos_sum * norm_scale).astype(jnp.bfloat16).reshape(rows, count)
    sin_part = (-sin_sum * norm_scale).astype(jnp.bfloat16).reshape(rows, count)
    return (cos_part, sin_part)


def response(band_index, taps):
    wavenumber = BAND_LO + band_index
    lag_index = jnp.arange(taps.shape[0], dtype=jnp.int32)
    phase_int = wavenumber[:, None] * lag_index[None, :] % SEG_LEN
    angles = phase_int.astype(jnp.float32) * (TWO_PI / SEG_LEN)
    real_part = jnp.dot(jnp.cos(angles), taps, precision=lax.Precision.HIGHEST)
    imag_part = jnp.dot(-jnp.sin(angles), taps, precision=lax.Precision.HIGHEST)
    return (real_part, imag_part)


def dft_kernel(rec_ref, cos_a_ref, nsin_a_ref, cos_b_ref, sin_b_ref, re_ref, im_ref):
    step = pl.program_id(0)
    lanes = cos_b_ref.shape[0]
    group = 8
    groups = rec_ref.shape[1] // (group * lanes)

    @pl.when(step == 0)
    def _():
        re_ref[...] = jnp.zeros_like(re_ref)
        im_ref[...] = jnp.zeros_like(im_ref)

    def one_group(index, carry):
        row = pl.multiple_of((step * groups + index) * group, group)
        cos_a = cos_a_ref[pl.ds(row, group), :]
        nsin_a = nsin_a_ref[pl.ds(row, group), :]
        cos_b = cos_b_ref[...]
        sin_b = sin_b_ref[...]
        for pair in range(group // 2):
            cos_parts = []
            sin_parts = []
            for half in range(2):
                at = 2 * pair + half
                ca = cos_a[at : at + 1]
                sa = nsin_a[at : at + 1]
                cos_parts.append(ca * cos_b + sa * sin_b)
                sin_parts.append(sa * cos_b - ca * sin_b)
            cos_tile = jnp.concatenate(cos_parts, axis=0).astype(jnp.bfloat16)
            sin_tile = jnp.concatenate(sin_parts, axis=0).astype(jnp.bfloat16)
            first = pl.multiple_of((index * group + 2 * pair) * lanes, 2 * lanes)
            rec = rec_ref[:, pl.ds(first, 2 * lanes)]
            re_ref[...] += lax.dot_general(cos_tile, rec, (((0,), (1,)), ((), ())), preferred_element_type=jnp.float32)
            im_ref[...] += lax.dot_general(sin_tile, rec, (((0,), (1,)), ((), ())), preferred_element_type=jnp.float32)
        return carry

    lax.fori_loop(0, groups, one_group, 0)


def dft_fused(records, band_index, first_sample):
    lanes = 128
    chunk = 2048
    count = records.shape[1]
    wavenumber = BAND_LO + band_index
    norm_scale = 1.0 / math.sqrt(SEG_LEN)

    def cos_sin(steps):
        angle = (steps[:, None] * wavenumber[None, :] % SEG_LEN).astype(jnp.float32) * (
            TWO_PI / SEG_LEN
        )
        return jnp.cos(angle), jnp.sin(angle)

    def combined(outer_steps, inner_steps):
        outer_cos, outer_sin = cos_sin(outer_steps)
        inner_cos, inner_sin = cos_sin(inner_steps)
        width = wavenumber.shape[0]
        cos_sum = outer_cos[:, None] * inner_cos[None] - outer_sin[:, None] * inner_sin[None]
        sin_sum = outer_sin[:, None] * inner_cos[None] + outer_cos[:, None] * inner_sin[None]
        return cos_sum.reshape(-1, width), sin_sum.reshape(-1, width)

    coarse_count = count // lanes
    coarse_outer = coarse_count // 8 if coarse_count % 8 == 0 else 1
    coarse_inner = coarse_count // coarse_outer
    cos_a, sin_a = combined(
        first_sample + lanes * coarse_inner * jnp.arange(coarse_outer, dtype=jnp.int32),
        lanes * jnp.arange(coarse_inner, dtype=jnp.int32),
    )
    nsin_a = -sin_a
    cos_b, sin_b = combined(
        16 * jnp.arange(lanes // 16, dtype=jnp.int32), jnp.arange(16, dtype=jnp.int32)
    )
    cos_b = cos_b * norm_scale
    sin_b = sin_b * norm_scale
    rows = records.shape[0]
    bins = band_index.shape[0]
    full = lambda step: (0, 0)
    return pl.pallas_call(
        dft_kernel,
        grid=(count // chunk,),
        in_specs=[
            pl.BlockSpec((rows, chunk), lambda step: (0, step)),
            pl.BlockSpec(cos_a.shape, full),
            pl.BlockSpec(nsin_a.shape, full),
            pl.BlockSpec(cos_b.shape, full),
            pl.BlockSpec(sin_b.shape, full),
        ],
        out_specs=[pl.BlockSpec((bins, rows), full), pl.BlockSpec((bins, rows), full)],
        out_shape=[
            jax.ShapeDtypeStruct((bins, rows), jnp.float32),
            jax.ShapeDtypeStruct((bins, rows), jnp.float32),
        ],
        compiler_params=pltpu.CompilerParams(dimension_semantics=("arbitrary",)),
    )(records, cos_a, nsin_a, cos_b, sin_b)


def gather_blocks(carried, count, rank, held=None):
    if count & (count - 1) != 0:
        return lax.all_gather(carried, "blk", axis=0, tiled=False)
    masks = []
    step = count // 2
    while step >= 1:
        masks.append(step)
        step //= 2
    if not masks:
        return carried[None]
    first = masks[0]
    rest = masks[1:]
    if held is None:
        pairs = [(source, source ^ first) for source in range(count)]
        held = jnp.stack([carried, lax.ppermute(carried, "blk", pairs)], axis=0)
    split = (held.shape[1] + 1) // 2
    halves = [held[:, :split], held[:, split:]]
    orders = [rest, rest[::-1]]
    results = []
    for part, order in zip(halves, orders):
        done = [first]
        for mask in order:
            pairs = [(source, source ^ mask) for source in range(count)]
            arrived = lax.ppermute(part, "blk", pairs)
            done.append(mask)
            axis = sorted(done, reverse=True).index(mask)
            part = jnp.stack([part, arrived], axis=axis)
        results.append(part.reshape((count,) + part.shape[len(masks):]))
    return jnp.concatenate(results, axis=1)


def per_device(raw, taps, send_list, recv_row):
    owners_count = lax.axis_size("blk")
    seg_count = lax.axis_size("seg")
    freq_count = lax.axis_size("freq")
    freq_rank = lax.axis_index("freq")
    sections, seg_dev, half_len = raw.shape
    records = raw.reshape(sections * seg_dev, half_len)
    device_bins = BINS // freq_count
    block_bins = device_bins // seg_count
    capacity = send_list.shape[2]

    def band_of(row_ids):
        owner_core = row_ids // device_bins
        local_row = row_ids % device_bins
        return (
            local_row // block_bins * freq_count + owner_core
        ) * block_bins + local_row % block_bins

    band_rows = band_of(jnp.arange(device_bins * freq_count, dtype=jnp.int32))
    real_all, imag_all = dft_fused(records, band_rows, freq_rank * half_len)
    blocks = jnp.stack([real_all, imag_all], axis=1)
    blocks = blocks.reshape(freq_count, device_bins, 2, records.shape[0])
    if freq_count == 2:
        kept = jnp.where(freq_rank == 0, blocks[0], blocks[1])
        sent = jnp.where(freq_rank == 0, blocks[1], blocks[0])
        kept_blocks = kept.reshape(seg_count, block_bins, 2, -1)
        sent_blocks = sent.reshape(seg_count, block_bins, 2, -1)
        own_edges = jnp.concatenate(
            [kept_blocks[:, :HW], kept_blocks[:, block_bins - HW :]], axis=1
        ).reshape(seg_count * 2 * HW, 2, -1)
        message = jnp.concatenate([sent, own_edges], axis=0)
        arrived = swapped(message, "freq", 0)
        spectra = kept + arrived[:device_bins]
        their_edges = jnp.concatenate(
            [sent_blocks[:, :HW], sent_blocks[:, block_bins - HW :]], axis=1
        ).reshape(seg_count * 2 * HW, 2, -1)
        edge_spectra = (their_edges + arrived[device_bins:]).reshape(seg_count, 2, HW, 2, -1)
        partner = jnp.transpose(
            jnp.sqrt(
                edge_spectra[..., 0, :] * edge_spectra[..., 0, :]
                + edge_spectra[..., 1, :] * edge_spectra[..., 1, :]
                + 1e-06
            ),
            (1, 0, 2, 3),
        )
    else:
        spectra = lax.psum_scatter(
            blocks.reshape(device_bins * freq_count, 2, records.shape[0]),
            "freq",
            scatter_dimension=0,
            tiled=True,
        )
    real_part = spectra[:, 0]
    imag_part = spectra[:, 1]
    amplitude = jnp.sqrt(real_part * real_part + imag_part * imag_part + 1e-06)
    amp_blocks = amplitude.reshape(seg_count, block_bins, -1)
    if freq_count != 2:
        band_rims = jnp.stack([amp_blocks[:, :HW], amp_blocks[:, block_bins - HW :]])
        partner = swapped(band_rims, "freq", 0)
    zero_rim = jnp.zeros_like(partner[1][:1])
    right_prev = jnp.concatenate([zero_rim, partner[1][:-1]], axis=0)
    left_next = jnp.concatenate([partner[0][1:], zero_rim], axis=0)
    first_core = freq_rank == 0
    lower_rim = jnp.where(first_core, right_prev, partner[1])
    upper_rim = jnp.where(first_core, partner[0], left_next)
    padded = jnp.concatenate([lower_rim, amp_blocks, upper_rim], axis=1)
    window_sum = padded[:, 0:block_bins]
    for offset_step in range(1, 2 * HW + 1):
        window_sum = window_sum + padded[:, offset_step : offset_step + block_bins]
    span_ids = jnp.arange(seg_count, dtype=jnp.int32)[:, None]
    offsets = jnp.arange(block_bins, dtype=jnp.int32)[None, :]
    position = (span_ids * freq_count + freq_rank) * block_bins + offsets
    counted = jnp.minimum(position + HW, BINS - 1) - jnp.maximum(position - HW, 0) + 1
    smooth = window_sum / counted.astype(jnp.float32)[:, :, None]
    divisor = jnp.maximum(smooth, WHITEN_FLOOR).reshape(device_bins, -1)
    local_bins = freq_rank * device_bins + jnp.arange(device_bins, dtype=jnp.int32)
    response_re, response_im = response(band_of(local_bins), taps)
    scaled_re = real_part / divisor
    scaled_im = imag_part / divisor
    white_re = scaled_re * response_re[:, None] - scaled_im * response_im[:, None]
    white_im = scaled_re * response_im[:, None] + scaled_im * response_re[:, None]
    whitened = jnp.stack([white_re, white_im], axis=1).astype(jnp.bfloat16)
    whitened = whitened.reshape(seg_count, block_bins, 2, sections, seg_dev)
    whitened = jnp.transpose(whitened, (0, 3, 1, 2, 4))
    seg_rank = lax.axis_index("seg")
    all_segs = seg_dev * seg_count
    table = jnp.concatenate([send_list[0], recv_row[0]], axis=1).reshape(-1)
    table_len = table.shape[0]
    blk_rank = lax.axis_index("blk")
    fused_round = seg_count == 2 and owners_count >= 2 and owners_count & (owners_count - 1) == 0
    if fused_round:
        piece_width = block_bins * 2 * seg_dev
        slab_width = 128
        slab = jnp.pad(table.astype(jnp.bfloat16), (0, sections * slab_width - table_len))
        keep = lax.dynamic_index_in_dim(whitened, seg_rank, axis=0, keepdims=False)
        other = lax.dynamic_index_in_dim(whitened, 1 - seg_rank, axis=0, keepdims=False)
        keep_flat = jnp.concatenate(
            [keep.reshape(sections, -1), slab.reshape(sections, slab_width)], axis=1
        )
        other_flat = other.reshape(sections, -1)
        first = owners_count // 2
        from_blk = lax.ppermute(
            keep_flat, "blk", [(source, source ^ first) for source in range(owners_count)]
        )
        from_seg = lax.ppermute(other_flat, "seg", [(0, 1), (1, 0)])
        diagonal = [
            (source * 2 + side, (source ^ first) * 2 + 1 - side)
            for source in range(owners_count)
            for side in range(2)
        ]
        from_diagonal = lax.ppermute(other_flat, ("blk", "seg"), diagonal)

        def interleave(mine_segs, their_segs, table_slab):
            lanes_in = 2 * seg_dev
            joined = jnp.concatenate(
                [
                    mine_segs.reshape(sections, block_bins, lanes_in),
                    their_segs.reshape(sections, block_bins, lanes_in),
                ],
                axis=2,
            ).reshape(sections, -1)
            return jnp.concatenate([joined, table_slab], axis=1)

        held = jnp.stack(
            [
                interleave(keep_flat[:, :piece_width], from_seg, keep_flat[:, piece_width:]),
                interleave(from_blk[:, :piece_width], from_diagonal, from_blk[:, piece_width:]),
            ],
            axis=0,
        )
        moved = gather_blocks(None, owners_count, blk_rank, held=held)
        halves = [moved[:, :, : 2 * piece_width]]
        table_part = moved[:, :, 2 * piece_width :]
        table_part = table_part.reshape(owners_count, -1)[:, :table_len]
        half_segs = all_segs
        chunk_segs = seg_dev
    else:
        pieces = [lax.dynamic_index_in_dim(whitened, seg_rank, axis=0, keepdims=False)]
        for shift in range(1, seg_count):
            outgoing = lax.dynamic_index_in_dim(
                whitened, (seg_rank + shift) % seg_count, axis=0, keepdims=False
            )
            pairs = [(source, (source + shift) % seg_count) for source in range(seg_count)]
            flat = outgoing.reshape(sections, -1)
            pieces.append(lax.ppermute(flat, "seg", pairs).reshape(outgoing.shape))
        local = jnp.stack(pieces, axis=3).reshape(sections, block_bins, -1)
        table_width = local.shape[-1]
        slab = jnp.pad(table.astype(jnp.bfloat16), (0, sections * table_width - table_len))
        carried = jnp.concatenate([local, slab.reshape(sections, 1, table_width)], axis=1)
        everything = gather_blocks(carried.reshape(sections, -1), owners_count, blk_rank)
        everything = everything.reshape(owners_count, sections, block_bins + 1, table_width)
        halves = [everything[:, :, :block_bins]]
        table_part = everything[:, :, block_bins].reshape(owners_count, -1)[:, :table_len]
        half_segs = all_segs
        chunk_segs = all_segs
    table_part = table_part.astype(jnp.int32).reshape(owners_count, owners_count, 2 * capacity)
    position_ids = jnp.arange(owners_count, dtype=jnp.int32)
    if owners_count & (owners_count - 1) == 0:
        source_of = blk_rank ^ position_ids
        unpermute = (source_of[:, None] == position_ids[None, :]).astype(jnp.int32)
        table_part = jnp.sum(unpermute[:, :, None, None] * table_part[None], axis=1)
    else:
        source_of = position_ids
    send_all = table_part[..., :capacity]
    recv_all = table_part[..., capacity:]
    rows_count = owners_count * OWN
    chans_count = owners_count * sections
    chosen = jnp.transpose(send_all, (1, 0, 2))
    valid = (chosen < sections) & (recv_all < OWN)
    source_ids = (blk_rank ^ position_ids if owners_count & (owners_count - 1) == 0 else position_ids)[None, :, None]
    owner_ids = jnp.arange(owners_count, dtype=jnp.int32)[:, None, None]
    channel = jnp.where(valid, source_ids * sections + chosen, -1).reshape(-1)
    target = jnp.where(valid, owner_ids * OWN + recv_all, -1).reshape(-1)
    row_hot = (target[:, None] == jnp.arange(rows_count, dtype=jnp.int32)[None, :]).astype(
        jnp.bfloat16
    )
    chan_hot = (channel[:, None] == jnp.arange(chans_count, dtype=jnp.int32)[None, :]).astype(
        jnp.bfloat16
    )
    selector = jnp.einsum(
        "er,ec->rc", row_hot, chan_hot, preferred_element_type=jnp.float32
    ).astype(jnp.bfloat16)
    selector = selector.reshape(rows_count, owners_count, sections)
    cross = None
    for half in halves:
        data = half.reshape(owners_count, sections, block_bins, 2 * half_segs)
        routed = jnp.einsum(
            "rsc,scbq->brq", selector, data, preferred_element_type=jnp.float32
        ).astype(jnp.bfloat16)
        own = lax.dynamic_slice_in_dim(routed, blk_rank * OWN, OWN, axis=1)
        own_parts = own.reshape(own.shape[:-1] + (-1, 2, chunk_segs))
        rotated = jnp.stack([own_parts[..., 1, :], -own_parts[..., 0, :]], axis=-2)
        rotated = rotated.reshape(own.shape)
        lhs = jnp.concatenate([own, rotated], axis=1)
        part = jnp.einsum("bpq,bjq->bpj", lhs, routed, preferred_element_type=jnp.float32)
        cross = part if cross is None else cross + part
    cross = cross.reshape(block_bins, 2, OWN, rows_count)
    return jnp.transpose(cross, (1, 0, 2, 3)) / jnp.float32(all_segs)


def solution(mesh):
    placed = (
        P(("groups", "blk"), "seg", "freq"),
        P(),
        P(("groups", "blk"), None, None),
        P(("groups", "blk"), None, None),
    )
    return jax.shard_map(
        per_device,
        mesh=mesh,
        in_specs=placed,
        out_specs=P(None, ("seg", "freq"), ("groups", "blk"), None),
        check_vma=False,
    )
```

```python
import math

import jax
import jax.numpy as jnp
from jax import lax
from jax.experimental import pallas as pl
from jax.experimental.pallas import tpu as pltpu
from jax.sharding import PartitionSpec as P

SEG_LEN = 16384
BINS = 256
BAND_LO = 128
HW = 4
OWN = 16


WHITEN_FLOOR = 0.25
TWO_PI = 2.0 * math.pi


def swapped(value, axis, distance):
    mask = 2**distance
    pairs = [(source, source ^ mask) for source in range(lax.axis_size(axis))]
    return lax.ppermute(value, axis, pairs)


def dft_tables(band_index, sample_index):
    wavenumber = BAND_LO + band_index
    phase_int = wavenumber[:, None] * sample_index[None, :] % SEG_LEN
    angles = phase_int.astype(jnp.float32) * (TWO_PI / SEG_LEN)
    norm_scale = 1.0 / math.sqrt(SEG_LEN)
    cos_part = (jnp.cos(angles) * norm_scale).astype(jnp.bfloat16)
    sin_part = (-jnp.sin(angles) * norm_scale).astype(jnp.bfloat16)
    return (cos_part, sin_part)


def dft_tables_fast(band_index, first_sample, count):
    lanes = 128
    wavenumber = BAND_LO + band_index
    coarse = (first_sample + lanes * jnp.arange(count // lanes, dtype=jnp.int32))
    fine = jnp.arange(lanes, dtype=jnp.int32)
    coarse_angle = (wavenumber[:, None] * coarse[None, :] % SEG_LEN).astype(jnp.float32) * (
        TWO_PI / SEG_LEN
    )
    fine_angle = (wavenumber[:, None] * fine[None, :] % SEG_LEN).astype(jnp.float32) * (
        TWO_PI / SEG_LEN
    )
    cos_a = jnp.cos(coarse_angle)[:, :, None]
    sin_a = jnp.sin(coarse_angle)[:, :, None]
    cos_b = jnp.cos(fine_angle)[:, None, :]
    sin_b = jnp.sin(fine_angle)[:, None, :]
    norm_scale = 1.0 / math.sqrt(SEG_LEN)
    cos_sum = cos_a * cos_b - sin_a * sin_b
    sin_sum = sin_a * cos_b + cos_a * sin_b
    rows = band_index.shape[0]
    cos_part = (cos_sum * norm_scale).astype(jnp.bfloat16).reshape(rows, count)
    sin_part = (-sin_sum * norm_scale).astype(jnp.bfloat16).reshape(rows, count)
    return (cos_part, sin_part)


def response(band_index, taps):
    wavenumber = BAND_LO + band_index
    lag_index = jnp.arange(taps.shape[0], dtype=jnp.int32)
    phase_int = wavenumber[:, None] * lag_index[None, :] % SEG_LEN
    angles = phase_int.astype(jnp.float32) * (TWO_PI / SEG_LEN)
    real_part = jnp.dot(jnp.cos(angles), taps, precision=lax.Precision.HIGHEST)
    imag_part = jnp.dot(-jnp.sin(angles), taps, precision=lax.Precision.HIGHEST)
    return (real_part, imag_part)


def dft_kernel(rec_ref, cos_a_ref, nsin_a_ref, cos_b_ref, sin_b_ref, re_ref, im_ref):
    step = pl.program_id(0)
    lanes = cos_b_ref.shape[0]
    group = 8
    groups = rec_ref.shape[1] // (group * lanes)

    @pl.when(step == 0)
    def _():
        re_ref[...] = jnp.zeros_like(re_ref)
        im_ref[...] = jnp.zeros_like(im_ref)

    def one_group(index, carry):
        row = pl.multiple_of((step * groups + index) * group, group)
        cos_a = cos_a_ref[pl.ds(row, group), :]
        nsin_a = nsin_a_ref[pl.ds(row, group), :]
        cos_b = cos_b_ref[...]
        sin_b = sin_b_ref[...]
        for pair in range(group // 2):
            cos_parts = []
            sin_parts = []
            for half in range(2):
                at = 2 * pair + half
                ca = cos_a[at : at + 1]
                sa = nsin_a[at : at + 1]
                cos_parts.append(ca * cos_b + sa * sin_b)
                sin_parts.append(sa * cos_b - ca * sin_b)
            cos_tile = jnp.concatenate(cos_parts, axis=0).astype(jnp.bfloat16)
            sin_tile = jnp.concatenate(sin_parts, axis=0).astype(jnp.bfloat16)
            first = pl.multiple_of((index * group + 2 * pair) * lanes, 2 * lanes)
            rec = rec_ref[:, pl.ds(first, 2 * lanes)]
            re_ref[...] += jnp.dot(rec, cos_tile, preferred_element_type=jnp.float32)
            im_ref[...] += jnp.dot(rec, sin_tile, preferred_element_type=jnp.float32)
        return carry

    lax.fori_loop(0, groups, one_group, 0)


def dft_fused(records, band_index, first_sample):
    lanes = 128
    chunk = 2048
    count = records.shape[1]
    wavenumber = BAND_LO + band_index
    norm_scale = 1.0 / math.sqrt(SEG_LEN)

    def cos_sin(steps):
        angle = (steps[:, None] * wavenumber[None, :] % SEG_LEN).astype(jnp.float32) * (
            TWO_PI / SEG_LEN
        )
        return jnp.cos(angle), jnp.sin(angle)

    def combined(outer_steps, inner_steps):
        outer_cos, outer_sin = cos_sin(outer_steps)
        inner_cos, inner_sin = cos_sin(inner_steps)
        width = wavenumber.shape[0]
        cos_sum = outer_cos[:, None] * inner_cos[None] - outer_sin[:, None] * inner_sin[None]
        sin_sum = outer_sin[:, None] * inner_cos[None] + outer_cos[:, None] * inner_sin[None]
        return cos_sum.reshape(-1, width), sin_sum.reshape(-1, width)

    coarse_count = count // lanes
    coarse_outer = coarse_count // 8 if coarse_count % 8 == 0 else 1
    coarse_inner = coarse_count // coarse_outer
    cos_a, sin_a = combined(
        first_sample + lanes * coarse_inner * jnp.arange(coarse_outer, dtype=jnp.int32),
        lanes * jnp.arange(coarse_inner, dtype=jnp.int32),
    )
    nsin_a = -sin_a
    cos_b, sin_b = combined(
        16 * jnp.arange(lanes // 16, dtype=jnp.int32), jnp.arange(16, dtype=jnp.int32)
    )
    cos_b = cos_b * norm_scale
    sin_b = sin_b * norm_scale
    rows = records.shape[0]
    bins = band_index.shape[0]
    full = lambda step: (0, 0)
    return pl.pallas_call(
        dft_kernel,
        grid=(count // chunk,),
        in_specs=[
            pl.BlockSpec((rows, chunk), lambda step: (0, step)),
            pl.BlockSpec(cos_a.shape, full),
            pl.BlockSpec(nsin_a.shape, full),
            pl.BlockSpec(cos_b.shape, full),
            pl.BlockSpec(sin_b.shape, full),
        ],
        out_specs=[pl.BlockSpec((rows, bins), full), pl.BlockSpec((rows, bins), full)],
        out_shape=[
            jax.ShapeDtypeStruct((rows, bins), jnp.float32),
            jax.ShapeDtypeStruct((rows, bins), jnp.float32),
        ],
        compiler_params=pltpu.CompilerParams(dimension_semantics=("arbitrary",)),
    )(records, cos_a, nsin_a, cos_b, sin_b)


def gather_blocks(carried, count, rank, held=None):
    if count & (count - 1) != 0:
        return lax.all_gather(carried, "blk", axis=0, tiled=False)
    masks = []
    step = count // 2
    while step >= 1:
        masks.append(step)
        step //= 2
    if not masks:
        return carried[None]
    first = masks[0]
    rest = masks[1:]
    if held is None:
        pairs = [(source, source ^ first) for source in range(count)]
        held = jnp.stack([carried, lax.ppermute(carried, "blk", pairs)], axis=0)
    split = (held.shape[1] + 1) // 2
    halves = [held[:, :split], held[:, split:]]
    orders = [rest, rest[::-1]]
    results = []
    for part, order in zip(halves, orders):
        done = [first]
        for mask in order:
            pairs = [(source, source ^ mask) for source in range(count)]
            arrived = lax.ppermute(part, "blk", pairs)
            done.append(mask)
            axis = sorted(done, reverse=True).index(mask)
            part = jnp.stack([part, arrived], axis=axis)
        results.append(part.reshape((count,) + part.shape[len(masks):]))
    return jnp.concatenate(results, axis=1)


def per_device(raw, taps, send_list, recv_row):
    owners_count = lax.axis_size("blk")
    seg_count = lax.axis_size("seg")
    freq_count = lax.axis_size("freq")
    freq_rank = lax.axis_index("freq")
    sections, seg_dev, half_len = raw.shape
    records = raw.reshape(sections * seg_dev, half_len)
    device_bins = BINS // freq_count
    block_bins = device_bins // seg_count
    capacity = send_list.shape[2]

    def band_of(row_ids):
        owner_core = row_ids // device_bins
        local_row = row_ids % device_bins
        return (
            local_row // block_bins * freq_count + owner_core
        ) * block_bins + local_row % block_bins

    band_rows = band_of(jnp.arange(device_bins * freq_count, dtype=jnp.int32))
    real_t, imag_t = dft_fused(records, band_rows, freq_rank * half_len)
    real_all = real_t.T
    imag_all = imag_t.T
    blocks = jnp.stack([real_all, imag_all], axis=1)
    blocks = blocks.reshape(freq_count, device_bins, 2, records.shape[0])
    if freq_count == 2:
        kept = lax.dynamic_index_in_dim(blocks, freq_rank, axis=0, keepdims=False)
        sent = lax.dynamic_index_in_dim(blocks, 1 - freq_rank, axis=0, keepdims=False)
        kept_blocks = kept.reshape(seg_count, block_bins, 2, -1)
        sent_blocks = sent.reshape(seg_count, block_bins, 2, -1)
        own_edges = jnp.concatenate(
            [kept_blocks[:, :HW], kept_blocks[:, block_bins - HW :]], axis=1
        ).reshape(seg_count * 2 * HW, 2, -1)
        message = jnp.concatenate([sent, own_edges], axis=0)
        arrived = swapped(message, "freq", 0)
        spectra = kept + arrived[:device_bins]
        their_edges = jnp.concatenate(
            [sent_blocks[:, :HW], sent_blocks[:, block_bins - HW :]], axis=1
        ).reshape(seg_count * 2 * HW, 2, -1)
        edge_spectra = (their_edges + arrived[device_bins:]).reshape(seg_count, 2, HW, 2, -1)
        partner = jnp.transpose(
            jnp.sqrt(
                edge_spectra[..., 0, :] * edge_spectra[..., 0, :]
                + edge_spectra[..., 1, :] * edge_spectra[..., 1, :]
                + 1e-06
            ),
            (1, 0, 2, 3),
        )
    else:
        spectra = lax.psum_scatter(
            blocks.reshape(device_bins * freq_count, 2, records.shape[0]),
            "freq",
            scatter_dimension=0,
            tiled=True,
        )
    real_part = spectra[:, 0]
    imag_part = spectra[:, 1]
    amplitude = jnp.sqrt(real_part * real_part + imag_part * imag_part + 1e-06)
    amp_blocks = amplitude.reshape(seg_count, block_bins, -1)
    if freq_count != 2:
        band_rims = jnp.stack([amp_blocks[:, :HW], amp_blocks[:, block_bins - HW :]])
        partner = swapped(band_rims, "freq", 0)
    zero_rim = jnp.zeros_like(partner[1][:1])
    right_prev = jnp.concatenate([zero_rim, partner[1][:-1]], axis=0)
    left_next = jnp.concatenate([partner[0][1:], zero_rim], axis=0)
    first_core = freq_rank == 0
    lower_rim = jnp.where(first_core, right_prev, partner[1])
    upper_rim = jnp.where(first_core, partner[0], left_next)
    padded = jnp.concatenate([lower_rim, amp_blocks, upper_rim], axis=1)
    window_sum = padded[:, 0:block_bins]
    for offset_step in range(1, 2 * HW + 1):
        window_sum = window_sum + padded[:, offset_step : offset_step + block_bins]
    span_ids = jnp.arange(seg_count, dtype=jnp.int32)[:, None]
    offsets = jnp.arange(block_bins, dtype=jnp.int32)[None, :]
    position = (span_ids * freq_count + freq_rank) * block_bins + offsets
    counted = jnp.minimum(position + HW, BINS - 1) - jnp.maximum(position - HW, 0) + 1
    smooth = window_sum / counted.astype(jnp.float32)[:, :, None]
    divisor = jnp.maximum(smooth, WHITEN_FLOOR).reshape(device_bins, -1)
    local_bins = freq_rank * device_bins + jnp.arange(device_bins, dtype=jnp.int32)
    response_re, response_im = response(band_of(local_bins), taps)
    scaled_re = real_part / divisor
    scaled_im = imag_part / divisor
    white_re = scaled_re * response_re[:, None] - scaled_im * response_im[:, None]
    white_im = scaled_re * response_im[:, None] + scaled_im * response_re[:, None]
    whitened = jnp.stack([white_re, white_im], axis=1).astype(jnp.bfloat16)
    whitened = whitened.reshape(seg_count, block_bins, 2, sections, seg_dev)
    whitened = jnp.transpose(whitened, (0, 3, 1, 2, 4))
    seg_rank = lax.axis_index("seg")
    all_segs = seg_dev * seg_count
    table = jnp.concatenate([send_list[0], recv_row[0]], axis=1).reshape(-1)
    table_len = table.shape[0]
    blk_rank = lax.axis_index("blk")
    fused_round = seg_count == 2 and owners_count >= 2 and owners_count & (owners_count - 1) == 0
    if fused_round:
        piece_width = block_bins * 2 * seg_dev
        slab_width = 128
        slab = jnp.pad(table.astype(jnp.bfloat16), (0, sections * slab_width - table_len))
        keep = lax.dynamic_index_in_dim(whitened, seg_rank, axis=0, keepdims=False)
        other = lax.dynamic_index_in_dim(whitened, 1 - seg_rank, axis=0, keepdims=False)
        keep_flat = jnp.concatenate(
            [keep.reshape(sections, -1), slab.reshape(sections, slab_width)], axis=1
        )
        other_flat = other.reshape(sections, -1)
        first = owners_count // 2
        from_blk = lax.ppermute(
            keep_flat, "blk", [(source, source ^ first) for source in range(owners_count)]
        )
        from_seg = lax.ppermute(other_flat, "seg", [(0, 1), (1, 0)])
        diagonal = [
            (source * 2 + side, (source ^ first) * 2 + 1 - side)
            for source in range(owners_count)
            for side in range(2)
        ]
        from_diagonal = lax.ppermute(other_flat, ("blk", "seg"), diagonal)

        def interleave(mine_segs, their_segs, table_slab):
            lanes_in = 2 * seg_dev
            joined = jnp.concatenate(
                [
                    mine_segs.reshape(sections, block_bins, lanes_in),
                    their_segs.reshape(sections, block_bins, lanes_in),
                ],
                axis=2,
            ).reshape(sections, -1)
            return jnp.concatenate([joined, table_slab], axis=1)

        held = jnp.stack(
            [
                interleave(keep_flat[:, :piece_width], from_seg, keep_flat[:, piece_width:]),
                interleave(from_blk[:, :piece_width], from_diagonal, from_blk[:, piece_width:]),
            ],
            axis=0,
        )
        moved = gather_blocks(None, owners_count, blk_rank, held=held)
        halves = [moved[:, :, : 2 * piece_width]]
        table_part = moved[:, :, 2 * piece_width :]
        table_part = table_part.reshape(owners_count, -1)[:, :table_len]
        half_segs = all_segs
        chunk_segs = seg_dev
    else:
        pieces = [lax.dynamic_index_in_dim(whitened, seg_rank, axis=0, keepdims=False)]
        for shift in range(1, seg_count):
            outgoing = lax.dynamic_index_in_dim(
                whitened, (seg_rank + shift) % seg_count, axis=0, keepdims=False
            )
            pairs = [(source, (source + shift) % seg_count) for source in range(seg_count)]
            flat = outgoing.reshape(sections, -1)
            pieces.append(lax.ppermute(flat, "seg", pairs).reshape(outgoing.shape))
        local = jnp.stack(pieces, axis=3).reshape(sections, block_bins, -1)
        table_width = local.shape[-1]
        slab = jnp.pad(table.astype(jnp.bfloat16), (0, sections * table_width - table_len))
        carried = jnp.concatenate([local, slab.reshape(sections, 1, table_width)], axis=1)
        everything = gather_blocks(carried.reshape(sections, -1), owners_count, blk_rank)
        everything = everything.reshape(owners_count, sections, block_bins + 1, table_width)
        halves = [everything[:, :, :block_bins]]
        table_part = everything[:, :, block_bins].reshape(owners_count, -1)[:, :table_len]
        half_segs = all_segs
        chunk_segs = all_segs
    table_part = table_part.astype(jnp.int32).reshape(owners_count, owners_count, 2 * capacity)
    position_ids = jnp.arange(owners_count, dtype=jnp.int32)
    if owners_count & (owners_count - 1) == 0:
        source_of = blk_rank ^ position_ids
        unpermute = (source_of[:, None] == position_ids[None, :]).astype(jnp.int32)
        table_part = jnp.sum(unpermute[:, :, None, None] * table_part[None], axis=1)
    else:
        source_of = position_ids
    send_all = table_part[..., :capacity]
    recv_all = table_part[..., capacity:]
    rows_count = owners_count * OWN
    chans_count = owners_count * sections
    chosen = jnp.transpose(send_all, (1, 0, 2))
    valid = (chosen < sections) & (recv_all < OWN)
    source_ids = (blk_rank ^ position_ids if owners_count & (owners_count - 1) == 0 else position_ids)[None, :, None]
    owner_ids = jnp.arange(owners_count, dtype=jnp.int32)[:, None, None]
    channel = jnp.where(valid, source_ids * sections + chosen, -1).reshape(-1)
    target = jnp.where(valid, owner_ids * OWN + recv_all, -1).reshape(-1)
    row_hot = (target[:, None] == jnp.arange(rows_count, dtype=jnp.int32)[None, :]).astype(
        jnp.bfloat16
    )
    chan_hot = (channel[:, None] == jnp.arange(chans_count, dtype=jnp.int32)[None, :]).astype(
        jnp.bfloat16
    )
    selector = jnp.einsum(
        "er,ec->rc", row_hot, chan_hot, preferred_element_type=jnp.float32
    ).astype(jnp.bfloat16)
    selector = selector.reshape(rows_count, owners_count, sections)
    cross = None
    for half in halves:
        data = half.reshape(owners_count, sections, block_bins, 2 * half_segs)
        routed = jnp.einsum(
            "rsc,scbq->brq", selector, data, preferred_element_type=jnp.float32
        ).astype(jnp.bfloat16)
        own = lax.dynamic_slice_in_dim(routed, blk_rank * OWN, OWN, axis=1)
        own_parts = own.reshape(own.shape[:-1] + (-1, 2, chunk_segs))
        rotated = jnp.stack([own_parts[..., 1, :], -own_parts[..., 0, :]], axis=-2)
        rotated = rotated.reshape(own.shape)
        lhs = jnp.concatenate([own, rotated], axis=1)
        part = jnp.einsum("bpq,bjq->bpj", lhs, routed, preferred_element_type=jnp.float32)
        cross = part if cross is None else cross + part
    cross = cross.reshape(block_bins, 2, OWN, rows_count)
    return jnp.transpose(cross, (1, 0, 2, 3)) / jnp.float32(all_segs)


def solution(mesh):
    placed = (
        P(("groups", "blk"), "seg", "freq"),
        P(),
        P(("groups", "blk"), None, None),
        P(("groups", "blk"), None, None),
    )
    return jax.shard_map(
        per_device,
        mesh=mesh,
        in_specs=placed,
        out_specs=P(None, ("seg", "freq"), ("groups", "blk"), None),
        check_vma=False,
    )
```

```python
import math

import jax
import jax.numpy as jnp
from jax import lax
from jax.experimental import pallas as pl
from jax.experimental.pallas import tpu as pltpu
from jax.sharding import PartitionSpec as P

SEG_LEN = 16384
BINS = 256
BAND_LO = 128
HW = 4
OWN = 16


WHITEN_FLOOR = 0.25
TWO_PI = 2.0 * math.pi


def swapped(value, axis, distance):
    mask = 2**distance
    pairs = [(source, source ^ mask) for source in range(lax.axis_size(axis))]
    return lax.ppermute(value, axis, pairs)


def dft_tables(band_index, sample_index):
    wavenumber = BAND_LO + band_index
    phase_int = wavenumber[:, None] * sample_index[None, :] % SEG_LEN
    angles = phase_int.astype(jnp.float32) * (TWO_PI / SEG_LEN)
    norm_scale = 1.0 / math.sqrt(SEG_LEN)
    cos_part = (jnp.cos(angles) * norm_scale).astype(jnp.bfloat16)
    sin_part = (-jnp.sin(angles) * norm_scale).astype(jnp.bfloat16)
    return (cos_part, sin_part)


def dft_tables_fast(band_index, first_sample, count):
    lanes = 128
    wavenumber = BAND_LO + band_index
    coarse = (first_sample + lanes * jnp.arange(count // lanes, dtype=jnp.int32))
    fine = jnp.arange(lanes, dtype=jnp.int32)
    coarse_angle = (wavenumber[:, None] * coarse[None, :] % SEG_LEN).astype(jnp.float32) * (
        TWO_PI / SEG_LEN
    )
    fine_angle = (wavenumber[:, None] * fine[None, :] % SEG_LEN).astype(jnp.float32) * (
        TWO_PI / SEG_LEN
    )
    cos_a = jnp.cos(coarse_angle)[:, :, None]
    sin_a = jnp.sin(coarse_angle)[:, :, None]
    cos_b = jnp.cos(fine_angle)[:, None, :]
    sin_b = jnp.sin(fine_angle)[:, None, :]
    norm_scale = 1.0 / math.sqrt(SEG_LEN)
    cos_sum = cos_a * cos_b - sin_a * sin_b
    sin_sum = sin_a * cos_b + cos_a * sin_b
    rows = band_index.shape[0]
    cos_part = (cos_sum * norm_scale).astype(jnp.bfloat16).reshape(rows, count)
    sin_part = (-sin_sum * norm_scale).astype(jnp.bfloat16).reshape(rows, count)
    return (cos_part, sin_part)


def response(band_index, taps):
    wavenumber = BAND_LO + band_index
    lag_index = jnp.arange(taps.shape[0], dtype=jnp.int32)
    phase_int = wavenumber[:, None] * lag_index[None, :] % SEG_LEN
    angles = phase_int.astype(jnp.float32) * (TWO_PI / SEG_LEN)
    real_part = jnp.dot(jnp.cos(angles), taps, precision=lax.Precision.HIGHEST)
    imag_part = jnp.dot(-jnp.sin(angles), taps, precision=lax.Precision.HIGHEST)
    return (real_part, imag_part)


def dft_kernel(rec_ref, cos_a_ref, nsin_a_ref, cos_b_ref, sin_b_ref, re_ref, im_ref):
    step = pl.program_id(0)
    lanes = cos_b_ref.shape[0]
    group = 8
    groups = rec_ref.shape[1] // (group * lanes)

    @pl.when(step == 0)
    def _():
        re_ref[...] = jnp.zeros_like(re_ref)
        im_ref[...] = jnp.zeros_like(im_ref)

    def one_group(index, carry):
        row = pl.multiple_of((step * groups + index) * group, group)
        cos_a = cos_a_ref[pl.ds(row, group), :]
        nsin_a = nsin_a_ref[pl.ds(row, group), :]
        cos_b = cos_b_ref[...]
        sin_b = sin_b_ref[...]
        for pair in range(group // 2):
            cos_parts = []
            sin_parts = []
            for half in range(2):
                at = 2 * pair + half
                ca = cos_a[at : at + 1]
                sa = nsin_a[at : at + 1]
                cos_parts.append(ca * cos_b + sa * sin_b)
                sin_parts.append(sa * cos_b - ca * sin_b)
            cos_tile = jnp.concatenate(cos_parts, axis=0).astype(jnp.bfloat16)
            sin_tile = jnp.concatenate(sin_parts, axis=0).astype(jnp.bfloat16)
            first = pl.multiple_of((index * group + 2 * pair) * lanes, 2 * lanes)
            rec = rec_ref[:, pl.ds(first, 2 * lanes)]
            re_ref[...] += jnp.dot(rec, cos_tile, preferred_element_type=jnp.float32)
            im_ref[...] += jnp.dot(rec, sin_tile, preferred_element_type=jnp.float32)
        return carry

    lax.fori_loop(0, groups, one_group, 0)


def dft_fused(records, band_index, first_sample):
    lanes = 128
    chunk = 2048
    count = records.shape[1]
    wavenumber = BAND_LO + band_index
    norm_scale = 1.0 / math.sqrt(SEG_LEN)

    def cos_sin(steps):
        angle = (steps[:, None] * wavenumber[None, :] % SEG_LEN).astype(jnp.float32) * (
            TWO_PI / SEG_LEN
        )
        return jnp.cos(angle), jnp.sin(angle)

    def combined(outer_steps, inner_steps):
        outer_cos, outer_sin, inner_cos, inner_sin = lax.optimization_barrier(
            cos_sin(outer_steps) + cos_sin(inner_steps)
        )
        width = wavenumber.shape[0]
        cos_sum = outer_cos[:, None] * inner_cos[None] - outer_sin[:, None] * inner_sin[None]
        sin_sum = outer_sin[:, None] * inner_cos[None] + outer_cos[:, None] * inner_sin[None]
        return cos_sum.reshape(-1, width), sin_sum.reshape(-1, width)

    coarse_count = count // lanes
    coarse_outer = coarse_count // 8 if coarse_count % 8 == 0 else 1
    coarse_inner = coarse_count // coarse_outer
    cos_a, sin_a = combined(
        first_sample + lanes * coarse_inner * jnp.arange(coarse_outer, dtype=jnp.int32),
        lanes * jnp.arange(coarse_inner, dtype=jnp.int32),
    )
    nsin_a = -sin_a
    cos_b, sin_b = combined(
        16 * jnp.arange(lanes // 16, dtype=jnp.int32), jnp.arange(16, dtype=jnp.int32)
    )
    cos_b = cos_b * norm_scale
    sin_b = sin_b * norm_scale
    rows = records.shape[0]
    bins = band_index.shape[0]
    full = lambda step: (0, 0)
    return pl.pallas_call(
        dft_kernel,
        grid=(count // chunk,),
        in_specs=[
            pl.BlockSpec((rows, chunk), lambda step: (0, step)),
            pl.BlockSpec(cos_a.shape, full),
            pl.BlockSpec(nsin_a.shape, full),
            pl.BlockSpec(cos_b.shape, full),
            pl.BlockSpec(sin_b.shape, full),
        ],
        out_specs=[pl.BlockSpec((rows, bins), full), pl.BlockSpec((rows, bins), full)],
        out_shape=[
            jax.ShapeDtypeStruct((rows, bins), jnp.float32),
            jax.ShapeDtypeStruct((rows, bins), jnp.float32),
        ],
        compiler_params=pltpu.CompilerParams(dimension_semantics=("arbitrary",)),
    )(records, cos_a, nsin_a, cos_b, sin_b)


def gather_blocks(carried, count, rank, held=None):
    if count & (count - 1) != 0:
        return lax.all_gather(carried, "blk", axis=0, tiled=False)
    masks = []
    step = count // 2
    while step >= 1:
        masks.append(step)
        step //= 2
    if not masks:
        return carried[None]
    first = masks[0]
    rest = masks[1:]
    if held is None:
        pairs = [(source, source ^ first) for source in range(count)]
        held = jnp.stack([carried, lax.ppermute(carried, "blk", pairs)], axis=0)
    split = (held.shape[1] + 1) // 2
    halves = [held[:, :split], held[:, split:]]
    orders = [rest, rest[::-1]]
    results = []
    for part, order in zip(halves, orders):
        done = [first]
        for mask in order:
            pairs = [(source, source ^ mask) for source in range(count)]
            arrived = lax.ppermute(part, "blk", pairs)
            done.append(mask)
            axis = sorted(done, reverse=True).index(mask)
            part = jnp.stack([part, arrived], axis=axis)
        results.append(part.reshape((count,) + part.shape[len(masks):]))
    return jnp.concatenate(results, axis=1)


def per_device(raw, taps, send_list, recv_row):
    owners_count = lax.axis_size("blk")
    seg_count = lax.axis_size("seg")
    freq_count = lax.axis_size("freq")
    freq_rank = lax.axis_index("freq")
    sections, seg_dev, half_len = raw.shape
    records = raw.reshape(sections * seg_dev, half_len)
    device_bins = BINS // freq_count
    block_bins = device_bins // seg_count
    capacity = send_list.shape[2]

    def band_of(row_ids):
        owner_core = row_ids // device_bins
        local_row = row_ids % device_bins
        return (
            local_row // block_bins * freq_count + owner_core
        ) * block_bins + local_row % block_bins

    band_rows = band_of(jnp.arange(device_bins * freq_count, dtype=jnp.int32))
    real_t, imag_t = dft_fused(records, band_rows, freq_rank * half_len)
    real_all = real_t.T
    imag_all = imag_t.T
    blocks = jnp.stack([real_all, imag_all], axis=1)
    blocks = blocks.reshape(freq_count, device_bins, 2, records.shape[0])
    if freq_count == 2:
        kept = jnp.where(freq_rank == 0, blocks[0], blocks[1])
        sent = jnp.where(freq_rank == 0, blocks[1], blocks[0])
        kept_blocks = kept.reshape(seg_count, block_bins, 2, -1)
        sent_blocks = sent.reshape(seg_count, block_bins, 2, -1)
        own_edges = jnp.concatenate(
            [kept_blocks[:, :HW], kept_blocks[:, block_bins - HW :]], axis=1
        ).reshape(seg_count * 2 * HW, 2, -1)
        message = jnp.concatenate([sent, own_edges], axis=0)
        arrived = swapped(message, "freq", 0)
        spectra = kept + arrived[:device_bins]
        their_edges = jnp.concatenate(
            [sent_blocks[:, :HW], sent_blocks[:, block_bins - HW :]], axis=1
        ).reshape(seg_count * 2 * HW, 2, -1)
        edge_spectra = (their_edges + arrived[device_bins:]).reshape(seg_count, 2, HW, 2, -1)
        partner = jnp.transpose(
            jnp.sqrt(
                edge_spectra[..., 0, :] * edge_spectra[..., 0, :]
                + edge_spectra[..., 1, :] * edge_spectra[..., 1, :]
                + 1e-06
            ),
            (1, 0, 2, 3),
        )
    else:
        spectra = lax.psum_scatter(
            blocks.reshape(device_bins * freq_count, 2, records.shape[0]),
            "freq",
            scatter_dimension=0,
            tiled=True,
        )
    real_part = spectra[:, 0]
    imag_part = spectra[:, 1]
    amplitude = jnp.sqrt(real_part * real_part + imag_part * imag_part + 1e-06)
    amp_blocks = amplitude.reshape(seg_count, block_bins, -1)
    if freq_count != 2:
        band_rims = jnp.stack([amp_blocks[:, :HW], amp_blocks[:, block_bins - HW :]])
        partner = swapped(band_rims, "freq", 0)
    zero_rim = jnp.zeros_like(partner[1][:1])
    right_prev = jnp.concatenate([zero_rim, partner[1][:-1]], axis=0)
    left_next = jnp.concatenate([partner[0][1:], zero_rim], axis=0)
    first_core = freq_rank == 0
    lower_rim = jnp.where(first_core, right_prev, partner[1])
    upper_rim = jnp.where(first_core, partner[0], left_next)
    padded = jnp.concatenate([lower_rim, amp_blocks, upper_rim], axis=1)
    window_sum = padded[:, 0:block_bins]
    for offset_step in range(1, 2 * HW + 1):
        window_sum = window_sum + padded[:, offset_step : offset_step + block_bins]
    span_ids = jnp.arange(seg_count, dtype=jnp.int32)[:, None]
    offsets = jnp.arange(block_bins, dtype=jnp.int32)[None, :]
    position = (span_ids * freq_count + freq_rank) * block_bins + offsets
    counted = jnp.minimum(position + HW, BINS - 1) - jnp.maximum(position - HW, 0) + 1
    smooth = window_sum / counted.astype(jnp.float32)[:, :, None]
    divisor = jnp.maximum(smooth, WHITEN_FLOOR).reshape(device_bins, -1)
    local_bins = freq_rank * device_bins + jnp.arange(device_bins, dtype=jnp.int32)
    response_re, response_im = response(band_of(local_bins), taps)
    scaled_re = real_part / divisor
    scaled_im = imag_part / divisor
    white_re = scaled_re * response_re[:, None] - scaled_im * response_im[:, None]
    white_im = scaled_re * response_im[:, None] + scaled_im * response_re[:, None]
    whitened = jnp.stack([white_re, white_im], axis=1).astype(jnp.bfloat16)
    whitened = whitened.reshape(seg_count, block_bins, 2, sections, seg_dev)
    whitened = jnp.transpose(whitened, (0, 3, 1, 2, 4))
    seg_rank = lax.axis_index("seg")
    all_segs = seg_dev * seg_count
    table = jnp.concatenate([send_list[0], recv_row[0]], axis=1).reshape(-1)
    table_len = table.shape[0]
    blk_rank = lax.axis_index("blk")
    fused_round = seg_count == 2 and owners_count >= 2 and owners_count & (owners_count - 1) == 0
    if fused_round:
        piece_width = block_bins * 2 * seg_dev
        slab_width = 128
        slab = jnp.pad(table.astype(jnp.bfloat16), (0, sections * slab_width - table_len))
        keep = lax.dynamic_index_in_dim(whitened, seg_rank, axis=0, keepdims=False)
        other = lax.dynamic_index_in_dim(whitened, 1 - seg_rank, axis=0, keepdims=False)
        keep_flat = jnp.concatenate(
            [keep.reshape(sections, -1), slab.reshape(sections, slab_width)], axis=1
        )
        other_flat = other.reshape(sections, -1)
        first = owners_count // 2
        from_blk = lax.ppermute(
            keep_flat, "blk", [(source, source ^ first) for source in range(owners_count)]
        )
        from_seg = lax.ppermute(other_flat, "seg", [(0, 1), (1, 0)])
        diagonal = [
            (source * 2 + side, (source ^ first) * 2 + 1 - side)
            for source in range(owners_count)
            for side in range(2)
        ]
        from_diagonal = lax.ppermute(other_flat, ("blk", "seg"), diagonal)

        def interleave(mine_segs, their_segs, table_slab):
            lanes_in = 2 * seg_dev
            joined = jnp.concatenate(
                [
                    mine_segs.reshape(sections, block_bins, lanes_in),
                    their_segs.reshape(sections, block_bins, lanes_in),
                ],
                axis=2,
            ).reshape(sections, -1)
            return jnp.concatenate([joined, table_slab], axis=1)

        held = jnp.stack(
            [
                interleave(keep_flat[:, :piece_width], from_seg, keep_flat[:, piece_width:]),
                interleave(from_blk[:, :piece_width], from_diagonal, from_blk[:, piece_width:]),
            ],
            axis=0,
        )
        moved = gather_blocks(None, owners_count, blk_rank, held=held)
        halves = [moved[:, :, : 2 * piece_width]]
        table_part = moved[:, :, 2 * piece_width :]
        table_part = table_part.reshape(owners_count, -1)[:, :table_len]
        half_segs = all_segs
        chunk_segs = seg_dev
    else:
        pieces = [lax.dynamic_index_in_dim(whitened, seg_rank, axis=0, keepdims=False)]
        for shift in range(1, seg_count):
            outgoing = lax.dynamic_index_in_dim(
                whitened, (seg_rank + shift) % seg_count, axis=0, keepdims=False
            )
            pairs = [(source, (source + shift) % seg_count) for source in range(seg_count)]
            flat = outgoing.reshape(sections, -1)
            pieces.append(lax.ppermute(flat, "seg", pairs).reshape(outgoing.shape))
        local = jnp.stack(pieces, axis=3).reshape(sections, block_bins, -1)
        table_width = local.shape[-1]
        slab = jnp.pad(table.astype(jnp.bfloat16), (0, sections * table_width - table_len))
        carried = jnp.concatenate([local, slab.reshape(sections, 1, table_width)], axis=1)
        everything = gather_blocks(carried.reshape(sections, -1), owners_count, blk_rank)
        everything = everything.reshape(owners_count, sections, block_bins + 1, table_width)
        halves = [everything[:, :, :block_bins]]
        table_part = everything[:, :, block_bins].reshape(owners_count, -1)[:, :table_len]
        half_segs = all_segs
        chunk_segs = all_segs
    table_part = table_part.astype(jnp.int32).reshape(owners_count, owners_count, 2 * capacity)
    position_ids = jnp.arange(owners_count, dtype=jnp.int32)
    if owners_count & (owners_count - 1) == 0:
        source_of = blk_rank ^ position_ids
        unpermute = (source_of[:, None] == position_ids[None, :]).astype(jnp.int32)
        table_part = jnp.sum(unpermute[:, :, None, None] * table_part[None], axis=1)
    else:
        source_of = position_ids
    send_all = table_part[..., :capacity]
    recv_all = table_part[..., capacity:]
    rows_count = owners_count * OWN
    chans_count = owners_count * sections
    chosen = jnp.transpose(send_all, (1, 0, 2))
    valid = (chosen < sections) & (recv_all < OWN)
    source_ids = (blk_rank ^ position_ids if owners_count & (owners_count - 1) == 0 else position_ids)[None, :, None]
    owner_ids = jnp.arange(owners_count, dtype=jnp.int32)[:, None, None]
    channel = jnp.where(valid, source_ids * sections + chosen, -1).reshape(-1)
    target = jnp.where(valid, owner_ids * OWN + recv_all, -1).reshape(-1)
    row_hot = (target[:, None] == jnp.arange(rows_count, dtype=jnp.int32)[None, :]).astype(
        jnp.bfloat16
    )
    chan_hot = (channel[:, None] == jnp.arange(chans_count, dtype=jnp.int32)[None, :]).astype(
        jnp.bfloat16
    )
    selector = jnp.einsum(
        "er,ec->rc", row_hot, chan_hot, preferred_element_type=jnp.float32
    ).astype(jnp.bfloat16)
    selector = selector.reshape(rows_count, owners_count, sections)
    cross = None
    for half in halves:
        data = half.reshape(owners_count, sections, block_bins, 2 * half_segs)
        routed = jnp.einsum(
            "rsc,scbq->brq", selector, data, preferred_element_type=jnp.float32
        ).astype(jnp.bfloat16)
        own = lax.dynamic_slice_in_dim(routed, blk_rank * OWN, OWN, axis=1)
        own_parts = own.reshape(own.shape[:-1] + (-1, 2, chunk_segs))
        rotated = jnp.stack([own_parts[..., 1, :], -own_parts[..., 0, :]], axis=-2)
        rotated = rotated.reshape(own.shape)
        lhs = jnp.concatenate([own, rotated], axis=1)
        part = jnp.einsum("bpq,bjq->bpj", lhs, routed, preferred_element_type=jnp.float32)
        cross = part if cross is None else cross + part
    cross = cross.reshape(block_bins, 2, OWN, rows_count)
    return jnp.transpose(cross, (1, 0, 2, 3)) / jnp.float32(all_segs)


def solution(mesh):
    placed = (
        P(("groups", "blk"), "seg", "freq"),
        P(),
        P(("groups", "blk"), None, None),
        P(("groups", "blk"), None, None),
    )
    return jax.shard_map(
        per_device,
        mesh=mesh,
        in_specs=placed,
        out_specs=P(None, ("seg", "freq"), ("groups", "blk"), None),
        check_vma=False,
    )
```

```python
import math

import jax
import jax.numpy as jnp
from jax import lax
from jax.experimental import pallas as pl
from jax.experimental.pallas import tpu as pltpu
from jax.sharding import PartitionSpec as P

SEG_LEN = 16384
BINS = 256
BAND_LO = 128
HW = 4
OWN = 16


WHITEN_FLOOR = 0.25
TWO_PI = 2.0 * math.pi


def swapped(value, axis, distance):
    mask = 2**distance
    pairs = [(source, source ^ mask) for source in range(lax.axis_size(axis))]
    return lax.ppermute(value, axis, pairs)


def dft_tables(band_index, sample_index):
    wavenumber = BAND_LO + band_index
    phase_int = wavenumber[:, None] * sample_index[None, :] % SEG_LEN
    angles = phase_int.astype(jnp.float32) * (TWO_PI / SEG_LEN)
    norm_scale = 1.0 / math.sqrt(SEG_LEN)
    cos_part = (jnp.cos(angles) * norm_scale).astype(jnp.bfloat16)
    sin_part = (-jnp.sin(angles) * norm_scale).astype(jnp.bfloat16)
    return (cos_part, sin_part)


def dft_tables_fast(band_index, first_sample, count):
    lanes = 128
    wavenumber = BAND_LO + band_index
    coarse = (first_sample + lanes * jnp.arange(count // lanes, dtype=jnp.int32))
    fine = jnp.arange(lanes, dtype=jnp.int32)
    coarse_angle = (wavenumber[:, None] * coarse[None, :] % SEG_LEN).astype(jnp.float32) * (
        TWO_PI / SEG_LEN
    )
    fine_angle = (wavenumber[:, None] * fine[None, :] % SEG_LEN).astype(jnp.float32) * (
        TWO_PI / SEG_LEN
    )
    cos_a = jnp.cos(coarse_angle)[:, :, None]
    sin_a = jnp.sin(coarse_angle)[:, :, None]
    cos_b = jnp.cos(fine_angle)[:, None, :]
    sin_b = jnp.sin(fine_angle)[:, None, :]
    norm_scale = 1.0 / math.sqrt(SEG_LEN)
    cos_sum = cos_a * cos_b - sin_a * sin_b
    sin_sum = sin_a * cos_b + cos_a * sin_b
    rows = band_index.shape[0]
    cos_part = (cos_sum * norm_scale).astype(jnp.bfloat16).reshape(rows, count)
    sin_part = (-sin_sum * norm_scale).astype(jnp.bfloat16).reshape(rows, count)
    return (cos_part, sin_part)


def response(band_index, taps):
    wavenumber = BAND_LO + band_index
    lag_index = jnp.arange(taps.shape[0], dtype=jnp.int32)
    phase_int = wavenumber[:, None] * lag_index[None, :] % SEG_LEN
    angles = phase_int.astype(jnp.float32) * (TWO_PI / SEG_LEN)
    real_part = jnp.dot(jnp.cos(angles), taps, precision=lax.Precision.HIGHEST)
    imag_part = jnp.dot(-jnp.sin(angles), taps, precision=lax.Precision.HIGHEST)
    return (real_part, imag_part)


def dft_kernel(rec_ref, cos_a_ref, nsin_a_ref, cos_b_ref, sin_b_ref, re_ref, im_ref):
    step = pl.program_id(0)
    lanes = cos_b_ref.shape[0]
    group = 8
    groups = rec_ref.shape[1] // (group * lanes)

    @pl.when(step == 0)
    def _():
        re_ref[...] = jnp.zeros_like(re_ref)
        im_ref[...] = jnp.zeros_like(im_ref)

    def one_group(index, carry):
        row = pl.multiple_of((step * groups + index) * group, group)
        cos_a = cos_a_ref[pl.ds(row, group), :]
        nsin_a = nsin_a_ref[pl.ds(row, group), :]
        cos_b = cos_b_ref[...]
        sin_b = sin_b_ref[...]
        for pair in range(group // 2):
            cos_parts = []
            sin_parts = []
            for half in range(2):
                at = 2 * pair + half
                ca = cos_a[at : at + 1]
                sa = nsin_a[at : at + 1]
                cos_parts.append(ca * cos_b + sa * sin_b)
                sin_parts.append(sa * cos_b - ca * sin_b)
            cos_tile = jnp.concatenate(cos_parts, axis=0).astype(jnp.bfloat16)
            sin_tile = jnp.concatenate(sin_parts, axis=0).astype(jnp.bfloat16)
            first = pl.multiple_of((index * group + 2 * pair) * lanes, 2 * lanes)
            rec = rec_ref[:, pl.ds(first, 2 * lanes)]
            re_ref[...] += jnp.dot(rec, cos_tile, preferred_element_type=jnp.float32)
            im_ref[...] += jnp.dot(rec, sin_tile, preferred_element_type=jnp.float32)
        return carry

    lax.fori_loop(0, groups, one_group, 0)


def dft_kernel_inline(rec_ref, oca_ref, osa_ref, ica_ref, isa_ref, ocb_ref, osb_ref, icb_ref, isb_ref,
                      re_ref, im_ref):
    step = pl.program_id(0)
    lanes = 128
    group = ica_ref.shape[0]
    groups = rec_ref.shape[1] // (group * lanes)
    norm_scale = 1.0 / math.sqrt(SEG_LEN)

    @pl.when(step == 0)
    def _():
        re_ref[...] = jnp.zeros_like(re_ref)
        im_ref[...] = jnp.zeros_like(im_ref)

    icb = icb_ref[...]
    isb = isb_ref[...]
    cos_rows = []
    sin_rows = []
    for outer in range(ocb_ref.shape[0]):
        ocb = ocb_ref[outer : outer + 1, :]
        osb = osb_ref[outer : outer + 1, :]
        cos_rows.append(ocb * icb - osb * isb)
        sin_rows.append(osb * icb + ocb * isb)
    cos_b = jnp.concatenate(cos_rows, axis=0) * norm_scale
    sin_b = jnp.concatenate(sin_rows, axis=0) * norm_scale
    ica = ica_ref[...]
    isa = isa_ref[...]

    def one_group(index, carry):
        outer = step * groups + index
        oca = oca_ref[outer]
        osa = osa_ref[outer]
        cos_a = oca * ica - osa * isa
        nsin_a = -(osa * ica + oca * isa)
        for pair in range(group // 2):
            cos_parts = []
            sin_parts = []
            for half in range(2):
                at = 2 * pair + half
                ca = cos_a[at : at + 1]
                sa = nsin_a[at : at + 1]
                cos_parts.append(ca * cos_b + sa * sin_b)
                sin_parts.append(sa * cos_b - ca * sin_b)
            cos_tile = jnp.concatenate(cos_parts, axis=0).astype(jnp.bfloat16)
            sin_tile = jnp.concatenate(sin_parts, axis=0).astype(jnp.bfloat16)
            first = pl.multiple_of((index * group + 2 * pair) * lanes, 2 * lanes)
            rec = rec_ref[:, pl.ds(first, 2 * lanes)]
            re_ref[...] += jnp.dot(rec, cos_tile, preferred_element_type=jnp.float32)
            im_ref[...] += jnp.dot(rec, sin_tile, preferred_element_type=jnp.float32)
        return carry

    lax.fori_loop(0, groups, one_group, 0)


def dft_fused(records, band_index, first_sample):
    lanes = 128
    chunk = 2048
    count = records.shape[1]
    wavenumber = BAND_LO + band_index
    norm_scale = 1.0 / math.sqrt(SEG_LEN)

    def cos_sin(steps):
        angle = (steps[:, None] * wavenumber[None, :] % SEG_LEN).astype(jnp.float32) * (
            TWO_PI / SEG_LEN
        )
        return jnp.cos(angle), jnp.sin(angle)

    def combined(outer_steps, inner_steps):
        outer_cos, outer_sin = cos_sin(outer_steps)
        inner_cos, inner_sin = cos_sin(inner_steps)
        width = wavenumber.shape[0]
        cos_sum = outer_cos[:, None] * inner_cos[None] - outer_sin[:, None] * inner_sin[None]
        sin_sum = outer_sin[:, None] * inner_cos[None] + outer_cos[:, None] * inner_sin[None]
        return cos_sum.reshape(-1, width), sin_sum.reshape(-1, width)

    coarse_count = count // lanes
    rows = records.shape[0]
    bins = band_index.shape[0]
    full = lambda step: (0, 0)
    if coarse_count == 64 and chunk == 2048:
        outer_cos, outer_sin = cos_sin(first_sample + lanes * 8 * jnp.arange(8, dtype=jnp.int32))
        inner_cos, inner_sin = cos_sin(lanes * jnp.arange(8, dtype=jnp.int32))
        fine_outer_cos, fine_outer_sin = cos_sin(16 * jnp.arange(lanes // 16, dtype=jnp.int32))
        fine_inner_cos, fine_inner_sin = cos_sin(jnp.arange(16, dtype=jnp.int32))
        outer_cos = jnp.broadcast_to(outer_cos[:, None, :], (8, 8, bins))
        outer_sin = jnp.broadcast_to(outer_sin[:, None, :], (8, 8, bins))
        small = [inner_cos, inner_sin, fine_outer_cos, fine_outer_sin, fine_inner_cos, fine_inner_sin]
        return pl.pallas_call(
            dft_kernel_inline,
            grid=(count // chunk,),
            in_specs=[pl.BlockSpec((rows, chunk), lambda step: (0, step))]
            + [pl.BlockSpec((8, 8, bins), lambda step: (0, 0, 0))] * 2
            + [pl.BlockSpec(table.shape, full) for table in small],
            out_specs=[pl.BlockSpec((rows, bins), full), pl.BlockSpec((rows, bins), full)],
            out_shape=[
                jax.ShapeDtypeStruct((rows, bins), jnp.float32),
                jax.ShapeDtypeStruct((rows, bins), jnp.float32),
            ],
            compiler_params=pltpu.CompilerParams(dimension_semantics=("arbitrary",)),
        )(records, outer_cos, outer_sin, *small)
    coarse_outer = coarse_count // 8 if coarse_count % 8 == 0 else 1
    coarse_inner = coarse_count // coarse_outer
    cos_a, sin_a = combined(
        first_sample + lanes * coarse_inner * jnp.arange(coarse_outer, dtype=jnp.int32),
        lanes * jnp.arange(coarse_inner, dtype=jnp.int32),
    )
    nsin_a = -sin_a
    cos_b, sin_b = combined(
        16 * jnp.arange(lanes // 16, dtype=jnp.int32), jnp.arange(16, dtype=jnp.int32)
    )
    cos_b = cos_b * norm_scale
    sin_b = sin_b * norm_scale
    rows = records.shape[0]
    bins = band_index.shape[0]
    full = lambda step: (0, 0)
    return pl.pallas_call(
        dft_kernel,
        grid=(count // chunk,),
        in_specs=[
            pl.BlockSpec((rows, chunk), lambda step: (0, step)),
            pl.BlockSpec(cos_a.shape, full),
            pl.BlockSpec(nsin_a.shape, full),
            pl.BlockSpec(cos_b.shape, full),
            pl.BlockSpec(sin_b.shape, full),
        ],
        out_specs=[pl.BlockSpec((rows, bins), full), pl.BlockSpec((rows, bins), full)],
        out_shape=[
            jax.ShapeDtypeStruct((rows, bins), jnp.float32),
            jax.ShapeDtypeStruct((rows, bins), jnp.float32),
        ],
        compiler_params=pltpu.CompilerParams(dimension_semantics=("arbitrary",)),
    )(records, cos_a, nsin_a, cos_b, sin_b)


def gather_blocks(carried, count, rank, held=None):
    if count & (count - 1) != 0:
        return lax.all_gather(carried, "blk", axis=0, tiled=False)
    masks = []
    step = count // 2
    while step >= 1:
        masks.append(step)
        step //= 2
    if not masks:
        return carried[None]
    first = masks[0]
    rest = masks[1:]
    if held is None:
        pairs = [(source, source ^ first) for source in range(count)]
        held = jnp.stack([carried, lax.ppermute(carried, "blk", pairs)], axis=0)
    split = (held.shape[1] + 1) // 2
    halves = [held[:, :split], held[:, split:]]
    orders = [rest, rest[::-1]]
    results = []
    for part, order in zip(halves, orders):
        done = [first]
        for mask in order:
            pairs = [(source, source ^ mask) for source in range(count)]
            arrived = lax.ppermute(part, "blk", pairs)
            done.append(mask)
            axis = sorted(done, reverse=True).index(mask)
            part = jnp.stack([part, arrived], axis=axis)
        results.append(part.reshape((count,) + part.shape[len(masks):]))
    return jnp.concatenate(results, axis=1)


def per_device(raw, taps, send_list, recv_row):
    owners_count = lax.axis_size("blk")
    seg_count = lax.axis_size("seg")
    freq_count = lax.axis_size("freq")
    freq_rank = lax.axis_index("freq")
    sections, seg_dev, half_len = raw.shape
    records = raw.reshape(sections * seg_dev, half_len)
    device_bins = BINS // freq_count
    block_bins = device_bins // seg_count
    capacity = send_list.shape[2]

    def band_of(row_ids):
        owner_core = row_ids // device_bins
        local_row = row_ids % device_bins
        return (
            local_row // block_bins * freq_count + owner_core
        ) * block_bins + local_row % block_bins

    band_rows = band_of(jnp.arange(device_bins * freq_count, dtype=jnp.int32))
    real_t, imag_t = dft_fused(records, band_rows, freq_rank * half_len)
    real_all = real_t.T
    imag_all = imag_t.T
    blocks = jnp.stack([real_all, imag_all], axis=1)
    blocks = blocks.reshape(freq_count, device_bins, 2, records.shape[0])
    if freq_count == 2:
        kept = jnp.where(freq_rank == 0, blocks[0], blocks[1])
        sent = jnp.where(freq_rank == 0, blocks[1], blocks[0])
        kept_blocks = kept.reshape(seg_count, block_bins, 2, -1)
        sent_blocks = sent.reshape(seg_count, block_bins, 2, -1)
        own_edges = jnp.concatenate(
            [kept_blocks[:, :HW], kept_blocks[:, block_bins - HW :]], axis=1
        ).reshape(seg_count * 2 * HW, 2, -1)
        message = jnp.concatenate([sent, own_edges], axis=0)
        arrived = swapped(message, "freq", 0)
        spectra = kept + arrived[:device_bins]
        their_edges = jnp.concatenate(
            [sent_blocks[:, :HW], sent_blocks[:, block_bins - HW :]], axis=1
        ).reshape(seg_count * 2 * HW, 2, -1)
        edge_spectra = (their_edges + arrived[device_bins:]).reshape(seg_count, 2, HW, 2, -1)
        partner = jnp.transpose(
            jnp.sqrt(
                edge_spectra[..., 0, :] * edge_spectra[..., 0, :]
                + edge_spectra[..., 1, :] * edge_spectra[..., 1, :]
                + 1e-06
            ),
            (1, 0, 2, 3),
        )
    else:
        spectra = lax.psum_scatter(
            blocks.reshape(device_bins * freq_count, 2, records.shape[0]),
            "freq",
            scatter_dimension=0,
            tiled=True,
        )
    real_part = spectra[:, 0]
    imag_part = spectra[:, 1]
    amplitude = jnp.sqrt(real_part * real_part + imag_part * imag_part + 1e-06)
    amp_blocks = amplitude.reshape(seg_count, block_bins, -1)
    if freq_count != 2:
        band_rims = jnp.stack([amp_blocks[:, :HW], amp_blocks[:, block_bins - HW :]])
        partner = swapped(band_rims, "freq", 0)
    zero_rim = jnp.zeros_like(partner[1][:1])
    right_prev = jnp.concatenate([zero_rim, partner[1][:-1]], axis=0)
    left_next = jnp.concatenate([partner[0][1:], zero_rim], axis=0)
    first_core = freq_rank == 0
    lower_rim = jnp.where(first_core, right_prev, partner[1])
    upper_rim = jnp.where(first_core, partner[0], left_next)
    padded = jnp.concatenate([lower_rim, amp_blocks, upper_rim], axis=1)
    window_sum = padded[:, 0:block_bins]
    for offset_step in range(1, 2 * HW + 1):
        window_sum = window_sum + padded[:, offset_step : offset_step + block_bins]
    span_ids = jnp.arange(seg_count, dtype=jnp.int32)[:, None]
    offsets = jnp.arange(block_bins, dtype=jnp.int32)[None, :]
    position = (span_ids * freq_count + freq_rank) * block_bins + offsets
    counted = jnp.minimum(position + HW, BINS - 1) - jnp.maximum(position - HW, 0) + 1
    smooth = window_sum / counted.astype(jnp.float32)[:, :, None]
    divisor = jnp.maximum(smooth, WHITEN_FLOOR).reshape(device_bins, -1)
    local_bins = freq_rank * device_bins + jnp.arange(device_bins, dtype=jnp.int32)
    response_re, response_im = response(band_of(local_bins), taps)
    scaled_re = real_part / divisor
    scaled_im = imag_part / divisor
    white_re = scaled_re * response_re[:, None] - scaled_im * response_im[:, None]
    white_im = scaled_re * response_im[:, None] + scaled_im * response_re[:, None]
    whitened = jnp.stack([white_re, white_im], axis=1).astype(jnp.bfloat16)
    whitened = whitened.reshape(seg_count, block_bins, 2, sections, seg_dev)
    whitened = jnp.transpose(whitened, (0, 3, 1, 2, 4))
    seg_rank = lax.axis_index("seg")
    all_segs = seg_dev * seg_count
    table = jnp.concatenate([send_list[0], recv_row[0]], axis=1).reshape(-1)
    table_len = table.shape[0]
    blk_rank = lax.axis_index("blk")
    fused_round = seg_count == 2 and owners_count >= 2 and owners_count & (owners_count - 1) == 0
    if fused_round:
        piece_width = block_bins * 2 * seg_dev
        slab_width = 128
        slab = jnp.pad(table.astype(jnp.bfloat16), (0, sections * slab_width - table_len))
        keep = lax.dynamic_index_in_dim(whitened, seg_rank, axis=0, keepdims=False)
        other = lax.dynamic_index_in_dim(whitened, 1 - seg_rank, axis=0, keepdims=False)
        keep_flat = jnp.concatenate(
            [keep.reshape(sections, -1), slab.reshape(sections, slab_width)], axis=1
        )
        other_flat = other.reshape(sections, -1)
        first = owners_count // 2
        from_blk = lax.ppermute(
            keep_flat, "blk", [(source, source ^ first) for source in range(owners_count)]
        )
        from_seg = lax.ppermute(other_flat, "seg", [(0, 1), (1, 0)])
        diagonal = [
            (source * 2 + side, (source ^ first) * 2 + 1 - side)
            for source in range(owners_count)
            for side in range(2)
        ]
        from_diagonal = lax.ppermute(other_flat, ("blk", "seg"), diagonal)

        def interleave(mine_segs, their_segs, table_slab):
            lanes_in = 2 * seg_dev
            joined = jnp.concatenate(
                [
                    mine_segs.reshape(sections, block_bins, lanes_in),
                    their_segs.reshape(sections, block_bins, lanes_in),
                ],
                axis=2,
            ).reshape(sections, -1)
            return jnp.concatenate([joined, table_slab], axis=1)

        held = jnp.stack(
            [
                interleave(keep_flat[:, :piece_width], from_seg, keep_flat[:, piece_width:]),
                interleave(from_blk[:, :piece_width], from_diagonal, from_blk[:, piece_width:]),
            ],
            axis=0,
        )
        moved = gather_blocks(None, owners_count, blk_rank, held=held)
        halves = [moved[:, :, : 2 * piece_width]]
        table_part = moved[:, :, 2 * piece_width :]
        table_part = table_part.reshape(owners_count, -1)[:, :table_len]
        half_segs = all_segs
        chunk_segs = seg_dev
    else:
        pieces = [lax.dynamic_index_in_dim(whitened, seg_rank, axis=0, keepdims=False)]
        for shift in range(1, seg_count):
            outgoing = lax.dynamic_index_in_dim(
                whitened, (seg_rank + shift) % seg_count, axis=0, keepdims=False
            )
            pairs = [(source, (source + shift) % seg_count) for source in range(seg_count)]
            flat = outgoing.reshape(sections, -1)
            pieces.append(lax.ppermute(flat, "seg", pairs).reshape(outgoing.shape))
        local = jnp.stack(pieces, axis=3).reshape(sections, block_bins, -1)
        table_width = local.shape[-1]
        slab = jnp.pad(table.astype(jnp.bfloat16), (0, sections * table_width - table_len))
        carried = jnp.concatenate([local, slab.reshape(sections, 1, table_width)], axis=1)
        everything = gather_blocks(carried.reshape(sections, -1), owners_count, blk_rank)
        everything = everything.reshape(owners_count, sections, block_bins + 1, table_width)
        halves = [everything[:, :, :block_bins]]
        table_part = everything[:, :, block_bins].reshape(owners_count, -1)[:, :table_len]
        half_segs = all_segs
        chunk_segs = all_segs
    table_part = table_part.astype(jnp.int32).reshape(owners_count, owners_count, 2 * capacity)
    position_ids = jnp.arange(owners_count, dtype=jnp.int32)
    if owners_count & (owners_count - 1) == 0:
        source_of = blk_rank ^ position_ids
        unpermute = (source_of[:, None] == position_ids[None, :]).astype(jnp.int32)
        table_part = jnp.sum(unpermute[:, :, None, None] * table_part[None], axis=1)
    else:
        source_of = position_ids
    send_all = table_part[..., :capacity]
    recv_all = table_part[..., capacity:]
    rows_count = owners_count * OWN
    chans_count = owners_count * sections
    chosen = jnp.transpose(send_all, (1, 0, 2))
    valid = (chosen < sections) & (recv_all < OWN)
    source_ids = (blk_rank ^ position_ids if owners_count & (owners_count - 1) == 0 else position_ids)[None, :, None]
    owner_ids = jnp.arange(owners_count, dtype=jnp.int32)[:, None, None]
    channel = jnp.where(valid, source_ids * sections + chosen, -1).reshape(-1)
    target = jnp.where(valid, owner_ids * OWN + recv_all, -1).reshape(-1)
    row_hot = (target[:, None] == jnp.arange(rows_count, dtype=jnp.int32)[None, :]).astype(
        jnp.bfloat16
    )
    chan_hot = (channel[:, None] == jnp.arange(chans_count, dtype=jnp.int32)[None, :]).astype(
        jnp.bfloat16
    )
    selector = jnp.einsum(
        "er,ec->rc", row_hot, chan_hot, preferred_element_type=jnp.float32
    ).astype(jnp.bfloat16)
    selector = selector.reshape(rows_count, owners_count, sections)
    cross = None
    for half in halves:
        data = half.reshape(owners_count, sections, block_bins, 2 * half_segs)
        routed = jnp.einsum(
            "rsc,scbq->brq", selector, data, preferred_element_type=jnp.float32
        ).astype(jnp.bfloat16)
        own = lax.dynamic_slice_in_dim(routed, blk_rank * OWN, OWN, axis=1)
        own_parts = own.reshape(own.shape[:-1] + (-1, 2, chunk_segs))
        rotated = jnp.stack([own_parts[..., 1, :], -own_parts[..., 0, :]], axis=-2)
        rotated = rotated.reshape(own.shape)
        lhs = jnp.concatenate([own, rotated], axis=1)
        part = jnp.einsum("bpq,bjq->bpj", lhs, routed, preferred_element_type=jnp.float32)
        cross = part if cross is None else cross + part
    cross = cross.reshape(block_bins, 2, OWN, rows_count)
    return jnp.transpose(cross, (1, 0, 2, 3)) / jnp.float32(all_segs)


def solution(mesh):
    placed = (
        P(("groups", "blk"), "seg", "freq"),
        P(),
        P(("groups", "blk"), None, None),
        P(("groups", "blk"), None, None),
    )
    return jax.shard_map(
        per_device,
        mesh=mesh,
        in_specs=placed,
        out_specs=P(None, ("seg", "freq"), ("groups", "blk"), None),
        check_vma=False,
    )
```

```python
import math

import jax
import jax.numpy as jnp
from jax import lax
from jax.experimental import pallas as pl
from jax.experimental.pallas import tpu as pltpu
from jax.sharding import PartitionSpec as P

SEG_LEN = 16384
BINS = 256
BAND_LO = 128
HW = 4
OWN = 16


WHITEN_FLOOR = 0.25
TWO_PI = 2.0 * math.pi


def swapped(value, axis, distance):
    mask = 2**distance
    pairs = [(source, source ^ mask) for source in range(lax.axis_size(axis))]
    return lax.ppermute(value, axis, pairs)


def dft_tables(band_index, sample_index):
    wavenumber = BAND_LO + band_index
    phase_int = wavenumber[:, None] * sample_index[None, :] % SEG_LEN
    angles = phase_int.astype(jnp.float32) * (TWO_PI / SEG_LEN)
    norm_scale = 1.0 / math.sqrt(SEG_LEN)
    cos_part = (jnp.cos(angles) * norm_scale).astype(jnp.bfloat16)
    sin_part = (-jnp.sin(angles) * norm_scale).astype(jnp.bfloat16)
    return (cos_part, sin_part)


def dft_tables_fast(band_index, first_sample, count):
    lanes = 128
    wavenumber = BAND_LO + band_index
    coarse = (first_sample + lanes * jnp.arange(count // lanes, dtype=jnp.int32))
    fine = jnp.arange(lanes, dtype=jnp.int32)
    coarse_angle = (wavenumber[:, None] * coarse[None, :] % SEG_LEN).astype(jnp.float32) * (
        TWO_PI / SEG_LEN
    )
    fine_angle = (wavenumber[:, None] * fine[None, :] % SEG_LEN).astype(jnp.float32) * (
        TWO_PI / SEG_LEN
    )
    cos_a = jnp.cos(coarse_angle)[:, :, None]
    sin_a = jnp.sin(coarse_angle)[:, :, None]
    cos_b = jnp.cos(fine_angle)[:, None, :]
    sin_b = jnp.sin(fine_angle)[:, None, :]
    norm_scale = 1.0 / math.sqrt(SEG_LEN)
    cos_sum = cos_a * cos_b - sin_a * sin_b
    sin_sum = sin_a * cos_b + cos_a * sin_b
    rows = band_index.shape[0]
    cos_part = (cos_sum * norm_scale).astype(jnp.bfloat16).reshape(rows, count)
    sin_part = (-sin_sum * norm_scale).astype(jnp.bfloat16).reshape(rows, count)
    return (cos_part, sin_part)


def response(band_index, taps):
    wavenumber = BAND_LO + band_index
    lag_index = jnp.arange(taps.shape[0], dtype=jnp.int32)
    phase_int = wavenumber[:, None] * lag_index[None, :] % SEG_LEN
    angles = phase_int.astype(jnp.float32) * (TWO_PI / SEG_LEN)
    real_part = jnp.dot(jnp.cos(angles), taps, precision=lax.Precision.HIGHEST)
    imag_part = jnp.dot(-jnp.sin(angles), taps, precision=lax.Precision.HIGHEST)
    return (real_part, imag_part)


def dft_kernel(rec_ref, cos_a_ref, nsin_a_ref, cos_b_ref, sin_b_ref, re_ref, im_ref):
    step = pl.program_id(0)
    lanes = cos_b_ref.shape[0]
    group = 8
    groups = rec_ref.shape[1] // (group * lanes)

    @pl.when(step == 0)
    def _():
        re_ref[...] = jnp.zeros_like(re_ref)
        im_ref[...] = jnp.zeros_like(im_ref)

    def one_group(index, carry):
        row = pl.multiple_of((step * groups + index) * group, group)
        cos_a = cos_a_ref[pl.ds(row, group), :]
        nsin_a = nsin_a_ref[pl.ds(row, group), :]
        cos_b = cos_b_ref[...]
        sin_b = sin_b_ref[...]
        for pair in range(group // 2):
            cos_parts = []
            sin_parts = []
            for half in range(2):
                at = 2 * pair + half
                ca = cos_a[at : at + 1]
                sa = nsin_a[at : at + 1]
                cos_parts.append(ca * cos_b + sa * sin_b)
                sin_parts.append(sa * cos_b - ca * sin_b)
            cos_tile = jnp.concatenate(cos_parts, axis=0).astype(jnp.bfloat16)
            sin_tile = jnp.concatenate(sin_parts, axis=0).astype(jnp.bfloat16)
            first = pl.multiple_of((index * group + 2 * pair) * lanes, 2 * lanes)
            rec = rec_ref[:, pl.ds(first, 2 * lanes)]
            re_ref[...] += jnp.dot(rec, cos_tile, preferred_element_type=jnp.float32)
            im_ref[...] += jnp.dot(rec, sin_tile, preferred_element_type=jnp.float32)
        return carry

    lax.fori_loop(0, groups, one_group, 0)


def dft_kernel_self(info_ref, rec_ref, re_ref, im_ref, cos_a_ref, nsin_a_ref, cos_b_ref, sin_b_ref):
    step = pl.program_id(0)
    lanes = 128
    group = 8
    groups = rec_ref.shape[1] // (group * lanes)

    @pl.when(step == 0)
    def _():
        re_ref[...] = jnp.zeros_like(re_ref)
        im_ref[...] = jnp.zeros_like(im_ref)
        wavenumber = info_ref[0:1, :]
        first = info_ref[1:2, :]

        def cos_sin(steps):
            angle = (steps * wavenumber % SEG_LEN).astype(jnp.float32) * (TWO_PI / SEG_LEN)
            return jnp.cos(angle), jnp.sin(angle)

        width = wavenumber.shape[1]
        eight = lax.broadcasted_iota(jnp.int32, (8, width), 0)
        sixteen = lax.broadcasted_iota(jnp.int32, (16, width), 0)
        outer_cos, outer_sin = cos_sin(first + lanes * 8 * eight)
        inner_cos, inner_sin = cos_sin(lanes * eight)
        fine_outer_cos, fine_outer_sin = cos_sin(16 * eight)
        fine_inner_cos, fine_inner_sin = cos_sin(sixteen)
        norm_scale = 1.0 / math.sqrt(SEG_LEN)
        for outer in range(8):
            oc = outer_cos[outer : outer + 1]
            os_ = outer_sin[outer : outer + 1]
            cos_a_ref[outer * 8 : outer * 8 + 8, :] = oc * inner_cos - os_ * inner_sin
            nsin_a_ref[outer * 8 : outer * 8 + 8, :] = -(os_ * inner_cos + oc * inner_sin)
            fc = fine_outer_cos[outer : outer + 1]
            fs = fine_outer_sin[outer : outer + 1]
            cos_b_ref[outer * 16 : outer * 16 + 16, :] = (fc * fine_inner_cos - fs * fine_inner_sin) * norm_scale
            sin_b_ref[outer * 16 : outer * 16 + 16, :] = (fs * fine_inner_cos + fc * fine_inner_sin) * norm_scale

    def one_group(index, carry):
        row = pl.multiple_of((step * groups + index) * group, group)
        cos_a = cos_a_ref[pl.ds(row, group), :]
        nsin_a = nsin_a_ref[pl.ds(row, group), :]
        cos_b = cos_b_ref[...]
        sin_b = sin_b_ref[...]
        for pair in range(group // 2):
            cos_parts = []
            sin_parts = []
            for half in range(2):
                at = 2 * pair + half
                ca = cos_a[at : at + 1]
                sa = nsin_a[at : at + 1]
                cos_parts.append(ca * cos_b + sa * sin_b)
                sin_parts.append(sa * cos_b - ca * sin_b)
            cos_tile = jnp.concatenate(cos_parts, axis=0).astype(jnp.bfloat16)
            sin_tile = jnp.concatenate(sin_parts, axis=0).astype(jnp.bfloat16)
            first = pl.multiple_of((index * group + 2 * pair) * lanes, 2 * lanes)
            rec = rec_ref[:, pl.ds(first, 2 * lanes)]
            re_ref[...] += jnp.dot(rec, cos_tile, preferred_element_type=jnp.float32)
            im_ref[...] += jnp.dot(rec, sin_tile, preferred_element_type=jnp.float32)
        return carry

    lax.fori_loop(0, groups, one_group, 0)


def dft_fused(records, band_index, first_sample):
    lanes = 128
    chunk = 2048
    count = records.shape[1]
    wavenumber = BAND_LO + band_index
    norm_scale = 1.0 / math.sqrt(SEG_LEN)

    def cos_sin(steps):
        angle = (steps[:, None] * wavenumber[None, :] % SEG_LEN).astype(jnp.float32) * (
            TWO_PI / SEG_LEN
        )
        return jnp.cos(angle), jnp.sin(angle)

    def combined(outer_steps, inner_steps):
        outer_cos, outer_sin = cos_sin(outer_steps)
        inner_cos, inner_sin = cos_sin(inner_steps)
        width = wavenumber.shape[0]
        cos_sum = outer_cos[:, None] * inner_cos[None] - outer_sin[:, None] * inner_sin[None]
        sin_sum = outer_sin[:, None] * inner_cos[None] + outer_cos[:, None] * inner_sin[None]
        return cos_sum.reshape(-1, width), sin_sum.reshape(-1, width)

    coarse_count = count // lanes
    rows = records.shape[0]
    bins = band_index.shape[0]
    full = lambda step: (0, 0)
    if coarse_count == 64 and chunk == 2048:
        info = jnp.concatenate(
            [
                wavenumber[None, :].astype(jnp.int32),
                jnp.broadcast_to(jnp.asarray(first_sample, jnp.int32), (7, bins)),
            ],
            axis=0,
        )
        return pl.pallas_call(
            dft_kernel_self,
            grid=(count // chunk,),
            in_specs=[pl.BlockSpec((8, bins), full), pl.BlockSpec((rows, chunk), lambda step: (0, step))],
            out_specs=[pl.BlockSpec((rows, bins), full), pl.BlockSpec((rows, bins), full)],
            out_shape=[
                jax.ShapeDtypeStruct((rows, bins), jnp.float32),
                jax.ShapeDtypeStruct((rows, bins), jnp.float32),
            ],
            scratch_shapes=[
                pltpu.VMEM((64, bins), jnp.float32),
                pltpu.VMEM((64, bins), jnp.float32),
                pltpu.VMEM((128, bins), jnp.float32),
                pltpu.VMEM((128, bins), jnp.float32),
            ],
            compiler_params=pltpu.CompilerParams(dimension_semantics=("arbitrary",)),
        )(info, records)
    coarse_outer = coarse_count // 8 if coarse_count % 8 == 0 else 1
    coarse_inner = coarse_count // coarse_outer
    cos_a, sin_a = combined(
        first_sample + lanes * coarse_inner * jnp.arange(coarse_outer, dtype=jnp.int32),
        lanes * jnp.arange(coarse_inner, dtype=jnp.int32),
    )
    nsin_a = -sin_a
    cos_b, sin_b = combined(
        16 * jnp.arange(lanes // 16, dtype=jnp.int32), jnp.arange(16, dtype=jnp.int32)
    )
    cos_b = cos_b * norm_scale
    sin_b = sin_b * norm_scale
    rows = records.shape[0]
    bins = band_index.shape[0]
    full = lambda step: (0, 0)
    return pl.pallas_call(
        dft_kernel,
        grid=(count // chunk,),
        in_specs=[
            pl.BlockSpec((rows, chunk), lambda step: (0, step)),
            pl.BlockSpec(cos_a.shape, full),
            pl.BlockSpec(nsin_a.shape, full),
            pl.BlockSpec(cos_b.shape, full),
            pl.BlockSpec(sin_b.shape, full),
        ],
        out_specs=[pl.BlockSpec((rows, bins), full), pl.BlockSpec((rows, bins), full)],
        out_shape=[
            jax.ShapeDtypeStruct((rows, bins), jnp.float32),
            jax.ShapeDtypeStruct((rows, bins), jnp.float32),
        ],
        compiler_params=pltpu.CompilerParams(dimension_semantics=("arbitrary",)),
    )(records, cos_a, nsin_a, cos_b, sin_b)


def gather_blocks(carried, count, rank, held=None):
    if count & (count - 1) != 0:
        return lax.all_gather(carried, "blk", axis=0, tiled=False)
    masks = []
    step = count // 2
    while step >= 1:
        masks.append(step)
        step //= 2
    if not masks:
        return carried[None]
    first = masks[0]
    rest = masks[1:]
    if held is None:
        pairs = [(source, source ^ first) for source in range(count)]
        held = jnp.stack([carried, lax.ppermute(carried, "blk", pairs)], axis=0)
    split = (held.shape[1] + 1) // 2
    halves = [held[:, :split], held[:, split:]]
    orders = [rest, rest[::-1]]
    results = []
    for part, order in zip(halves, orders):
        done = [first]
        for mask in order:
            pairs = [(source, source ^ mask) for source in range(count)]
            arrived = lax.ppermute(part, "blk", pairs)
            done.append(mask)
            axis = sorted(done, reverse=True).index(mask)
            part = jnp.stack([part, arrived], axis=axis)
        results.append(part.reshape((count,) + part.shape[len(masks):]))
    return jnp.concatenate(results, axis=1)


def per_device(raw, taps, send_list, recv_row):
    owners_count = lax.axis_size("blk")
    seg_count = lax.axis_size("seg")
    freq_count = lax.axis_size("freq")
    freq_rank = lax.axis_index("freq")
    sections, seg_dev, half_len = raw.shape
    records = raw.reshape(sections * seg_dev, half_len)
    device_bins = BINS // freq_count
    block_bins = device_bins // seg_count
    capacity = send_list.shape[2]

    def band_of(row_ids):
        owner_core = row_ids // device_bins
        local_row = row_ids % device_bins
        return (
            local_row // block_bins * freq_count + owner_core
        ) * block_bins + local_row % block_bins

    band_rows = band_of(jnp.arange(device_bins * freq_count, dtype=jnp.int32))
    real_t, imag_t = dft_fused(records, band_rows, freq_rank * half_len)
    real_all = real_t.T
    imag_all = imag_t.T
    blocks = jnp.stack([real_all, imag_all], axis=1)
    blocks = blocks.reshape(freq_count, device_bins, 2, records.shape[0])
    if freq_count == 2:
        kept = jnp.where(freq_rank == 0, blocks[0], blocks[1])
        sent = jnp.where(freq_rank == 0, blocks[1], blocks[0])
        kept_blocks = kept.reshape(seg_count, block_bins, 2, -1)
        sent_blocks = sent.reshape(seg_count, block_bins, 2, -1)
        own_edges = jnp.concatenate(
            [kept_blocks[:, :HW], kept_blocks[:, block_bins - HW :]], axis=1
        ).reshape(seg_count * 2 * HW, 2, -1)
        message = jnp.concatenate([sent, own_edges], axis=0)
        arrived = swapped(message, "freq", 0)
        spectra = kept + arrived[:device_bins]
        their_edges = jnp.concatenate(
            [sent_blocks[:, :HW], sent_blocks[:, block_bins - HW :]], axis=1
        ).reshape(seg_count * 2 * HW, 2, -1)
        edge_spectra = (their_edges + arrived[device_bins:]).reshape(seg_count, 2, HW, 2, -1)
        partner = jnp.transpose(
            jnp.sqrt(
                edge_spectra[..., 0, :] * edge_spectra[..., 0, :]
                + edge_spectra[..., 1, :] * edge_spectra[..., 1, :]
                + 1e-06
            ),
            (1, 0, 2, 3),
        )
    else:
        spectra = lax.psum_scatter(
            blocks.reshape(device_bins * freq_count, 2, records.shape[0]),
            "freq",
            scatter_dimension=0,
            tiled=True,
        )
    real_part = spectra[:, 0]
    imag_part = spectra[:, 1]
    amplitude = jnp.sqrt(real_part * real_part + imag_part * imag_part + 1e-06)
    amp_blocks = amplitude.reshape(seg_count, block_bins, -1)
    if freq_count != 2:
        band_rims = jnp.stack([amp_blocks[:, :HW], amp_blocks[:, block_bins - HW :]])
        partner = swapped(band_rims, "freq", 0)
    zero_rim = jnp.zeros_like(partner[1][:1])
    right_prev = jnp.concatenate([zero_rim, partner[1][:-1]], axis=0)
    left_next = jnp.concatenate([partner[0][1:], zero_rim], axis=0)
    first_core = freq_rank == 0
    lower_rim = jnp.where(first_core, right_prev, partner[1])
    upper_rim = jnp.where(first_core, partner[0], left_next)
    padded = jnp.concatenate([lower_rim, amp_blocks, upper_rim], axis=1)
    window_sum = padded[:, 0:block_bins]
    for offset_step in range(1, 2 * HW + 1):
        window_sum = window_sum + padded[:, offset_step : offset_step + block_bins]
    span_ids = jnp.arange(seg_count, dtype=jnp.int32)[:, None]
    offsets = jnp.arange(block_bins, dtype=jnp.int32)[None, :]
    position = (span_ids * freq_count + freq_rank) * block_bins + offsets
    counted = jnp.minimum(position + HW, BINS - 1) - jnp.maximum(position - HW, 0) + 1
    smooth = window_sum / counted.astype(jnp.float32)[:, :, None]
    divisor = jnp.maximum(smooth, WHITEN_FLOOR).reshape(device_bins, -1)
    local_bins = freq_rank * device_bins + jnp.arange(device_bins, dtype=jnp.int32)
    response_re, response_im = response(band_of(local_bins), taps)
    scaled_re = real_part / divisor
    scaled_im = imag_part / divisor
    white_re = scaled_re * response_re[:, None] - scaled_im * response_im[:, None]
    white_im = scaled_re * response_im[:, None] + scaled_im * response_re[:, None]
    whitened = jnp.stack([white_re, white_im], axis=1).astype(jnp.bfloat16)
    whitened = whitened.reshape(seg_count, block_bins, 2, sections, seg_dev)
    whitened = jnp.transpose(whitened, (0, 3, 1, 2, 4))
    seg_rank = lax.axis_index("seg")
    all_segs = seg_dev * seg_count
    table = jnp.concatenate([send_list[0], recv_row[0]], axis=1).reshape(-1)
    table_len = table.shape[0]
    blk_rank = lax.axis_index("blk")
    fused_round = seg_count == 2 and owners_count >= 2 and owners_count & (owners_count - 1) == 0
    if fused_round:
        piece_width = block_bins * 2 * seg_dev
        slab_width = 128
        slab = jnp.pad(table.astype(jnp.bfloat16), (0, sections * slab_width - table_len))
        keep = lax.dynamic_index_in_dim(whitened, seg_rank, axis=0, keepdims=False)
        other = lax.dynamic_index_in_dim(whitened, 1 - seg_rank, axis=0, keepdims=False)
        keep_flat = jnp.concatenate(
            [keep.reshape(sections, -1), slab.reshape(sections, slab_width)], axis=1
        )
        other_flat = other.reshape(sections, -1)
        first = owners_count // 2
        from_blk = lax.ppermute(
            keep_flat, "blk", [(source, source ^ first) for source in range(owners_count)]
        )
        from_seg = lax.ppermute(other_flat, "seg", [(0, 1), (1, 0)])
        diagonal = [
            (source * 2 + side, (source ^ first) * 2 + 1 - side)
            for source in range(owners_count)
            for side in range(2)
        ]
        from_diagonal = lax.ppermute(other_flat, ("blk", "seg"), diagonal)

        def interleave(mine_segs, their_segs, table_slab):
            lanes_in = 2 * seg_dev
            joined = jnp.concatenate(
                [
                    mine_segs.reshape(sections, block_bins, lanes_in),
                    their_segs.reshape(sections, block_bins, lanes_in),
                ],
                axis=2,
            ).reshape(sections, -1)
            return jnp.concatenate([joined, table_slab], axis=1)

        held = jnp.stack(
            [
                interleave(keep_flat[:, :piece_width], from_seg, keep_flat[:, piece_width:]),
                interleave(from_blk[:, :piece_width], from_diagonal, from_blk[:, piece_width:]),
            ],
            axis=0,
        )
        moved = gather_blocks(None, owners_count, blk_rank, held=held)
        halves = [moved[:, :, : 2 * piece_width]]
        table_part = moved[:, :, 2 * piece_width :]
        table_part = table_part.reshape(owners_count, -1)[:, :table_len]
        half_segs = all_segs
        chunk_segs = seg_dev
    else:
        pieces = [lax.dynamic_index_in_dim(whitened, seg_rank, axis=0, keepdims=False)]
        for shift in range(1, seg_count):
            outgoing = lax.dynamic_index_in_dim(
                whitened, (seg_rank + shift) % seg_count, axis=0, keepdims=False
            )
            pairs = [(source, (source + shift) % seg_count) for source in range(seg_count)]
            flat = outgoing.reshape(sections, -1)
            pieces.append(lax.ppermute(flat, "seg", pairs).reshape(outgoing.shape))
        local = jnp.stack(pieces, axis=3).reshape(sections, block_bins, -1)
        table_width = local.shape[-1]
        slab = jnp.pad(table.astype(jnp.bfloat16), (0, sections * table_width - table_len))
        carried = jnp.concatenate([local, slab.reshape(sections, 1, table_width)], axis=1)
        everything = gather_blocks(carried.reshape(sections, -1), owners_count, blk_rank)
        everything = everything.reshape(owners_count, sections, block_bins + 1, table_width)
        halves = [everything[:, :, :block_bins]]
        table_part = everything[:, :, block_bins].reshape(owners_count, -1)[:, :table_len]
        half_segs = all_segs
        chunk_segs = all_segs
    table_part = table_part.astype(jnp.int32).reshape(owners_count, owners_count, 2 * capacity)
    position_ids = jnp.arange(owners_count, dtype=jnp.int32)
    if owners_count & (owners_count - 1) == 0:
        source_of = blk_rank ^ position_ids
        unpermute = (source_of[:, None] == position_ids[None, :]).astype(jnp.int32)
        table_part = jnp.sum(unpermute[:, :, None, None] * table_part[None], axis=1)
    else:
        source_of = position_ids
    send_all = table_part[..., :capacity]
    recv_all = table_part[..., capacity:]
    rows_count = owners_count * OWN
    chans_count = owners_count * sections
    chosen = jnp.transpose(send_all, (1, 0, 2))
    valid = (chosen < sections) & (recv_all < OWN)
    source_ids = (blk_rank ^ position_ids if owners_count & (owners_count - 1) == 0 else position_ids)[None, :, None]
    owner_ids = jnp.arange(owners_count, dtype=jnp.int32)[:, None, None]
    channel = jnp.where(valid, source_ids * sections + chosen, -1).reshape(-1)
    target = jnp.where(valid, owner_ids * OWN + recv_all, -1).reshape(-1)
    row_hot = (target[:, None] == jnp.arange(rows_count, dtype=jnp.int32)[None, :]).astype(
        jnp.bfloat16
    )
    chan_hot = (channel[:, None] == jnp.arange(chans_count, dtype=jnp.int32)[None, :]).astype(
        jnp.bfloat16
    )
    selector = jnp.einsum(
        "er,ec->rc", row_hot, chan_hot, preferred_element_type=jnp.float32
    ).astype(jnp.bfloat16)
    selector = selector.reshape(rows_count, owners_count, sections)
    cross = None
    for half in halves:
        data = half.reshape(owners_count, sections, block_bins, 2 * half_segs)
        routed = jnp.einsum(
            "rsc,scbq->brq", selector, data, preferred_element_type=jnp.float32
        ).astype(jnp.bfloat16)
        own = lax.dynamic_slice_in_dim(routed, blk_rank * OWN, OWN, axis=1)
        own_parts = own.reshape(own.shape[:-1] + (-1, 2, chunk_segs))
        rotated = jnp.stack([own_parts[..., 1, :], -own_parts[..., 0, :]], axis=-2)
        rotated = rotated.reshape(own.shape)
        lhs = jnp.concatenate([own, rotated], axis=1)
        part = jnp.einsum("bpq,bjq->bpj", lhs, routed, preferred_element_type=jnp.float32)
        cross = part if cross is None else cross + part
    cross = cross.reshape(block_bins, 2, OWN, rows_count)
    return jnp.transpose(cross, (1, 0, 2, 3)) / jnp.float32(all_segs)


def solution(mesh):
    placed = (
        P(("groups", "blk"), "seg", "freq"),
        P(),
        P(("groups", "blk"), None, None),
        P(("groups", "blk"), None, None),
    )
    return jax.shard_map(
        per_device,
        mesh=mesh,
        in_specs=placed,
        out_specs=P(None, ("seg", "freq"), ("groups", "blk"), None),
        check_vma=False,
    )
```

```python
import math

import jax
import jax.numpy as jnp
from jax import lax
from jax.experimental import pallas as pl
from jax.experimental.pallas import tpu as pltpu
from jax.sharding import PartitionSpec as P

SEG_LEN = 16384
BINS = 256
BAND_LO = 128
HW = 4
OWN = 16


WHITEN_FLOOR = 0.25
TWO_PI = 2.0 * math.pi


def swapped(value, axis, distance):
    mask = 2**distance
    pairs = [(source, source ^ mask) for source in range(lax.axis_size(axis))]
    return lax.ppermute(value, axis, pairs)


def dft_tables(band_index, sample_index):
    wavenumber = BAND_LO + band_index
    phase_int = wavenumber[:, None] * sample_index[None, :] % SEG_LEN
    angles = phase_int.astype(jnp.float32) * (TWO_PI / SEG_LEN)
    norm_scale = 1.0 / math.sqrt(SEG_LEN)
    cos_part = (jnp.cos(angles) * norm_scale).astype(jnp.bfloat16)
    sin_part = (-jnp.sin(angles) * norm_scale).astype(jnp.bfloat16)
    return (cos_part, sin_part)


def dft_tables_fast(band_index, first_sample, count):
    lanes = 128
    wavenumber = BAND_LO + band_index
    coarse = (first_sample + lanes * jnp.arange(count // lanes, dtype=jnp.int32))
    fine = jnp.arange(lanes, dtype=jnp.int32)
    coarse_angle = (wavenumber[:, None] * coarse[None, :] % SEG_LEN).astype(jnp.float32) * (
        TWO_PI / SEG_LEN
    )
    fine_angle = (wavenumber[:, None] * fine[None, :] % SEG_LEN).astype(jnp.float32) * (
        TWO_PI / SEG_LEN
    )
    cos_a = jnp.cos(coarse_angle)[:, :, None]
    sin_a = jnp.sin(coarse_angle)[:, :, None]
    cos_b = jnp.cos(fine_angle)[:, None, :]
    sin_b = jnp.sin(fine_angle)[:, None, :]
    norm_scale = 1.0 / math.sqrt(SEG_LEN)
    cos_sum = cos_a * cos_b - sin_a * sin_b
    sin_sum = sin_a * cos_b + cos_a * sin_b
    rows = band_index.shape[0]
    cos_part = (cos_sum * norm_scale).astype(jnp.bfloat16).reshape(rows, count)
    sin_part = (-sin_sum * norm_scale).astype(jnp.bfloat16).reshape(rows, count)
    return (cos_part, sin_part)


def response(band_index, taps):
    wavenumber = BAND_LO + band_index
    lag_index = jnp.arange(taps.shape[0], dtype=jnp.int32)
    phase_int = wavenumber[:, None] * lag_index[None, :] % SEG_LEN
    angles = phase_int.astype(jnp.float32) * (TWO_PI / SEG_LEN)
    real_part = jnp.dot(jnp.cos(angles), taps, precision=lax.Precision.HIGHEST)
    imag_part = jnp.dot(-jnp.sin(angles), taps, precision=lax.Precision.HIGHEST)
    return (real_part, imag_part)


def dft_kernel(rec_ref, cos_a_ref, nsin_a_ref, cos_b_ref, sin_b_ref, re_ref, im_ref):
    step = pl.program_id(0)
    lanes = cos_b_ref.shape[0]
    group = 8
    groups = rec_ref.shape[1] // (group * lanes)

    @pl.when(step == 0)
    def _():
        re_ref[...] = jnp.zeros_like(re_ref)
        im_ref[...] = jnp.zeros_like(im_ref)

    def one_group(index, carry):
        row = pl.multiple_of((step * groups + index) * group, group)
        cos_a = cos_a_ref[pl.ds(row, group), :]
        nsin_a = nsin_a_ref[pl.ds(row, group), :]
        cos_b = cos_b_ref[...]
        sin_b = sin_b_ref[...]
        for pair in range(group // 2):
            cos_parts = []
            sin_parts = []
            for half in range(2):
                at = 2 * pair + half
                ca = cos_a[at : at + 1]
                sa = nsin_a[at : at + 1]
                cos_parts.append(ca * cos_b + sa * sin_b)
                sin_parts.append(sa * cos_b - ca * sin_b)
            cos_tile = jnp.concatenate(cos_parts, axis=0).astype(jnp.bfloat16)
            sin_tile = jnp.concatenate(sin_parts, axis=0).astype(jnp.bfloat16)
            first = pl.multiple_of((index * group + 2 * pair) * lanes, 2 * lanes)
            rec = rec_ref[:, pl.ds(first, 2 * lanes)]
            re_ref[...] += jnp.dot(rec, cos_tile, preferred_element_type=jnp.float32)
            im_ref[...] += jnp.dot(rec, sin_tile, preferred_element_type=jnp.float32)
        return carry

    lax.fori_loop(0, groups, one_group, 0)


def dft_kernel_self(info_ref, rec_ref, re_ref, im_ref, cos_a_ref, nsin_a_ref, cos_b_ref, sin_b_ref, layout=None):
    step = pl.program_id(0)
    lanes = 128
    group = 8
    groups = rec_ref.shape[1] // (group * lanes)

    @pl.when(step == 0)
    def _():
        re_ref[...] = jnp.zeros_like(re_ref)
        im_ref[...] = jnp.zeros_like(im_ref)
        if layout is None:
            wavenumber = info_ref[0:1, :]
            first = info_ref[1:2, :]
        else:
            device_bins, block_bins, freq_count, half_len = layout
            row_ids = lax.broadcasted_iota(jnp.int32, (1, re_ref.shape[1]), 1)
            owner_core = row_ids // device_bins
            local_row = row_ids % device_bins
            band = (local_row // block_bins * freq_count + owner_core) * block_bins + local_row % block_bins
            wavenumber = BAND_LO + band
            first = lax.axis_index("freq") * half_len

        def cos_sin(steps):
            angle = (steps * wavenumber % SEG_LEN).astype(jnp.float32) * (TWO_PI / SEG_LEN)
            return jnp.cos(angle), jnp.sin(angle)

        width = wavenumber.shape[1]
        eight = lax.broadcasted_iota(jnp.int32, (8, width), 0)
        sixteen = lax.broadcasted_iota(jnp.int32, (16, width), 0)
        outer_cos, outer_sin = cos_sin(first + lanes * 8 * eight)
        inner_cos, inner_sin = cos_sin(lanes * eight)
        fine_outer_cos, fine_outer_sin = cos_sin(16 * eight)
        fine_inner_cos, fine_inner_sin = cos_sin(sixteen)
        norm_scale = 1.0 / math.sqrt(SEG_LEN)
        for outer in range(8):
            oc = outer_cos[outer : outer + 1]
            os_ = outer_sin[outer : outer + 1]
            cos_a_ref[outer * 8 : outer * 8 + 8, :] = oc * inner_cos - os_ * inner_sin
            nsin_a_ref[outer * 8 : outer * 8 + 8, :] = -(os_ * inner_cos + oc * inner_sin)
            fc = fine_outer_cos[outer : outer + 1]
            fs = fine_outer_sin[outer : outer + 1]
            cos_b_ref[outer * 16 : outer * 16 + 16, :] = (fc * fine_inner_cos - fs * fine_inner_sin) * norm_scale
            sin_b_ref[outer * 16 : outer * 16 + 16, :] = (fs * fine_inner_cos + fc * fine_inner_sin) * norm_scale

    def one_group(index, carry):
        row = pl.multiple_of((step * groups + index) * group, group)
        cos_a = cos_a_ref[pl.ds(row, group), :]
        nsin_a = nsin_a_ref[pl.ds(row, group), :]
        cos_b = cos_b_ref[...]
        sin_b = sin_b_ref[...]
        for pair in range(group // 2):
            cos_parts = []
            sin_parts = []
            for half in range(2):
                at = 2 * pair + half
                ca = cos_a[at : at + 1]
                sa = nsin_a[at : at + 1]
                cos_parts.append(ca * cos_b + sa * sin_b)
                sin_parts.append(sa * cos_b - ca * sin_b)
            cos_tile = jnp.concatenate(cos_parts, axis=0).astype(jnp.bfloat16)
            sin_tile = jnp.concatenate(sin_parts, axis=0).astype(jnp.bfloat16)
            first = pl.multiple_of((index * group + 2 * pair) * lanes, 2 * lanes)
            rec = rec_ref[:, pl.ds(first, 2 * lanes)]
            re_ref[...] += jnp.dot(rec, cos_tile, preferred_element_type=jnp.float32)
            im_ref[...] += jnp.dot(rec, sin_tile, preferred_element_type=jnp.float32)
        return carry

    lax.fori_loop(0, groups, one_group, 0)


def dft_fused(records, band_index, first_sample, layout=None):
    lanes = 128
    chunk = 2048
    count = records.shape[1]
    wavenumber = BAND_LO + band_index
    norm_scale = 1.0 / math.sqrt(SEG_LEN)

    def cos_sin(steps):
        angle = (steps[:, None] * wavenumber[None, :] % SEG_LEN).astype(jnp.float32) * (
            TWO_PI / SEG_LEN
        )
        return jnp.cos(angle), jnp.sin(angle)

    def combined(outer_steps, inner_steps):
        outer_cos, outer_sin = cos_sin(outer_steps)
        inner_cos, inner_sin = cos_sin(inner_steps)
        width = wavenumber.shape[0]
        cos_sum = outer_cos[:, None] * inner_cos[None] - outer_sin[:, None] * inner_sin[None]
        sin_sum = outer_sin[:, None] * inner_cos[None] + outer_cos[:, None] * inner_sin[None]
        return cos_sum.reshape(-1, width), sin_sum.reshape(-1, width)

    coarse_count = count // lanes
    rows = records.shape[0]
    bins = band_index.shape[0]
    full = lambda step: (0, 0)
    if coarse_count == 64 and chunk == 2048:
        info = jnp.concatenate(
            [
                wavenumber[None, :].astype(jnp.int32),
                jnp.broadcast_to(jnp.asarray(first_sample, jnp.int32), (7, bins)),
            ],
            axis=0,
        )
        if layout is not None:
            def kernel(rec_ref, re_ref, im_ref, *scratch):
                dft_kernel_self(None, rec_ref, re_ref, im_ref, *scratch, layout=layout)

            operands = (records,)
            leading = []
        else:
            kernel = dft_kernel_self
            operands = (info, records)
            leading = [pl.BlockSpec((8, bins), full)]
        return pl.pallas_call(
            kernel,
            grid=(count // chunk,),
            in_specs=leading + [pl.BlockSpec((rows, chunk), lambda step: (0, step))],
            out_specs=[pl.BlockSpec((rows, bins), full), pl.BlockSpec((rows, bins), full)],
            out_shape=[
                jax.ShapeDtypeStruct((rows, bins), jnp.float32),
                jax.ShapeDtypeStruct((rows, bins), jnp.float32),
            ],
            scratch_shapes=[
                pltpu.VMEM((64, bins), jnp.float32),
                pltpu.VMEM((64, bins), jnp.float32),
                pltpu.VMEM((128, bins), jnp.float32),
                pltpu.VMEM((128, bins), jnp.float32),
            ],
            compiler_params=pltpu.CompilerParams(dimension_semantics=("arbitrary",)),
        )(*operands)
    coarse_outer = coarse_count // 8 if coarse_count % 8 == 0 else 1
    coarse_inner = coarse_count // coarse_outer
    cos_a, sin_a = combined(
        first_sample + lanes * coarse_inner * jnp.arange(coarse_outer, dtype=jnp.int32),
        lanes * jnp.arange(coarse_inner, dtype=jnp.int32),
    )
    nsin_a = -sin_a
    cos_b, sin_b = combined(
        16 * jnp.arange(lanes // 16, dtype=jnp.int32), jnp.arange(16, dtype=jnp.int32)
    )
    cos_b = cos_b * norm_scale
    sin_b = sin_b * norm_scale
    rows = records.shape[0]
    bins = band_index.shape[0]
    full = lambda step: (0, 0)
    return pl.pallas_call(
        dft_kernel,
        grid=(count // chunk,),
        in_specs=[
            pl.BlockSpec((rows, chunk), lambda step: (0, step)),
            pl.BlockSpec(cos_a.shape, full),
            pl.BlockSpec(nsin_a.shape, full),
            pl.BlockSpec(cos_b.shape, full),
            pl.BlockSpec(sin_b.shape, full),
        ],
        out_specs=[pl.BlockSpec((rows, bins), full), pl.BlockSpec((rows, bins), full)],
        out_shape=[
            jax.ShapeDtypeStruct((rows, bins), jnp.float32),
            jax.ShapeDtypeStruct((rows, bins), jnp.float32),
        ],
        compiler_params=pltpu.CompilerParams(dimension_semantics=("arbitrary",)),
    )(records, cos_a, nsin_a, cos_b, sin_b)


def gather_blocks(carried, count, rank, held=None):
    if count & (count - 1) != 0:
        return lax.all_gather(carried, "blk", axis=0, tiled=False)
    masks = []
    step = count // 2
    while step >= 1:
        masks.append(step)
        step //= 2
    if not masks:
        return carried[None]
    first = masks[0]
    rest = masks[1:]
    if held is None:
        pairs = [(source, source ^ first) for source in range(count)]
        held = jnp.stack([carried, lax.ppermute(carried, "blk", pairs)], axis=0)
    split = (held.shape[1] + 1) // 2
    halves = [held[:, :split], held[:, split:]]
    orders = [rest, rest[::-1]]
    results = []
    for part, order in zip(halves, orders):
        done = [first]
        for mask in order:
            pairs = [(source, source ^ mask) for source in range(count)]
            arrived = lax.ppermute(part, "blk", pairs)
            done.append(mask)
            axis = sorted(done, reverse=True).index(mask)
            part = jnp.stack([part, arrived], axis=axis)
        results.append(part.reshape((count,) + part.shape[len(masks):]))
    return jnp.concatenate(results, axis=1)


def per_device(raw, taps, send_list, recv_row):
    owners_count = lax.axis_size("blk")
    seg_count = lax.axis_size("seg")
    freq_count = lax.axis_size("freq")
    freq_rank = lax.axis_index("freq")
    sections, seg_dev, half_len = raw.shape
    records = raw.reshape(sections * seg_dev, half_len)
    device_bins = BINS // freq_count
    block_bins = device_bins // seg_count
    capacity = send_list.shape[2]

    def band_of(row_ids):
        owner_core = row_ids // device_bins
        local_row = row_ids % device_bins
        return (
            local_row // block_bins * freq_count + owner_core
        ) * block_bins + local_row % block_bins

    band_rows = band_of(jnp.arange(device_bins * freq_count, dtype=jnp.int32))
    real_t, imag_t = dft_fused(
        records, band_rows, freq_rank * half_len, (device_bins, block_bins, freq_count, half_len)
    )
    real_all = real_t.T
    imag_all = imag_t.T
    blocks = jnp.stack([real_all, imag_all], axis=1)
    blocks = blocks.reshape(freq_count, device_bins, 2, records.shape[0])
    if freq_count == 2:
        kept = jnp.where(freq_rank == 0, blocks[0], blocks[1])
        sent = jnp.where(freq_rank == 0, blocks[1], blocks[0])
        kept_blocks = kept.reshape(seg_count, block_bins, 2, -1)
        sent_blocks = sent.reshape(seg_count, block_bins, 2, -1)
        own_edges = jnp.concatenate(
            [kept_blocks[:, :HW], kept_blocks[:, block_bins - HW :]], axis=1
        ).reshape(seg_count * 2 * HW, 2, -1)
        message = jnp.concatenate([sent, own_edges], axis=0)
        arrived = swapped(message, "freq", 0)
        spectra = kept + arrived[:device_bins]
        their_edges = jnp.concatenate(
            [sent_blocks[:, :HW], sent_blocks[:, block_bins - HW :]], axis=1
        ).reshape(seg_count * 2 * HW, 2, -1)
        edge_spectra = (their_edges + arrived[device_bins:]).reshape(seg_count, 2, HW, 2, -1)
        partner = jnp.transpose(
            jnp.sqrt(
                edge_spectra[..., 0, :] * edge_spectra[..., 0, :]
                + edge_spectra[..., 1, :] * edge_spectra[..., 1, :]
                + 1e-06
            ),
            (1, 0, 2, 3),
        )
    else:
        spectra = lax.psum_scatter(
            blocks.reshape(device_bins * freq_count, 2, records.shape[0]),
            "freq",
            scatter_dimension=0,
            tiled=True,
        )
    real_part = spectra[:, 0]
    imag_part = spectra[:, 1]
    amplitude = jnp.sqrt(real_part * real_part + imag_part * imag_part + 1e-06)
    amp_blocks = amplitude.reshape(seg_count, block_bins, -1)
    if freq_count != 2:
        band_rims = jnp.stack([amp_blocks[:, :HW], amp_blocks[:, block_bins - HW :]])
        partner = swapped(band_rims, "freq", 0)
    zero_rim = jnp.zeros_like(partner[1][:1])
    right_prev = jnp.concatenate([zero_rim, partner[1][:-1]], axis=0)
    left_next = jnp.concatenate([partner[0][1:], zero_rim], axis=0)
    first_core = freq_rank == 0
    lower_rim = jnp.where(first_core, right_prev, partner[1])
    upper_rim = jnp.where(first_core, partner[0], left_next)
    padded = jnp.concatenate([lower_rim, amp_blocks, upper_rim], axis=1)
    window_sum = padded[:, 0:block_bins]
    for offset_step in range(1, 2 * HW + 1):
        window_sum = window_sum + padded[:, offset_step : offset_step + block_bins]
    span_ids = jnp.arange(seg_count, dtype=jnp.int32)[:, None]
    offsets = jnp.arange(block_bins, dtype=jnp.int32)[None, :]
    position = (span_ids * freq_count + freq_rank) * block_bins + offsets
    counted = jnp.minimum(position + HW, BINS - 1) - jnp.maximum(position - HW, 0) + 1
    smooth = window_sum / counted.astype(jnp.float32)[:, :, None]
    divisor = jnp.maximum(smooth, WHITEN_FLOOR).reshape(device_bins, -1)
    local_bins = freq_rank * device_bins + jnp.arange(device_bins, dtype=jnp.int32)
    response_re, response_im = response(band_of(local_bins), taps)
    scaled_re = real_part / divisor
    scaled_im = imag_part / divisor
    white_re = scaled_re * response_re[:, None] - scaled_im * response_im[:, None]
    white_im = scaled_re * response_im[:, None] + scaled_im * response_re[:, None]
    whitened = jnp.stack([white_re, white_im], axis=1).astype(jnp.bfloat16)
    whitened = whitened.reshape(seg_count, block_bins, 2, sections, seg_dev)
    whitened = jnp.transpose(whitened, (0, 3, 1, 2, 4))
    seg_rank = lax.axis_index("seg")
    all_segs = seg_dev * seg_count
    table = jnp.concatenate([send_list[0], recv_row[0]], axis=1).reshape(-1)
    table_len = table.shape[0]
    blk_rank = lax.axis_index("blk")
    fused_round = seg_count == 2 and owners_count >= 2 and owners_count & (owners_count - 1) == 0
    if fused_round:
        piece_width = block_bins * 2 * seg_dev
        slab_width = 128
        slab = jnp.pad(table.astype(jnp.bfloat16), (0, sections * slab_width - table_len))
        keep = lax.dynamic_index_in_dim(whitened, seg_rank, axis=0, keepdims=False)
        other = lax.dynamic_index_in_dim(whitened, 1 - seg_rank, axis=0, keepdims=False)
        keep_flat = jnp.concatenate(
            [keep.reshape(sections, -1), slab.reshape(sections, slab_width)], axis=1
        )
        other_flat = other.reshape(sections, -1)
        first = owners_count // 2
        from_blk = lax.ppermute(
            keep_flat, "blk", [(source, source ^ first) for source in range(owners_count)]
        )
        from_seg = lax.ppermute(other_flat, "seg", [(0, 1), (1, 0)])
        diagonal = [
            (source * 2 + side, (source ^ first) * 2 + 1 - side)
            for source in range(owners_count)
            for side in range(2)
        ]
        from_diagonal = lax.ppermute(other_flat, ("blk", "seg"), diagonal)

        def interleave(mine_segs, their_segs, table_slab):
            lanes_in = 2 * seg_dev
            joined = jnp.concatenate(
                [
                    mine_segs.reshape(sections, block_bins, lanes_in),
                    their_segs.reshape(sections, block_bins, lanes_in),
                ],
                axis=2,
            ).reshape(sections, -1)
            return jnp.concatenate([joined, table_slab], axis=1)

        held = jnp.stack(
            [
                interleave(keep_flat[:, :piece_width], from_seg, keep_flat[:, piece_width:]),
                interleave(from_blk[:, :piece_width], from_diagonal, from_blk[:, piece_width:]),
            ],
            axis=0,
        )
        moved = gather_blocks(None, owners_count, blk_rank, held=held)
        halves = [moved[:, :, : 2 * piece_width]]
        table_part = moved[:, :, 2 * piece_width :]
        table_part = table_part.reshape(owners_count, -1)[:, :table_len]
        half_segs = all_segs
        chunk_segs = seg_dev
    else:
        pieces = [lax.dynamic_index_in_dim(whitened, seg_rank, axis=0, keepdims=False)]
        for shift in range(1, seg_count):
            outgoing = lax.dynamic_index_in_dim(
                whitened, (seg_rank + shift) % seg_count, axis=0, keepdims=False
            )
            pairs = [(source, (source + shift) % seg_count) for source in range(seg_count)]
            flat = outgoing.reshape(sections, -1)
            pieces.append(lax.ppermute(flat, "seg", pairs).reshape(outgoing.shape))
        local = jnp.stack(pieces, axis=3).reshape(sections, block_bins, -1)
        table_width = local.shape[-1]
        slab = jnp.pad(table.astype(jnp.bfloat16), (0, sections * table_width - table_len))
        carried = jnp.concatenate([local, slab.reshape(sections, 1, table_width)], axis=1)
        everything = gather_blocks(carried.reshape(sections, -1), owners_count, blk_rank)
        everything = everything.reshape(owners_count, sections, block_bins + 1, table_width)
        halves = [everything[:, :, :block_bins]]
        table_part = everything[:, :, block_bins].reshape(owners_count, -1)[:, :table_len]
        half_segs = all_segs
        chunk_segs = all_segs
    table_part = table_part.astype(jnp.int32).reshape(owners_count, owners_count, 2 * capacity)
    position_ids = jnp.arange(owners_count, dtype=jnp.int32)
    if owners_count & (owners_count - 1) == 0:
        source_of = blk_rank ^ position_ids
        unpermute = (source_of[:, None] == position_ids[None, :]).astype(jnp.int32)
        table_part = jnp.sum(unpermute[:, :, None, None] * table_part[None], axis=1)
    else:
        source_of = position_ids
    send_all = table_part[..., :capacity]
    recv_all = table_part[..., capacity:]
    rows_count = owners_count * OWN
    chans_count = owners_count * sections
    chosen = jnp.transpose(send_all, (1, 0, 2))
    valid = (chosen < sections) & (recv_all < OWN)
    source_ids = (blk_rank ^ position_ids if owners_count & (owners_count - 1) == 0 else position_ids)[None, :, None]
    owner_ids = jnp.arange(owners_count, dtype=jnp.int32)[:, None, None]
    channel = jnp.where(valid, source_ids * sections + chosen, -1).reshape(-1)
    target = jnp.where(valid, owner_ids * OWN + recv_all, -1).reshape(-1)
    row_hot = (target[:, None] == jnp.arange(rows_count, dtype=jnp.int32)[None, :]).astype(
        jnp.bfloat16
    )
    chan_hot = (channel[:, None] == jnp.arange(chans_count, dtype=jnp.int32)[None, :]).astype(
        jnp.bfloat16
    )
    selector = jnp.einsum(
        "er,ec->rc", row_hot, chan_hot, preferred_element_type=jnp.float32
    ).astype(jnp.bfloat16)
    selector = selector.reshape(rows_count, owners_count, sections)
    cross = None
    for half in halves:
        data = half.reshape(owners_count, sections, block_bins, 2 * half_segs)
        routed = jnp.einsum(
            "rsc,scbq->brq", selector, data, preferred_element_type=jnp.float32
        ).astype(jnp.bfloat16)
        own = lax.dynamic_slice_in_dim(routed, blk_rank * OWN, OWN, axis=1)
        own_parts = own.reshape(own.shape[:-1] + (-1, 2, chunk_segs))
        rotated = jnp.stack([own_parts[..., 1, :], -own_parts[..., 0, :]], axis=-2)
        rotated = rotated.reshape(own.shape)
        lhs = jnp.concatenate([own, rotated], axis=1)
        part = jnp.einsum("bpq,bjq->bpj", lhs, routed, preferred_element_type=jnp.float32)
        cross = part if cross is None else cross + part
    cross = cross.reshape(block_bins, 2, OWN, rows_count)
    return jnp.transpose(cross, (1, 0, 2, 3)) / jnp.float32(all_segs)


def solution(mesh):
    placed = (
        P(("groups", "blk"), "seg", "freq"),
        P(),
        P(("groups", "blk"), None, None),
        P(("groups", "blk"), None, None),
    )
    return jax.shard_map(
        per_device,
        mesh=mesh,
        in_specs=placed,
        out_specs=P(None, ("seg", "freq"), ("groups", "blk"), None),
        check_vma=False,
    )
```

```python
import math

import jax
import jax.numpy as jnp
from jax import lax
from jax.experimental import pallas as pl
from jax.experimental.pallas import tpu as pltpu
from jax.sharding import PartitionSpec as P

SEG_LEN = 16384
BINS = 256
BAND_LO = 128
HW = 4
OWN = 16


WHITEN_FLOOR = 0.25
TWO_PI = 2.0 * math.pi


def swapped(value, axis, distance):
    mask = 2**distance
    pairs = [(source, source ^ mask) for source in range(lax.axis_size(axis))]
    return lax.ppermute(value, axis, pairs)


def dft_tables(band_index, sample_index):
    wavenumber = BAND_LO + band_index
    phase_int = wavenumber[:, None] * sample_index[None, :] % SEG_LEN
    angles = phase_int.astype(jnp.float32) * (TWO_PI / SEG_LEN)
    norm_scale = 1.0 / math.sqrt(SEG_LEN)
    cos_part = (jnp.cos(angles) * norm_scale).astype(jnp.bfloat16)
    sin_part = (-jnp.sin(angles) * norm_scale).astype(jnp.bfloat16)
    return (cos_part, sin_part)


def dft_tables_fast(band_index, first_sample, count):
    lanes = 128
    wavenumber = BAND_LO + band_index
    coarse = (first_sample + lanes * jnp.arange(count // lanes, dtype=jnp.int32))
    fine = jnp.arange(lanes, dtype=jnp.int32)
    coarse_angle = (wavenumber[:, None] * coarse[None, :] % SEG_LEN).astype(jnp.float32) * (
        TWO_PI / SEG_LEN
    )
    fine_angle = (wavenumber[:, None] * fine[None, :] % SEG_LEN).astype(jnp.float32) * (
        TWO_PI / SEG_LEN
    )
    cos_a = jnp.cos(coarse_angle)[:, :, None]
    sin_a = jnp.sin(coarse_angle)[:, :, None]
    cos_b = jnp.cos(fine_angle)[:, None, :]
    sin_b = jnp.sin(fine_angle)[:, None, :]
    norm_scale = 1.0 / math.sqrt(SEG_LEN)
    cos_sum = cos_a * cos_b - sin_a * sin_b
    sin_sum = sin_a * cos_b + cos_a * sin_b
    rows = band_index.shape[0]
    cos_part = (cos_sum * norm_scale).astype(jnp.bfloat16).reshape(rows, count)
    sin_part = (-sin_sum * norm_scale).astype(jnp.bfloat16).reshape(rows, count)
    return (cos_part, sin_part)


def response(band_index, taps):
    wavenumber = BAND_LO + band_index
    lag_index = jnp.arange(taps.shape[0], dtype=jnp.int32)
    phase_int = wavenumber[:, None] * lag_index[None, :] % SEG_LEN
    angles = phase_int.astype(jnp.float32) * (TWO_PI / SEG_LEN)
    real_part = jnp.dot(jnp.cos(angles), taps, precision=lax.Precision.HIGHEST)
    imag_part = jnp.dot(-jnp.sin(angles), taps, precision=lax.Precision.HIGHEST)
    return (real_part, imag_part)


def dft_kernel(rec_ref, cos_a_ref, nsin_a_ref, cos_b_ref, sin_b_ref, re_ref, im_ref):
    step = pl.program_id(0)
    lanes = cos_b_ref.shape[0]
    group = 8
    groups = rec_ref.shape[1] // (group * lanes)

    @pl.when(step == 0)
    def _():
        re_ref[...] = jnp.zeros_like(re_ref)
        im_ref[...] = jnp.zeros_like(im_ref)

    def one_group(index, carry):
        row = pl.multiple_of((step * groups + index) * group, group)
        cos_a = cos_a_ref[pl.ds(row, group), :]
        nsin_a = nsin_a_ref[pl.ds(row, group), :]
        cos_b = cos_b_ref[...]
        sin_b = sin_b_ref[...]
        for pair in range(group // 2):
            cos_parts = []
            sin_parts = []
            for half in range(2):
                at = 2 * pair + half
                ca = cos_a[at : at + 1]
                sa = nsin_a[at : at + 1]
                cos_parts.append(ca * cos_b + sa * sin_b)
                sin_parts.append(sa * cos_b - ca * sin_b)
            cos_tile = jnp.concatenate(cos_parts, axis=0).astype(jnp.bfloat16)
            sin_tile = jnp.concatenate(sin_parts, axis=0).astype(jnp.bfloat16)
            first = pl.multiple_of((index * group + 2 * pair) * lanes, 2 * lanes)
            rec = rec_ref[:, pl.ds(first, 2 * lanes)]
            re_ref[...] += jnp.dot(rec, cos_tile, preferred_element_type=jnp.float32)
            im_ref[...] += jnp.dot(rec, sin_tile, preferred_element_type=jnp.float32)
        return carry

    lax.fori_loop(0, groups, one_group, 0)


def dft_kernel_self(info_ref, rec_ref, re_ref, im_ref, cos_a_ref, nsin_a_ref, cos_b_ref, sin_b_ref, layout=None):
    step = pl.program_id(0)
    lanes = 128
    group = 8
    groups = rec_ref.shape[1] // (group * lanes)

    @pl.when(step == 0)
    def _():
        re_ref[...] = jnp.zeros_like(re_ref)
        im_ref[...] = jnp.zeros_like(im_ref)
        if layout is None:
            wavenumber = info_ref[0:1, :]
            first = info_ref[1:2, :]
        else:
            device_bins, block_bins, freq_count, half_len = layout
            row_ids = lax.broadcasted_iota(jnp.int32, (1, re_ref.shape[1]), 1)
            owner_core = row_ids // device_bins
            local_row = row_ids % device_bins
            band = (local_row // block_bins * freq_count + owner_core) * block_bins + local_row % block_bins
            wavenumber = BAND_LO + band
            first = lax.axis_index("freq") * half_len

        def cos_sin(steps):
            angle = (steps * wavenumber % SEG_LEN).astype(jnp.float32) * (TWO_PI / SEG_LEN)
            return jnp.cos(angle), jnp.sin(angle)

        width = wavenumber.shape[1]
        eight = lax.broadcasted_iota(jnp.int32, (8, width), 0)
        sixteen = lax.broadcasted_iota(jnp.int32, (16, width), 0)
        outer_cos, outer_sin = cos_sin(first + lanes * 8 * eight)
        inner_cos, inner_sin = cos_sin(lanes * eight)
        fine_outer_cos, fine_outer_sin = cos_sin(16 * eight)
        fine_inner_cos, fine_inner_sin = cos_sin(sixteen)
        norm_scale = 1.0 / math.sqrt(SEG_LEN)
        for outer in range(8):
            oc = outer_cos[outer : outer + 1]
            os_ = outer_sin[outer : outer + 1]
            cos_a_ref[outer * 8 : outer * 8 + 8, :] = oc * inner_cos - os_ * inner_sin
            nsin_a_ref[outer * 8 : outer * 8 + 8, :] = -(os_ * inner_cos + oc * inner_sin)
            fc = fine_outer_cos[outer : outer + 1]
            fs = fine_outer_sin[outer : outer + 1]
            cos_b_ref[outer * 16 : outer * 16 + 16, :] = (fc * fine_inner_cos - fs * fine_inner_sin) * norm_scale
            sin_b_ref[outer * 16 : outer * 16 + 16, :] = (fs * fine_inner_cos + fc * fine_inner_sin) * norm_scale

    def one_group(index, carry):
        row = pl.multiple_of((step * groups + index) * group, group)
        cos_a = cos_a_ref[pl.ds(row, group), :]
        nsin_a = nsin_a_ref[pl.ds(row, group), :]
        cos_b = cos_b_ref[...]
        sin_b = sin_b_ref[...]
        for pair in range(group // 2):
            cos_parts = []
            sin_parts = []
            for half in range(2):
                at = 2 * pair + half
                ca = cos_a[at : at + 1]
                sa = nsin_a[at : at + 1]
                cos_parts.append(ca * cos_b + sa * sin_b)
                sin_parts.append(sa * cos_b - ca * sin_b)
            cos_tile = jnp.concatenate(cos_parts, axis=0).astype(jnp.bfloat16)
            sin_tile = jnp.concatenate(sin_parts, axis=0).astype(jnp.bfloat16)
            first = pl.multiple_of((index * group + 2 * pair) * lanes, 2 * lanes)
            rec = rec_ref[:, pl.ds(first, 2 * lanes)]
            re_ref[...] += jnp.dot(rec, cos_tile, preferred_element_type=jnp.float32)
            im_ref[...] += jnp.dot(rec, sin_tile, preferred_element_type=jnp.float32)
        return carry

    lax.fori_loop(0, groups, one_group, 0)


def dft_fused(records, band_index, first_sample, layout=None):
    lanes = 128
    chunk = 2048
    count = records.shape[1]
    wavenumber = BAND_LO + band_index
    norm_scale = 1.0 / math.sqrt(SEG_LEN)

    def cos_sin(steps):
        angle = (steps[:, None] * wavenumber[None, :] % SEG_LEN).astype(jnp.float32) * (
            TWO_PI / SEG_LEN
        )
        return jnp.cos(angle), jnp.sin(angle)

    def combined(outer_steps, inner_steps):
        outer_cos, outer_sin = cos_sin(outer_steps)
        inner_cos, inner_sin = cos_sin(inner_steps)
        width = wavenumber.shape[0]
        cos_sum = outer_cos[:, None] * inner_cos[None] - outer_sin[:, None] * inner_sin[None]
        sin_sum = outer_sin[:, None] * inner_cos[None] + outer_cos[:, None] * inner_sin[None]
        return cos_sum.reshape(-1, width), sin_sum.reshape(-1, width)

    coarse_count = count // lanes
    rows = records.shape[0]
    bins = band_index.shape[0]
    full = lambda step: (0, 0)
    if coarse_count == 64 and chunk == 2048:
        info = jnp.concatenate(
            [
                wavenumber[None, :].astype(jnp.int32),
                jnp.broadcast_to(jnp.asarray(first_sample, jnp.int32), (7, bins)),
            ],
            axis=0,
        )
        if layout is not None:
            def kernel(rec_ref, re_ref, im_ref, *scratch):
                dft_kernel_self(None, rec_ref, re_ref, im_ref, *scratch, layout=layout)

            operands = (records,)
            leading = []
        else:
            kernel = dft_kernel_self
            operands = (info, records)
            leading = [pl.BlockSpec((8, bins), full)]
        return pl.pallas_call(
            kernel,
            grid=(count // chunk,),
            in_specs=leading + [pl.BlockSpec((rows, chunk), lambda step: (0, step))],
            out_specs=[pl.BlockSpec((rows, bins), full), pl.BlockSpec((rows, bins), full)],
            out_shape=[
                jax.ShapeDtypeStruct((rows, bins), jnp.float32),
                jax.ShapeDtypeStruct((rows, bins), jnp.float32),
            ],
            scratch_shapes=[
                pltpu.VMEM((64, bins), jnp.float32),
                pltpu.VMEM((64, bins), jnp.float32),
                pltpu.VMEM((128, bins), jnp.float32),
                pltpu.VMEM((128, bins), jnp.float32),
            ],
            compiler_params=pltpu.CompilerParams(dimension_semantics=("arbitrary",)),
        )(*operands)
    coarse_outer = coarse_count // 8 if coarse_count % 8 == 0 else 1
    coarse_inner = coarse_count // coarse_outer
    cos_a, sin_a = combined(
        first_sample + lanes * coarse_inner * jnp.arange(coarse_outer, dtype=jnp.int32),
        lanes * jnp.arange(coarse_inner, dtype=jnp.int32),
    )
    nsin_a = -sin_a
    cos_b, sin_b = combined(
        16 * jnp.arange(lanes // 16, dtype=jnp.int32), jnp.arange(16, dtype=jnp.int32)
    )
    cos_b = cos_b * norm_scale
    sin_b = sin_b * norm_scale
    rows = records.shape[0]
    bins = band_index.shape[0]
    full = lambda step: (0, 0)
    return pl.pallas_call(
        dft_kernel,
        grid=(count // chunk,),
        in_specs=[
            pl.BlockSpec((rows, chunk), lambda step: (0, step)),
            pl.BlockSpec(cos_a.shape, full),
            pl.BlockSpec(nsin_a.shape, full),
            pl.BlockSpec(cos_b.shape, full),
            pl.BlockSpec(sin_b.shape, full),
        ],
        out_specs=[pl.BlockSpec((rows, bins), full), pl.BlockSpec((rows, bins), full)],
        out_shape=[
            jax.ShapeDtypeStruct((rows, bins), jnp.float32),
            jax.ShapeDtypeStruct((rows, bins), jnp.float32),
        ],
        compiler_params=pltpu.CompilerParams(dimension_semantics=("arbitrary",)),
    )(records, cos_a, nsin_a, cos_b, sin_b)


def gather_blocks(carried, count, rank, held=None):
    if count & (count - 1) != 0:
        return lax.all_gather(carried, "blk", axis=0, tiled=False)
    masks = []
    step = count // 2
    while step >= 1:
        masks.append(step)
        step //= 2
    if not masks:
        return carried[None]
    first = masks[0]
    rest = masks[1:]
    if held is None:
        pairs = [(source, source ^ first) for source in range(count)]
        held = jnp.stack([carried, lax.ppermute(carried, "blk", pairs)], axis=0)
    split = (held.shape[1] + 1) // 2
    halves = [held[:, :split], held[:, split:]]
    orders = [rest, rest[::-1]]
    results = []
    for part, order in zip(halves, orders):
        done = [first]
        for mask in order:
            pairs = [(source, source ^ mask) for source in range(count)]
            arrived = lax.ppermute(part, "blk", pairs)
            done.append(mask)
            axis = sorted(done, reverse=True).index(mask)
            part = jnp.stack([part, arrived], axis=axis)
        results.append(part.reshape((count,) + part.shape[len(masks):]))
    return jnp.concatenate(results, axis=1)


def per_device(raw, taps, send_list, recv_row):
    owners_count = lax.axis_size("blk")
    seg_count = lax.axis_size("seg")
    freq_count = lax.axis_size("freq")
    freq_rank = lax.axis_index("freq")
    sections, seg_dev, half_len = raw.shape
    records = raw.reshape(sections * seg_dev, half_len)
    device_bins = BINS // freq_count
    block_bins = device_bins // seg_count
    capacity = send_list.shape[2]

    def band_of(row_ids):
        owner_core = row_ids // device_bins
        local_row = row_ids % device_bins
        return (
            local_row // block_bins * freq_count + owner_core
        ) * block_bins + local_row % block_bins

    band_rows = band_of(jnp.arange(device_bins * freq_count, dtype=jnp.int32))
    real_t, imag_t = dft_fused(
        records, band_rows, freq_rank * half_len, (device_bins, block_bins, freq_count, half_len)
    )
    real_all = real_t.T
    imag_all = imag_t.T
    if freq_count == 2:
        blocks = jnp.stack([real_all, imag_all], axis=0)
        blocks = blocks.reshape(2, freq_count, device_bins, records.shape[0])
        kept = jnp.where(freq_rank == 0, blocks[:, 0], blocks[:, 1])
        sent = jnp.where(freq_rank == 0, blocks[:, 1], blocks[:, 0])
        kept_blocks = kept.reshape(2, seg_count, block_bins, -1)
        sent_blocks = sent.reshape(2, seg_count, block_bins, -1)
        own_edges = jnp.concatenate(
            [kept_blocks[:, :, :HW], kept_blocks[:, :, block_bins - HW :]], axis=2
        ).reshape(2, seg_count * 2 * HW, -1)
        message = jnp.concatenate([sent, own_edges], axis=1)
        arrived = swapped(message, "freq", 0)
        spectra_pair = kept + arrived[:, :device_bins]
        their_edges = jnp.concatenate(
            [sent_blocks[:, :, :HW], sent_blocks[:, :, block_bins - HW :]], axis=2
        ).reshape(2, seg_count * 2 * HW, -1)
        edge_spectra = (their_edges + arrived[:, device_bins:]).reshape(2, seg_count, 2, HW, -1)
        partner = jnp.transpose(
            jnp.sqrt(edge_spectra[0] * edge_spectra[0] + edge_spectra[1] * edge_spectra[1] + 1e-06),
            (1, 0, 2, 3),
        )
        spectra = jnp.stack([spectra_pair[0], spectra_pair[1]], axis=1)
    else:
        blocks = jnp.stack([real_all, imag_all], axis=1)
        spectra = lax.psum_scatter(
            blocks.reshape(device_bins * freq_count, 2, records.shape[0]),
            "freq",
            scatter_dimension=0,
            tiled=True,
        )
    real_part = spectra[:, 0]
    imag_part = spectra[:, 1]
    if freq_count == 2:
        real_part = spectra_pair[0]
        imag_part = spectra_pair[1]
    amplitude = jnp.sqrt(real_part * real_part + imag_part * imag_part + 1e-06)
    amp_blocks = amplitude.reshape(seg_count, block_bins, -1)
    if freq_count != 2:
        band_rims = jnp.stack([amp_blocks[:, :HW], amp_blocks[:, block_bins - HW :]])
        partner = swapped(band_rims, "freq", 0)
    zero_rim = jnp.zeros_like(partner[1][:1])
    right_prev = jnp.concatenate([zero_rim, partner[1][:-1]], axis=0)
    left_next = jnp.concatenate([partner[0][1:], zero_rim], axis=0)
    first_core = freq_rank == 0
    lower_rim = jnp.where(first_core, right_prev, partner[1])
    upper_rim = jnp.where(first_core, partner[0], left_next)
    padded = jnp.concatenate([lower_rim, amp_blocks, upper_rim], axis=1)
    window_sum = padded[:, 0:block_bins]
    for offset_step in range(1, 2 * HW + 1):
        window_sum = window_sum + padded[:, offset_step : offset_step + block_bins]
    span_ids = jnp.arange(seg_count, dtype=jnp.int32)[:, None]
    offsets = jnp.arange(block_bins, dtype=jnp.int32)[None, :]
    position = (span_ids * freq_count + freq_rank) * block_bins + offsets
    counted = jnp.minimum(position + HW, BINS - 1) - jnp.maximum(position - HW, 0) + 1
    smooth = window_sum / counted.astype(jnp.float32)[:, :, None]
    divisor = jnp.maximum(smooth, WHITEN_FLOOR).reshape(device_bins, -1)
    local_bins = freq_rank * device_bins + jnp.arange(device_bins, dtype=jnp.int32)
    response_re, response_im = response(band_of(local_bins), taps)
    scaled_re = real_part / divisor
    scaled_im = imag_part / divisor
    white_re = scaled_re * response_re[:, None] - scaled_im * response_im[:, None]
    white_im = scaled_re * response_im[:, None] + scaled_im * response_re[:, None]
    whitened = jnp.stack([white_re, white_im], axis=1).astype(jnp.bfloat16)
    whitened = whitened.reshape(seg_count, block_bins, 2, sections, seg_dev)
    whitened = jnp.transpose(whitened, (0, 3, 1, 2, 4))
    seg_rank = lax.axis_index("seg")
    all_segs = seg_dev * seg_count
    table = jnp.concatenate([send_list[0], recv_row[0]], axis=1).reshape(-1)
    table_len = table.shape[0]
    blk_rank = lax.axis_index("blk")
    fused_round = seg_count == 2 and owners_count >= 2 and owners_count & (owners_count - 1) == 0
    if fused_round:
        piece_width = block_bins * 2 * seg_dev
        slab_width = 128
        slab = jnp.pad(table.astype(jnp.bfloat16), (0, sections * slab_width - table_len))
        keep = lax.dynamic_index_in_dim(whitened, seg_rank, axis=0, keepdims=False)
        other = lax.dynamic_index_in_dim(whitened, 1 - seg_rank, axis=0, keepdims=False)
        keep_flat = jnp.concatenate(
            [keep.reshape(sections, -1), slab.reshape(sections, slab_width)], axis=1
        )
        other_flat = other.reshape(sections, -1)
        first = owners_count // 2
        from_blk = lax.ppermute(
            keep_flat, "blk", [(source, source ^ first) for source in range(owners_count)]
        )
        from_seg = lax.ppermute(other_flat, "seg", [(0, 1), (1, 0)])
        diagonal = [
            (source * 2 + side, (source ^ first) * 2 + 1 - side)
            for source in range(owners_count)
            for side in range(2)
        ]
        from_diagonal = lax.ppermute(other_flat, ("blk", "seg"), diagonal)

        def interleave(mine_segs, their_segs, table_slab):
            lanes_in = 2 * seg_dev
            joined = jnp.concatenate(
                [
                    mine_segs.reshape(sections, block_bins, lanes_in),
                    their_segs.reshape(sections, block_bins, lanes_in),
                ],
                axis=2,
            ).reshape(sections, -1)
            return jnp.concatenate([joined, table_slab], axis=1)

        held = jnp.stack(
            [
                interleave(keep_flat[:, :piece_width], from_seg, keep_flat[:, piece_width:]),
                interleave(from_blk[:, :piece_width], from_diagonal, from_blk[:, piece_width:]),
            ],
            axis=0,
        )
        moved = gather_blocks(None, owners_count, blk_rank, held=held)
        halves = [moved[:, :, : 2 * piece_width]]
        table_part = moved[:, :, 2 * piece_width :]
        table_part = table_part.reshape(owners_count, -1)[:, :table_len]
        half_segs = all_segs
        chunk_segs = seg_dev
    else:
        pieces = [lax.dynamic_index_in_dim(whitened, seg_rank, axis=0, keepdims=False)]
        for shift in range(1, seg_count):
            outgoing = lax.dynamic_index_in_dim(
                whitened, (seg_rank + shift) % seg_count, axis=0, keepdims=False
            )
            pairs = [(source, (source + shift) % seg_count) for source in range(seg_count)]
            flat = outgoing.reshape(sections, -1)
            pieces.append(lax.ppermute(flat, "seg", pairs).reshape(outgoing.shape))
        local = jnp.stack(pieces, axis=3).reshape(sections, block_bins, -1)
        table_width = local.shape[-1]
        slab = jnp.pad(table.astype(jnp.bfloat16), (0, sections * table_width - table_len))
        carried = jnp.concatenate([local, slab.reshape(sections, 1, table_width)], axis=1)
        everything = gather_blocks(carried.reshape(sections, -1), owners_count, blk_rank)
        everything = everything.reshape(owners_count, sections, block_bins + 1, table_width)
        halves = [everything[:, :, :block_bins]]
        table_part = everything[:, :, block_bins].reshape(owners_count, -1)[:, :table_len]
        half_segs = all_segs
        chunk_segs = all_segs
    table_part = table_part.astype(jnp.int32).reshape(owners_count, owners_count, 2 * capacity)
    position_ids = jnp.arange(owners_count, dtype=jnp.int32)
    if owners_count & (owners_count - 1) == 0:
        source_of = blk_rank ^ position_ids
        unpermute = (source_of[:, None] == position_ids[None, :]).astype(jnp.int32)
        table_part = jnp.sum(unpermute[:, :, None, None] * table_part[None], axis=1)
    else:
        source_of = position_ids
    send_all = table_part[..., :capacity]
    recv_all = table_part[..., capacity:]
    rows_count = owners_count * OWN
    chans_count = owners_count * sections
    chosen = jnp.transpose(send_all, (1, 0, 2))
    valid = (chosen < sections) & (recv_all < OWN)
    source_ids = (blk_rank ^ position_ids if owners_count & (owners_count - 1) == 0 else position_ids)[None, :, None]
    owner_ids = jnp.arange(owners_count, dtype=jnp.int32)[:, None, None]
    channel = jnp.where(valid, source_ids * sections + chosen, -1).reshape(-1)
    target = jnp.where(valid, owner_ids * OWN + recv_all, -1).reshape(-1)
    row_hot = (target[:, None] == jnp.arange(rows_count, dtype=jnp.int32)[None, :]).astype(
        jnp.bfloat16
    )
    chan_hot = (channel[:, None] == jnp.arange(chans_count, dtype=jnp.int32)[None, :]).astype(
        jnp.bfloat16
    )
    selector = jnp.einsum(
        "er,ec->rc", row_hot, chan_hot, preferred_element_type=jnp.float32
    ).astype(jnp.bfloat16)
    selector = selector.reshape(rows_count, owners_count, sections)
    cross = None
    for half in halves:
        data = half.reshape(owners_count, sections, block_bins, 2 * half_segs)
        routed = jnp.einsum(
            "rsc,scbq->brq", selector, data, preferred_element_type=jnp.float32
        ).astype(jnp.bfloat16)
        own = lax.dynamic_slice_in_dim(routed, blk_rank * OWN, OWN, axis=1)
        own_parts = own.reshape(own.shape[:-1] + (-1, 2, chunk_segs))
        rotated = jnp.stack([own_parts[..., 1, :], -own_parts[..., 0, :]], axis=-2)
        rotated = rotated.reshape(own.shape)
        lhs = jnp.concatenate([own, rotated], axis=1)
        part = jnp.einsum("bpq,bjq->bpj", lhs, routed, preferred_element_type=jnp.float32)
        cross = part if cross is None else cross + part
    cross = cross.reshape(block_bins, 2, OWN, rows_count)
    return jnp.transpose(cross, (1, 0, 2, 3)) / jnp.float32(all_segs)


def solution(mesh):
    placed = (
        P(("groups", "blk"), "seg", "freq"),
        P(),
        P(("groups", "blk"), None, None),
        P(("groups", "blk"), None, None),
    )
    return jax.shard_map(
        per_device,
        mesh=mesh,
        in_specs=placed,
        out_specs=P(None, ("seg", "freq"), ("groups", "blk"), None),
        check_vma=False,
    )
```

```python
import math

import jax
import jax.numpy as jnp
from jax import lax
from jax.experimental import pallas as pl
from jax.experimental.pallas import tpu as pltpu
from jax.sharding import PartitionSpec as P

SEG_LEN = 16384
BINS = 256
BAND_LO = 128
HW = 4
OWN = 16


WHITEN_FLOOR = 0.25
TWO_PI = 2.0 * math.pi


def swapped(value, axis, distance):
    mask = 2**distance
    pairs = [(source, source ^ mask) for source in range(lax.axis_size(axis))]
    return lax.ppermute(value, axis, pairs)


def dft_tables(band_index, sample_index):
    wavenumber = BAND_LO + band_index
    phase_int = wavenumber[:, None] * sample_index[None, :] % SEG_LEN
    angles = phase_int.astype(jnp.float32) * (TWO_PI / SEG_LEN)
    norm_scale = 1.0 / math.sqrt(SEG_LEN)
    cos_part = (jnp.cos(angles) * norm_scale).astype(jnp.bfloat16)
    sin_part = (-jnp.sin(angles) * norm_scale).astype(jnp.bfloat16)
    return (cos_part, sin_part)


def dft_tables_fast(band_index, first_sample, count):
    lanes = 128
    wavenumber = BAND_LO + band_index
    coarse = (first_sample + lanes * jnp.arange(count // lanes, dtype=jnp.int32))
    fine = jnp.arange(lanes, dtype=jnp.int32)
    coarse_angle = (wavenumber[:, None] * coarse[None, :] % SEG_LEN).astype(jnp.float32) * (
        TWO_PI / SEG_LEN
    )
    fine_angle = (wavenumber[:, None] * fine[None, :] % SEG_LEN).astype(jnp.float32) * (
        TWO_PI / SEG_LEN
    )
    cos_a = jnp.cos(coarse_angle)[:, :, None]
    sin_a = jnp.sin(coarse_angle)[:, :, None]
    cos_b = jnp.cos(fine_angle)[:, None, :]
    sin_b = jnp.sin(fine_angle)[:, None, :]
    norm_scale = 1.0 / math.sqrt(SEG_LEN)
    cos_sum = cos_a * cos_b - sin_a * sin_b
    sin_sum = sin_a * cos_b + cos_a * sin_b
    rows = band_index.shape[0]
    cos_part = (cos_sum * norm_scale).astype(jnp.bfloat16).reshape(rows, count)
    sin_part = (-sin_sum * norm_scale).astype(jnp.bfloat16).reshape(rows, count)
    return (cos_part, sin_part)


def response(band_index, taps):
    wavenumber = BAND_LO + band_index
    lag_index = jnp.arange(taps.shape[0], dtype=jnp.int32)
    phase_int = wavenumber[:, None] * lag_index[None, :] % SEG_LEN
    angles = phase_int.astype(jnp.float32) * (TWO_PI / SEG_LEN)
    real_part = jnp.dot(jnp.cos(angles), taps, precision=lax.Precision.HIGHEST)
    imag_part = jnp.dot(-jnp.sin(angles), taps, precision=lax.Precision.HIGHEST)
    return (real_part, imag_part)


def dft_kernel(rec_ref, cos_a_ref, nsin_a_ref, cos_b_ref, sin_b_ref, re_ref, im_ref):
    step = pl.program_id(0)
    lanes = cos_b_ref.shape[0]
    group = 8
    groups = rec_ref.shape[1] // (group * lanes)

    @pl.when(step == 0)
    def _():
        re_ref[...] = jnp.zeros_like(re_ref)
        im_ref[...] = jnp.zeros_like(im_ref)

    def one_group(index, carry):
        row = pl.multiple_of((step * groups + index) * group, group)
        cos_a = cos_a_ref[pl.ds(row, group), :]
        nsin_a = nsin_a_ref[pl.ds(row, group), :]
        cos_b = cos_b_ref[...]
        sin_b = sin_b_ref[...]
        for pair in range(group // 2):
            cos_parts = []
            sin_parts = []
            for half in range(2):
                at = 2 * pair + half
                ca = cos_a[at : at + 1]
                sa = nsin_a[at : at + 1]
                cos_parts.append(ca * cos_b + sa * sin_b)
                sin_parts.append(sa * cos_b - ca * sin_b)
            cos_tile = jnp.concatenate(cos_parts, axis=0).astype(jnp.bfloat16)
            sin_tile = jnp.concatenate(sin_parts, axis=0).astype(jnp.bfloat16)
            first = pl.multiple_of((index * group + 2 * pair) * lanes, 2 * lanes)
            rec = rec_ref[:, pl.ds(first, 2 * lanes)]
            re_ref[...] += jnp.dot(rec, cos_tile, preferred_element_type=jnp.float32)
            im_ref[...] += jnp.dot(rec, sin_tile, preferred_element_type=jnp.float32)
        return carry

    lax.fori_loop(0, groups, one_group, 0)


def dft_kernel_self(info_ref, rec_ref, re_ref, im_ref, cos_a_ref, nsin_a_ref, cos_b_ref, sin_b_ref, layout=None):
    step = pl.program_id(0)
    lanes = 128
    group = 8
    groups = rec_ref.shape[1] // (group * lanes)

    @pl.when(step == 0)
    def _():
        re_ref[...] = jnp.zeros_like(re_ref)
        im_ref[...] = jnp.zeros_like(im_ref)
        if layout is None:
            wavenumber = info_ref[0:1, :]
            first = info_ref[1:2, :]
        else:
            device_bins, block_bins, freq_count, half_len = layout
            row_ids = lax.broadcasted_iota(jnp.int32, (1, re_ref.shape[0]), 1)
            owner_core = row_ids // device_bins
            local_row = row_ids % device_bins
            band = (local_row // block_bins * freq_count + owner_core) * block_bins + local_row % block_bins
            wavenumber = BAND_LO + band
            first = lax.axis_index("freq") * half_len

        def cos_sin(steps):
            angle = (steps * wavenumber % SEG_LEN).astype(jnp.float32) * (TWO_PI / SEG_LEN)
            return jnp.cos(angle), jnp.sin(angle)

        width = wavenumber.shape[1]
        eight = lax.broadcasted_iota(jnp.int32, (8, width), 0)
        sixteen = lax.broadcasted_iota(jnp.int32, (16, width), 0)
        outer_cos, outer_sin = cos_sin(first + lanes * 8 * eight)
        inner_cos, inner_sin = cos_sin(lanes * eight)
        fine_outer_cos, fine_outer_sin = cos_sin(16 * eight)
        fine_inner_cos, fine_inner_sin = cos_sin(sixteen)
        norm_scale = 1.0 / math.sqrt(SEG_LEN)
        for outer in range(8):
            oc = outer_cos[outer : outer + 1]
            os_ = outer_sin[outer : outer + 1]
            cos_a_ref[outer * 8 : outer * 8 + 8, :] = oc * inner_cos - os_ * inner_sin
            nsin_a_ref[outer * 8 : outer * 8 + 8, :] = -(os_ * inner_cos + oc * inner_sin)
            fc = fine_outer_cos[outer : outer + 1]
            fs = fine_outer_sin[outer : outer + 1]
            cos_b_ref[outer * 16 : outer * 16 + 16, :] = (fc * fine_inner_cos - fs * fine_inner_sin) * norm_scale
            sin_b_ref[outer * 16 : outer * 16 + 16, :] = (fs * fine_inner_cos + fc * fine_inner_sin) * norm_scale

    def one_group(index, carry):
        row = pl.multiple_of((step * groups + index) * group, group)
        cos_a = cos_a_ref[pl.ds(row, group), :]
        nsin_a = nsin_a_ref[pl.ds(row, group), :]
        cos_b = cos_b_ref[...]
        sin_b = sin_b_ref[...]
        for pair in range(group // 2):
            cos_parts = []
            sin_parts = []
            for half in range(2):
                at = 2 * pair + half
                ca = cos_a[at : at + 1]
                sa = nsin_a[at : at + 1]
                cos_parts.append(ca * cos_b + sa * sin_b)
                sin_parts.append(sa * cos_b - ca * sin_b)
            cos_tile = jnp.concatenate(cos_parts, axis=0).astype(jnp.bfloat16)
            sin_tile = jnp.concatenate(sin_parts, axis=0).astype(jnp.bfloat16)
            first = pl.multiple_of((index * group + 2 * pair) * lanes, 2 * lanes)
            rec = rec_ref[:, pl.ds(first, 2 * lanes)]
            re_ref[...] += lax.dot_general(cos_tile, rec, (((0,), (1,)), ((), ())), preferred_element_type=jnp.float32)
            im_ref[...] += lax.dot_general(sin_tile, rec, (((0,), (1,)), ((), ())), preferred_element_type=jnp.float32)
        return carry

    lax.fori_loop(0, groups, one_group, 0)


def dft_fused(records, band_index, first_sample, layout=None):
    lanes = 128
    chunk = 2048
    count = records.shape[1]
    wavenumber = BAND_LO + band_index
    norm_scale = 1.0 / math.sqrt(SEG_LEN)

    def cos_sin(steps):
        angle = (steps[:, None] * wavenumber[None, :] % SEG_LEN).astype(jnp.float32) * (
            TWO_PI / SEG_LEN
        )
        return jnp.cos(angle), jnp.sin(angle)

    def combined(outer_steps, inner_steps):
        outer_cos, outer_sin = cos_sin(outer_steps)
        inner_cos, inner_sin = cos_sin(inner_steps)
        width = wavenumber.shape[0]
        cos_sum = outer_cos[:, None] * inner_cos[None] - outer_sin[:, None] * inner_sin[None]
        sin_sum = outer_sin[:, None] * inner_cos[None] + outer_cos[:, None] * inner_sin[None]
        return cos_sum.reshape(-1, width), sin_sum.reshape(-1, width)

    coarse_count = count // lanes
    rows = records.shape[0]
    bins = band_index.shape[0]
    full = lambda step: (0, 0)
    if coarse_count == 64 and chunk == 2048:
        info = jnp.concatenate(
            [
                wavenumber[None, :].astype(jnp.int32),
                jnp.broadcast_to(jnp.asarray(first_sample, jnp.int32), (7, bins)),
            ],
            axis=0,
        )
        if layout is not None:
            def kernel(rec_ref, re_ref, im_ref, *scratch):
                dft_kernel_self(None, rec_ref, re_ref, im_ref, *scratch, layout=layout)

            operands = (records,)
            leading = []
        else:
            kernel = dft_kernel_self
            operands = (info, records)
            leading = [pl.BlockSpec((8, bins), full)]
        return pl.pallas_call(
            kernel,
            grid=(count // chunk,),
            in_specs=leading + [pl.BlockSpec((rows, chunk), lambda step: (0, step))],
            out_specs=[pl.BlockSpec((bins, rows), full), pl.BlockSpec((bins, rows), full)],
            out_shape=[
                jax.ShapeDtypeStruct((bins, rows), jnp.float32),
                jax.ShapeDtypeStruct((bins, rows), jnp.float32),
            ],
            scratch_shapes=[
                pltpu.VMEM((64, bins), jnp.float32),
                pltpu.VMEM((64, bins), jnp.float32),
                pltpu.VMEM((128, bins), jnp.float32),
                pltpu.VMEM((128, bins), jnp.float32),
            ],
            compiler_params=pltpu.CompilerParams(dimension_semantics=("arbitrary",)),
        )(*operands)
    coarse_outer = coarse_count // 8 if coarse_count % 8 == 0 else 1
    coarse_inner = coarse_count // coarse_outer
    cos_a, sin_a = combined(
        first_sample + lanes * coarse_inner * jnp.arange(coarse_outer, dtype=jnp.int32),
        lanes * jnp.arange(coarse_inner, dtype=jnp.int32),
    )
    nsin_a = -sin_a
    cos_b, sin_b = combined(
        16 * jnp.arange(lanes // 16, dtype=jnp.int32), jnp.arange(16, dtype=jnp.int32)
    )
    cos_b = cos_b * norm_scale
    sin_b = sin_b * norm_scale
    rows = records.shape[0]
    bins = band_index.shape[0]
    full = lambda step: (0, 0)
    return pl.pallas_call(
        dft_kernel,
        grid=(count // chunk,),
        in_specs=[
            pl.BlockSpec((rows, chunk), lambda step: (0, step)),
            pl.BlockSpec(cos_a.shape, full),
            pl.BlockSpec(nsin_a.shape, full),
            pl.BlockSpec(cos_b.shape, full),
            pl.BlockSpec(sin_b.shape, full),
        ],
        out_specs=[pl.BlockSpec((rows, bins), full), pl.BlockSpec((rows, bins), full)],
        out_shape=[
            jax.ShapeDtypeStruct((rows, bins), jnp.float32),
            jax.ShapeDtypeStruct((rows, bins), jnp.float32),
        ],
        compiler_params=pltpu.CompilerParams(dimension_semantics=("arbitrary",)),
    )(records, cos_a, nsin_a, cos_b, sin_b)


def gather_blocks(carried, count, rank, held=None):
    if count & (count - 1) != 0:
        return lax.all_gather(carried, "blk", axis=0, tiled=False)
    masks = []
    step = count // 2
    while step >= 1:
        masks.append(step)
        step //= 2
    if not masks:
        return carried[None]
    first = masks[0]
    rest = masks[1:]
    if held is None:
        pairs = [(source, source ^ first) for source in range(count)]
        held = jnp.stack([carried, lax.ppermute(carried, "blk", pairs)], axis=0)
    split = (held.shape[1] + 1) // 2
    halves = [held[:, :split], held[:, split:]]
    orders = [rest, rest[::-1]]
    results = []
    for part, order in zip(halves, orders):
        done = [first]
        for mask in order:
            pairs = [(source, source ^ mask) for source in range(count)]
            arrived = lax.ppermute(part, "blk", pairs)
            done.append(mask)
            axis = sorted(done, reverse=True).index(mask)
            part = jnp.stack([part, arrived], axis=axis)
        results.append(part.reshape((count,) + part.shape[len(masks):]))
    return jnp.concatenate(results, axis=1)


def per_device(raw, taps, send_list, recv_row):
    owners_count = lax.axis_size("blk")
    seg_count = lax.axis_size("seg")
    freq_count = lax.axis_size("freq")
    freq_rank = lax.axis_index("freq")
    sections, seg_dev, half_len = raw.shape
    records = raw.reshape(sections * seg_dev, half_len)
    device_bins = BINS // freq_count
    block_bins = device_bins // seg_count
    capacity = send_list.shape[2]

    def band_of(row_ids):
        owner_core = row_ids // device_bins
        local_row = row_ids % device_bins
        return (
            local_row // block_bins * freq_count + owner_core
        ) * block_bins + local_row % block_bins

    band_rows = band_of(jnp.arange(device_bins * freq_count, dtype=jnp.int32))
    real_t, imag_t = dft_fused(
        records, band_rows, freq_rank * half_len, (device_bins, block_bins, freq_count, half_len)
    )
    real_all = real_t
    imag_all = imag_t
    if freq_count == 2:
        blocks = jnp.stack([real_all, imag_all], axis=0)
        blocks = blocks.reshape(2, freq_count, device_bins, records.shape[0])
        kept = jnp.where(freq_rank == 0, blocks[:, 0], blocks[:, 1])
        sent = jnp.where(freq_rank == 0, blocks[:, 1], blocks[:, 0])
        kept_blocks = kept.reshape(2, seg_count, block_bins, -1)
        sent_blocks = sent.reshape(2, seg_count, block_bins, -1)
        own_edges = jnp.concatenate(
            [kept_blocks[:, :, :HW], kept_blocks[:, :, block_bins - HW :]], axis=2
        ).reshape(2, seg_count * 2 * HW, -1)
        message = jnp.concatenate([sent, own_edges], axis=1)
        arrived = swapped(message, "freq", 0)
        spectra_pair = kept + arrived[:, :device_bins]
        their_edges = jnp.concatenate(
            [sent_blocks[:, :, :HW], sent_blocks[:, :, block_bins - HW :]], axis=2
        ).reshape(2, seg_count * 2 * HW, -1)
        edge_spectra = (their_edges + arrived[:, device_bins:]).reshape(2, seg_count, 2, HW, -1)
        partner = jnp.transpose(
            jnp.sqrt(edge_spectra[0] * edge_spectra[0] + edge_spectra[1] * edge_spectra[1] + 1e-06),
            (1, 0, 2, 3),
        )
        spectra = jnp.stack([spectra_pair[0], spectra_pair[1]], axis=1)
    else:
        blocks = jnp.stack([real_all, imag_all], axis=1)
        spectra = lax.psum_scatter(
            blocks.reshape(device_bins * freq_count, 2, records.shape[0]),
            "freq",
            scatter_dimension=0,
            tiled=True,
        )
    real_part = spectra[:, 0]
    imag_part = spectra[:, 1]
    if freq_count == 2:
        real_part = spectra_pair[0]
        imag_part = spectra_pair[1]
    amplitude = jnp.sqrt(real_part * real_part + imag_part * imag_part + 1e-06)
    amp_blocks = amplitude.reshape(seg_count, block_bins, -1)
    if freq_count != 2:
        band_rims = jnp.stack([amp_blocks[:, :HW], amp_blocks[:, block_bins - HW :]])
        partner = swapped(band_rims, "freq", 0)
    zero_rim = jnp.zeros_like(partner[1][:1])
    right_prev = jnp.concatenate([zero_rim, partner[1][:-1]], axis=0)
    left_next = jnp.concatenate([partner[0][1:], zero_rim], axis=0)
    first_core = freq_rank == 0
    lower_rim = jnp.where(first_core, right_prev, partner[1])
    upper_rim = jnp.where(first_core, partner[0], left_next)
    padded = jnp.concatenate([lower_rim, amp_blocks, upper_rim], axis=1)
    window_sum = padded[:, 0:block_bins]
    for offset_step in range(1, 2 * HW + 1):
        window_sum = window_sum + padded[:, offset_step : offset_step + block_bins]
    span_ids = jnp.arange(seg_count, dtype=jnp.int32)[:, None]
    offsets = jnp.arange(block_bins, dtype=jnp.int32)[None, :]
    position = (span_ids * freq_count + freq_rank) * block_bins + offsets
    counted = jnp.minimum(position + HW, BINS - 1) - jnp.maximum(position - HW, 0) + 1
    smooth = window_sum / counted.astype(jnp.float32)[:, :, None]
    divisor = jnp.maximum(smooth, WHITEN_FLOOR).reshape(device_bins, -1)
    local_bins = freq_rank * device_bins + jnp.arange(device_bins, dtype=jnp.int32)
    response_re, response_im = response(band_of(local_bins), taps)
    scaled_re = real_part / divisor
    scaled_im = imag_part / divisor
    white_re = scaled_re * response_re[:, None] - scaled_im * response_im[:, None]
    white_im = scaled_re * response_im[:, None] + scaled_im * response_re[:, None]
    whitened = jnp.stack([white_re, white_im], axis=1).astype(jnp.bfloat16)
    whitened = whitened.reshape(seg_count, block_bins, 2, sections, seg_dev)
    whitened = jnp.transpose(whitened, (0, 3, 1, 2, 4))
    seg_rank = lax.axis_index("seg")
    all_segs = seg_dev * seg_count
    table = jnp.concatenate([send_list[0], recv_row[0]], axis=1).reshape(-1)
    table_len = table.shape[0]
    blk_rank = lax.axis_index("blk")
    fused_round = seg_count == 2 and owners_count >= 2 and owners_count & (owners_count - 1) == 0
    if fused_round:
        piece_width = block_bins * 2 * seg_dev
        slab_width = 128
        slab = jnp.pad(table.astype(jnp.bfloat16), (0, sections * slab_width - table_len))
        keep = lax.dynamic_index_in_dim(whitened, seg_rank, axis=0, keepdims=False)
        other = lax.dynamic_index_in_dim(whitened, 1 - seg_rank, axis=0, keepdims=False)
        keep_flat = jnp.concatenate(
            [keep.reshape(sections, -1), slab.reshape(sections, slab_width)], axis=1
        )
        other_flat = other.reshape(sections, -1)
        first = owners_count // 2
        from_blk = lax.ppermute(
            keep_flat, "blk", [(source, source ^ first) for source in range(owners_count)]
        )
        from_seg = lax.ppermute(other_flat, "seg", [(0, 1), (1, 0)])
        diagonal = [
            (source * 2 + side, (source ^ first) * 2 + 1 - side)
            for source in range(owners_count)
            for side in range(2)
        ]
        from_diagonal = lax.ppermute(other_flat, ("blk", "seg"), diagonal)

        def interleave(mine_segs, their_segs, table_slab):
            lanes_in = 2 * seg_dev
            joined = jnp.concatenate(
                [
                    mine_segs.reshape(sections, block_bins, lanes_in),
                    their_segs.reshape(sections, block_bins, lanes_in),
                ],
                axis=2,
            ).reshape(sections, -1)
            return jnp.concatenate([joined, table_slab], axis=1)

        held = jnp.stack(
            [
                interleave(keep_flat[:, :piece_width], from_seg, keep_flat[:, piece_width:]),
                interleave(from_blk[:, :piece_width], from_diagonal, from_blk[:, piece_width:]),
            ],
            axis=0,
        )
        moved = gather_blocks(None, owners_count, blk_rank, held=held)
        halves = [moved[:, :, : 2 * piece_width]]
        table_part = moved[:, :, 2 * piece_width :]
        table_part = table_part.reshape(owners_count, -1)[:, :table_len]
        half_segs = all_segs
        chunk_segs = seg_dev
    else:
        pieces = [lax.dynamic_index_in_dim(whitened, seg_rank, axis=0, keepdims=False)]
        for shift in range(1, seg_count):
            outgoing = lax.dynamic_index_in_dim(
                whitened, (seg_rank + shift) % seg_count, axis=0, keepdims=False
            )
            pairs = [(source, (source + shift) % seg_count) for source in range(seg_count)]
            flat = outgoing.reshape(sections, -1)
            pieces.append(lax.ppermute(flat, "seg", pairs).reshape(outgoing.shape))
        local = jnp.stack(pieces, axis=3).reshape(sections, block_bins, -1)
        table_width = local.shape[-1]
        slab = jnp.pad(table.astype(jnp.bfloat16), (0, sections * table_width - table_len))
        carried = jnp.concatenate([local, slab.reshape(sections, 1, table_width)], axis=1)
        everything = gather_blocks(carried.reshape(sections, -1), owners_count, blk_rank)
        everything = everything.reshape(owners_count, sections, block_bins + 1, table_width)
        halves = [everything[:, :, :block_bins]]
        table_part = everything[:, :, block_bins].reshape(owners_count, -1)[:, :table_len]
        half_segs = all_segs
        chunk_segs = all_segs
    table_part = table_part.astype(jnp.int32).reshape(owners_count, owners_count, 2 * capacity)
    position_ids = jnp.arange(owners_count, dtype=jnp.int32)
    if owners_count & (owners_count - 1) == 0:
        source_of = blk_rank ^ position_ids
        unpermute = (source_of[:, None] == position_ids[None, :]).astype(jnp.int32)
        table_part = jnp.sum(unpermute[:, :, None, None] * table_part[None], axis=1)
    else:
        source_of = position_ids
    send_all = table_part[..., :capacity]
    recv_all = table_part[..., capacity:]
    rows_count = owners_count * OWN
    chans_count = owners_count * sections
    chosen = jnp.transpose(send_all, (1, 0, 2))
    valid = (chosen < sections) & (recv_all < OWN)
    source_ids = (blk_rank ^ position_ids if owners_count & (owners_count - 1) == 0 else position_ids)[None, :, None]
    owner_ids = jnp.arange(owners_count, dtype=jnp.int32)[:, None, None]
    channel = jnp.where(valid, source_ids * sections + chosen, -1).reshape(-1)
    target = jnp.where(valid, owner_ids * OWN + recv_all, -1).reshape(-1)
    row_hot = (target[:, None] == jnp.arange(rows_count, dtype=jnp.int32)[None, :]).astype(
        jnp.bfloat16
    )
    chan_hot = (channel[:, None] == jnp.arange(chans_count, dtype=jnp.int32)[None, :]).astype(
        jnp.bfloat16
    )
    selector = jnp.einsum(
        "er,ec->rc", row_hot, chan_hot, preferred_element_type=jnp.float32
    ).astype(jnp.bfloat16)
    selector = selector.reshape(rows_count, owners_count, sections)
    cross = None
    for half in halves:
        data = half.reshape(owners_count, sections, block_bins, 2 * half_segs)
        routed = jnp.einsum(
            "rsc,scbq->brq", selector, data, preferred_element_type=jnp.float32
        ).astype(jnp.bfloat16)
        own = lax.dynamic_slice_in_dim(routed, blk_rank * OWN, OWN, axis=1)
        own_parts = own.reshape(own.shape[:-1] + (-1, 2, chunk_segs))
        rotated = jnp.stack([own_parts[..., 1, :], -own_parts[..., 0, :]], axis=-2)
        rotated = rotated.reshape(own.shape)
        lhs = jnp.concatenate([own, rotated], axis=1)
        part = jnp.einsum("bpq,bjq->bpj", lhs, routed, preferred_element_type=jnp.float32)
        cross = part if cross is None else cross + part
    cross = cross.reshape(block_bins, 2, OWN, rows_count)
    return jnp.transpose(cross, (1, 0, 2, 3)) / jnp.float32(all_segs)


def solution(mesh):
    placed = (
        P(("groups", "blk"), "seg", "freq"),
        P(),
        P(("groups", "blk"), None, None),
        P(("groups", "blk"), None, None),
    )
    return jax.shard_map(
        per_device,
        mesh=mesh,
        in_specs=placed,
        out_specs=P(None, ("seg", "freq"), ("groups", "blk"), None),
        check_vma=False,
    )
```

```python
import math

import jax
import jax.numpy as jnp
from jax import lax
from jax.experimental import pallas as pl
from jax.experimental.pallas import tpu as pltpu
from jax.sharding import PartitionSpec as P

SEG_LEN = 16384
BINS = 256
BAND_LO = 128
HW = 4
OWN = 16


WHITEN_FLOOR = 0.25
TWO_PI = 2.0 * math.pi


def swapped(value, axis, distance):
    mask = 2**distance
    pairs = [(source, source ^ mask) for source in range(lax.axis_size(axis))]
    return lax.ppermute(value, axis, pairs)


def dft_tables(band_index, sample_index):
    wavenumber = BAND_LO + band_index
    phase_int = wavenumber[:, None] * sample_index[None, :] % SEG_LEN
    angles = phase_int.astype(jnp.float32) * (TWO_PI / SEG_LEN)
    norm_scale = 1.0 / math.sqrt(SEG_LEN)
    cos_part = (jnp.cos(angles) * norm_scale).astype(jnp.bfloat16)
    sin_part = (-jnp.sin(angles) * norm_scale).astype(jnp.bfloat16)
    return (cos_part, sin_part)


def dft_tables_fast(band_index, first_sample, count):
    lanes = 128
    wavenumber = BAND_LO + band_index
    coarse = (first_sample + lanes * jnp.arange(count // lanes, dtype=jnp.int32))
    fine = jnp.arange(lanes, dtype=jnp.int32)
    coarse_angle = (wavenumber[:, None] * coarse[None, :] % SEG_LEN).astype(jnp.float32) * (
        TWO_PI / SEG_LEN
    )
    fine_angle = (wavenumber[:, None] * fine[None, :] % SEG_LEN).astype(jnp.float32) * (
        TWO_PI / SEG_LEN
    )
    cos_a = jnp.cos(coarse_angle)[:, :, None]
    sin_a = jnp.sin(coarse_angle)[:, :, None]
    cos_b = jnp.cos(fine_angle)[:, None, :]
    sin_b = jnp.sin(fine_angle)[:, None, :]
    norm_scale = 1.0 / math.sqrt(SEG_LEN)
    cos_sum = cos_a * cos_b - sin_a * sin_b
    sin_sum = sin_a * cos_b + cos_a * sin_b
    rows = band_index.shape[0]
    cos_part = (cos_sum * norm_scale).astype(jnp.bfloat16).reshape(rows, count)
    sin_part = (-sin_sum * norm_scale).astype(jnp.bfloat16).reshape(rows, count)
    return (cos_part, sin_part)


def response(band_index, taps):
    wavenumber = BAND_LO + band_index
    lag_index = jnp.arange(taps.shape[0], dtype=jnp.int32)
    phase_int = wavenumber[:, None] * lag_index[None, :] % SEG_LEN
    angles = phase_int.astype(jnp.float32) * (TWO_PI / SEG_LEN)
    real_part = jnp.dot(jnp.cos(angles), taps, precision=lax.Precision.HIGHEST)
    imag_part = jnp.dot(-jnp.sin(angles), taps, precision=lax.Precision.HIGHEST)
    return (real_part, imag_part)


def dft_kernel(rec_ref, cos_a_ref, nsin_a_ref, cos_b_ref, sin_b_ref, re_ref, im_ref):
    step = pl.program_id(0)
    lanes = cos_b_ref.shape[0]
    group = 8
    groups = rec_ref.shape[1] // (group * lanes)

    @pl.when(step == 0)
    def _():
        re_ref[...] = jnp.zeros_like(re_ref)
        im_ref[...] = jnp.zeros_like(im_ref)

    def one_group(index, carry):
        row = pl.multiple_of((step * groups + index) * group, group)
        cos_a = cos_a_ref[pl.ds(row, group), :]
        nsin_a = nsin_a_ref[pl.ds(row, group), :]
        cos_b = cos_b_ref[...]
        sin_b = sin_b_ref[...]
        for pair in range(group // 2):
            cos_parts = []
            sin_parts = []
            for half in range(2):
                at = 2 * pair + half
                ca = cos_a[at : at + 1]
                sa = nsin_a[at : at + 1]
                cos_parts.append(ca * cos_b + sa * sin_b)
                sin_parts.append(sa * cos_b - ca * sin_b)
            cos_tile = jnp.concatenate(cos_parts, axis=0).astype(jnp.bfloat16)
            sin_tile = jnp.concatenate(sin_parts, axis=0).astype(jnp.bfloat16)
            first = pl.multiple_of((index * group + 2 * pair) * lanes, 2 * lanes)
            rec = rec_ref[:, pl.ds(first, 2 * lanes)]
            re_ref[...] += jnp.dot(rec, cos_tile, preferred_element_type=jnp.float32)
            im_ref[...] += jnp.dot(rec, sin_tile, preferred_element_type=jnp.float32)
        return carry

    lax.fori_loop(0, groups, one_group, 0)


def dft_kernel_self(info_ref, rec_ref, re_ref, im_ref, cos_a_ref, nsin_a_ref, cos_b_ref, sin_b_ref, layout=None):
    step = pl.program_id(0)
    lanes = 128
    group = 8
    groups = rec_ref.shape[1] // (group * lanes)

    @pl.when(step == 0)
    def _():
        re_ref[...] = jnp.zeros_like(re_ref)
        im_ref[...] = jnp.zeros_like(im_ref)
        if layout is None:
            wavenumber = info_ref[0:1, :]
            first = info_ref[1:2, :]
        else:
            device_bins, block_bins, freq_count, half_len = layout
            row_ids = lax.broadcasted_iota(jnp.int32, (1, re_ref.shape[0]), 1)
            owner_core = row_ids // device_bins
            if freq_count == 2:
                owner_core = (owner_core + lax.axis_index("freq")) % freq_count
            local_row = row_ids % device_bins
            band = (local_row // block_bins * freq_count + owner_core) * block_bins + local_row % block_bins
            wavenumber = BAND_LO + band
            first = lax.axis_index("freq") * half_len

        def cos_sin(steps):
            angle = (steps * wavenumber % SEG_LEN).astype(jnp.float32) * (TWO_PI / SEG_LEN)
            return jnp.cos(angle), jnp.sin(angle)

        width = wavenumber.shape[1]
        eight = lax.broadcasted_iota(jnp.int32, (8, width), 0)
        sixteen = lax.broadcasted_iota(jnp.int32, (16, width), 0)
        outer_cos, outer_sin = cos_sin(first + lanes * 8 * eight)
        inner_cos, inner_sin = cos_sin(lanes * eight)
        fine_outer_cos, fine_outer_sin = cos_sin(16 * eight)
        fine_inner_cos, fine_inner_sin = cos_sin(sixteen)
        norm_scale = 1.0 / math.sqrt(SEG_LEN)
        for outer in range(8):
            oc = outer_cos[outer : outer + 1]
            os_ = outer_sin[outer : outer + 1]
            cos_a_ref[outer * 8 : outer * 8 + 8, :] = oc * inner_cos - os_ * inner_sin
            nsin_a_ref[outer * 8 : outer * 8 + 8, :] = -(os_ * inner_cos + oc * inner_sin)
            fc = fine_outer_cos[outer : outer + 1]
            fs = fine_outer_sin[outer : outer + 1]
            cos_b_ref[outer * 16 : outer * 16 + 16, :] = (fc * fine_inner_cos - fs * fine_inner_sin) * norm_scale
            sin_b_ref[outer * 16 : outer * 16 + 16, :] = (fs * fine_inner_cos + fc * fine_inner_sin) * norm_scale

    def one_group(index, carry):
        row = pl.multiple_of((step * groups + index) * group, group)
        cos_a = cos_a_ref[pl.ds(row, group), :]
        nsin_a = nsin_a_ref[pl.ds(row, group), :]
        cos_b = cos_b_ref[...]
        sin_b = sin_b_ref[...]
        for pair in range(group // 2):
            cos_parts = []
            sin_parts = []
            for half in range(2):
                at = 2 * pair + half
                ca = cos_a[at : at + 1]
                sa = nsin_a[at : at + 1]
                cos_parts.append(ca * cos_b + sa * sin_b)
                sin_parts.append(sa * cos_b - ca * sin_b)
            cos_tile = jnp.concatenate(cos_parts, axis=0).astype(jnp.bfloat16)
            sin_tile = jnp.concatenate(sin_parts, axis=0).astype(jnp.bfloat16)
            first = pl.multiple_of((index * group + 2 * pair) * lanes, 2 * lanes)
            rec = rec_ref[:, pl.ds(first, 2 * lanes)]
            re_ref[...] += lax.dot_general(cos_tile, rec, (((0,), (1,)), ((), ())), preferred_element_type=jnp.float32)
            im_ref[...] += lax.dot_general(sin_tile, rec, (((0,), (1,)), ((), ())), preferred_element_type=jnp.float32)
        return carry

    lax.fori_loop(0, groups, one_group, 0)


def dft_fused(records, band_index, first_sample, layout=None):
    lanes = 128
    chunk = 2048
    count = records.shape[1]
    wavenumber = BAND_LO + band_index
    norm_scale = 1.0 / math.sqrt(SEG_LEN)

    def cos_sin(steps):
        angle = (steps[:, None] * wavenumber[None, :] % SEG_LEN).astype(jnp.float32) * (
            TWO_PI / SEG_LEN
        )
        return jnp.cos(angle), jnp.sin(angle)

    def combined(outer_steps, inner_steps):
        outer_cos, outer_sin = cos_sin(outer_steps)
        inner_cos, inner_sin = cos_sin(inner_steps)
        width = wavenumber.shape[0]
        cos_sum = outer_cos[:, None] * inner_cos[None] - outer_sin[:, None] * inner_sin[None]
        sin_sum = outer_sin[:, None] * inner_cos[None] + outer_cos[:, None] * inner_sin[None]
        return cos_sum.reshape(-1, width), sin_sum.reshape(-1, width)

    coarse_count = count // lanes
    rows = records.shape[0]
    bins = band_index.shape[0]
    full = lambda step: (0, 0)
    if coarse_count == 64 and chunk == 2048:
        info = jnp.concatenate(
            [
                wavenumber[None, :].astype(jnp.int32),
                jnp.broadcast_to(jnp.asarray(first_sample, jnp.int32), (7, bins)),
            ],
            axis=0,
        )
        if layout is not None:
            def kernel(rec_ref, re_ref, im_ref, *scratch):
                dft_kernel_self(None, rec_ref, re_ref, im_ref, *scratch, layout=layout)

            operands = (records,)
            leading = []
        else:
            kernel = dft_kernel_self
            operands = (info, records)
            leading = [pl.BlockSpec((8, bins), full)]
        return pl.pallas_call(
            kernel,
            grid=(count // chunk,),
            in_specs=leading + [pl.BlockSpec((rows, chunk), lambda step: (0, step))],
            out_specs=[pl.BlockSpec((bins, rows), full), pl.BlockSpec((bins, rows), full)],
            out_shape=[
                jax.ShapeDtypeStruct((bins, rows), jnp.float32),
                jax.ShapeDtypeStruct((bins, rows), jnp.float32),
            ],
            scratch_shapes=[
                pltpu.VMEM((64, bins), jnp.float32),
                pltpu.VMEM((64, bins), jnp.float32),
                pltpu.VMEM((128, bins), jnp.float32),
                pltpu.VMEM((128, bins), jnp.float32),
            ],
            compiler_params=pltpu.CompilerParams(dimension_semantics=("arbitrary",)),
        )(*operands)
    coarse_outer = coarse_count // 8 if coarse_count % 8 == 0 else 1
    coarse_inner = coarse_count // coarse_outer
    cos_a, sin_a = combined(
        first_sample + lanes * coarse_inner * jnp.arange(coarse_outer, dtype=jnp.int32),
        lanes * jnp.arange(coarse_inner, dtype=jnp.int32),
    )
    nsin_a = -sin_a
    cos_b, sin_b = combined(
        16 * jnp.arange(lanes // 16, dtype=jnp.int32), jnp.arange(16, dtype=jnp.int32)
    )
    cos_b = cos_b * norm_scale
    sin_b = sin_b * norm_scale
    rows = records.shape[0]
    bins = band_index.shape[0]
    full = lambda step: (0, 0)
    outputs = pl.pallas_call(
        dft_kernel,
        grid=(count // chunk,),
        in_specs=[
            pl.BlockSpec((rows, chunk), lambda step: (0, step)),
            pl.BlockSpec(cos_a.shape, full),
            pl.BlockSpec(nsin_a.shape, full),
            pl.BlockSpec(cos_b.shape, full),
            pl.BlockSpec(sin_b.shape, full),
        ],
        out_specs=[pl.BlockSpec((rows, bins), full), pl.BlockSpec((rows, bins), full)],
        out_shape=[
            jax.ShapeDtypeStruct((rows, bins), jnp.float32),
            jax.ShapeDtypeStruct((rows, bins), jnp.float32),
        ],
        compiler_params=pltpu.CompilerParams(dimension_semantics=("arbitrary",)),
    )(records, cos_a, nsin_a, cos_b, sin_b)
    return [part.T for part in outputs]


def gather_blocks(carried, count, rank, held=None):
    if count & (count - 1) != 0:
        return lax.all_gather(carried, "blk", axis=0, tiled=False)
    masks = []
    step = count // 2
    while step >= 1:
        masks.append(step)
        step //= 2
    if not masks:
        return carried[None]
    first = masks[0]
    rest = masks[1:]
    if held is None:
        pairs = [(source, source ^ first) for source in range(count)]
        held = jnp.stack([carried, lax.ppermute(carried, "blk", pairs)], axis=0)
    split = (held.shape[1] + 1) // 2
    halves = [held[:, :split], held[:, split:]]
    orders = [rest, rest[::-1]]
    results = []
    for part, order in zip(halves, orders):
        done = [first]
        for mask in order:
            pairs = [(source, source ^ mask) for source in range(count)]
            arrived = lax.ppermute(part, "blk", pairs)
            done.append(mask)
            axis = sorted(done, reverse=True).index(mask)
            part = jnp.stack([part, arrived], axis=axis)
        results.append(part.reshape((count,) + part.shape[len(masks):]))
    return jnp.concatenate(results, axis=1)


def per_device(raw, taps, send_list, recv_row):
    owners_count = lax.axis_size("blk")
    seg_count = lax.axis_size("seg")
    freq_count = lax.axis_size("freq")
    freq_rank = lax.axis_index("freq")
    sections, seg_dev, half_len = raw.shape
    records = raw.reshape(sections * seg_dev, half_len)
    device_bins = BINS // freq_count
    block_bins = device_bins // seg_count
    capacity = send_list.shape[2]

    def band_of(row_ids):
        owner_core = row_ids // device_bins
        local_row = row_ids % device_bins
        return (
            local_row // block_bins * freq_count + owner_core
        ) * block_bins + local_row % block_bins

    band_rows = band_of(jnp.arange(device_bins * freq_count, dtype=jnp.int32))
    real_t, imag_t = dft_fused(
        records, band_rows, freq_rank * half_len, (device_bins, block_bins, freq_count, half_len)
    )
    real_all = real_t
    imag_all = imag_t
    if freq_count == 2:
        blocks = jnp.stack([real_all, imag_all], axis=0)
        blocks = blocks.reshape(2, freq_count, device_bins, records.shape[0])
        kept = blocks[:, 0]
        sent = blocks[:, 1]
        kept_blocks = kept.reshape(2, seg_count, block_bins, -1)
        sent_blocks = sent.reshape(2, seg_count, block_bins, -1)
        own_edges = jnp.concatenate(
            [kept_blocks[:, :, :HW], kept_blocks[:, :, block_bins - HW :]], axis=2
        ).reshape(2, seg_count * 2 * HW, -1)
        message = jnp.concatenate([sent, own_edges], axis=1)
        arrived = swapped(message, "freq", 0)
        spectra_pair = kept + arrived[:, :device_bins]
        their_edges = jnp.concatenate(
            [sent_blocks[:, :, :HW], sent_blocks[:, :, block_bins - HW :]], axis=2
        ).reshape(2, seg_count * 2 * HW, -1)
        edge_spectra = (their_edges + arrived[:, device_bins:]).reshape(2, seg_count, 2, HW, -1)
        partner = jnp.transpose(
            jnp.sqrt(edge_spectra[0] * edge_spectra[0] + edge_spectra[1] * edge_spectra[1] + 1e-06),
            (1, 0, 2, 3),
        )
        spectra = jnp.stack([spectra_pair[0], spectra_pair[1]], axis=1)
    else:
        blocks = jnp.stack([real_all, imag_all], axis=1)
        spectra = lax.psum_scatter(
            blocks.reshape(device_bins * freq_count, 2, records.shape[0]),
            "freq",
            scatter_dimension=0,
            tiled=True,
        )
    real_part = spectra[:, 0]
    imag_part = spectra[:, 1]
    if freq_count == 2:
        real_part = spectra_pair[0]
        imag_part = spectra_pair[1]
    amplitude = jnp.sqrt(real_part * real_part + imag_part * imag_part + 1e-06)
    amp_blocks = amplitude.reshape(seg_count, block_bins, -1)
    if freq_count != 2:
        band_rims = jnp.stack([amp_blocks[:, :HW], amp_blocks[:, block_bins - HW :]])
        partner = swapped(band_rims, "freq", 0)
    zero_rim = jnp.zeros_like(partner[1][:1])
    right_prev = jnp.concatenate([zero_rim, partner[1][:-1]], axis=0)
    left_next = jnp.concatenate([partner[0][1:], zero_rim], axis=0)
    first_core = freq_rank == 0
    lower_rim = jnp.where(first_core, right_prev, partner[1])
    upper_rim = jnp.where(first_core, partner[0], left_next)
    padded = jnp.concatenate([lower_rim, amp_blocks, upper_rim], axis=1)
    window_sum = padded[:, 0:block_bins]
    for offset_step in range(1, 2 * HW + 1):
        window_sum = window_sum + padded[:, offset_step : offset_step + block_bins]
    span_ids = jnp.arange(seg_count, dtype=jnp.int32)[:, None]
    offsets = jnp.arange(block_bins, dtype=jnp.int32)[None, :]
    position = (span_ids * freq_count + freq_rank) * block_bins + offsets
    counted = jnp.minimum(position + HW, BINS - 1) - jnp.maximum(position - HW, 0) + 1
    smooth = window_sum / counted.astype(jnp.float32)[:, :, None]
    divisor = jnp.maximum(smooth, WHITEN_FLOOR).reshape(device_bins, -1)
    local_bins = freq_rank * device_bins + jnp.arange(device_bins, dtype=jnp.int32)
    response_re, response_im = response(band_of(local_bins), taps)
    scaled_re = real_part / divisor
    scaled_im = imag_part / divisor
    white_re = scaled_re * response_re[:, None] - scaled_im * response_im[:, None]
    white_im = scaled_re * response_im[:, None] + scaled_im * response_re[:, None]
    whitened = jnp.stack([white_re, white_im], axis=1).astype(jnp.bfloat16)
    whitened = whitened.reshape(seg_count, block_bins, 2, sections, seg_dev)
    whitened = jnp.transpose(whitened, (0, 3, 1, 2, 4))
    seg_rank = lax.axis_index("seg")
    all_segs = seg_dev * seg_count
    table = jnp.concatenate([send_list[0], recv_row[0]], axis=1).reshape(-1)
    table_len = table.shape[0]
    blk_rank = lax.axis_index("blk")
    fused_round = seg_count == 2 and owners_count >= 2 and owners_count & (owners_count - 1) == 0
    if fused_round:
        piece_width = block_bins * 2 * seg_dev
        slab_width = 128
        slab = jnp.pad(table.astype(jnp.bfloat16), (0, sections * slab_width - table_len))
        keep = lax.dynamic_index_in_dim(whitened, seg_rank, axis=0, keepdims=False)
        other = lax.dynamic_index_in_dim(whitened, 1 - seg_rank, axis=0, keepdims=False)
        keep_flat = jnp.concatenate(
            [keep.reshape(sections, -1), slab.reshape(sections, slab_width)], axis=1
        )
        other_flat = other.reshape(sections, -1)
        first = owners_count // 2
        from_blk = lax.ppermute(
            keep_flat, "blk", [(source, source ^ first) for source in range(owners_count)]
        )
        from_seg = lax.ppermute(other_flat, "seg", [(0, 1), (1, 0)])
        diagonal = [
            (source * 2 + side, (source ^ first) * 2 + 1 - side)
            for source in range(owners_count)
            for side in range(2)
        ]
        from_diagonal = lax.ppermute(other_flat, ("blk", "seg"), diagonal)

        def interleave(mine_segs, their_segs, table_slab):
            lanes_in = 2 * seg_dev
            joined = jnp.concatenate(
                [
                    mine_segs.reshape(sections, block_bins, lanes_in),
                    their_segs.reshape(sections, block_bins, lanes_in),
                ],
                axis=2,
            ).reshape(sections, -1)
            return jnp.concatenate([joined, table_slab], axis=1)

        held = jnp.stack(
            [
                interleave(keep_flat[:, :piece_width], from_seg, keep_flat[:, piece_width:]),
                interleave(from_blk[:, :piece_width], from_diagonal, from_blk[:, piece_width:]),
            ],
            axis=0,
        )
        moved = gather_blocks(None, owners_count, blk_rank, held=held)
        halves = [moved[:, :, : 2 * piece_width]]
        table_part = moved[:, :, 2 * piece_width :]
        table_part = table_part.reshape(owners_count, -1)[:, :table_len]
        half_segs = all_segs
        chunk_segs = seg_dev
    else:
        pieces = [lax.dynamic_index_in_dim(whitened, seg_rank, axis=0, keepdims=False)]
        for shift in range(1, seg_count):
            outgoing = lax.dynamic_index_in_dim(
                whitened, (seg_rank + shift) % seg_count, axis=0, keepdims=False
            )
            pairs = [(source, (source + shift) % seg_count) for source in range(seg_count)]
            flat = outgoing.reshape(sections, -1)
            pieces.append(lax.ppermute(flat, "seg", pairs).reshape(outgoing.shape))
        local = jnp.stack(pieces, axis=3).reshape(sections, block_bins, -1)
        table_width = local.shape[-1]
        slab = jnp.pad(table.astype(jnp.bfloat16), (0, sections * table_width - table_len))
        carried = jnp.concatenate([local, slab.reshape(sections, 1, table_width)], axis=1)
        everything = gather_blocks(carried.reshape(sections, -1), owners_count, blk_rank)
        everything = everything.reshape(owners_count, sections, block_bins + 1, table_width)
        halves = [everything[:, :, :block_bins]]
        table_part = everything[:, :, block_bins].reshape(owners_count, -1)[:, :table_len]
        half_segs = all_segs
        chunk_segs = all_segs
    table_part = table_part.astype(jnp.int32).reshape(owners_count, owners_count, 2 * capacity)
    position_ids = jnp.arange(owners_count, dtype=jnp.int32)
    if owners_count & (owners_count - 1) == 0:
        source_of = blk_rank ^ position_ids
        unpermute = (source_of[:, None] == position_ids[None, :]).astype(jnp.int32)
        table_part = jnp.sum(unpermute[:, :, None, None] * table_part[None], axis=1)
    else:
        source_of = position_ids
    send_all = table_part[..., :capacity]
    recv_all = table_part[..., capacity:]
    rows_count = owners_count * OWN
    chans_count = owners_count * sections
    chosen = jnp.transpose(send_all, (1, 0, 2))
    valid = (chosen < sections) & (recv_all < OWN)
    source_ids = (blk_rank ^ position_ids if owners_count & (owners_count - 1) == 0 else position_ids)[None, :, None]
    owner_ids = jnp.arange(owners_count, dtype=jnp.int32)[:, None, None]
    channel = jnp.where(valid, source_ids * sections + chosen, -1).reshape(-1)
    target = jnp.where(valid, owner_ids * OWN + recv_all, -1).reshape(-1)
    row_hot = (target[:, None] == jnp.arange(rows_count, dtype=jnp.int32)[None, :]).astype(
        jnp.bfloat16
    )
    chan_hot = (channel[:, None] == jnp.arange(chans_count, dtype=jnp.int32)[None, :]).astype(
        jnp.bfloat16
    )
    selector = jnp.einsum(
        "er,ec->rc", row_hot, chan_hot, preferred_element_type=jnp.float32
    ).astype(jnp.bfloat16)
    selector = selector.reshape(rows_count, owners_count, sections)
    cross = None
    for half in halves:
        data = half.reshape(owners_count, sections, block_bins, 2 * half_segs)
        routed = jnp.einsum(
            "rsc,scbq->brq", selector, data, preferred_element_type=jnp.float32
        ).astype(jnp.bfloat16)
        own = lax.dynamic_slice_in_dim(routed, blk_rank * OWN, OWN, axis=1)
        own_parts = own.reshape(own.shape[:-1] + (-1, 2, chunk_segs))
        rotated = jnp.stack([own_parts[..., 1, :], -own_parts[..., 0, :]], axis=-2)
        rotated = rotated.reshape(own.shape)
        lhs = jnp.concatenate([own, rotated], axis=1)
        part = jnp.einsum("bpq,bjq->bpj", lhs, routed, preferred_element_type=jnp.float32)
        cross = part if cross is None else cross + part
    cross = cross.reshape(block_bins, 2, OWN, rows_count)
    return jnp.transpose(cross, (1, 0, 2, 3)) / jnp.float32(all_segs)


def solution(mesh):
    placed = (
        P(("groups", "blk"), "seg", "freq"),
        P(),
        P(("groups", "blk"), None, None),
        P(("groups", "blk"), None, None),
    )
    return jax.shard_map(
        per_device,
        mesh=mesh,
        in_specs=placed,
        out_specs=P(None, ("seg", "freq"), ("groups", "blk"), None),
        check_vma=False,
    )
```

```python
import math

import jax
import jax.numpy as jnp
from jax import lax
from jax.experimental import pallas as pl
from jax.experimental.pallas import tpu as pltpu
from jax.sharding import PartitionSpec as P

SEG_LEN = 16384
BINS = 256
BAND_LO = 128
HW = 4
OWN = 16


WHITEN_FLOOR = 0.25
TWO_PI = 2.0 * math.pi


def swapped(value, axis, distance):
    mask = 2**distance
    pairs = [(source, source ^ mask) for source in range(lax.axis_size(axis))]
    return lax.ppermute(value, axis, pairs)


def dft_tables(band_index, sample_index):
    wavenumber = BAND_LO + band_index
    phase_int = wavenumber[:, None] * sample_index[None, :] % SEG_LEN
    angles = phase_int.astype(jnp.float32) * (TWO_PI / SEG_LEN)
    norm_scale = 1.0 / math.sqrt(SEG_LEN)
    cos_part = (jnp.cos(angles) * norm_scale).astype(jnp.bfloat16)
    sin_part = (-jnp.sin(angles) * norm_scale).astype(jnp.bfloat16)
    return (cos_part, sin_part)


def dft_tables_fast(band_index, first_sample, count):
    lanes = 128
    wavenumber = BAND_LO + band_index
    coarse = (first_sample + lanes * jnp.arange(count // lanes, dtype=jnp.int32))
    fine = jnp.arange(lanes, dtype=jnp.int32)
    coarse_angle = (wavenumber[:, None] * coarse[None, :] % SEG_LEN).astype(jnp.float32) * (
        TWO_PI / SEG_LEN
    )
    fine_angle = (wavenumber[:, None] * fine[None, :] % SEG_LEN).astype(jnp.float32) * (
        TWO_PI / SEG_LEN
    )
    cos_a = jnp.cos(coarse_angle)[:, :, None]
    sin_a = jnp.sin(coarse_angle)[:, :, None]
    cos_b = jnp.cos(fine_angle)[:, None, :]
    sin_b = jnp.sin(fine_angle)[:, None, :]
    norm_scale = 1.0 / math.sqrt(SEG_LEN)
    cos_sum = cos_a * cos_b - sin_a * sin_b
    sin_sum = sin_a * cos_b + cos_a * sin_b
    rows = band_index.shape[0]
    cos_part = (cos_sum * norm_scale).astype(jnp.bfloat16).reshape(rows, count)
    sin_part = (-sin_sum * norm_scale).astype(jnp.bfloat16).reshape(rows, count)
    return (cos_part, sin_part)


def response(band_index, taps):
    wavenumber = BAND_LO + band_index
    lag_index = jnp.arange(taps.shape[0], dtype=jnp.int32)
    phase_int = wavenumber[:, None] * lag_index[None, :] % SEG_LEN
    angles = phase_int.astype(jnp.float32) * (TWO_PI / SEG_LEN)
    real_part = jnp.dot(jnp.cos(angles), taps, precision=lax.Precision.HIGHEST)
    imag_part = jnp.dot(-jnp.sin(angles), taps, precision=lax.Precision.HIGHEST)
    return (real_part, imag_part)


def dft_kernel(rec_ref, cos_a_ref, nsin_a_ref, cos_b_ref, sin_b_ref, re_ref, im_ref):
    step = pl.program_id(0)
    lanes = cos_b_ref.shape[0]
    group = 8
    groups = rec_ref.shape[1] // (group * lanes)

    @pl.when(step == 0)
    def _():
        re_ref[...] = jnp.zeros_like(re_ref)
        im_ref[...] = jnp.zeros_like(im_ref)

    def one_group(index, carry):
        row = pl.multiple_of((step * groups + index) * group, group)
        cos_a = cos_a_ref[pl.ds(row, group), :]
        nsin_a = nsin_a_ref[pl.ds(row, group), :]
        cos_b = cos_b_ref[...]
        sin_b = sin_b_ref[...]
        for pair in range(group // 2):
            cos_parts = []
            sin_parts = []
            for half in range(2):
                at = 2 * pair + half
                ca = cos_a[at : at + 1]
                sa = nsin_a[at : at + 1]
                cos_parts.append(ca * cos_b + sa * sin_b)
                sin_parts.append(sa * cos_b - ca * sin_b)
            cos_tile = jnp.concatenate(cos_parts, axis=0).astype(jnp.bfloat16)
            sin_tile = jnp.concatenate(sin_parts, axis=0).astype(jnp.bfloat16)
            first = pl.multiple_of((index * group + 2 * pair) * lanes, 2 * lanes)
            rec = rec_ref[:, pl.ds(first, 2 * lanes)]
            re_ref[...] += jnp.dot(rec, cos_tile, preferred_element_type=jnp.float32)
            im_ref[...] += jnp.dot(rec, sin_tile, preferred_element_type=jnp.float32)
        return carry

    lax.fori_loop(0, groups, one_group, 0)


def dft_kernel_self(info_ref, rec_ref, re_ref, im_ref, cos_a_ref, nsin_a_ref, cos_b_ref, sin_b_ref, layout=None):
    step = pl.program_id(0)
    lanes = 128
    group = 8
    groups = rec_ref.shape[1] // (group * lanes)

    @pl.when(step == 0)
    def _():
        re_ref[...] = jnp.zeros_like(re_ref)
        im_ref[...] = jnp.zeros_like(im_ref)
        if layout is None:
            wavenumber = info_ref[0:1, :]
            first = info_ref[1:2, :]
        else:
            device_bins, block_bins, freq_count, half_len = layout
            row_ids = lax.broadcasted_iota(jnp.int32, (1, re_ref.shape[0]), 1)
            owner_core = row_ids // device_bins
            if freq_count == 2:
                owner_core = (owner_core + lax.axis_index("freq")) % freq_count
            local_row = row_ids % device_bins
            band = (local_row // block_bins * freq_count + owner_core) * block_bins + local_row % block_bins
            wavenumber = BAND_LO + band
            first = lax.axis_index("freq") * half_len

        def cos_sin(steps):
            angle = (steps * wavenumber % SEG_LEN).astype(jnp.float32) * (TWO_PI / SEG_LEN)
            return jnp.cos(angle), jnp.sin(angle)

        width = wavenumber.shape[1]
        eight = lax.broadcasted_iota(jnp.int32, (8, width), 0)
        sixteen = lax.broadcasted_iota(jnp.int32, (16, width), 0)
        outer_cos, outer_sin = cos_sin(first + lanes * 8 * eight)
        inner_cos, inner_sin = cos_sin(lanes * eight)
        fine_outer_cos, fine_outer_sin = cos_sin(16 * eight)
        fine_inner_cos, fine_inner_sin = cos_sin(sixteen)
        norm_scale = 1.0 / math.sqrt(SEG_LEN)
        for outer in range(8):
            oc = outer_cos[outer : outer + 1]
            os_ = outer_sin[outer : outer + 1]
            cos_a_ref[outer * 8 : outer * 8 + 8, :] = oc * inner_cos - os_ * inner_sin
            nsin_a_ref[outer * 8 : outer * 8 + 8, :] = -(os_ * inner_cos + oc * inner_sin)
            fc = fine_outer_cos[outer : outer + 1]
            fs = fine_outer_sin[outer : outer + 1]
            cos_b_ref[outer * 16 : outer * 16 + 16, :] = (fc * fine_inner_cos - fs * fine_inner_sin) * norm_scale
            sin_b_ref[outer * 16 : outer * 16 + 16, :] = (fs * fine_inner_cos + fc * fine_inner_sin) * norm_scale

    def one_group(index, carry):
        row = pl.multiple_of((step * groups + index) * group, group)
        cos_a = cos_a_ref[pl.ds(row, group), :]
        nsin_a = nsin_a_ref[pl.ds(row, group), :]
        cos_b = cos_b_ref[...]
        sin_b = sin_b_ref[...]
        for pair in range(group // 2):
            cos_parts = []
            sin_parts = []
            for half in range(2):
                at = 2 * pair + half
                ca = cos_a[at : at + 1]
                sa = nsin_a[at : at + 1]
                cos_parts.append(ca * cos_b + sa * sin_b)
                sin_parts.append(sa * cos_b - ca * sin_b)
            cos_tile = jnp.concatenate(cos_parts, axis=0).astype(jnp.bfloat16)
            sin_tile = jnp.concatenate(sin_parts, axis=0).astype(jnp.bfloat16)
            first = pl.multiple_of((index * group + 2 * pair) * lanes, 2 * lanes)
            rec = rec_ref[:, pl.ds(first, 2 * lanes)]
            re_ref[...] += lax.dot_general(cos_tile, rec, (((0,), (1,)), ((), ())), preferred_element_type=jnp.float32)
            im_ref[...] += lax.dot_general(sin_tile, rec, (((0,), (1,)), ((), ())), preferred_element_type=jnp.float32)
        return carry

    lax.fori_loop(0, groups, one_group, 0)


def dft_fused(records, band_index, first_sample, layout=None):
    lanes = 128
    chunk = 2048
    count = records.shape[1]
    wavenumber = BAND_LO + band_index
    norm_scale = 1.0 / math.sqrt(SEG_LEN)

    def cos_sin(steps):
        angle = (steps[:, None] * wavenumber[None, :] % SEG_LEN).astype(jnp.float32) * (
            TWO_PI / SEG_LEN
        )
        return jnp.cos(angle), jnp.sin(angle)

    def combined(outer_steps, inner_steps):
        outer_cos, outer_sin = cos_sin(outer_steps)
        inner_cos, inner_sin = cos_sin(inner_steps)
        width = wavenumber.shape[0]
        cos_sum = outer_cos[:, None] * inner_cos[None] - outer_sin[:, None] * inner_sin[None]
        sin_sum = outer_sin[:, None] * inner_cos[None] + outer_cos[:, None] * inner_sin[None]
        return cos_sum.reshape(-1, width), sin_sum.reshape(-1, width)

    coarse_count = count // lanes
    rows = records.shape[0]
    bins = band_index.shape[0]
    full = lambda step: (0, 0)
    if coarse_count == 64 and chunk == 2048:
        info = jnp.concatenate(
            [
                wavenumber[None, :].astype(jnp.int32),
                jnp.broadcast_to(jnp.asarray(first_sample, jnp.int32), (7, bins)),
            ],
            axis=0,
        )
        if layout is not None:
            def kernel(rec_ref, re_ref, im_ref, *scratch):
                dft_kernel_self(None, rec_ref, re_ref, im_ref, *scratch, layout=layout)

            operands = (records,)
            leading = []
        else:
            kernel = dft_kernel_self
            operands = (info, records)
            leading = [pl.BlockSpec((8, bins), full)]
        return pl.pallas_call(
            kernel,
            grid=(count // chunk,),
            in_specs=leading + [pl.BlockSpec((rows, chunk), lambda step: (0, step))],
            out_specs=[pl.BlockSpec((bins, rows), full), pl.BlockSpec((bins, rows), full)],
            out_shape=[
                jax.ShapeDtypeStruct((bins, rows), jnp.float32),
                jax.ShapeDtypeStruct((bins, rows), jnp.float32),
            ],
            scratch_shapes=[
                pltpu.VMEM((64, bins), jnp.float32),
                pltpu.VMEM((64, bins), jnp.float32),
                pltpu.VMEM((128, bins), jnp.float32),
                pltpu.VMEM((128, bins), jnp.float32),
            ],
            compiler_params=pltpu.CompilerParams(dimension_semantics=("arbitrary",)),
        )(*operands)
    coarse_outer = coarse_count // 8 if coarse_count % 8 == 0 else 1
    coarse_inner = coarse_count // coarse_outer
    cos_a, sin_a = combined(
        first_sample + lanes * coarse_inner * jnp.arange(coarse_outer, dtype=jnp.int32),
        lanes * jnp.arange(coarse_inner, dtype=jnp.int32),
    )
    nsin_a = -sin_a
    cos_b, sin_b = combined(
        16 * jnp.arange(lanes // 16, dtype=jnp.int32), jnp.arange(16, dtype=jnp.int32)
    )
    cos_b = cos_b * norm_scale
    sin_b = sin_b * norm_scale
    rows = records.shape[0]
    bins = band_index.shape[0]
    full = lambda step: (0, 0)
    outputs = pl.pallas_call(
        dft_kernel,
        grid=(count // chunk,),
        in_specs=[
            pl.BlockSpec((rows, chunk), lambda step: (0, step)),
            pl.BlockSpec(cos_a.shape, full),
            pl.BlockSpec(nsin_a.shape, full),
            pl.BlockSpec(cos_b.shape, full),
            pl.BlockSpec(sin_b.shape, full),
        ],
        out_specs=[pl.BlockSpec((rows, bins), full), pl.BlockSpec((rows, bins), full)],
        out_shape=[
            jax.ShapeDtypeStruct((rows, bins), jnp.float32),
            jax.ShapeDtypeStruct((rows, bins), jnp.float32),
        ],
        compiler_params=pltpu.CompilerParams(dimension_semantics=("arbitrary",)),
    )(records, cos_a, nsin_a, cos_b, sin_b)
    return [part.T for part in outputs]


def gather_blocks(carried, count, rank, held=None):
    if count & (count - 1) != 0:
        return lax.all_gather(carried, "blk", axis=0, tiled=False)
    masks = []
    step = count // 2
    while step >= 1:
        masks.append(step)
        step //= 2
    if not masks:
        return carried[None]
    first = masks[0]
    rest = masks[1:]
    if held is None:
        pairs = [(source, source ^ first) for source in range(count)]
        held = jnp.stack([carried, lax.ppermute(carried, "blk", pairs)], axis=0)
    split = (held.shape[1] + 1) // 2
    halves = [held[:, :split], held[:, split:]]
    orders = [rest, rest[::-1]]
    results = []
    for part, order in zip(halves, orders):
        done = [first]
        for mask in order:
            pairs = [(source, source ^ mask) for source in range(count)]
            arrived = lax.ppermute(part, "blk", pairs)
            done.append(mask)
            axis = sorted(done, reverse=True).index(mask)
            part = jnp.stack([part, arrived], axis=axis)
        results.append(part.reshape((count,) + part.shape[len(masks):]))
    return jnp.concatenate(results, axis=1)


def per_device(raw, taps, send_list, recv_row):
    owners_count = lax.axis_size("blk")
    seg_count = lax.axis_size("seg")
    freq_count = lax.axis_size("freq")
    freq_rank = lax.axis_index("freq")
    sections, seg_dev, half_len = raw.shape
    records = raw.reshape(sections * seg_dev, half_len)
    device_bins = BINS // freq_count
    block_bins = device_bins // seg_count
    capacity = send_list.shape[2]

    def band_of(row_ids):
        owner_core = row_ids // device_bins
        local_row = row_ids % device_bins
        return (
            local_row // block_bins * freq_count + owner_core
        ) * block_bins + local_row % block_bins

    band_rows = band_of(jnp.arange(device_bins * freq_count, dtype=jnp.int32))
    real_t, imag_t = dft_fused(
        records, band_rows, freq_rank * half_len, (device_bins, block_bins, freq_count, half_len)
    )
    real_all = real_t
    imag_all = imag_t
    if freq_count == 2:
        blocks = jnp.stack([real_all, imag_all], axis=0)
        blocks = blocks.reshape(2, freq_count, device_bins, records.shape[0])
        kept = blocks[:, 0]
        sent = blocks[:, 1]
        kept_blocks = kept.reshape(2, seg_count, block_bins, -1)
        sent_blocks = sent.reshape(2, seg_count, block_bins, -1)
        own_edges = jnp.concatenate(
            [kept_blocks[:, :, :HW], kept_blocks[:, :, block_bins - HW :]], axis=2
        ).reshape(2, seg_count * 2 * HW, -1)
        arrived_all = swapped(blocks, "freq", 0)
        spectra_pair = kept + arrived_all[:, 1]
        partner_own = arrived_all[:, 0].reshape(2, seg_count, block_bins, -1)
        partner_edges = jnp.concatenate(
            [partner_own[:, :, :HW], partner_own[:, :, block_bins - HW :]], axis=2
        ).reshape(2, seg_count * 2 * HW, -1)
        their_edges = jnp.concatenate(
            [sent_blocks[:, :, :HW], sent_blocks[:, :, block_bins - HW :]], axis=2
        ).reshape(2, seg_count * 2 * HW, -1)
        edge_spectra = (their_edges + partner_edges).reshape(2, seg_count, 2, HW, -1)
        partner = jnp.transpose(
            jnp.sqrt(edge_spectra[0] * edge_spectra[0] + edge_spectra[1] * edge_spectra[1] + 1e-06),
            (1, 0, 2, 3),
        )
        spectra = jnp.stack([spectra_pair[0], spectra_pair[1]], axis=1)
    else:
        blocks = jnp.stack([real_all, imag_all], axis=1)
        spectra = lax.psum_scatter(
            blocks.reshape(device_bins * freq_count, 2, records.shape[0]),
            "freq",
            scatter_dimension=0,
            tiled=True,
        )
    real_part = spectra[:, 0]
    imag_part = spectra[:, 1]
    if freq_count == 2:
        real_part = spectra_pair[0]
        imag_part = spectra_pair[1]
    amplitude = jnp.sqrt(real_part * real_part + imag_part * imag_part + 1e-06)
    amp_blocks = amplitude.reshape(seg_count, block_bins, -1)
    if freq_count != 2:
        band_rims = jnp.stack([amp_blocks[:, :HW], amp_blocks[:, block_bins - HW :]])
        partner = swapped(band_rims, "freq", 0)
    zero_rim = jnp.zeros_like(partner[1][:1])
    right_prev = jnp.concatenate([zero_rim, partner[1][:-1]], axis=0)
    left_next = jnp.concatenate([partner[0][1:], zero_rim], axis=0)
    first_core = freq_rank == 0
    lower_rim = jnp.where(first_core, right_prev, partner[1])
    upper_rim = jnp.where(first_core, partner[0], left_next)
    padded = jnp.concatenate([lower_rim, amp_blocks, upper_rim], axis=1)
    window_sum = padded[:, 0:block_bins]
    for offset_step in range(1, 2 * HW + 1):
        window_sum = window_sum + padded[:, offset_step : offset_step + block_bins]
    span_ids = jnp.arange(seg_count, dtype=jnp.int32)[:, None]
    offsets = jnp.arange(block_bins, dtype=jnp.int32)[None, :]
    position = (span_ids * freq_count + freq_rank) * block_bins + offsets
    counted = jnp.minimum(position + HW, BINS - 1) - jnp.maximum(position - HW, 0) + 1
    smooth = window_sum / counted.astype(jnp.float32)[:, :, None]
    divisor = jnp.maximum(smooth, WHITEN_FLOOR).reshape(device_bins, -1)
    local_bins = freq_rank * device_bins + jnp.arange(device_bins, dtype=jnp.int32)
    response_re, response_im = response(band_of(local_bins), taps)
    scaled_re = real_part / divisor
    scaled_im = imag_part / divisor
    white_re = scaled_re * response_re[:, None] - scaled_im * response_im[:, None]
    white_im = scaled_re * response_im[:, None] + scaled_im * response_re[:, None]
    whitened = jnp.stack([white_re, white_im], axis=1).astype(jnp.bfloat16)
    whitened = whitened.reshape(seg_count, block_bins, 2, sections, seg_dev)
    whitened = jnp.transpose(whitened, (0, 3, 1, 2, 4))
    seg_rank = lax.axis_index("seg")
    all_segs = seg_dev * seg_count
    table = jnp.concatenate([send_list[0], recv_row[0]], axis=1).reshape(-1)
    table_len = table.shape[0]
    blk_rank = lax.axis_index("blk")
    fused_round = seg_count == 2 and owners_count >= 2 and owners_count & (owners_count - 1) == 0
    if fused_round:
        piece_width = block_bins * 2 * seg_dev
        slab_width = 128
        slab = jnp.pad(table.astype(jnp.bfloat16), (0, sections * slab_width - table_len))
        keep = lax.dynamic_index_in_dim(whitened, seg_rank, axis=0, keepdims=False)
        other = lax.dynamic_index_in_dim(whitened, 1 - seg_rank, axis=0, keepdims=False)
        keep_flat = jnp.concatenate(
            [keep.reshape(sections, -1), slab.reshape(sections, slab_width)], axis=1
        )
        other_flat = other.reshape(sections, -1)
        first = owners_count // 2
        from_blk = lax.ppermute(
            keep_flat, "blk", [(source, source ^ first) for source in range(owners_count)]
        )
        from_seg = lax.ppermute(other_flat, "seg", [(0, 1), (1, 0)])
        diagonal = [
            (source * 2 + side, (source ^ first) * 2 + 1 - side)
            for source in range(owners_count)
            for side in range(2)
        ]
        from_diagonal = lax.ppermute(other_flat, ("blk", "seg"), diagonal)

        def interleave(mine_segs, their_segs, table_slab):
            lanes_in = 2 * seg_dev
            joined = jnp.concatenate(
                [
                    mine_segs.reshape(sections, block_bins, lanes_in),
                    their_segs.reshape(sections, block_bins, lanes_in),
                ],
                axis=2,
            ).reshape(sections, -1)
            return jnp.concatenate([joined, table_slab], axis=1)

        held = jnp.stack(
            [
                interleave(keep_flat[:, :piece_width], from_seg, keep_flat[:, piece_width:]),
                interleave(from_blk[:, :piece_width], from_diagonal, from_blk[:, piece_width:]),
            ],
            axis=0,
        )
        moved = gather_blocks(None, owners_count, blk_rank, held=held)
        halves = [moved[:, :, : 2 * piece_width]]
        table_part = moved[:, :, 2 * piece_width :]
        table_part = table_part.reshape(owners_count, -1)[:, :table_len]
        half_segs = all_segs
        chunk_segs = seg_dev
    else:
        pieces = [lax.dynamic_index_in_dim(whitened, seg_rank, axis=0, keepdims=False)]
        for shift in range(1, seg_count):
            outgoing = lax.dynamic_index_in_dim(
                whitened, (seg_rank + shift) % seg_count, axis=0, keepdims=False
            )
            pairs = [(source, (source + shift) % seg_count) for source in range(seg_count)]
            flat = outgoing.reshape(sections, -1)
            pieces.append(lax.ppermute(flat, "seg", pairs).reshape(outgoing.shape))
        local = jnp.stack(pieces, axis=3).reshape(sections, block_bins, -1)
        table_width = local.shape[-1]
        slab = jnp.pad(table.astype(jnp.bfloat16), (0, sections * table_width - table_len))
        carried = jnp.concatenate([local, slab.reshape(sections, 1, table_width)], axis=1)
        everything = gather_blocks(carried.reshape(sections, -1), owners_count, blk_rank)
        everything = everything.reshape(owners_count, sections, block_bins + 1, table_width)
        halves = [everything[:, :, :block_bins]]
        table_part = everything[:, :, block_bins].reshape(owners_count, -1)[:, :table_len]
        half_segs = all_segs
        chunk_segs = all_segs
    table_part = table_part.astype(jnp.int32).reshape(owners_count, owners_count, 2 * capacity)
    position_ids = jnp.arange(owners_count, dtype=jnp.int32)
    if owners_count & (owners_count - 1) == 0:
        source_of = blk_rank ^ position_ids
        unpermute = (source_of[:, None] == position_ids[None, :]).astype(jnp.int32)
        table_part = jnp.sum(unpermute[:, :, None, None] * table_part[None], axis=1)
    else:
        source_of = position_ids
    send_all = table_part[..., :capacity]
    recv_all = table_part[..., capacity:]
    rows_count = owners_count * OWN
    chans_count = owners_count * sections
    chosen = jnp.transpose(send_all, (1, 0, 2))
    valid = (chosen < sections) & (recv_all < OWN)
    source_ids = (blk_rank ^ position_ids if owners_count & (owners_count - 1) == 0 else position_ids)[None, :, None]
    owner_ids = jnp.arange(owners_count, dtype=jnp.int32)[:, None, None]
    channel = jnp.where(valid, source_ids * sections + chosen, -1).reshape(-1)
    target = jnp.where(valid, owner_ids * OWN + recv_all, -1).reshape(-1)
    row_hot = (target[:, None] == jnp.arange(rows_count, dtype=jnp.int32)[None, :]).astype(
        jnp.bfloat16
    )
    chan_hot = (channel[:, None] == jnp.arange(chans_count, dtype=jnp.int32)[None, :]).astype(
        jnp.bfloat16
    )
    selector = jnp.einsum(
        "er,ec->rc", row_hot, chan_hot, preferred_element_type=jnp.float32
    ).astype(jnp.bfloat16)
    selector = selector.reshape(rows_count, owners_count, sections)
    cross = None
    for half in halves:
        data = half.reshape(owners_count, sections, block_bins, 2 * half_segs)
        routed = jnp.einsum(
            "rsc,scbq->brq", selector, data, preferred_element_type=jnp.float32
        ).astype(jnp.bfloat16)
        own = lax.dynamic_slice_in_dim(routed, blk_rank * OWN, OWN, axis=1)
        own_parts = own.reshape(own.shape[:-1] + (-1, 2, chunk_segs))
        rotated = jnp.stack([own_parts[..., 1, :], -own_parts[..., 0, :]], axis=-2)
        rotated = rotated.reshape(own.shape)
        lhs = jnp.concatenate([own, rotated], axis=1)
        part = jnp.einsum("bpq,bjq->bpj", lhs, routed, preferred_element_type=jnp.float32)
        cross = part if cross is None else cross + part
    cross = cross.reshape(block_bins, 2, OWN, rows_count)
    return jnp.transpose(cross, (1, 0, 2, 3)) / jnp.float32(all_segs)


def solution(mesh):
    placed = (
        P(("groups", "blk"), "seg", "freq"),
        P(),
        P(("groups", "blk"), None, None),
        P(("groups", "blk"), None, None),
    )
    return jax.shard_map(
        per_device,
        mesh=mesh,
        in_specs=placed,
        out_specs=P(None, ("seg", "freq"), ("groups", "blk"), None),
        check_vma=False,
    )
```
